32 devices in a mesh: dp: 8 (over z, x), mp: 4 (over y, core).
Axes of the slice: x: 2, y: 2, z: 4, core: 2. Of those that a mesh axis runs over, the one named last changes fastest.
Arguments:
- tokens: bfloat16 [4096, 2048], P('dp'), may hold values from -6 to 6
- segment_ids: int32 [8, 512], P('dp'), may hold values from 0 to 3, never falling along the last dimension, each value on 1 to 256 neighbouring positions
- valid_lengths: int32 [8], P('dp'), may hold values from 256 to 512, as said below
- cotangent: bfloat16 [4096, 2048], P('dp'), may hold values from -6 to 6
- w_query: bfloat16 [2048, 2048], P('dp', 'mp'), may hold values from -0.125 to 0.125
- w_key: bfloat16 [2048, 2048], P('dp', 'mp'), may hold values from -0.125 to 0.125
- w_value: bfloat16 [2048, 2048], P('dp', 'mp'), may hold values from -0.125 to 0.125
- w_out: bfloat16 [2048, 2048], P('mp', 'dp'), may hold values from -0.125 to 0.125
- query_gain: bfloat16 [2048], P(('mp', 'dp')), may hold values from 0.25 to 1.75
- key_gain: bfloat16 [2048], P(('mp', 'dp')), may hold values from 0.25 to 1.75
- attn_gain: bfloat16 [2048], P('dp'), may hold values from 0.25 to 1.75
- w_gate: bfloat16 [2048, 8192], P('dp', 'mp'), may hold values from -0.125 to 0.125
- w_up: bfloat16 [2048, 8192], P('dp', 'mp'), may hold values from -0.125 to 0.125
- w_down: bfloat16 [8192, 2048], P('mp', 'dp'), may hold values from -0.0625 to 0.0625
- mlp_gain: bfloat16 [2048], P('dp'), may hold values from 0.25 to 1.75
Outputs:
- layer_out: bfloat16 [4096, 2048], P('dp')
- input_grad: float32 [4096, 2048], P('dp')
- grad_w_query: float32 [2048, 2048], P('dp', 'mp')
- grad_w_key: float32 [2048, 2048], P('dp', 'mp')
- grad_w_value: float32 [2048, 2048], P('dp', 'mp')
- grad_w_out: float32 [2048, 2048], P('mp', 'dp')
- grad_query_gain: float32 [2048], P(('mp', 'dp'))
- grad_key_gain: float32 [2048], P(('mp', 'dp'))
- grad_attn_gain: float32 [2048], P('dp')
- grad_w_gate: float32 [2048, 8192], P('dp', 'mp')
- grad_w_up: float32 [2048, 8192], P('dp', 'mp')
- grad_w_down: float32 [8192, 2048], P('mp', 'dp')
- grad_mlp_gain: float32 [2048], P('dp')
The draws below stay inside these ranges and needn't reach their ends.
Inputs may be any that keep to these rules, and one draw needn't show every extreme that they name: `valid_lengths`: each sequence has at least half of 512 valid tokens; some sequence is full in every draw.
All inputs are finite; a program needn't handle non-finite values.
Results may differ from the reference program's by a relative error of at most 0.015.
Values may be sent and summed in bfloat16 or wider, within the bound.
No kernel may reach another device: no remote copies, remote signals or barrier semaphores. Data moves between devices by JAX's collectives and lax.ppermute only.
A program may use at most 256 MiB of HBM per device.

```python
import math
import jax
import jax.numpy as jnp
import numpy as np
from jax import lax

D = 2048
HEADS = 16
HEAD_DIM = 128
FF = 8192
TOK_DEV = 512
SEQS = 8
TOKENS = 4096


def draw_valid_lengths(key, part):
    first, second = jax.random.split(jax.random.fold_in(key, 11))
    short = jax.random.randint(first, (SEQS,), 0, TOK_DEV // 2 + 1)
    full = jax.random.randint(second, (), 0, SEQS)
    return jnp.where(jnp.arange(SEQS) == full, TOK_DEV, TOK_DEV - short).astype(jnp.int32)


def block_scale(rng, shape, cuts, low, largest):
    loudness, own = 1.0, jax.random.fold_in(rng, 6)
    for position, shards_of in cuts:
        heights = jnp.exp(jax.random.uniform(jax.random.fold_in(own, position), (shards_of,), jnp.float32, low / len(cuts), largest / len(cuts)))
        loudness = loudness * jnp.repeat(heights, shape[position] // shards_of).reshape([-1 if axis == position else 1 for axis in range(len(shape))])
    return loudness


def profile(amount, total, limit, slope):
    weights = [(1 << 20) // math.isqrt(grade ** slope) + 1 for grade in range(2, amount + 1)]
    spare, counts = total - limit - (amount - 1), [1] * (amount - 1)
    while spare > 0:
        free = [i for i in range(amount - 1) if counts[i] < limit]
        pool, budget = sum([weights[i] for i in free]), spare
        for i in free:
            addition = min(limit - counts[i], max(1, budget * weights[i] // pool), spare)
            counts[i] = counts[i] + addition
            spare = spare - addition
    return np.array([limit] + counts)


def uneven_parts(key, count, total, limit, slope):
    if count == 2:
        one = jax.random.randint(key, (), max(1, total - limit), min(limit, total - 1) + 1)
        return jnp.stack([one, total - one])
    lengths = jnp.asarray(profile(count, total, limit, slope), jnp.int32)
    couples = (count - 1) // 2
    giver, receiver = lengths[1:1 + 2 * couples:2], lengths[2:2 + 2 * couples:2]
    slack = jnp.minimum(giver - 1, limit - receiver)
    shifted = jax.random.randint(jax.random.fold_in(key, 1), (couples,), 0, 1 << 20) % (slack + 1)
    lengths = lengths.at[1:1 + 2 * couples:2].set(giver - shifted).at[2:2 + 2 * couples:2].set(receiver + shifted)
    return lengths[jax.random.permutation(jax.random.fold_in(key, 2), count)]


def scatter_about(rng, extent, spread, reach, cuts=(), held_as=jnp.bfloat16):
    level = block_scale(rng, extent, cuts, -0.22, 0.18) if cuts else 1.0
    array = jax.random.normal(rng, extent, jnp.float32) * spread * level
    return jnp.minimum(jnp.maximum(array, -reach), reach).astype(held_as)


def setup_inputs(seed: int = 0) -> dict:
    splits = jax.random.split(jax.random.key(seed), 16)
    tokens = scatter_about(splits[0], (TOKENS, D), 1.0, 6.0, ((0, 8),))
    segment_ids = jax.vmap(lambda own: jnp.searchsorted(jnp.cumsum(uneven_parts(own, 4, TOK_DEV, TOK_DEV // 2, 0)), jnp.arange(TOK_DEV), side="right"))(jax.random.split(splits[1], SEQS)).reshape((SEQS, TOK_DEV)).astype(jnp.int32)
    valid_lengths = draw_valid_lengths(jax.random.fold_in(splits[15], 71), 0)
    cotangent = scatter_about(splits[3], (TOKENS, D), 1.0, 6.0, ((0, 8),))
    w_query = scatter_about(splits[4], (D, D), D ** -0.5, 0.125, ((0, 8), (1, 4)))
    w_key = scatter_about(splits[5], (D, D), D ** -0.5, 0.125, ((0, 8), (1, 4)))
    w_value = scatter_about(splits[6], (D, D), D ** -0.5, 0.125, ((0, 8), (1, 4)))
    w_out = scatter_about(splits[7], (D, D), D ** -0.5, 0.125, ((0, 4), (1, 8)))
    query_gain = jnp.clip(1.0 + 0.15 * jax.random.normal(splits[8], (D,), jnp.float32), 0.25, 1.75).astype(jnp.bfloat16)
    key_gain = jnp.clip(1.0 + 0.15 * jax.random.normal(splits[9], (D,), jnp.float32), 0.25, 1.75).astype(jnp.bfloat16)
    attn_gain = jnp.clip(1.0 + 0.15 * jax.random.normal(splits[10], (D,), jnp.float32), 0.25, 1.75).astype(jnp.bfloat16)
    w_gate = scatter_about(splits[11], (D, FF), D ** -0.5, 0.125, ((0, 8), (1, 4)))
    w_up = scatter_about(splits[12], (D, FF), D ** -0.5, 0.125, ((0, 8), (1, 4)))
    w_down = scatter_about(splits[13], (FF, D), FF ** -0.5, 0.0625, ((0, 4), (1, 8)))
    mlp_gain = jnp.clip(1.0 + 0.15 * jax.random.normal(splits[14], (D,), jnp.float32), 0.25, 1.75).astype(jnp.bfloat16)
    return {"tokens": tokens, "segment_ids": segment_ids, "valid_lengths": valid_lengths, "cotangent": cotangent, "w_query": w_query, "w_key": w_key, "w_value": w_value, "w_out": w_out, "query_gain": query_gain, "key_gain": key_gain, "attn_gain": attn_gain, "w_gate": w_gate, "w_up": w_up, "w_down": w_down, "mlp_gain": mlp_gain}


EPS = 1e-06
THETA = 500000.0
HIGH = lax.Precision.HIGHEST

@jax.custom_vjp
def low(v):
    return lax.optimization_barrier(v.astype(jnp.bfloat16)).astype(jnp.float32)

@jax.custom_vjp
def low_back(v):
    return v

def low_keep(v):
    return (low(v), None)

def low_pass(kept, grad):
    return (grad,)

def back_keep(v):
    return (v, None)

def back_low(kept, grad):
    return (low(grad),)
low.defvjp(low_keep, low_pass)
low_back.defvjp(back_keep, back_low)

def matmul(left, right):
    return jnp.dot(left, right, precision=HIGH, preferred_element_type=jnp.float32)

def rms_norm(value, gain):
    return value * lax.rsqrt(lax.optimization_barrier(jnp.mean(value * value, axis=-1, keepdims=True)) + EPS) * gain

def rope_tables(rows, head_dim):
    half = head_dim // 2
    inverse = THETA ** (-(jnp.arange(half).astype(jnp.float32) * 2.0) / head_dim)
    angles = jnp.arange(rows).astype(jnp.float32)[:, None] * inverse[None, :]
    return (jnp.cos(angles)[:, None, :], jnp.sin(angles)[:, None, :])

def rotate(value, cosine, sine):
    half = value.shape[-1] // 2
    first, second = (value[..., :half], value[..., half:])
    return jnp.concatenate([first * cosine - second * sine, second * cosine + first * sine], axis=-1)

def allowed_block(start, block, seg_row, length):
    query_pos = start + jnp.arange(block).astype(jnp.int32)
    key_pos = jnp.arange(seg_row.shape[0]).astype(jnp.int32)
    query_seg = lax.dynamic_slice_in_dim(seg_row, start, block, 0)
    same = query_seg[:, None] == seg_row[None, :]
    causal = key_pos[None, :] <= query_pos[:, None]
    inside = key_pos[None, :] < length
    return same & causal & inside | (key_pos[None, :] == query_pos[:, None])

def attention(query_rot, key_rot, values, seg_row, length):
    rows = query_rot.shape[0]
    block = min(512, rows)
    count = rows // block
    scale = HEAD_DIM ** (-0.5)

    @jax.checkpoint
    def one_block(start):
        q_blk = lax.dynamic_slice_in_dim(query_rot, start, block, 0)
        raw = jnp.einsum('qhe,khe->hqk', q_blk, key_rot, precision=HIGH) * scale
        scores = low_back(raw)
        mask = allowed_block(start, block, seg_row, length)
        scores = jnp.where(mask[None], scores, -1e+30)
        probs = low(jax.nn.softmax(scores, axis=-1))
        return jnp.einsum('hqk,khe->qhe', probs, values, precision=HIGH)
    starts = jnp.arange(count).astype(jnp.int32) * block
    out = lax.map(one_block, starts)
    return out.reshape(rows, -1)

def layer(weights, row, seg_row, length):
    wq, wk, wv, wo, gq, gk, ga, wg, wu, wd, gm = weights
    rows = row.shape[0]
    xb = low(row)
    query = low_back(matmul(xb, wq))
    keys = low_back(matmul(xb, wk))
    values = low(low_back(matmul(xb, wv)))
    cosine, sine = rope_tables(rows, HEAD_DIM)
    query_rot = low(rotate(rms_norm(query, gq).reshape(rows, HEADS, HEAD_DIM), cosine, sine))
    key_rot = low(rotate(rms_norm(keys, gk).reshape(rows, HEADS, HEAD_DIM), cosine, sine))
    attended = attention(query_rot, key_rot, values.reshape(rows, HEADS, HEAD_DIM), seg_row, length)
    attended = low(low_back(attended))
    branch = low_back(matmul(attended, wo))
    hidden = row + rms_norm(branch, ga)
    hidden_b = low(hidden)
    gate = low_back(matmul(hidden_b, wg))
    up = low_back(matmul(hidden_b, wu))
    mixed = low(jax.nn.silu(gate) * up)
    mlp = low_back(matmul(mixed, wd))
    return hidden + rms_norm(mlp, gm)

def reference(tokens, segment_ids, valid_lengths, cotangent, w_query, w_key, w_value, w_out, query_gain, key_gain, attn_gain, w_gate, w_up, w_down, mlp_gain):
    weights = tuple((w.astype(jnp.float32) for w in (w_query, w_key, w_value, w_out, query_gain, key_gain, attn_gain, w_gate, w_up, w_down, mlp_gain)))
    inputs = tokens.astype(jnp.float32).reshape(SEQS, TOK_DEV, D)
    checked = jax.checkpoint(layer)

    def forward(inputs, weights):

        def one_sequence(item):
            row, seg_row, length = item
            return checked(weights, row, seg_row, length)
        return lax.map(one_sequence, (inputs, segment_ids, valid_lengths))
    outputs, pullback = jax.vjp(forward, inputs, weights)
    grad_inputs, grads = pullback(cotangent.astype(jnp.float32).reshape(SEQS, TOK_DEV, D))
    return (outputs.reshape(TOKENS, D).astype(jnp.bfloat16), grad_inputs.reshape(TOKENS, D), grads[0], grads[1], grads[2], grads[3], grads[4], grads[5], grads[6], grads[7], grads[8], grads[9], grads[10])
```

```python
import jax
import jax.numpy as jnp
from jax import lax
from jax.sharding import PartitionSpec as P

HEAD_DIM = 128


EPS = 1e-06
THETA = 500000.0


def rope_tables(rows, head_dim):
    half = head_dim // 2
    inverse = THETA ** (-(jnp.arange(half).astype(jnp.float32) * 2.0) / head_dim)
    angles = jnp.arange(rows).astype(jnp.float32)[:, None] * inverse[None, :]
    return (jnp.cos(angles)[:, None, :], jnp.sin(angles)[:, None, :])


def rotate(value, cosine, sine):
    half = value.shape[-1] // 2
    first, second = (value[..., :half], value[..., half:])
    return jnp.concatenate(
        [first * cosine - second * sine, second * cosine + first * sine], axis=-1
    )


def rotate_back(grad, cosine, sine):
    half = grad.shape[-1] // 2
    first, second = (grad[..., :half], grad[..., half:])
    return jnp.concatenate(
        [first * cosine + second * sine, second * cosine - first * sine], axis=-1
    )


def allowed_block(start, block, seg_row, length):
    query_pos = start + jnp.arange(block)
    key_pos = jnp.arange(seg_row.shape[0])
    same = seg_row[:, None] == seg_row[None, :]
    causal = key_pos[None, :] <= query_pos[:, None]
    inside = key_pos[None, :] < length
    return same & causal & inside | (key_pos[None, :] == query_pos[:, None])


MP_LOW = False


def branch_total(partial_sum):
    if MP_LOW:
        return lax.psum(partial_sum.astype(jnp.bfloat16), "mp").astype(jnp.float32)
    return lax.psum(partial_sum, "mp")


def input_total(partial_sum):
    if MP_LOW:
        return lax.psum(partial_sum.astype(jnp.bfloat16), "mp").astype(jnp.float32)
    return lax.psum(partial_sum, "mp")


def grad_scatter(grad, dim):
    low = grad.astype(jnp.bfloat16)
    return lax.psum_scatter(low, "dp", scatter_dimension=dim, tiled=True).astype(jnp.float32)


def norm_forward(total):
    factor = lax.rsqrt(jnp.mean(total * total, axis=1, keepdims=True) + EPS)
    return (total * factor, factor)


def norm_back(grad, normed, factor, gain):
    grad_gain = jnp.sum(grad * normed, axis=0)
    scaled = grad * gain
    inner = jnp.mean(scaled * normed, axis=1, keepdims=True)
    return (factor * (scaled - normed * inner), grad_gain)


def per_device(
    tokens,
    segment_ids,
    valid_lengths,
    cotangent,
    w_query,
    w_key,
    w_value,
    w_out,
    query_gain,
    key_gain,
    attn_gain,
    w_gate,
    w_up,
    w_down,
    mlp_gain,
):
    f32 = jnp.float32
    bf16 = jnp.bfloat16
    rows, width = tokens.shape
    seg_row = segment_ids[0]
    length = valid_lengths[0]
    block = min(512, rows)
    count = rows // block
    scale = HEAD_DIM ** (-0.5)
    attn_set = (
        lax.all_gather(w_query, "dp", axis=0, tiled=True),
        lax.all_gather(w_key, "dp", axis=0, tiled=True),
        lax.all_gather(w_value, "dp", axis=0, tiled=True),
        lax.all_gather(w_out, "dp", axis=1, tiled=True),
        lax.all_gather(query_gain, "dp", axis=0, tiled=True),
        lax.all_gather(key_gain, "dp", axis=0, tiled=True),
        lax.all_gather(attn_gain, "dp", axis=0, tiled=True),
    )
    mlp_set = (
        lax.all_gather(w_gate, "dp", axis=0, tiled=True),
        lax.all_gather(w_up, "dp", axis=0, tiled=True),
        lax.all_gather(w_down, "dp", axis=1, tiled=True),
        lax.all_gather(mlp_gain, "dp", axis=0, tiled=True),
    )
    wq, wk, wv, wo, gq, gk, ga = attn_set
    wg, wu, wd, gm = mlp_set
    gq32 = gq.astype(f32)
    gk32 = gk.astype(f32)
    ga32 = ga.astype(f32)
    gm32 = gm.astype(f32)
    query = jnp.dot(tokens, wq, preferred_element_type=f32)
    keys = jnp.dot(tokens, wk, preferred_element_type=f32)
    values = jnp.dot(tokens, wv, preferred_element_type=f32).astype(bf16)
    query_sq, key_sq = lax.psum(
        (jnp.sum(query * query, axis=1), jnp.sum(keys * keys, axis=1)), "mp"
    )
    query_factor = lax.rsqrt(query_sq / width + EPS)[:, None]
    key_factor = lax.rsqrt(key_sq / width + EPS)[:, None]
    query_hat = query * query_factor
    key_hat = keys * key_factor
    heads = query.shape[1] // HEAD_DIM
    cosine, sine = rope_tables(rows, HEAD_DIM)
    query_rot = rotate((query_hat * gq32).reshape(rows, heads, HEAD_DIM), cosine, sine).astype(bf16)
    key_rot = rotate((key_hat * gk32).reshape(rows, heads, HEAD_DIM), cosine, sine).astype(bf16)
    values_h = values.reshape(rows, heads, HEAD_DIM)

    def block_scores(start):
        scores = jnp.einsum("qhe,khe->hqk", query_rot, key_rot, preferred_element_type=f32) * scale
        mask = allowed_block(start, block, seg_row, length)
        return (query_rot, jnp.where(mask[None], scores, -1e30))

    def forward_block(index):
        start = index * block
        q_blk, scores = block_scores(start)
        top = jnp.max(scores, axis=-1, keepdims=True)
        total = jnp.sum(jnp.exp(scores - top), axis=-1, keepdims=True)
        logsum = top + jnp.log(total)
        probs = jnp.exp(scores - logsum).astype(bf16)
        attended = jnp.einsum("hqk,khe->qhe", probs, values_h, preferred_element_type=f32)
        return (attended, logsum[..., 0])

    attended, logsums = lax.map(forward_block, jnp.arange(count))
    attended_b = attended.reshape(rows, heads * HEAD_DIM).astype(bf16)
    attn_partial = jnp.dot(attended_b, wo, preferred_element_type=f32)
    attn_total = branch_total(attn_partial)
    attn_hat, attn_factor = norm_forward(attn_total)
    hidden = tokens.astype(f32) + attn_hat * ga32
    hidden_b = hidden.astype(bf16)
    gate = jnp.dot(hidden_b, wg, preferred_element_type=f32)
    up = jnp.dot(hidden_b, wu, preferred_element_type=f32)
    active = jax.nn.silu(gate)
    mixed_b = (active * up).astype(bf16)
    mlp_partial = jnp.dot(mixed_b, wd, preferred_element_type=f32)
    mlp_total = branch_total(mlp_partial)
    mlp_hat, mlp_factor = norm_forward(mlp_total)
    layer_out = (hidden + mlp_hat * gm32).astype(bf16)
    attn_set = (
        lax.all_gather(w_query, "dp", axis=0, tiled=True),
        lax.all_gather(w_key, "dp", axis=0, tiled=True),
        lax.all_gather(w_value, "dp", axis=0, tiled=True),
        lax.all_gather(w_out, "dp", axis=1, tiled=True),
        lax.all_gather(query_gain, "dp", axis=0, tiled=True),
        lax.all_gather(key_gain, "dp", axis=0, tiled=True),
        lax.all_gather(attn_gain, "dp", axis=0, tiled=True),
    )
    mlp_set = (
        lax.all_gather(w_gate, "dp", axis=0, tiled=True),
        lax.all_gather(w_up, "dp", axis=0, tiled=True),
        lax.all_gather(w_down, "dp", axis=1, tiled=True),
        lax.all_gather(mlp_gain, "dp", axis=0, tiled=True),
    )
    wq, wk, wv, wo, gq, gk, ga = attn_set
    wg, wu, wd, gm = mlp_set
    grad_out = cotangent.astype(f32)
    d_mlp, grad_mg = norm_back(grad_out, mlp_hat, mlp_factor, gm32)
    d_mlp_b = d_mlp.astype(bf16)
    grad_wd = jnp.einsum("rf,rd->fd", mixed_b, d_mlp_b, preferred_element_type=f32)
    d_mixed = jnp.einsum("rd,fd->rf", d_mlp_b, wd, preferred_element_type=f32)
    sigma = jax.nn.sigmoid(gate)
    d_gate = (d_mixed * up * sigma * (1.0 + gate * (1.0 - sigma))).astype(bf16)
    d_up = (d_mixed * active).astype(bf16)
    grad_wg = jnp.einsum("rd,rf->df", hidden_b, d_gate, preferred_element_type=f32)
    grad_wu = jnp.einsum("rd,rf->df", hidden_b, d_up, preferred_element_type=f32)
    hidden_partial = jnp.einsum("rf,df->rd", d_gate, wg, preferred_element_type=f32) + jnp.einsum(
        "rf,df->rd", d_up, wu, preferred_element_type=f32
    )
    d_hidden = grad_out + input_total(hidden_partial)
    d_attn, grad_ag = norm_back(d_hidden, attn_hat, attn_factor, ga32)
    d_attn_b = d_attn.astype(bf16)
    grad_wo = jnp.einsum("rc,rd->cd", attended_b, d_attn_b, preferred_element_type=f32)
    d_attended = jnp.einsum("rd,cd->rc", d_attn_b, wo, preferred_element_type=f32).astype(bf16)
    d_attended = d_attended.reshape(rows, heads, HEAD_DIM)

    def backward_block(carry, index):
        key_acc, value_acc = carry
        start = index * block
        q_blk, scores = block_scores(start)
        logsum = lax.dynamic_index_in_dim(logsums, index, 0, keepdims=False)
        probs = jnp.exp(scores - logsum[..., None])
        value_acc = value_acc + jnp.einsum(
            "hqk,qhe->khe", probs.astype(bf16), d_attended, preferred_element_type=f32
        )
        d_probs = jnp.einsum("qhe,khe->hqk", d_attended, values_h, preferred_element_type=f32)
        delta = jnp.sum(probs * d_probs, axis=-1, keepdims=True)
        d_scores = (probs * (d_probs - delta)).astype(bf16)
        d_query_blk = (
            jnp.einsum("hqk,khe->qhe", d_scores, key_rot, preferred_element_type=f32) * scale
        )
        key_acc = (
            key_acc
            + jnp.einsum("hqk,qhe->khe", d_scores, q_blk, preferred_element_type=f32) * scale
        )
        return ((key_acc, value_acc), d_query_blk)

    empty = jnp.zeros((rows, heads, HEAD_DIM), f32)
    (d_key_rot, d_values), d_query_rot = lax.scan(backward_block, (empty, empty), jnp.arange(count))
    d_query_rot = d_query_rot.reshape(rows, heads, HEAD_DIM)
    d_values_b = d_values.reshape(rows, heads * HEAD_DIM).astype(bf16)
    d_query_n = rotate_back(d_query_rot, cosine, sine).reshape(rows, heads * HEAD_DIM)
    d_key_n = rotate_back(d_key_rot, cosine, sine).reshape(rows, heads * HEAD_DIM)
    grad_gq = jnp.sum(d_query_n * query_hat, axis=0)
    grad_gk = jnp.sum(d_key_n * key_hat, axis=0)
    d_query_hat = d_query_n * gq32
    d_key_hat = d_key_n * gk32
    query_inner, key_inner = lax.psum(
        (jnp.sum(d_query_hat * query_hat, axis=1), jnp.sum(d_key_hat * key_hat, axis=1)), "mp"
    )
    d_query_b = (query_factor * (d_query_hat - query_hat * (query_inner / width)[:, None])).astype(
        bf16
    )
    d_key_b = (key_factor * (d_key_hat - key_hat * (key_inner / width)[:, None])).astype(bf16)
    grad_wq = jnp.einsum("rd,rc->dc", tokens, d_query_b, preferred_element_type=f32)
    grad_wk = jnp.einsum("rd,rc->dc", tokens, d_key_b, preferred_element_type=f32)
    grad_wv = jnp.einsum("rd,rc->dc", tokens, d_values_b, preferred_element_type=f32)
    input_part = jnp.einsum("rc,dc->rd", d_query_b, wq, preferred_element_type=f32)
    input_part = input_part + jnp.einsum("rc,dc->rd", d_key_b, wk, preferred_element_type=f32)
    input_part = input_part + jnp.einsum("rc,dc->rd", d_values_b, wv, preferred_element_type=f32)
    input_grad = d_hidden + input_total(input_part)
    every = (
        grad_scatter(grad_wq, 0),
        grad_scatter(grad_wk, 0),
        grad_scatter(grad_wv, 0),
        grad_scatter(grad_wo, 1),
        lax.psum_scatter(grad_gq, "dp", scatter_dimension=0, tiled=True),
        lax.psum_scatter(grad_gk, "dp", scatter_dimension=0, tiled=True),
        lax.psum_scatter(grad_ag, "dp", scatter_dimension=0, tiled=True),
        grad_scatter(grad_wg, 0),
        grad_scatter(grad_wu, 0),
        grad_scatter(grad_wd, 1),
        lax.psum_scatter(grad_mg, "dp", scatter_dimension=0, tiled=True),
    )
    attn_parts = every[:7]
    mlp_parts = every[7:]
    return (
        layer_out,
        input_grad,
        attn_parts[0],
        attn_parts[1],
        attn_parts[2],
        attn_parts[3],
        attn_parts[4],
        attn_parts[5],
        attn_parts[6],
        mlp_parts[0],
        mlp_parts[1],
        mlp_parts[2],
        mlp_parts[3],
    )


def solution(mesh):
    placed = (
        P("dp", None),
        P("dp", None),
        P("dp"),
        P("dp", None),
        P("dp", "mp"),
        P("dp", "mp"),
        P("dp", "mp"),
        P("mp", "dp"),
        P(("mp", "dp")),
        P(("mp", "dp")),
        P("dp"),
        P("dp", "mp"),
        P("dp", "mp"),
        P("mp", "dp"),
        P("dp"),
    )
    return jax.shard_map(
        per_device,
        mesh=mesh,
        in_specs=placed,
        out_specs=(
            P("dp", None),
            P("dp", None),
            P("dp", "mp"),
            P("dp", "mp"),
            P("dp", "mp"),
            P("mp", "dp"),
            P(("mp", "dp")),
            P(("mp", "dp")),
            P("dp"),
            P("dp", "mp"),
            P("dp", "mp"),
            P("mp", "dp"),
            P("dp"),
        ),
        check_vma=False,
    )
```

```python
import functools

import jax
import jax.numpy as jnp
import numpy as np
from jax import lax
from jax.sharding import PartitionSpec as P

HEAD_DIM = 128


EPS = 1e-06
THETA = 500000.0


def rope_tables(rows, head_dim):
    half = head_dim // 2
    inverse = THETA ** (-(jnp.arange(half).astype(jnp.float32) * 2.0) / head_dim)
    angles = jnp.arange(rows).astype(jnp.float32)[:, None] * inverse[None, :]
    return (jnp.cos(angles)[:, None, :], jnp.sin(angles)[:, None, :])


def rotate(value, cosine, sine):
    half = value.shape[-1] // 2
    first, second = (value[..., :half], value[..., half:])
    return jnp.concatenate(
        [first * cosine - second * sine, second * cosine + first * sine], axis=-1
    )


def rotate_back(grad, cosine, sine):
    half = grad.shape[-1] // 2
    first, second = (grad[..., :half], grad[..., half:])
    return jnp.concatenate(
        [first * cosine + second * sine, second * cosine - first * sine], axis=-1
    )


def allowed_block(start, block, seg_row, length):
    query_pos = start + jnp.arange(block)
    key_pos = jnp.arange(seg_row.shape[0])
    same = seg_row[:, None] == seg_row[None, :]
    causal = key_pos[None, :] <= query_pos[:, None]
    inside = key_pos[None, :] < length
    return same & causal & inside | (key_pos[None, :] == query_pos[:, None])


def branch_total(partial_sum):
    return lax.psum(partial_sum, "mp")


def input_total(partial_sum):
    return lax.psum(partial_sum, "mp")


def norm_forward(total):
    factor = lax.rsqrt(jnp.mean(total * total, axis=1, keepdims=True) + EPS)
    return (total * factor, factor)


def norm_back(grad, normed, factor, gain):
    grad_gain = jnp.sum(grad * normed, axis=0)
    scaled = grad * gain
    inner = jnp.mean(scaled * normed, axis=1, keepdims=True)
    return (factor * (scaled - normed * inner), grad_gain)


def ring_order(mesh):
    column = [mesh.devices[i, 0] for i in range(mesh.devices.shape[0])]
    count = len(column)
    try:
        coords = [tuple(d.coords) for d in column]
    except AttributeError:
        return list(range(count))
    axes = [a for a in range(len(coords[0])) if len({c[a] for c in coords}) > 1]
    if len(axes) != 2:
        return list(range(count))
    sizes = {a: len({c[a] for c in coords}) for a in axes}
    even = [a for a in axes if sizes[a] % 2 == 0]
    if not even:
        return list(range(count))
    outer = min(even, key=lambda a: sizes[a])
    inner = [a for a in axes if a != outer][0]
    lo = {a: min(c[a] for c in coords) for a in axes}
    where = {(c[outer] - lo[outer], c[inner] - lo[inner]): i for i, c in enumerate(coords)}
    order = []
    for o in range(sizes[outer]):
        steps = range(sizes[inner]) if o % 2 == 0 else reversed(range(sizes[inner]))
        for k in steps:
            order.append(where[(o, k)])
    if sorted(order) != list(range(count)):
        return list(range(count))
    return order


def ring_gather(flat, ring):
    n = len(ring)
    if n == 1:
        return flat[None]
    pos_of = [ring.index(d) for d in range(n)]
    mypos = jnp.asarray(pos_of, jnp.int32)[lax.axis_index("dp")]
    fwd = [(ring[p], ring[(p + 1) % n]) for p in range(n)]
    bwd = [(ring[p], ring[(p - 1) % n]) for p in range(n)]
    nf = n // 2
    nb = n - 1 - nf
    parts = {0: flat}
    a = flat
    for s in range(nf):
        a = lax.ppermute(a, "dp", fwd)
        parts[-(s + 1)] = a
    b = flat
    for s in range(nb):
        b = lax.ppermute(b, "dp", bwd)
        parts[s + 1] = b
    stack = jnp.stack([parts[k] for k in range(-nf, nb + 1)])
    index = (jnp.asarray(pos_of, jnp.int32) - mypos + nf) % n
    return jnp.take(stack, index, axis=0)


def ring_scatter(chunks, ring, carry=jnp.bfloat16):
    n = len(ring)
    if n == 1:
        return chunks[0]
    pos_of = [ring.index(d) for d in range(n)]
    ring_arr = jnp.asarray(ring, jnp.int32)
    mypos = jnp.asarray(pos_of, jnp.int32)[lax.axis_index("dp")]
    fwd = [(ring[p], ring[(p + 1) % n]) for p in range(n)]
    bwd = [(ring[p], ring[(p - 1) % n]) for p in range(n)]
    nf = n // 2
    nb = n - 1 - nf

    def own(q):
        return lax.dynamic_index_in_dim(chunks, ring_arr[q % n], 0, keepdims=False)

    got_f = None
    for s in range(nf):
        val = own(mypos + nf - s)
        if got_f is not None:
            val = val + got_f.astype(jnp.float32)
        got_f = lax.ppermute(val.astype(carry), "dp", fwd)
    got_b = None
    for s in range(nb):
        val = own(mypos - nb + s)
        if got_b is not None:
            val = val + got_b.astype(jnp.float32)
        got_b = lax.ppermute(val.astype(carry), "dp", bwd)
    total = own(mypos) + got_f.astype(jnp.float32)
    if got_b is not None:
        total = total + got_b.astype(jnp.float32)
    return total


def gather_group(pieces, ring, after=None):
    n = len(ring)
    flat = jnp.concatenate([p.astype(jnp.bfloat16).reshape(-1) for p, _ in pieces])
    if after is not None:
        flat, _ = lax.optimization_barrier((flat, after))
    full = ring_gather(flat, ring)
    out = []
    start = 0
    for p, axis in pieces:
        size = p.size
        block = full[:, start:start + size].reshape((n,) + p.shape)
        start += size
        block = jnp.moveaxis(block, 0, axis)
        shape = list(p.shape)
        shape[axis] *= n
        out.append(block.reshape(shape))
    return out


def scatter_group(pieces, ring):
    n = len(ring)
    rows = []
    shapes = []
    for g, axis in pieces:
        shape = list(g.shape)
        shape[axis] //= n
        split = g.reshape(g.shape[:axis] + (n, shape[axis]) + g.shape[axis + 1:])
        split = jnp.moveaxis(split, axis, 0)
        rows.append(split.reshape(n, -1).astype(jnp.float32))
        shapes.append(tuple(shape))
    chunks = jnp.concatenate(rows, axis=1)
    total = ring_scatter(chunks, ring)
    out = []
    start = 0
    for shape in shapes:
        size = int(np.prod(shape))
        out.append(total[start:start + size].reshape(shape))
        start += size
    return out


def per_device(
    tokens,
    segment_ids,
    valid_lengths,
    cotangent,
    w_query,
    w_key,
    w_value,
    w_out,
    query_gain,
    key_gain,
    attn_gain,
    w_gate,
    w_up,
    w_down,
    mlp_gain,
    ring,
):
    f32 = jnp.float32
    bf16 = jnp.bfloat16
    rows, width = tokens.shape
    seg_row = segment_ids[0]
    length = valid_lengths[0]
    block = min(512, rows)
    count = rows // block
    scale = HEAD_DIM ** (-0.5)
    wq, wk, wv = gather_group([(w_query, 0), (w_key, 0), (w_value, 0)], ring)
    wo, gq, gk, ga = gather_group(
        [(w_out, 1), (query_gain, 0), (key_gain, 0), (attn_gain, 0)], ring, after=wv
    )
    wg, wu, gm = gather_group([(w_gate, 0), (w_up, 0), (mlp_gain, 0)], ring, after=wo)
    (wd,) = gather_group([(w_down, 1)], ring, after=wu)
    gq32 = gq.astype(f32)
    gk32 = gk.astype(f32)
    ga32 = ga.astype(f32)
    gm32 = gm.astype(f32)
    query = jnp.dot(tokens, wq, preferred_element_type=f32)
    keys = jnp.dot(tokens, wk, preferred_element_type=f32)
    values = jnp.dot(tokens, wv, preferred_element_type=f32).astype(bf16)
    query_sq, key_sq = lax.psum(
        (jnp.sum(query * query, axis=1), jnp.sum(keys * keys, axis=1)), "mp"
    )
    query_factor = lax.rsqrt(query_sq / width + EPS)[:, None]
    key_factor = lax.rsqrt(key_sq / width + EPS)[:, None]
    query_hat = query * query_factor
    key_hat = keys * key_factor
    heads = query.shape[1] // HEAD_DIM
    cosine, sine = rope_tables(rows, HEAD_DIM)
    query_rot = rotate((query_hat * gq32).reshape(rows, heads, HEAD_DIM), cosine, sine).astype(bf16)
    key_rot = rotate((key_hat * gk32).reshape(rows, heads, HEAD_DIM), cosine, sine).astype(bf16)
    values_h = values.reshape(rows, heads, HEAD_DIM)

    def block_scores(start):
        scores = jnp.einsum("qhe,khe->hqk", query_rot, key_rot, preferred_element_type=f32) * scale
        mask = allowed_block(start, block, seg_row, length)
        return (query_rot, jnp.where(mask[None], scores, -1e30))

    def forward_block(index):
        start = index * block
        q_blk, scores = block_scores(start)
        top = jnp.max(scores, axis=-1, keepdims=True)
        total = jnp.sum(jnp.exp(scores - top), axis=-1, keepdims=True)
        logsum = top + jnp.log(total)
        probs = jnp.exp(scores - logsum).astype(bf16)
        attended = jnp.einsum("hqk,khe->qhe", probs, values_h, preferred_element_type=f32)
        return (attended, logsum[..., 0])

    attended, logsums = lax.map(forward_block, jnp.arange(count))
    attended_b = attended.reshape(rows, heads * HEAD_DIM).astype(bf16)
    attn_partial = jnp.dot(attended_b, wo, preferred_element_type=f32)
    attn_total = branch_total(attn_partial)
    attn_hat, attn_factor = norm_forward(attn_total)
    hidden = tokens.astype(f32) + attn_hat * ga32
    hidden_b = hidden.astype(bf16)
    gate = jnp.dot(hidden_b, wg, preferred_element_type=f32)
    up = jnp.dot(hidden_b, wu, preferred_element_type=f32)
    active = jax.nn.silu(gate)
    mixed_b = (active * up).astype(bf16)
    mlp_partial = jnp.dot(mixed_b, wd, preferred_element_type=f32)
    mlp_total = branch_total(mlp_partial)
    mlp_hat, mlp_factor = norm_forward(mlp_total)
    layer_out = (hidden + mlp_hat * gm32).astype(bf16)
    grad_out = cotangent.astype(f32)
    d_mlp, grad_mg = norm_back(grad_out, mlp_hat, mlp_factor, gm32)
    d_mlp_b = d_mlp.astype(bf16)
    grad_wd = jnp.einsum("rf,rd->fd", mixed_b, d_mlp_b, preferred_element_type=f32)
    grad_wd_s, grad_mg_s = scatter_group([(grad_wd, 1), (grad_mg, 0)], ring)
    d_mixed = jnp.einsum("rd,fd->rf", d_mlp_b, wd, preferred_element_type=f32)
    sigma = jax.nn.sigmoid(gate)
    d_gate = (d_mixed * up * sigma * (1.0 + gate * (1.0 - sigma))).astype(bf16)
    d_up = (d_mixed * active).astype(bf16)
    grad_wg = jnp.einsum("rd,rf->df", hidden_b, d_gate, preferred_element_type=f32)
    grad_wu = jnp.einsum("rd,rf->df", hidden_b, d_up, preferred_element_type=f32)
    grad_wg_s, grad_wu_s = scatter_group([(grad_wg, 0), (grad_wu, 0)], ring)
    hidden_partial = jnp.einsum("rf,df->rd", d_gate, wg, preferred_element_type=f32) + jnp.einsum(
        "rf,df->rd", d_up, wu, preferred_element_type=f32
    )
    d_hidden = grad_out + input_total(hidden_partial)
    d_attn, grad_ag = norm_back(d_hidden, attn_hat, attn_factor, ga32)
    d_attn_b = d_attn.astype(bf16)
    grad_wo = jnp.einsum("rc,rd->cd", attended_b, d_attn_b, preferred_element_type=f32)
    grad_wo_s, grad_ag_s = scatter_group([(grad_wo, 1), (grad_ag, 0)], ring)
    d_attended = jnp.einsum("rd,cd->rc", d_attn_b, wo, preferred_element_type=f32).astype(bf16)
    d_attended = d_attended.reshape(rows, heads, HEAD_DIM)

    def backward_block(carry, index):
        key_acc, value_acc = carry
        start = index * block
        q_blk, scores = block_scores(start)
        logsum = lax.dynamic_index_in_dim(logsums, index, 0, keepdims=False)
        probs = jnp.exp(scores - logsum[..., None])
        value_acc = value_acc + jnp.einsum(
            "hqk,qhe->khe", probs.astype(bf16), d_attended, preferred_element_type=f32
        )
        d_probs = jnp.einsum("qhe,khe->hqk", d_attended, values_h, preferred_element_type=f32)
        delta = jnp.sum(probs * d_probs, axis=-1, keepdims=True)
        d_scores = (probs * (d_probs - delta)).astype(bf16)
        d_query_blk = (
            jnp.einsum("hqk,khe->qhe", d_scores, key_rot, preferred_element_type=f32) * scale
        )
        key_acc = (
            key_acc
            + jnp.einsum("hqk,qhe->khe", d_scores, q_blk, preferred_element_type=f32) * scale
        )
        return ((key_acc, value_acc), d_query_blk)

    empty = jnp.zeros((rows, heads, HEAD_DIM), f32)
    (d_key_rot, d_values), d_query_rot = lax.scan(backward_block, (empty, empty), jnp.arange(count))
    d_query_rot = d_query_rot.reshape(rows, heads, HEAD_DIM)
    d_values_b = d_values.reshape(rows, heads * HEAD_DIM).astype(bf16)
    d_query_n = rotate_back(d_query_rot, cosine, sine).reshape(rows, heads * HEAD_DIM)
    d_key_n = rotate_back(d_key_rot, cosine, sine).reshape(rows, heads * HEAD_DIM)
    grad_gq = jnp.sum(d_query_n * query_hat, axis=0)
    grad_gk = jnp.sum(d_key_n * key_hat, axis=0)
    d_query_hat = d_query_n * gq32
    d_key_hat = d_key_n * gk32
    query_inner, key_inner = lax.psum(
        (jnp.sum(d_query_hat * query_hat, axis=1), jnp.sum(d_key_hat * key_hat, axis=1)), "mp"
    )
    d_query_b = (query_factor * (d_query_hat - query_hat * (query_inner / width)[:, None])).astype(
        bf16
    )
    d_key_b = (key_factor * (d_key_hat - key_hat * (key_inner / width)[:, None])).astype(bf16)
    grad_wq = jnp.einsum("rd,rc->dc", tokens, d_query_b, preferred_element_type=f32)
    grad_wk = jnp.einsum("rd,rc->dc", tokens, d_key_b, preferred_element_type=f32)
    grad_wv = jnp.einsum("rd,rc->dc", tokens, d_values_b, preferred_element_type=f32)
    grad_wq_s, grad_wk_s, grad_wv_s, grad_gq_s, grad_gk_s = scatter_group(
        [(grad_wq, 0), (grad_wk, 0), (grad_wv, 0), (grad_gq, 0), (grad_gk, 0)], ring
    )
    input_part = jnp.einsum("rc,dc->rd", d_query_b, wq, preferred_element_type=f32)
    input_part = input_part + jnp.einsum("rc,dc->rd", d_key_b, wk, preferred_element_type=f32)
    input_part = input_part + jnp.einsum("rc,dc->rd", d_values_b, wv, preferred_element_type=f32)
    input_grad = d_hidden + input_total(input_part)
    return (
        layer_out,
        input_grad,
        grad_wq_s,
        grad_wk_s,
        grad_wv_s,
        grad_wo_s,
        grad_gq_s,
        grad_gk_s,
        grad_ag_s,
        grad_wg_s,
        grad_wu_s,
        grad_wd_s,
        grad_mg_s,
    )


def solution(mesh):
    placed = (
        P("dp", None),
        P("dp", None),
        P("dp"),
        P("dp", None),
        P("dp", "mp"),
        P("dp", "mp"),
        P("dp", "mp"),
        P("mp", "dp"),
        P(("mp", "dp")),
        P(("mp", "dp")),
        P("dp"),
        P("dp", "mp"),
        P("dp", "mp"),
        P("mp", "dp"),
        P("dp"),
    )
    ring = ring_order(mesh)
    return jax.shard_map(
        functools.partial(per_device, ring=ring),
        mesh=mesh,
        in_specs=placed,
        out_specs=(
            P("dp", None),
            P("dp", None),
            P("dp", "mp"),
            P("dp", "mp"),
            P("dp", "mp"),
            P("mp", "dp"),
            P(("mp", "dp")),
            P(("mp", "dp")),
            P("dp"),
            P("dp", "mp"),
            P("dp", "mp"),
            P("mp", "dp"),
            P("dp"),
        ),
        check_vma=False,
    )
```

```python
import functools

import jax
import jax.numpy as jnp
import numpy as np
from jax import lax
from jax.sharding import PartitionSpec as P

HEAD_DIM = 128


EPS = 1e-06
THETA = 500000.0


def rope_tables(rows, head_dim):
    half = head_dim // 2
    inverse = THETA ** (-(jnp.arange(half).astype(jnp.float32) * 2.0) / head_dim)
    angles = jnp.arange(rows).astype(jnp.float32)[:, None] * inverse[None, :]
    return (jnp.cos(angles)[:, None, :], jnp.sin(angles)[:, None, :])


def rotate(value, cosine, sine):
    half = value.shape[-1] // 2
    first, second = (value[..., :half], value[..., half:])
    return jnp.concatenate(
        [first * cosine - second * sine, second * cosine + first * sine], axis=-1
    )


def rotate_back(grad, cosine, sine):
    half = grad.shape[-1] // 2
    first, second = (grad[..., :half], grad[..., half:])
    return jnp.concatenate(
        [first * cosine + second * sine, second * cosine - first * sine], axis=-1
    )


def allowed_block(start, block, seg_row, length):
    query_pos = start + jnp.arange(block)
    key_pos = jnp.arange(seg_row.shape[0])
    same = seg_row[:, None] == seg_row[None, :]
    causal = key_pos[None, :] <= query_pos[:, None]
    inside = key_pos[None, :] < length
    return same & causal & inside | (key_pos[None, :] == query_pos[:, None])


def branch_total(partial_sum):
    return lax.psum(partial_sum, "mp")


def input_total(partial_sum):
    return lax.psum(partial_sum, "mp")


def norm_forward(total):
    factor = lax.rsqrt(jnp.mean(total * total, axis=1, keepdims=True) + EPS)
    return (total * factor, factor)


def norm_back(grad, normed, factor, gain):
    grad_gain = jnp.sum(grad * normed, axis=0)
    scaled = grad * gain
    inner = jnp.mean(scaled * normed, axis=1, keepdims=True)
    return (factor * (scaled - normed * inner), grad_gain)


def ring_order(mesh):
    column = [mesh.devices[i, 0] for i in range(mesh.devices.shape[0])]
    count = len(column)
    try:
        coords = [tuple(d.coords) for d in column]
    except AttributeError:
        return list(range(count))
    axes = [a for a in range(len(coords[0])) if len({c[a] for c in coords}) > 1]
    if len(axes) != 2:
        return list(range(count))
    sizes = {a: len({c[a] for c in coords}) for a in axes}
    even = [a for a in axes if sizes[a] % 2 == 0]
    if not even:
        return list(range(count))
    outer = min(even, key=lambda a: sizes[a])
    inner = [a for a in axes if a != outer][0]
    lo = {a: min(c[a] for c in coords) for a in axes}
    where = {(c[outer] - lo[outer], c[inner] - lo[inner]): i for i, c in enumerate(coords)}
    order = []
    for o in range(sizes[outer]):
        steps = range(sizes[inner]) if o % 2 == 0 else reversed(range(sizes[inner]))
        for k in steps:
            order.append(where[(o, k)])
    if sorted(order) != list(range(count)):
        return list(range(count))
    return order


def ring_steps(ring):
    n = len(ring)
    pos_of = [ring.index(d) for d in range(n)]
    mypos = jnp.asarray(pos_of, jnp.int32)[lax.axis_index("dp")]
    fwd = [(ring[p], ring[(p + 1) % n]) for p in range(n)]
    bwd = [(ring[p], ring[(p - 1) % n]) for p in range(n)]
    nf = n // 2
    return n, mypos, fwd, bwd, nf, n - 1 - nf


def gather_group(pieces, ring, after=None):
    locals_ = tuple(p.astype(jnp.bfloat16) for p, _ in pieces)
    if after is not None:
        locals_, _ = lax.optimization_barrier((locals_, after))
    n, mypos, fwd, bwd, nf, nb = ring_steps(ring)
    ring_arr = jnp.asarray(ring, jnp.int32)
    parts = {0: locals_}
    a = locals_
    for s in range(nf):
        a = lax.ppermute(a, "dp", fwd)
        parts[-(s + 1)] = a
    b = locals_
    for s in range(nb):
        b = lax.ppermute(b, "dp", bwd)
        parts[s + 1] = b
    out = []
    for i, (p, axis) in enumerate(pieces):
        shape = list(p.shape)
        width = shape[axis]
        shape[axis] *= n
        full = jnp.zeros(shape, jnp.bfloat16)
        for k in range(-nf, nb + 1):
            owner = ring_arr[(mypos + k) % n]
            full = lax.dynamic_update_slice_in_dim(full, parts[k][i], owner * width, axis)
        out.append(full)
    return out


def scatter_group(pieces, ring, carry=jnp.bfloat16):
    n, mypos, fwd, bwd, nf, nb = ring_steps(ring)
    ring_arr = jnp.asarray(ring, jnp.int32)
    widths = [g.shape[axis] // n for g, axis in pieces]

    def own(q):
        owner = ring_arr[q % n]
        return tuple(
            lax.dynamic_slice_in_dim(g, owner * w, w, axis).astype(jnp.float32)
            for (g, axis), w in zip(pieces, widths)
        )

    def send(vals, got, perm):
        if got is not None:
            vals = tuple(v + r.astype(jnp.float32) for v, r in zip(vals, got))
        return lax.ppermute(tuple(v.astype(carry) for v in vals), "dp", perm)

    got_f = None
    for s in range(nf):
        got_f = send(own(mypos + nf - s), got_f, fwd)
    got_b = None
    for s in range(nb):
        got_b = send(own(mypos - nb + s), got_b, bwd)
    total = own(mypos)
    total = tuple(t + r.astype(jnp.float32) for t, r in zip(total, got_f))
    if got_b is not None:
        total = tuple(t + r.astype(jnp.float32) for t, r in zip(total, got_b))
    return list(total)


def per_device(
    tokens,
    segment_ids,
    valid_lengths,
    cotangent,
    w_query,
    w_key,
    w_value,
    w_out,
    query_gain,
    key_gain,
    attn_gain,
    w_gate,
    w_up,
    w_down,
    mlp_gain,
    ring,
):
    f32 = jnp.float32
    bf16 = jnp.bfloat16
    rows, width = tokens.shape
    seg_row = segment_ids[0]
    length = valid_lengths[0]
    block = min(512, rows)
    count = rows // block
    scale = HEAD_DIM ** (-0.5)
    wq, wk, wv = gather_group([(w_query, 0), (w_key, 0), (w_value, 0)], ring)
    wo, gq, gk, ga = gather_group(
        [(w_out, 1), (query_gain, 0), (key_gain, 0), (attn_gain, 0)], ring, after=wv
    )
    wg, wu, gm = gather_group([(w_gate, 0), (w_up, 0), (mlp_gain, 0)], ring, after=wo)
    (wd,) = gather_group([(w_down, 1)], ring, after=wu)
    gq32 = gq.astype(f32)
    gk32 = gk.astype(f32)
    ga32 = ga.astype(f32)
    gm32 = gm.astype(f32)
    query = jnp.dot(tokens, wq, preferred_element_type=f32)
    keys = jnp.dot(tokens, wk, preferred_element_type=f32)
    values = jnp.dot(tokens, wv, preferred_element_type=f32).astype(bf16)
    query_sq, key_sq = lax.psum(
        (jnp.sum(query * query, axis=1), jnp.sum(keys * keys, axis=1)), "mp"
    )
    query_factor = lax.rsqrt(query_sq / width + EPS)[:, None]
    key_factor = lax.rsqrt(key_sq / width + EPS)[:, None]
    query_hat = query * query_factor
    key_hat = keys * key_factor
    heads = query.shape[1] // HEAD_DIM
    cosine, sine = rope_tables(rows, HEAD_DIM)
    query_rot = rotate((query_hat * gq32).reshape(rows, heads, HEAD_DIM), cosine, sine).astype(bf16)
    key_rot = rotate((key_hat * gk32).reshape(rows, heads, HEAD_DIM), cosine, sine).astype(bf16)
    values_h = values.reshape(rows, heads, HEAD_DIM)

    def block_scores(start):
        scores = jnp.einsum("qhe,khe->hqk", query_rot, key_rot, preferred_element_type=f32) * scale
        mask = allowed_block(start, block, seg_row, length)
        return (query_rot, jnp.where(mask[None], scores, -1e30))

    def forward_block(index):
        start = index * block
        q_blk, scores = block_scores(start)
        top = jnp.max(scores, axis=-1, keepdims=True)
        total = jnp.sum(jnp.exp(scores - top), axis=-1, keepdims=True)
        logsum = top + jnp.log(total)
        probs = jnp.exp(scores - logsum).astype(bf16)
        attended = jnp.einsum("hqk,khe->qhe", probs, values_h, preferred_element_type=f32)
        return (attended, logsum[..., 0])

    attended, logsums = lax.map(forward_block, jnp.arange(count))
    attended_b = attended.reshape(rows, heads * HEAD_DIM).astype(bf16)
    attn_partial = jnp.dot(attended_b, wo, preferred_element_type=f32)
    attn_total = branch_total(attn_partial)
    attn_hat, attn_factor = norm_forward(attn_total)
    hidden = tokens.astype(f32) + attn_hat * ga32
    hidden_b = hidden.astype(bf16)
    gate = jnp.dot(hidden_b, wg, preferred_element_type=f32)
    up = jnp.dot(hidden_b, wu, preferred_element_type=f32)
    active = jax.nn.silu(gate)
    mixed_b = (active * up).astype(bf16)
    mlp_partial = jnp.dot(mixed_b, wd, preferred_element_type=f32)
    mlp_total = branch_total(mlp_partial)
    mlp_hat, mlp_factor = norm_forward(mlp_total)
    layer_out = (hidden + mlp_hat * gm32).astype(bf16)
    grad_out = cotangent.astype(f32)
    d_mlp, grad_mg = norm_back(grad_out, mlp_hat, mlp_factor, gm32)
    d_mlp_b = d_mlp.astype(bf16)
    grad_wd = jnp.einsum("rf,rd->fd", mixed_b, d_mlp_b, preferred_element_type=f32)
    grad_wd_s, grad_mg_s = scatter_group([(grad_wd, 1), (grad_mg, 0)], ring)
    d_mixed = jnp.einsum("rd,fd->rf", d_mlp_b, wd, preferred_element_type=f32)
    sigma = jax.nn.sigmoid(gate)
    d_gate = (d_mixed * up * sigma * (1.0 + gate * (1.0 - sigma))).astype(bf16)
    d_up = (d_mixed * active).astype(bf16)
    grad_wg = jnp.einsum("rd,rf->df", hidden_b, d_gate, preferred_element_type=f32)
    grad_wu = jnp.einsum("rd,rf->df", hidden_b, d_up, preferred_element_type=f32)
    grad_wg_s, grad_wu_s = scatter_group([(grad_wg, 0), (grad_wu, 0)], ring)
    hidden_partial = jnp.einsum("rf,df->rd", d_gate, wg, preferred_element_type=f32) + jnp.einsum(
        "rf,df->rd", d_up, wu, preferred_element_type=f32
    )
    d_hidden = grad_out + input_total(hidden_partial)
    d_attn, grad_ag = norm_back(d_hidden, attn_hat, attn_factor, ga32)
    d_attn_b = d_attn.astype(bf16)
    grad_wo = jnp.einsum("rc,rd->cd", attended_b, d_attn_b, preferred_element_type=f32)
    grad_wo_s, grad_ag_s = scatter_group([(grad_wo, 1), (grad_ag, 0)], ring)
    d_attended = jnp.einsum("rd,cd->rc", d_attn_b, wo, preferred_element_type=f32).astype(bf16)
    d_attended = d_attended.reshape(rows, heads, HEAD_DIM)

    def backward_block(carry, index):
        key_acc, value_acc = carry
        start = index * block
        q_blk, scores = block_scores(start)
        logsum = lax.dynamic_index_in_dim(logsums, index, 0, keepdims=False)
        probs = jnp.exp(scores - logsum[..., None])
        value_acc = value_acc + jnp.einsum(
            "hqk,qhe->khe", probs.astype(bf16), d_attended, preferred_element_type=f32
        )
        d_probs = jnp.einsum("qhe,khe->hqk", d_attended, values_h, preferred_element_type=f32)
        delta = jnp.sum(probs * d_probs, axis=-1, keepdims=True)
        d_scores = (probs * (d_probs - delta)).astype(bf16)
        d_query_blk = (
            jnp.einsum("hqk,khe->qhe", d_scores, key_rot, preferred_element_type=f32) * scale
        )
        key_acc = (
            key_acc
            + jnp.einsum("hqk,qhe->khe", d_scores, q_blk, preferred_element_type=f32) * scale
        )
        return ((key_acc, value_acc), d_query_blk)

    empty = jnp.zeros((rows, heads, HEAD_DIM), f32)
    (d_key_rot, d_values), d_query_rot = lax.scan(backward_block, (empty, empty), jnp.arange(count))
    d_query_rot = d_query_rot.reshape(rows, heads, HEAD_DIM)
    d_values_b = d_values.reshape(rows, heads * HEAD_DIM).astype(bf16)
    d_query_n = rotate_back(d_query_rot, cosine, sine).reshape(rows, heads * HEAD_DIM)
    d_key_n = rotate_back(d_key_rot, cosine, sine).reshape(rows, heads * HEAD_DIM)
    grad_gq = jnp.sum(d_query_n * query_hat, axis=0)
    grad_gk = jnp.sum(d_key_n * key_hat, axis=0)
    d_query_hat = d_query_n * gq32
    d_key_hat = d_key_n * gk32
    query_inner, key_inner = lax.psum(
        (jnp.sum(d_query_hat * query_hat, axis=1), jnp.sum(d_key_hat * key_hat, axis=1)), "mp"
    )
    d_query_b = (query_factor * (d_query_hat - query_hat * (query_inner / width)[:, None])).astype(
        bf16
    )
    d_key_b = (key_factor * (d_key_hat - key_hat * (key_inner / width)[:, None])).astype(bf16)
    grad_wq = jnp.einsum("rd,rc->dc", tokens, d_query_b, preferred_element_type=f32)
    grad_wk = jnp.einsum("rd,rc->dc", tokens, d_key_b, preferred_element_type=f32)
    grad_wv = jnp.einsum("rd,rc->dc", tokens, d_values_b, preferred_element_type=f32)
    grad_wq_s, grad_wk_s, grad_wv_s, grad_gq_s, grad_gk_s = scatter_group(
        [(grad_wq, 0), (grad_wk, 0), (grad_wv, 0), (grad_gq, 0), (grad_gk, 0)], ring
    )
    input_part = jnp.einsum("rc,dc->rd", d_query_b, wq, preferred_element_type=f32)
    input_part = input_part + jnp.einsum("rc,dc->rd", d_key_b, wk, preferred_element_type=f32)
    input_part = input_part + jnp.einsum("rc,dc->rd", d_values_b, wv, preferred_element_type=f32)
    input_grad = d_hidden + input_total(input_part)
    return (
        layer_out,
        input_grad,
        grad_wq_s,
        grad_wk_s,
        grad_wv_s,
        grad_wo_s,
        grad_gq_s,
        grad_gk_s,
        grad_ag_s,
        grad_wg_s,
        grad_wu_s,
        grad_wd_s,
        grad_mg_s,
    )


def solution(mesh):
    placed = (
        P("dp", None),
        P("dp", None),
        P("dp"),
        P("dp", None),
        P("dp", "mp"),
        P("dp", "mp"),
        P("dp", "mp"),
        P("mp", "dp"),
        P(("mp", "dp")),
        P(("mp", "dp")),
        P("dp"),
        P("dp", "mp"),
        P("dp", "mp"),
        P("mp", "dp"),
        P("dp"),
    )
    ring = ring_order(mesh)
    return jax.shard_map(
        functools.partial(per_device, ring=ring),
        mesh=mesh,
        in_specs=placed,
        out_specs=(
            P("dp", None),
            P("dp", None),
            P("dp", "mp"),
            P("dp", "mp"),
            P("dp", "mp"),
            P("mp", "dp"),
            P(("mp", "dp")),
            P(("mp", "dp")),
            P("dp"),
            P("dp", "mp"),
            P("dp", "mp"),
            P("mp", "dp"),
            P("dp"),
        ),
        check_vma=False,
    )
```

```python
import functools

import jax
import jax.numpy as jnp
import numpy as np
from jax import lax
from jax.sharding import PartitionSpec as P

HEAD_DIM = 128


EPS = 1e-06
THETA = 500000.0


def rope_tables(rows, head_dim):
    half = head_dim // 2
    inverse = THETA ** (-(jnp.arange(half).astype(jnp.float32) * 2.0) / head_dim)
    angles = jnp.arange(rows).astype(jnp.float32)[:, None] * inverse[None, :]
    return (jnp.cos(angles)[:, None, :], jnp.sin(angles)[:, None, :])


def rotate(value, cosine, sine):
    half = value.shape[-1] // 2
    first, second = (value[..., :half], value[..., half:])
    return jnp.concatenate(
        [first * cosine - second * sine, second * cosine + first * sine], axis=-1
    )


def rotate_back(grad, cosine, sine):
    half = grad.shape[-1] // 2
    first, second = (grad[..., :half], grad[..., half:])
    return jnp.concatenate(
        [first * cosine + second * sine, second * cosine - first * sine], axis=-1
    )


def allowed_block(start, block, seg_row, length):
    query_pos = start + jnp.arange(block)
    key_pos = jnp.arange(seg_row.shape[0])
    same = seg_row[:, None] == seg_row[None, :]
    causal = key_pos[None, :] <= query_pos[:, None]
    inside = key_pos[None, :] < length
    return same & causal & inside | (key_pos[None, :] == query_pos[:, None])


def mp_allreduce(x, carry=jnp.bfloat16):
    m = lax.axis_size("mp")
    me = lax.axis_index("mp")
    core = me % 2
    chips = m // 2
    chip = me // 2
    half = x.shape[1] // 2
    pair = [(i, i ^ 1) for i in range(m)]
    mine = lax.dynamic_slice_in_dim(x, core * half, half, 1)
    other = lax.dynamic_slice_in_dim(x, (1 - core) * half, half, 1)
    part = mine + lax.ppermute(other, "mp", pair)
    if chips > 1:
        low = part.astype(carry)
        got = [low]
        for k in range(1, chips):
            perm = [(c * 2 + r, ((c + k) % chips) * 2 + r) for c in range(chips) for r in range(2)]
            got.append(lax.ppermute(low, "mp", perm))
        stack = jnp.stack(got)
        order = (chip - jnp.arange(chips)) % chips
        ordered = jnp.take(stack, order, axis=0).astype(jnp.float32)
        part = ordered[0]
        for k in range(1, chips):
            part = part + ordered[k]
    swapped = lax.ppermute(part, "mp", pair)
    full = jnp.zeros(x.shape, jnp.float32)
    full = lax.dynamic_update_slice_in_dim(full, part, core * half, 1)
    full = lax.dynamic_update_slice_in_dim(full, swapped, (1 - core) * half, 1)
    return full


def branch_total(partial_sum):
    return mp_allreduce(partial_sum)


def input_total(partial_sum):
    return mp_allreduce(partial_sum)


def norm_forward(total):
    factor = lax.rsqrt(jnp.mean(total * total, axis=1, keepdims=True) + EPS)
    return (total * factor, factor)


def norm_back(grad, normed, factor, gain):
    grad_gain = jnp.sum(grad * normed, axis=0)
    scaled = grad * gain
    inner = jnp.mean(scaled * normed, axis=1, keepdims=True)
    return (factor * (scaled - normed * inner), grad_gain)


def ring_order(mesh):
    column = [mesh.devices[i, 0] for i in range(mesh.devices.shape[0])]
    count = len(column)
    try:
        coords = [tuple(d.coords) for d in column]
    except AttributeError:
        return list(range(count))
    axes = [a for a in range(len(coords[0])) if len({c[a] for c in coords}) > 1]
    if len(axes) != 2:
        return list(range(count))
    sizes = {a: len({c[a] for c in coords}) for a in axes}
    even = [a for a in axes if sizes[a] % 2 == 0]
    if not even:
        return list(range(count))
    outer = min(even, key=lambda a: sizes[a])
    inner = [a for a in axes if a != outer][0]
    lo = {a: min(c[a] for c in coords) for a in axes}
    where = {(c[outer] - lo[outer], c[inner] - lo[inner]): i for i, c in enumerate(coords)}
    order = []
    for o in range(sizes[outer]):
        steps = range(sizes[inner]) if o % 2 == 0 else reversed(range(sizes[inner]))
        for k in steps:
            order.append(where[(o, k)])
    if sorted(order) != list(range(count)):
        return list(range(count))
    return order


def ring_steps(ring):
    n = len(ring)
    pos_of = [ring.index(d) for d in range(n)]
    mypos = jnp.asarray(pos_of, jnp.int32)[lax.axis_index("dp")]
    fwd = [(ring[p], ring[(p + 1) % n]) for p in range(n)]
    bwd = [(ring[p], ring[(p - 1) % n]) for p in range(n)]
    nf = n // 2
    return n, mypos, fwd, bwd, nf, n - 1 - nf


def gather_group(pieces, ring, after=None):
    locals_ = tuple(p.astype(jnp.bfloat16) for p, _ in pieces)
    if after is not None:
        locals_, _ = lax.optimization_barrier((locals_, after))
    n, mypos, fwd, bwd, nf, nb = ring_steps(ring)
    ring_arr = jnp.asarray(ring, jnp.int32)
    parts = {0: locals_}
    a = locals_
    for s in range(nf):
        a = lax.ppermute(a, "dp", fwd)
        parts[-(s + 1)] = a
    b = locals_
    for s in range(nb):
        b = lax.ppermute(b, "dp", bwd)
        parts[s + 1] = b
    out = []
    last = parts[-nf] if nf else locals_
    for i, (p, axis) in enumerate(pieces):
        shape = list(p.shape)
        width = shape[axis]
        shape[axis] *= n
        full = jnp.zeros(shape, jnp.bfloat16)
        for k in range(-nf, nb + 1):
            owner = ring_arr[(mypos + k) % n]
            full = lax.dynamic_update_slice_in_dim(full, parts[k][i], owner * width, axis)
        out.append(full)
    return out, last


def scatter_group(pieces, ring, carry=jnp.bfloat16):
    n, mypos, fwd, bwd, nf, nb = ring_steps(ring)
    ring_arr = jnp.asarray(ring, jnp.int32)
    widths = [g.shape[axis] // n for g, axis in pieces]

    def own(q):
        owner = ring_arr[q % n]
        return tuple(
            lax.dynamic_slice_in_dim(g, owner * w, w, axis).astype(jnp.float32)
            for (g, axis), w in zip(pieces, widths)
        )

    def send(vals, got, perm):
        if got is not None:
            vals = tuple(v + r.astype(jnp.float32) for v, r in zip(vals, got))
        return lax.ppermute(tuple(v.astype(carry) for v in vals), "dp", perm)

    got_f = None
    for s in range(nf):
        got_f = send(own(mypos + nf - s), got_f, fwd)
    got_b = None
    for s in range(nb):
        got_b = send(own(mypos - nb + s), got_b, bwd)
    total = own(mypos)
    total = tuple(t + r.astype(jnp.float32) for t, r in zip(total, got_f))
    if got_b is not None:
        total = tuple(t + r.astype(jnp.float32) for t, r in zip(total, got_b))
    return list(total)


def per_device(
    tokens,
    segment_ids,
    valid_lengths,
    cotangent,
    w_query,
    w_key,
    w_value,
    w_out,
    query_gain,
    key_gain,
    attn_gain,
    w_gate,
    w_up,
    w_down,
    mlp_gain,
    ring,
):
    f32 = jnp.float32
    bf16 = jnp.bfloat16
    rows, width = tokens.shape
    seg_row = segment_ids[0]
    length = valid_lengths[0]
    block = min(512, rows)
    count = rows // block
    scale = HEAD_DIM ** (-0.5)
    (wq, wk, wv), seen = gather_group([(w_query, 0), (w_key, 0), (w_value, 0)], ring)
    (wo, gq, gk, ga), seen = gather_group(
        [(w_out, 1), (query_gain, 0), (key_gain, 0), (attn_gain, 0)], ring, after=seen
    )
    (wg, wu, gm), seen = gather_group([(w_gate, 0), (w_up, 0), (mlp_gain, 0)], ring, after=seen)
    (wd,), seen = gather_group([(w_down, 1)], ring, after=seen)
    gq32 = gq.astype(f32)
    gk32 = gk.astype(f32)
    ga32 = ga.astype(f32)
    gm32 = gm.astype(f32)
    query = jnp.dot(tokens, wq, preferred_element_type=f32)
    keys = jnp.dot(tokens, wk, preferred_element_type=f32)
    values = jnp.dot(tokens, wv, preferred_element_type=f32).astype(bf16)
    query_sq, key_sq = lax.psum(
        (jnp.sum(query * query, axis=1), jnp.sum(keys * keys, axis=1)), "mp"
    )
    query_factor = lax.rsqrt(query_sq / width + EPS)[:, None]
    key_factor = lax.rsqrt(key_sq / width + EPS)[:, None]
    query_hat = query * query_factor
    key_hat = keys * key_factor
    heads = query.shape[1] // HEAD_DIM
    cosine, sine = rope_tables(rows, HEAD_DIM)
    query_rot = rotate((query_hat * gq32).reshape(rows, heads, HEAD_DIM), cosine, sine).astype(bf16)
    key_rot = rotate((key_hat * gk32).reshape(rows, heads, HEAD_DIM), cosine, sine).astype(bf16)
    values_h = values.reshape(rows, heads, HEAD_DIM)

    def block_scores(start):
        scores = jnp.einsum("qhe,khe->hqk", query_rot, key_rot, preferred_element_type=f32) * scale
        mask = allowed_block(start, block, seg_row, length)
        return (query_rot, jnp.where(mask[None], scores, -1e30))

    def forward_block(index):
        start = index * block
        q_blk, scores = block_scores(start)
        top = jnp.max(scores, axis=-1, keepdims=True)
        total = jnp.sum(jnp.exp(scores - top), axis=-1, keepdims=True)
        logsum = top + jnp.log(total)
        probs = jnp.exp(scores - logsum).astype(bf16)
        attended = jnp.einsum("hqk,khe->qhe", probs, values_h, preferred_element_type=f32)
        return (attended, logsum[..., 0])

    attended, logsums = lax.map(forward_block, jnp.arange(count))
    attended_b = attended.reshape(rows, heads * HEAD_DIM).astype(bf16)
    attn_partial = jnp.dot(attended_b, wo, preferred_element_type=f32)
    attn_total = branch_total(attn_partial)
    attn_hat, attn_factor = norm_forward(attn_total)
    hidden = tokens.astype(f32) + attn_hat * ga32
    hidden_b = hidden.astype(bf16)
    gate = jnp.dot(hidden_b, wg, preferred_element_type=f32)
    up = jnp.dot(hidden_b, wu, preferred_element_type=f32)
    active = jax.nn.silu(gate)
    mixed_b = (active * up).astype(bf16)
    mlp_partial = jnp.dot(mixed_b, wd, preferred_element_type=f32)
    mlp_total = branch_total(mlp_partial)
    mlp_hat, mlp_factor = norm_forward(mlp_total)
    layer_out = (hidden + mlp_hat * gm32).astype(bf16)
    grad_out = cotangent.astype(f32)
    d_mlp, grad_mg = norm_back(grad_out, mlp_hat, mlp_factor, gm32)
    d_mlp_b = d_mlp.astype(bf16)
    grad_wd = jnp.einsum("rf,rd->fd", mixed_b, d_mlp_b, preferred_element_type=f32)
    grad_wd_s, grad_mg_s = scatter_group([(grad_wd, 1), (grad_mg, 0)], ring)
    d_mixed = jnp.einsum("rd,fd->rf", d_mlp_b, wd, preferred_element_type=f32)
    sigma = jax.nn.sigmoid(gate)
    d_gate = (d_mixed * up * sigma * (1.0 + gate * (1.0 - sigma))).astype(bf16)
    d_up = (d_mixed * active).astype(bf16)
    grad_wg = jnp.einsum("rd,rf->df", hidden_b, d_gate, preferred_element_type=f32)
    grad_wu = jnp.einsum("rd,rf->df", hidden_b, d_up, preferred_element_type=f32)
    grad_wg_s, grad_wu_s = scatter_group([(grad_wg, 0), (grad_wu, 0)], ring)
    hidden_partial = jnp.einsum("rf,df->rd", d_gate, wg, preferred_element_type=f32) + jnp.einsum(
        "rf,df->rd", d_up, wu, preferred_element_type=f32
    )
    d_hidden = grad_out + input_total(hidden_partial)
    d_attn, grad_ag = norm_back(d_hidden, attn_hat, attn_factor, ga32)
    d_attn_b = d_attn.astype(bf16)
    grad_wo = jnp.einsum("rc,rd->cd", attended_b, d_attn_b, preferred_element_type=f32)
    grad_wo_s, grad_ag_s = scatter_group([(grad_wo, 1), (grad_ag, 0)], ring)
    d_attended = jnp.einsum("rd,cd->rc", d_attn_b, wo, preferred_element_type=f32).astype(bf16)
    d_attended = d_attended.reshape(rows, heads, HEAD_DIM)

    def backward_block(carry, index):
        key_acc, value_acc = carry
        start = index * block
        q_blk, scores = block_scores(start)
        logsum = lax.dynamic_index_in_dim(logsums, index, 0, keepdims=False)
        probs = jnp.exp(scores - logsum[..., None])
        value_acc = value_acc + jnp.einsum(
            "hqk,qhe->khe", probs.astype(bf16), d_attended, preferred_element_type=f32
        )
        d_probs = jnp.einsum("qhe,khe->hqk", d_attended, values_h, preferred_element_type=f32)
        delta = jnp.sum(probs * d_probs, axis=-1, keepdims=True)
        d_scores = (probs * (d_probs - delta)).astype(bf16)
        d_query_blk = (
            jnp.einsum("hqk,khe->qhe", d_scores, key_rot, preferred_element_type=f32) * scale
        )
        key_acc = (
            key_acc
            + jnp.einsum("hqk,qhe->khe", d_scores, q_blk, preferred_element_type=f32) * scale
        )
        return ((key_acc, value_acc), d_query_blk)

    empty = jnp.zeros((rows, heads, HEAD_DIM), f32)
    (d_key_rot, d_values), d_query_rot = lax.scan(backward_block, (empty, empty), jnp.arange(count))
    d_query_rot = d_query_rot.reshape(rows, heads, HEAD_DIM)
    d_values_b = d_values.reshape(rows, heads * HEAD_DIM).astype(bf16)
    d_query_n = rotate_back(d_query_rot, cosine, sine).reshape(rows, heads * HEAD_DIM)
    d_key_n = rotate_back(d_key_rot, cosine, sine).reshape(rows, heads * HEAD_DIM)
    grad_gq = jnp.sum(d_query_n * query_hat, axis=0)
    grad_gk = jnp.sum(d_key_n * key_hat, axis=0)
    d_query_hat = d_query_n * gq32
    d_key_hat = d_key_n * gk32
    query_inner, key_inner = lax.psum(
        (jnp.sum(d_query_hat * query_hat, axis=1), jnp.sum(d_key_hat * key_hat, axis=1)), "mp"
    )
    d_query_b = (query_factor * (d_query_hat - query_hat * (query_inner / width)[:, None])).astype(
        bf16
    )
    d_key_b = (key_factor * (d_key_hat - key_hat * (key_inner / width)[:, None])).astype(bf16)
    grad_wq = jnp.einsum("rd,rc->dc", tokens, d_query_b, preferred_element_type=f32)
    grad_wk = jnp.einsum("rd,rc->dc", tokens, d_key_b, preferred_element_type=f32)
    grad_wv = jnp.einsum("rd,rc->dc", tokens, d_values_b, preferred_element_type=f32)
    grad_wq_s, grad_wk_s, grad_wv_s, grad_gq_s, grad_gk_s = scatter_group(
        [(grad_wq, 0), (grad_wk, 0), (grad_wv, 0), (grad_gq, 0), (grad_gk, 0)], ring
    )
    input_part = jnp.einsum("rc,dc->rd", d_query_b, wq, preferred_element_type=f32)
    input_part = input_part + jnp.einsum("rc,dc->rd", d_key_b, wk, preferred_element_type=f32)
    input_part = input_part + jnp.einsum("rc,dc->rd", d_values_b, wv, preferred_element_type=f32)
    input_grad = d_hidden + input_total(input_part)
    return (
        layer_out,
        input_grad,
        grad_wq_s,
        grad_wk_s,
        grad_wv_s,
        grad_wo_s,
        grad_gq_s,
        grad_gk_s,
        grad_ag_s,
        grad_wg_s,
        grad_wu_s,
        grad_wd_s,
        grad_mg_s,
    )


def solution(mesh):
    placed = (
        P("dp", None),
        P("dp", None),
        P("dp"),
        P("dp", None),
        P("dp", "mp"),
        P("dp", "mp"),
        P("dp", "mp"),
        P("mp", "dp"),
        P(("mp", "dp")),
        P(("mp", "dp")),
        P("dp"),
        P("dp", "mp"),
        P("dp", "mp"),
        P("mp", "dp"),
        P("dp"),
    )
    ring = ring_order(mesh)
    return jax.shard_map(
        functools.partial(per_device, ring=ring),
        mesh=mesh,
        in_specs=placed,
        out_specs=(
            P("dp", None),
            P("dp", None),
            P("dp", "mp"),
            P("dp", "mp"),
            P("dp", "mp"),
            P("mp", "dp"),
            P(("mp", "dp")),
            P(("mp", "dp")),
            P("dp"),
            P("dp", "mp"),
            P("dp", "mp"),
            P("mp", "dp"),
            P("dp"),
        ),
        check_vma=False,
    )
```

```python
import functools

import jax
import jax.numpy as jnp
import numpy as np
from jax import lax
from jax.sharding import PartitionSpec as P

HEAD_DIM = 128


EPS = 1e-06
THETA = 500000.0


def rope_tables(rows, head_dim):
    half = head_dim // 2
    inverse = THETA ** (-(jnp.arange(half).astype(jnp.float32) * 2.0) / head_dim)
    angles = jnp.arange(rows).astype(jnp.float32)[:, None] * inverse[None, :]
    return (jnp.cos(angles)[:, None, :], jnp.sin(angles)[:, None, :])


def rotate(value, cosine, sine):
    half = value.shape[-1] // 2
    first, second = (value[..., :half], value[..., half:])
    return jnp.concatenate(
        [first * cosine - second * sine, second * cosine + first * sine], axis=-1
    )


def rotate_back(grad, cosine, sine):
    half = grad.shape[-1] // 2
    first, second = (grad[..., :half], grad[..., half:])
    return jnp.concatenate(
        [first * cosine + second * sine, second * cosine - first * sine], axis=-1
    )


def allowed_block(start, block, seg_row, length):
    query_pos = start + jnp.arange(block)
    key_pos = jnp.arange(seg_row.shape[0])
    same = seg_row[:, None] == seg_row[None, :]
    causal = key_pos[None, :] <= query_pos[:, None]
    inside = key_pos[None, :] < length
    return same & causal & inside | (key_pos[None, :] == query_pos[:, None])


def mp_allreduce(x, carry=jnp.bfloat16):
    m = lax.axis_size("mp")
    me = lax.axis_index("mp")
    core = me % 2
    chips = m // 2
    chip = me // 2
    half = x.shape[1] // 2
    pair = [(i, i ^ 1) for i in range(m)]
    mine = lax.dynamic_slice_in_dim(x, core * half, half, 1)
    other = lax.dynamic_slice_in_dim(x, (1 - core) * half, half, 1)
    part = mine + lax.ppermute(other, "mp", pair)
    if chips > 1:
        low = part.astype(carry)
        got = [low]
        for k in range(1, chips):
            perm = [(c * 2 + r, ((c + k) % chips) * 2 + r) for c in range(chips) for r in range(2)]
            got.append(lax.ppermute(low, "mp", perm))
        stack = jnp.stack(got)
        order = (chip - jnp.arange(chips)) % chips
        ordered = jnp.take(stack, order, axis=0).astype(jnp.float32)
        part = ordered[0]
        for k in range(1, chips):
            part = part + ordered[k]
    swapped = lax.ppermute(part, "mp", pair)
    full = jnp.zeros(x.shape, jnp.float32)
    full = lax.dynamic_update_slice_in_dim(full, part, core * half, 1)
    full = lax.dynamic_update_slice_in_dim(full, swapped, (1 - core) * half, 1)
    return full


def branch_total(partial_sum):
    return mp_allreduce(partial_sum)


def input_total(partial_sum):
    return mp_allreduce(partial_sum)


def norm_forward(total):
    factor = lax.rsqrt(jnp.mean(total * total, axis=1, keepdims=True) + EPS)
    return (total * factor, factor)


def norm_back(grad, normed, factor, gain):
    grad_gain = jnp.sum(grad * normed, axis=0)
    scaled = grad * gain
    inner = jnp.mean(scaled * normed, axis=1, keepdims=True)
    return (factor * (scaled - normed * inner), grad_gain)


def ring_order(mesh):
    column = [mesh.devices[i, 0] for i in range(mesh.devices.shape[0])]
    count = len(column)
    try:
        coords = [tuple(d.coords) for d in column]
    except AttributeError:
        return list(range(count))
    axes = [a for a in range(len(coords[0])) if len({c[a] for c in coords}) > 1]
    if len(axes) != 2:
        return list(range(count))
    sizes = {a: len({c[a] for c in coords}) for a in axes}
    even = [a for a in axes if sizes[a] % 2 == 0]
    if not even:
        return list(range(count))
    outer = min(even, key=lambda a: sizes[a])
    inner = [a for a in axes if a != outer][0]
    lo = {a: min(c[a] for c in coords) for a in axes}
    where = {(c[outer] - lo[outer], c[inner] - lo[inner]): i for i, c in enumerate(coords)}
    order = []
    for o in range(sizes[outer]):
        steps = range(sizes[inner]) if o % 2 == 0 else reversed(range(sizes[inner]))
        for k in steps:
            order.append(where[(o, k)])
    if sorted(order) != list(range(count)):
        return list(range(count))
    return order


def ring_steps(ring):
    n = len(ring)
    pos_of = [ring.index(d) for d in range(n)]
    mypos = jnp.asarray(pos_of, jnp.int32)[lax.axis_index("dp")]
    fwd = [(ring[p], ring[(p + 1) % n]) for p in range(n)]
    bwd = [(ring[p], ring[(p - 1) % n]) for p in range(n)]
    nf = n // 2
    return n, mypos, fwd, bwd, nf, n - 1 - nf


def gather_group(pieces, ring, after=None):
    locals_ = tuple(p.astype(jnp.bfloat16) for p, _ in pieces)
    if after is not None:
        locals_, _ = lax.optimization_barrier((locals_, after))
    n, mypos, fwd, bwd, nf, nb = ring_steps(ring)
    ring_arr = jnp.asarray(ring, jnp.int32)
    parts = {0: locals_}
    a = locals_
    for s in range(nf):
        a = lax.ppermute(a, "dp", fwd)
        parts[-(s + 1)] = a
    b = locals_
    for s in range(nb):
        b = lax.ppermute(b, "dp", bwd)
        parts[s + 1] = b
    out = []
    last = parts[-nf] if nf else locals_
    for i, (p, axis) in enumerate(pieces):
        shape = list(p.shape)
        width = shape[axis]
        shape[axis] *= n
        full = jnp.zeros(shape, jnp.bfloat16)
        for k in range(-nf, nb + 1):
            owner = ring_arr[(mypos + k) % n]
            full = lax.dynamic_update_slice_in_dim(full, parts[k][i], owner * width, axis)
        out.append(full)
    return out, last


def scatter_group(pieces, ring, carry=jnp.bfloat16):
    n, mypos, fwd, bwd, nf, nb = ring_steps(ring)
    ring_arr = jnp.asarray(ring, jnp.int32)
    widths = [g.shape[axis] // n for g, axis in pieces]

    def own(q):
        owner = ring_arr[q % n]
        return tuple(
            lax.dynamic_slice_in_dim(g, owner * w, w, axis).astype(jnp.float32)
            for (g, axis), w in zip(pieces, widths)
        )

    def send(vals, got, perm):
        if got is not None:
            vals = tuple(v + r.astype(jnp.float32) for v, r in zip(vals, got))
        return lax.ppermute(tuple(v.astype(carry) for v in vals), "dp", perm)

    got_f = None
    for s in range(nf):
        got_f = send(own(mypos + nf - s), got_f, fwd)
    got_b = None
    for s in range(nb):
        got_b = send(own(mypos - nb + s), got_b, bwd)
    total = own(mypos)
    total = tuple(t + r.astype(jnp.float32) for t, r in zip(total, got_f))
    if got_b is not None:
        total = tuple(t + r.astype(jnp.float32) for t, r in zip(total, got_b))
    return list(total)


def per_device(
    tokens,
    segment_ids,
    valid_lengths,
    cotangent,
    w_query,
    w_key,
    w_value,
    w_out,
    query_gain,
    key_gain,
    attn_gain,
    w_gate,
    w_up,
    w_down,
    mlp_gain,
    ring,
):
    f32 = jnp.float32
    bf16 = jnp.bfloat16
    rows, width = tokens.shape
    seg_row = segment_ids[0]
    length = valid_lengths[0]
    block = min(512, rows)
    count = rows // block
    scale = HEAD_DIM ** (-0.5)
    n_dp = len(ring)
    slab = attn_gain.shape[0]
    head_piece = query_gain.shape[0]

    def padded(g):
        return jnp.pad(g, (0, slab - g.shape[0]))

    gains = jnp.stack([padded(query_gain), padded(key_gain), attn_gain, mlp_gain])
    (qkv, gains_full), seen = gather_group(
        [(jnp.stack([w_query, w_key, w_value]), 1), (gains, 1)], ring
    )
    wq, wk, wv = qkv[0], qkv[1], qkv[2]
    gq = gains_full[0].reshape(n_dp, slab)[:, :head_piece].reshape(-1)
    gk = gains_full[1].reshape(n_dp, slab)[:, :head_piece].reshape(-1)
    ga = gains_full[2]
    gm = gains_full[3]
    (wo,), seen = gather_group([(w_out, 1)], ring, after=seen)
    (gu,), seen = gather_group([(jnp.stack([w_gate, w_up]), 1)], ring, after=seen)
    wg, wu = gu[0], gu[1]
    (wd,), seen = gather_group([(w_down, 1)], ring, after=seen)
    gq32 = gq.astype(f32)
    gk32 = gk.astype(f32)
    ga32 = ga.astype(f32)
    gm32 = gm.astype(f32)
    query = jnp.dot(tokens, wq, preferred_element_type=f32)
    keys = jnp.dot(tokens, wk, preferred_element_type=f32)
    values = jnp.dot(tokens, wv, preferred_element_type=f32).astype(bf16)
    query_sq, key_sq = lax.psum(
        (jnp.sum(query * query, axis=1), jnp.sum(keys * keys, axis=1)), "mp"
    )
    query_factor = lax.rsqrt(query_sq / width + EPS)[:, None]
    key_factor = lax.rsqrt(key_sq / width + EPS)[:, None]
    query_hat = query * query_factor
    key_hat = keys * key_factor
    heads = query.shape[1] // HEAD_DIM
    cosine, sine = rope_tables(rows, HEAD_DIM)
    query_rot = rotate((query_hat * gq32).reshape(rows, heads, HEAD_DIM), cosine, sine).astype(bf16)
    key_rot = rotate((key_hat * gk32).reshape(rows, heads, HEAD_DIM), cosine, sine).astype(bf16)
    values_h = values.reshape(rows, heads, HEAD_DIM)

    def block_scores(start):
        scores = jnp.einsum("qhe,khe->hqk", query_rot, key_rot, preferred_element_type=f32) * scale
        mask = allowed_block(start, block, seg_row, length)
        return (query_rot, jnp.where(mask[None], scores, -1e30))

    def forward_block(index):
        start = index * block
        q_blk, scores = block_scores(start)
        top = jnp.max(scores, axis=-1, keepdims=True)
        total = jnp.sum(jnp.exp(scores - top), axis=-1, keepdims=True)
        logsum = top + jnp.log(total)
        probs = jnp.exp(scores - logsum).astype(bf16)
        attended = jnp.einsum("hqk,khe->qhe", probs, values_h, preferred_element_type=f32)
        return (attended, logsum[..., 0])

    attended, logsums = lax.map(forward_block, jnp.arange(count))
    attended_b = attended.reshape(rows, heads * HEAD_DIM).astype(bf16)
    attn_partial = jnp.dot(attended_b, wo, preferred_element_type=f32)
    attn_total = branch_total(attn_partial)
    attn_hat, attn_factor = norm_forward(attn_total)
    hidden = tokens.astype(f32) + attn_hat * ga32
    hidden_b = hidden.astype(bf16)
    gate = jnp.dot(hidden_b, wg, preferred_element_type=f32)
    up = jnp.dot(hidden_b, wu, preferred_element_type=f32)
    active = jax.nn.silu(gate)
    mixed_b = (active * up).astype(bf16)
    mlp_partial = jnp.dot(mixed_b, wd, preferred_element_type=f32)
    mlp_total = branch_total(mlp_partial)
    mlp_hat, mlp_factor = norm_forward(mlp_total)
    layer_out = (hidden + mlp_hat * gm32).astype(bf16)
    grad_out = cotangent.astype(f32)
    d_mlp, grad_mg = norm_back(grad_out, mlp_hat, mlp_factor, gm32)
    d_mlp_b = d_mlp.astype(bf16)
    grad_wd = jnp.einsum("rf,rd->fd", mixed_b, d_mlp_b, preferred_element_type=f32)
    (grad_wd_s,) = scatter_group([(grad_wd, 1)], ring)
    d_mixed = jnp.einsum("rd,fd->rf", d_mlp_b, wd, preferred_element_type=f32)
    sigma = jax.nn.sigmoid(gate)
    d_gate = (d_mixed * up * sigma * (1.0 + gate * (1.0 - sigma))).astype(bf16)
    d_up = (d_mixed * active).astype(bf16)
    grad_gu = jnp.einsum(
        "rd,xrf->xdf", hidden_b, jnp.stack([d_gate, d_up]), preferred_element_type=f32
    )
    (grad_gu_s,) = scatter_group([(grad_gu, 1)], ring)
    grad_wg_s, grad_wu_s = grad_gu_s[0], grad_gu_s[1]
    hidden_partial = jnp.einsum("rf,df->rd", d_gate, wg, preferred_element_type=f32) + jnp.einsum(
        "rf,df->rd", d_up, wu, preferred_element_type=f32
    )
    d_hidden = grad_out + input_total(hidden_partial)
    d_attn, grad_ag = norm_back(d_hidden, attn_hat, attn_factor, ga32)
    d_attn_b = d_attn.astype(bf16)
    grad_wo = jnp.einsum("rc,rd->cd", attended_b, d_attn_b, preferred_element_type=f32)
    (grad_wo_s,) = scatter_group([(grad_wo, 1)], ring)
    d_attended = jnp.einsum("rd,cd->rc", d_attn_b, wo, preferred_element_type=f32).astype(bf16)
    d_attended = d_attended.reshape(rows, heads, HEAD_DIM)

    def backward_block(carry, index):
        key_acc, value_acc = carry
        start = index * block
        q_blk, scores = block_scores(start)
        logsum = lax.dynamic_index_in_dim(logsums, index, 0, keepdims=False)
        probs = jnp.exp(scores - logsum[..., None])
        value_acc = value_acc + jnp.einsum(
            "hqk,qhe->khe", probs.astype(bf16), d_attended, preferred_element_type=f32
        )
        d_probs = jnp.einsum("qhe,khe->hqk", d_attended, values_h, preferred_element_type=f32)
        delta = jnp.sum(probs * d_probs, axis=-1, keepdims=True)
        d_scores = (probs * (d_probs - delta)).astype(bf16)
        d_query_blk = (
            jnp.einsum("hqk,khe->qhe", d_scores, key_rot, preferred_element_type=f32) * scale
        )
        key_acc = (
            key_acc
            + jnp.einsum("hqk,qhe->khe", d_scores, q_blk, preferred_element_type=f32) * scale
        )
        return ((key_acc, value_acc), d_query_blk)

    empty = jnp.zeros((rows, heads, HEAD_DIM), f32)
    (d_key_rot, d_values), d_query_rot = lax.scan(backward_block, (empty, empty), jnp.arange(count))
    d_query_rot = d_query_rot.reshape(rows, heads, HEAD_DIM)
    d_values_b = d_values.reshape(rows, heads * HEAD_DIM).astype(bf16)
    d_query_n = rotate_back(d_query_rot, cosine, sine).reshape(rows, heads * HEAD_DIM)
    d_key_n = rotate_back(d_key_rot, cosine, sine).reshape(rows, heads * HEAD_DIM)
    grad_gq = jnp.sum(d_query_n * query_hat, axis=0)
    grad_gk = jnp.sum(d_key_n * key_hat, axis=0)
    d_query_hat = d_query_n * gq32
    d_key_hat = d_key_n * gk32
    query_inner, key_inner = lax.psum(
        (jnp.sum(d_query_hat * query_hat, axis=1), jnp.sum(d_key_hat * key_hat, axis=1)), "mp"
    )
    d_query_b = (query_factor * (d_query_hat - query_hat * (query_inner / width)[:, None])).astype(
        bf16
    )
    d_key_b = (key_factor * (d_key_hat - key_hat * (key_inner / width)[:, None])).astype(bf16)
    grad_qkv = jnp.einsum(
        "rd,xrc->xdc", tokens, jnp.stack([d_query_b, d_key_b, d_values_b]),
        preferred_element_type=f32,
    )
    (grad_qkv_s,) = scatter_group([(grad_qkv, 1)], ring)
    grad_wq_s, grad_wk_s, grad_wv_s = grad_qkv_s[0], grad_qkv_s[1], grad_qkv_s[2]

    def spread(g):
        return jnp.pad(g.reshape(n_dp, -1), ((0, 0), (0, slab - g.shape[0] // n_dp))).reshape(-1)

    grad_gains = jnp.stack([spread(grad_gq), spread(grad_gk), grad_ag, grad_mg])
    (grad_gains_s,) = scatter_group([(grad_gains, 1)], ring, carry=jnp.float32)
    grad_gq_s = grad_gains_s[0, :head_piece]
    grad_gk_s = grad_gains_s[1, :head_piece]
    grad_ag_s = grad_gains_s[2]
    grad_mg_s = grad_gains_s[3]
    input_part = jnp.einsum("rc,dc->rd", d_query_b, wq, preferred_element_type=f32)
    input_part = input_part + jnp.einsum("rc,dc->rd", d_key_b, wk, preferred_element_type=f32)
    input_part = input_part + jnp.einsum("rc,dc->rd", d_values_b, wv, preferred_element_type=f32)
    input_grad = d_hidden + input_total(input_part)
    return (
        layer_out,
        input_grad,
        grad_wq_s,
        grad_wk_s,
        grad_wv_s,
        grad_wo_s,
        grad_gq_s,
        grad_gk_s,
        grad_ag_s,
        grad_wg_s,
        grad_wu_s,
        grad_wd_s,
        grad_mg_s,
    )


def solution(mesh):
    placed = (
        P("dp", None),
        P("dp", None),
        P("dp"),
        P("dp", None),
        P("dp", "mp"),
        P("dp", "mp"),
        P("dp", "mp"),
        P("mp", "dp"),
        P(("mp", "dp")),
        P(("mp", "dp")),
        P("dp"),
        P("dp", "mp"),
        P("dp", "mp"),
        P("mp", "dp"),
        P("dp"),
    )
    ring = ring_order(mesh)
    return jax.shard_map(
        functools.partial(per_device, ring=ring),
        mesh=mesh,
        in_specs=placed,
        out_specs=(
            P("dp", None),
            P("dp", None),
            P("dp", "mp"),
            P("dp", "mp"),
            P("dp", "mp"),
            P("mp", "dp"),
            P(("mp", "dp")),
            P(("mp", "dp")),
            P("dp"),
            P("dp", "mp"),
            P("dp", "mp"),
            P("mp", "dp"),
            P("dp"),
        ),
        check_vma=False,
    )
```

```python
import functools

import jax
import jax.numpy as jnp
import numpy as np
from jax import lax
from jax.sharding import PartitionSpec as P

HEAD_DIM = 128


EPS = 1e-06
THETA = 500000.0


def rope_tables(rows, head_dim):
    half = head_dim // 2
    inverse = THETA ** (-(jnp.arange(half).astype(jnp.float32) * 2.0) / head_dim)
    angles = jnp.arange(rows).astype(jnp.float32)[:, None] * inverse[None, :]
    return (jnp.cos(angles)[:, None, :], jnp.sin(angles)[:, None, :])


def rotate(value, cosine, sine):
    half = value.shape[-1] // 2
    first, second = (value[..., :half], value[..., half:])
    return jnp.concatenate(
        [first * cosine - second * sine, second * cosine + first * sine], axis=-1
    )


def rotate_back(grad, cosine, sine):
    half = grad.shape[-1] // 2
    first, second = (grad[..., :half], grad[..., half:])
    return jnp.concatenate(
        [first * cosine + second * sine, second * cosine - first * sine], axis=-1
    )


def allowed_block(start, block, seg_row, length):
    query_pos = start + jnp.arange(block)
    key_pos = jnp.arange(seg_row.shape[0])
    same = seg_row[:, None] == seg_row[None, :]
    causal = key_pos[None, :] <= query_pos[:, None]
    inside = key_pos[None, :] < length
    return same & causal & inside | (key_pos[None, :] == query_pos[:, None])


def mp_allreduce(x, carry=jnp.bfloat16):
    m = lax.axis_size("mp")
    me = lax.axis_index("mp")
    core = me % 2
    chips = m // 2
    chip = me // 2
    half = x.shape[1] // 2
    pair = [(i, i ^ 1) for i in range(m)]
    mine = lax.dynamic_slice_in_dim(x, core * half, half, 1)
    other = lax.dynamic_slice_in_dim(x, (1 - core) * half, half, 1)
    part = mine + lax.ppermute(other, "mp", pair)
    if chips > 1:
        low = part.astype(carry)
        got = [low]
        for k in range(1, chips):
            perm = [(c * 2 + r, ((c + k) % chips) * 2 + r) for c in range(chips) for r in range(2)]
            got.append(lax.ppermute(low, "mp", perm))
        stack = jnp.stack(got)
        order = (chip - jnp.arange(chips)) % chips
        ordered = jnp.take(stack, order, axis=0).astype(jnp.float32)
        part = ordered[0]
        for k in range(1, chips):
            part = part + ordered[k]
    swapped = lax.ppermute(part, "mp", pair)
    full = jnp.zeros(x.shape, jnp.float32)
    full = lax.dynamic_update_slice_in_dim(full, part, core * half, 1)
    full = lax.dynamic_update_slice_in_dim(full, swapped, (1 - core) * half, 1)
    return full


def branch_total(partial_sum):
    return mp_allreduce(partial_sum)


def input_total(partial_sum):
    return mp_allreduce(partial_sum)


def norm_forward(total):
    factor = lax.rsqrt(jnp.mean(total * total, axis=1, keepdims=True) + EPS)
    return (total * factor, factor)


def norm_back(grad, normed, factor, gain):
    grad_gain = jnp.sum(grad * normed, axis=0)
    scaled = grad * gain
    inner = jnp.mean(scaled * normed, axis=1, keepdims=True)
    return (factor * (scaled - normed * inner), grad_gain)


def ring_order(mesh):
    column = [mesh.devices[i, 0] for i in range(mesh.devices.shape[0])]
    count = len(column)
    try:
        coords = [tuple(d.coords) for d in column]
    except AttributeError:
        return list(range(count))
    axes = [a for a in range(len(coords[0])) if len({c[a] for c in coords}) > 1]
    if len(axes) != 2:
        return list(range(count))
    sizes = {a: len({c[a] for c in coords}) for a in axes}
    even = [a for a in axes if sizes[a] % 2 == 0]
    if not even:
        return list(range(count))
    outer = min(even, key=lambda a: sizes[a])
    inner = [a for a in axes if a != outer][0]
    lo = {a: min(c[a] for c in coords) for a in axes}
    where = {(c[outer] - lo[outer], c[inner] - lo[inner]): i for i, c in enumerate(coords)}
    order = []
    for o in range(sizes[outer]):
        steps = range(sizes[inner]) if o % 2 == 0 else reversed(range(sizes[inner]))
        for k in steps:
            order.append(where[(o, k)])
    if sorted(order) != list(range(count)):
        return list(range(count))
    return order


def ring_steps(ring):
    n = len(ring)
    pos_of = [ring.index(d) for d in range(n)]
    mypos = jnp.asarray(pos_of, jnp.int32)[lax.axis_index("dp")]
    fwd = [(ring[p], ring[(p + 1) % n]) for p in range(n)]
    bwd = [(ring[p], ring[(p - 1) % n]) for p in range(n)]
    nf = n // 2
    return n, mypos, fwd, bwd, nf, n - 1 - nf


def gather_group(pieces, ring, after=None):
    locals_ = tuple(p.astype(jnp.bfloat16) for p, _ in pieces)
    if after is not None:
        locals_, _ = lax.optimization_barrier((locals_, after))
    n, mypos, fwd, bwd, nf, nb = ring_steps(ring)
    ring_arr = jnp.asarray(ring, jnp.int32)
    parts = {0: locals_}
    a = locals_
    for s in range(nf):
        a = lax.ppermute(a, "dp", fwd)
        parts[-(s + 1)] = a
    b = locals_
    for s in range(nb):
        b = lax.ppermute(b, "dp", bwd)
        parts[s + 1] = b
    out = []
    last = parts[-nf] if nf else locals_
    for i, (p, axis) in enumerate(pieces):
        shape = list(p.shape)
        width = shape[axis]
        shape[axis] *= n
        full = jnp.zeros(shape, jnp.bfloat16)
        for k in range(-nf, nb + 1):
            owner = ring_arr[(mypos + k) % n]
            full = lax.dynamic_update_slice_in_dim(full, parts[k][i], owner * width, axis)
        out.append(full)
    return out, last


def scatter_group(pieces, ring, carry=jnp.bfloat16):
    n, mypos, fwd, bwd, nf, nb = ring_steps(ring)
    ring_arr = jnp.asarray(ring, jnp.int32)
    widths = [g.shape[axis] // n for g, axis in pieces]

    def own(q):
        owner = ring_arr[q % n]
        return tuple(
            lax.dynamic_slice_in_dim(g, owner * w, w, axis).astype(jnp.float32)
            for (g, axis), w in zip(pieces, widths)
        )

    def send(vals, got, perm):
        if got is not None:
            vals = tuple(v + r.astype(jnp.float32) for v, r in zip(vals, got))
        return lax.ppermute(tuple(v.astype(carry) for v in vals), "dp", perm)

    got_f = None
    for s in range(nf):
        got_f = send(own(mypos + nf - s), got_f, fwd)
    got_b = None
    for s in range(nb):
        got_b = send(own(mypos - nb + s), got_b, bwd)
    total = own(mypos)
    total = tuple(t + r.astype(jnp.float32) for t, r in zip(total, got_f))
    if got_b is not None:
        total = tuple(t + r.astype(jnp.float32) for t, r in zip(total, got_b))
    return list(total)


def per_device(
    tokens,
    segment_ids,
    valid_lengths,
    cotangent,
    w_query,
    w_key,
    w_value,
    w_out,
    query_gain,
    key_gain,
    attn_gain,
    w_gate,
    w_up,
    w_down,
    mlp_gain,
    ring,
):
    f32 = jnp.float32
    bf16 = jnp.bfloat16
    rows, width = tokens.shape
    seg_row = segment_ids[0]
    length = valid_lengths[0]
    block = min(512, rows)
    count = rows // block
    scale = HEAD_DIM ** (-0.5)
    n_dp = len(ring)
    slab = attn_gain.shape[0]
    head_piece = query_gain.shape[0]

    def padded(g):
        return jnp.pad(g, (0, slab - g.shape[0]))

    gains = jnp.stack([padded(query_gain), padded(key_gain), attn_gain, mlp_gain])
    (qkvo, gains_full), seen = gather_group(
        [(jnp.stack([w_query, w_key, w_value, w_out.T]), 1), (gains, 1)], ring
    )
    wq, wk, wv, wo_t = qkvo[0], qkvo[1], qkvo[2], qkvo[3]
    gq = gains_full[0].reshape(n_dp, slab)[:, :head_piece].reshape(-1)
    gk = gains_full[1].reshape(n_dp, slab)[:, :head_piece].reshape(-1)
    ga = gains_full[2]
    gm = gains_full[3]
    (gud,), seen = gather_group([(jnp.stack([w_gate, w_up, w_down.T]), 1)], ring, after=seen)
    wg, wu, wd_t = gud[0], gud[1], gud[2]
    gq32 = gq.astype(f32)
    gk32 = gk.astype(f32)
    ga32 = ga.astype(f32)
    gm32 = gm.astype(f32)
    query = jnp.dot(tokens, wq, preferred_element_type=f32)
    keys = jnp.dot(tokens, wk, preferred_element_type=f32)
    values = jnp.dot(tokens, wv, preferred_element_type=f32).astype(bf16)
    query_sq, key_sq = lax.psum(
        (jnp.sum(query * query, axis=1), jnp.sum(keys * keys, axis=1)), "mp"
    )
    query_factor = lax.rsqrt(query_sq / width + EPS)[:, None]
    key_factor = lax.rsqrt(key_sq / width + EPS)[:, None]
    query_hat = query * query_factor
    key_hat = keys * key_factor
    heads = query.shape[1] // HEAD_DIM
    cosine, sine = rope_tables(rows, HEAD_DIM)
    query_rot = rotate((query_hat * gq32).reshape(rows, heads, HEAD_DIM), cosine, sine).astype(bf16)
    key_rot = rotate((key_hat * gk32).reshape(rows, heads, HEAD_DIM), cosine, sine).astype(bf16)
    values_h = values.reshape(rows, heads, HEAD_DIM)

    def block_scores(start):
        scores = jnp.einsum("qhe,khe->hqk", query_rot, key_rot, preferred_element_type=f32) * scale
        mask = allowed_block(start, block, seg_row, length)
        return (query_rot, jnp.where(mask[None], scores, -1e30))

    def forward_block(index):
        start = index * block
        q_blk, scores = block_scores(start)
        top = jnp.max(scores, axis=-1, keepdims=True)
        total = jnp.sum(jnp.exp(scores - top), axis=-1, keepdims=True)
        logsum = top + jnp.log(total)
        probs = jnp.exp(scores - logsum).astype(bf16)
        attended = jnp.einsum("hqk,khe->qhe", probs, values_h, preferred_element_type=f32)
        return (attended, logsum[..., 0])

    attended, logsums = lax.map(forward_block, jnp.arange(count))
    attended_b = attended.reshape(rows, heads * HEAD_DIM).astype(bf16)
    attn_partial = jnp.einsum("rc,dc->rd", attended_b, wo_t, preferred_element_type=f32)
    attn_total = branch_total(attn_partial)
    attn_hat, attn_factor = norm_forward(attn_total)
    hidden = tokens.astype(f32) + attn_hat * ga32
    hidden_b = hidden.astype(bf16)
    gate = jnp.dot(hidden_b, wg, preferred_element_type=f32)
    up = jnp.dot(hidden_b, wu, preferred_element_type=f32)
    active = jax.nn.silu(gate)
    mixed_b = (active * up).astype(bf16)
    mlp_partial = jnp.einsum("rf,df->rd", mixed_b, wd_t, preferred_element_type=f32)
    mlp_total = branch_total(mlp_partial)
    mlp_hat, mlp_factor = norm_forward(mlp_total)
    layer_out = (hidden + mlp_hat * gm32).astype(bf16)
    grad_out = cotangent.astype(f32)
    d_mlp, grad_mg = norm_back(grad_out, mlp_hat, mlp_factor, gm32)
    d_mlp_b = d_mlp.astype(bf16)
    d_mixed = jnp.einsum("rd,df->rf", d_mlp_b, wd_t, preferred_element_type=f32)
    sigma = jax.nn.sigmoid(gate)
    d_gate = (d_mixed * up * sigma * (1.0 + gate * (1.0 - sigma))).astype(bf16)
    d_up = (d_mixed * active).astype(bf16)
    grad_gud = jnp.einsum(
        "xrd,xrf->xdf",
        jnp.stack([hidden_b, hidden_b, d_mlp_b]),
        jnp.stack([d_gate, d_up, mixed_b]),
        preferred_element_type=f32,
    )
    (grad_gud_s,) = scatter_group([(grad_gud, 1)], ring)
    grad_wg_s, grad_wu_s, grad_wd_s = grad_gud_s[0], grad_gud_s[1], grad_gud_s[2].T
    hidden_partial = jnp.einsum("rf,df->rd", d_gate, wg, preferred_element_type=f32) + jnp.einsum(
        "rf,df->rd", d_up, wu, preferred_element_type=f32
    )
    d_hidden = grad_out + input_total(hidden_partial)
    d_attn, grad_ag = norm_back(d_hidden, attn_hat, attn_factor, ga32)
    d_attn_b = d_attn.astype(bf16)
    grad_wo_t = jnp.einsum("rd,rc->dc", d_attn_b, attended_b, preferred_element_type=f32)
    (grad_wo_t_s,) = scatter_group([(grad_wo_t, 0)], ring)
    grad_wo_s = grad_wo_t_s.T
    d_attended = jnp.einsum("rd,dc->rc", d_attn_b, wo_t, preferred_element_type=f32).astype(bf16)
    d_attended = d_attended.reshape(rows, heads, HEAD_DIM)

    def backward_block(carry, index):
        key_acc, value_acc = carry
        start = index * block
        q_blk, scores = block_scores(start)
        logsum = lax.dynamic_index_in_dim(logsums, index, 0, keepdims=False)
        probs = jnp.exp(scores - logsum[..., None])
        value_acc = value_acc + jnp.einsum(
            "hqk,qhe->khe", probs.astype(bf16), d_attended, preferred_element_type=f32
        )
        d_probs = jnp.einsum("qhe,khe->hqk", d_attended, values_h, preferred_element_type=f32)
        delta = jnp.sum(probs * d_probs, axis=-1, keepdims=True)
        d_scores = (probs * (d_probs - delta)).astype(bf16)
        d_query_blk = (
            jnp.einsum("hqk,khe->qhe", d_scores, key_rot, preferred_element_type=f32) * scale
        )
        key_acc = (
            key_acc
            + jnp.einsum("hqk,qhe->khe", d_scores, q_blk, preferred_element_type=f32) * scale
        )
        return ((key_acc, value_acc), d_query_blk)

    empty = jnp.zeros((rows, heads, HEAD_DIM), f32)
    (d_key_rot, d_values), d_query_rot = lax.scan(backward_block, (empty, empty), jnp.arange(count))
    d_query_rot = d_query_rot.reshape(rows, heads, HEAD_DIM)
    d_values_b = d_values.reshape(rows, heads * HEAD_DIM).astype(bf16)
    d_query_n = rotate_back(d_query_rot, cosine, sine).reshape(rows, heads * HEAD_DIM)
    d_key_n = rotate_back(d_key_rot, cosine, sine).reshape(rows, heads * HEAD_DIM)
    grad_gq = jnp.sum(d_query_n * query_hat, axis=0)
    grad_gk = jnp.sum(d_key_n * key_hat, axis=0)
    d_query_hat = d_query_n * gq32
    d_key_hat = d_key_n * gk32
    query_inner, key_inner = lax.psum(
        (jnp.sum(d_query_hat * query_hat, axis=1), jnp.sum(d_key_hat * key_hat, axis=1)), "mp"
    )
    d_query_b = (query_factor * (d_query_hat - query_hat * (query_inner / width)[:, None])).astype(
        bf16
    )
    d_key_b = (key_factor * (d_key_hat - key_hat * (key_inner / width)[:, None])).astype(bf16)
    grad_qkv = jnp.einsum(
        "rd,xrc->xdc", tokens, jnp.stack([d_query_b, d_key_b, d_values_b]),
        preferred_element_type=f32,
    )
    (grad_qkv_s,) = scatter_group([(grad_qkv, 1)], ring)
    grad_wq_s, grad_wk_s, grad_wv_s = grad_qkv_s[0], grad_qkv_s[1], grad_qkv_s[2]

    def spread(g):
        return jnp.pad(g.reshape(n_dp, -1), ((0, 0), (0, slab - g.shape[0] // n_dp))).reshape(-1)

    grad_gains = jnp.stack([spread(grad_gq), spread(grad_gk), grad_ag, grad_mg])
    (grad_gains_s,) = scatter_group([(grad_gains, 1)], ring, carry=jnp.float32)
    grad_gq_s = grad_gains_s[0, :head_piece]
    grad_gk_s = grad_gains_s[1, :head_piece]
    grad_ag_s = grad_gains_s[2]
    grad_mg_s = grad_gains_s[3]
    input_part = jnp.einsum("rc,dc->rd", d_query_b, wq, preferred_element_type=f32)
    input_part = input_part + jnp.einsum("rc,dc->rd", d_key_b, wk, preferred_element_type=f32)
    input_part = input_part + jnp.einsum("rc,dc->rd", d_values_b, wv, preferred_element_type=f32)
    input_grad = d_hidden + input_total(input_part)
    return (
        layer_out,
        input_grad,
        grad_wq_s,
        grad_wk_s,
        grad_wv_s,
        grad_wo_s,
        grad_gq_s,
        grad_gk_s,
        grad_ag_s,
        grad_wg_s,
        grad_wu_s,
        grad_wd_s,
        grad_mg_s,
    )


def solution(mesh):
    placed = (
        P("dp", None),
        P("dp", None),
        P("dp"),
        P("dp", None),
        P("dp", "mp"),
        P("dp", "mp"),
        P("dp", "mp"),
        P("mp", "dp"),
        P(("mp", "dp")),
        P(("mp", "dp")),
        P("dp"),
        P("dp", "mp"),
        P("dp", "mp"),
        P("mp", "dp"),
        P("dp"),
    )
    ring = ring_order(mesh)
    return jax.shard_map(
        functools.partial(per_device, ring=ring),
        mesh=mesh,
        in_specs=placed,
        out_specs=(
            P("dp", None),
            P("dp", None),
            P("dp", "mp"),
            P("dp", "mp"),
            P("dp", "mp"),
            P("mp", "dp"),
            P(("mp", "dp")),
            P(("mp", "dp")),
            P("dp"),
            P("dp", "mp"),
            P("dp", "mp"),
            P("mp", "dp"),
            P("dp"),
        ),
        check_vma=False,
    )
```

```python
import functools

import jax
import jax.numpy as jnp
import numpy as np
from jax import lax
from jax.sharding import PartitionSpec as P

HEAD_DIM = 128


EPS = 1e-06
THETA = 500000.0


def rope_tables(rows, head_dim):
    half = head_dim // 2
    inverse = THETA ** (-(jnp.arange(half).astype(jnp.float32) * 2.0) / head_dim)
    angles = jnp.arange(rows).astype(jnp.float32)[:, None] * inverse[None, :]
    return (jnp.cos(angles)[:, None, :], jnp.sin(angles)[:, None, :])


def rotate(value, cosine, sine):
    half = value.shape[-1] // 2
    first, second = (value[..., :half], value[..., half:])
    return jnp.concatenate(
        [first * cosine - second * sine, second * cosine + first * sine], axis=-1
    )


def rotate_back(grad, cosine, sine):
    half = grad.shape[-1] // 2
    first, second = (grad[..., :half], grad[..., half:])
    return jnp.concatenate(
        [first * cosine + second * sine, second * cosine - first * sine], axis=-1
    )


def allowed_block(start, block, seg_row, length):
    query_pos = start + jnp.arange(block)
    key_pos = jnp.arange(seg_row.shape[0])
    same = seg_row[:, None] == seg_row[None, :]
    causal = key_pos[None, :] <= query_pos[:, None]
    inside = key_pos[None, :] < length
    return same & causal & inside | (key_pos[None, :] == query_pos[:, None])


def mp_allreduce(x, carry=jnp.bfloat16):
    m = lax.axis_size("mp")
    me = lax.axis_index("mp")
    core = me % 2
    chips = m // 2
    chip = me // 2
    half = x.shape[1] // 2
    pair = [(i, i ^ 1) for i in range(m)]
    mine = lax.dynamic_slice_in_dim(x, core * half, half, 1)
    other = lax.dynamic_slice_in_dim(x, (1 - core) * half, half, 1)
    part = mine + lax.ppermute(other, "mp", pair)
    if chips > 1:
        low = part.astype(carry)
        got = [low]
        for k in range(1, chips):
            perm = [(c * 2 + r, ((c + k) % chips) * 2 + r) for c in range(chips) for r in range(2)]
            got.append(lax.ppermute(low, "mp", perm))
        stack = jnp.stack(got)
        order = (chip - jnp.arange(chips)) % chips
        ordered = jnp.take(stack, order, axis=0).astype(jnp.float32)
        part = ordered[0]
        for k in range(1, chips):
            part = part + ordered[k]
    swapped = lax.ppermute(part, "mp", pair)
    full = jnp.zeros(x.shape, jnp.float32)
    full = lax.dynamic_update_slice_in_dim(full, part, core * half, 1)
    full = lax.dynamic_update_slice_in_dim(full, swapped, (1 - core) * half, 1)
    return full


def branch_total(partial_sum):
    return mp_allreduce(partial_sum)


def input_total(partial_sum):
    return mp_allreduce(partial_sum)


def norm_forward(total):
    factor = lax.rsqrt(jnp.mean(total * total, axis=1, keepdims=True) + EPS)
    return (total * factor, factor)


def norm_back(grad, normed, factor, gain):
    grad_gain = jnp.sum(grad * normed, axis=0)
    scaled = grad * gain
    inner = jnp.mean(scaled * normed, axis=1, keepdims=True)
    return (factor * (scaled - normed * inner), grad_gain)


def ring_order(mesh):
    column = [mesh.devices[i, 0] for i in range(mesh.devices.shape[0])]
    count = len(column)
    try:
        coords = [tuple(d.coords) for d in column]
    except AttributeError:
        return list(range(count))
    axes = [a for a in range(len(coords[0])) if len({c[a] for c in coords}) > 1]
    if len(axes) != 2:
        return list(range(count))
    sizes = {a: len({c[a] for c in coords}) for a in axes}
    even = [a for a in axes if sizes[a] % 2 == 0]
    if not even:
        return list(range(count))
    outer = min(even, key=lambda a: sizes[a])
    inner = [a for a in axes if a != outer][0]
    lo = {a: min(c[a] for c in coords) for a in axes}
    where = {(c[outer] - lo[outer], c[inner] - lo[inner]): i for i, c in enumerate(coords)}
    order = []
    for o in range(sizes[outer]):
        steps = range(sizes[inner]) if o % 2 == 0 else reversed(range(sizes[inner]))
        for k in steps:
            order.append(where[(o, k)])
    if sorted(order) != list(range(count)):
        return list(range(count))
    return order


def ring_steps(ring):
    n = len(ring)
    pos_of = [ring.index(d) for d in range(n)]
    mypos = jnp.asarray(pos_of, jnp.int32)[lax.axis_index("dp")]
    fwd = [(ring[p], ring[(p + 1) % n]) for p in range(n)]
    bwd = [(ring[p], ring[(p - 1) % n]) for p in range(n)]
    nf = n // 2
    return n, mypos, fwd, bwd, nf, n - 1 - nf


def gather_group(pieces, ring, after=None):
    locals_ = tuple(p.astype(jnp.bfloat16) for p, _ in pieces)
    if after is not None:
        locals_, _ = lax.optimization_barrier((locals_, after))
    n, mypos, fwd, bwd, nf, nb = ring_steps(ring)
    ring_arr = jnp.asarray(ring, jnp.int32)
    parts = {0: locals_}
    a = locals_
    for s in range(nf):
        a = lax.ppermute(a, "dp", fwd)
        parts[-(s + 1)] = a
    b = locals_
    for s in range(nb):
        b = lax.ppermute(b, "dp", bwd)
        parts[s + 1] = b
    out = []
    last = parts[-nf] if nf else locals_
    for i, (p, axis) in enumerate(pieces):
        shape = list(p.shape)
        width = shape[axis]
        shape[axis] *= n
        full = jnp.zeros(shape, jnp.bfloat16)
        for k in range(-nf, nb + 1):
            owner = ring_arr[(mypos + k) % n]
            full = lax.dynamic_update_slice_in_dim(full, parts[k][i], owner * width, axis)
        out.append(full)
    return out, last


def scatter_group(pieces, ring, carry=jnp.bfloat16, after=None):
    if after is not None:
        grads, _ = lax.optimization_barrier((tuple(g for g, _ in pieces), after))
        pieces = [(g, axis) for g, (_, axis) in zip(grads, pieces)]
    n, mypos, fwd, bwd, nf, nb = ring_steps(ring)
    ring_arr = jnp.asarray(ring, jnp.int32)
    widths = [g.shape[axis] // n for g, axis in pieces]

    def own(q):
        owner = ring_arr[q % n]
        return tuple(
            lax.dynamic_slice_in_dim(g, owner * w, w, axis).astype(jnp.float32)
            for (g, axis), w in zip(pieces, widths)
        )

    def send(vals, got, perm):
        if got is not None:
            vals = tuple(v + r.astype(jnp.float32) for v, r in zip(vals, got))
        return lax.ppermute(tuple(v.astype(carry) for v in vals), "dp", perm)

    got_f = None
    for s in range(nf):
        got_f = send(own(mypos + nf - s), got_f, fwd)
    got_b = None
    for s in range(nb):
        got_b = send(own(mypos - nb + s), got_b, bwd)
    last = got_f
    total = own(mypos)
    total = tuple(t + r.astype(jnp.float32) for t, r in zip(total, got_f))
    if got_b is not None:
        total = tuple(t + r.astype(jnp.float32) for t, r in zip(total, got_b))
    return list(total), last


def per_device(
    tokens,
    segment_ids,
    valid_lengths,
    cotangent,
    w_query,
    w_key,
    w_value,
    w_out,
    query_gain,
    key_gain,
    attn_gain,
    w_gate,
    w_up,
    w_down,
    mlp_gain,
    ring,
):
    f32 = jnp.float32
    bf16 = jnp.bfloat16
    rows, width = tokens.shape
    seg_row = segment_ids[0]
    length = valid_lengths[0]
    block = min(512, rows)
    count = rows // block
    scale = HEAD_DIM ** (-0.5)
    n_dp = len(ring)
    slab = attn_gain.shape[0]
    head_piece = query_gain.shape[0]

    def padded(g):
        return jnp.pad(g, (0, slab - g.shape[0]))

    gains = jnp.stack([padded(query_gain), padded(key_gain), attn_gain, mlp_gain])
    (qkvo, gains_full), seen = gather_group(
        [(jnp.stack([w_query, w_key, w_value, w_out.T]), 1), (gains, 1)], ring
    )
    wq, wk, wv, wo_t = qkvo[0], qkvo[1], qkvo[2], qkvo[3]
    gq = gains_full[0].reshape(n_dp, slab)[:, :head_piece].reshape(-1)
    gk = gains_full[1].reshape(n_dp, slab)[:, :head_piece].reshape(-1)
    ga = gains_full[2]
    gm = gains_full[3]
    (gud,), seen = gather_group([(jnp.stack([w_gate, w_up, w_down.T]), 1)], ring, after=seen)
    wg, wu, wd_t = gud[0], gud[1], gud[2]
    gq32 = gq.astype(f32)
    gk32 = gk.astype(f32)
    ga32 = ga.astype(f32)
    gm32 = gm.astype(f32)
    query = jnp.dot(tokens, wq, preferred_element_type=f32)
    keys = jnp.dot(tokens, wk, preferred_element_type=f32)
    values = jnp.dot(tokens, wv, preferred_element_type=f32).astype(bf16)
    query_sq, key_sq = lax.psum(
        (jnp.sum(query * query, axis=1), jnp.sum(keys * keys, axis=1)), "mp"
    )
    query_factor = lax.rsqrt(query_sq / width + EPS)[:, None]
    key_factor = lax.rsqrt(key_sq / width + EPS)[:, None]
    query_hat = query * query_factor
    key_hat = keys * key_factor
    heads = query.shape[1] // HEAD_DIM
    cosine, sine = rope_tables(rows, HEAD_DIM)
    query_rot = rotate((query_hat * gq32).reshape(rows, heads, HEAD_DIM), cosine, sine).astype(bf16)
    key_rot = rotate((key_hat * gk32).reshape(rows, heads, HEAD_DIM), cosine, sine).astype(bf16)
    values_h = values.reshape(rows, heads, HEAD_DIM)

    def block_scores(start):
        scores = jnp.einsum("qhe,khe->hqk", query_rot, key_rot, preferred_element_type=f32) * scale
        mask = allowed_block(start, block, seg_row, length)
        return (query_rot, jnp.where(mask[None], scores, -1e30))

    def forward_block(index):
        start = index * block
        q_blk, scores = block_scores(start)
        top = jnp.max(scores, axis=-1, keepdims=True)
        total = jnp.sum(jnp.exp(scores - top), axis=-1, keepdims=True)
        logsum = top + jnp.log(total)
        probs = jnp.exp(scores - logsum).astype(bf16)
        attended = jnp.einsum("hqk,khe->qhe", probs, values_h, preferred_element_type=f32)
        return (attended, logsum[..., 0])

    attended, logsums = lax.map(forward_block, jnp.arange(count))
    attended_b = attended.reshape(rows, heads * HEAD_DIM).astype(bf16)
    attn_partial = jnp.einsum("rc,dc->rd", attended_b, wo_t, preferred_element_type=f32)
    attn_total = branch_total(attn_partial)
    attn_hat, attn_factor = norm_forward(attn_total)
    hidden = tokens.astype(f32) + attn_hat * ga32
    hidden_b = hidden.astype(bf16)
    gate = jnp.dot(hidden_b, wg, preferred_element_type=f32)
    up = jnp.dot(hidden_b, wu, preferred_element_type=f32)
    active = jax.nn.silu(gate)
    mixed_b = (active * up).astype(bf16)
    mlp_partial = jnp.einsum("rf,df->rd", mixed_b, wd_t, preferred_element_type=f32)
    mlp_total = branch_total(mlp_partial)
    mlp_hat, mlp_factor = norm_forward(mlp_total)
    layer_out = (hidden + mlp_hat * gm32).astype(bf16)
    grad_out = cotangent.astype(f32)
    d_mlp, grad_mg = norm_back(grad_out, mlp_hat, mlp_factor, gm32)
    d_mlp_b = d_mlp.astype(bf16)
    d_mixed = jnp.einsum("rd,df->rf", d_mlp_b, wd_t, preferred_element_type=f32)
    sigma = jax.nn.sigmoid(gate)
    d_gate = (d_mixed * up * sigma * (1.0 + gate * (1.0 - sigma))).astype(bf16)
    d_up = (d_mixed * active).astype(bf16)
    grad_gud = jnp.einsum(
        "xrd,xrf->xdf",
        jnp.stack([hidden_b, hidden_b, d_mlp_b]),
        jnp.stack([d_gate, d_up, mixed_b]),
        preferred_element_type=f32,
    )
    (grad_gud_s,), sent = scatter_group([(grad_gud, 1)], ring)
    grad_wg_s, grad_wu_s, grad_wd_s = grad_gud_s[0], grad_gud_s[1], grad_gud_s[2].T
    hidden_partial = jnp.einsum("rf,df->rd", d_gate, wg, preferred_element_type=f32) + jnp.einsum(
        "rf,df->rd", d_up, wu, preferred_element_type=f32
    )
    d_hidden = grad_out + input_total(hidden_partial)
    d_attn, grad_ag = norm_back(d_hidden, attn_hat, attn_factor, ga32)
    d_attn_b = d_attn.astype(bf16)
    d_attended = jnp.einsum("rd,dc->rc", d_attn_b, wo_t, preferred_element_type=f32).astype(bf16)
    d_attended = d_attended.reshape(rows, heads, HEAD_DIM)

    def backward_block(carry, index):
        key_acc, value_acc = carry
        start = index * block
        q_blk, scores = block_scores(start)
        logsum = lax.dynamic_index_in_dim(logsums, index, 0, keepdims=False)
        probs = jnp.exp(scores - logsum[..., None])
        value_acc = value_acc + jnp.einsum(
            "hqk,qhe->khe", probs.astype(bf16), d_attended, preferred_element_type=f32
        )
        d_probs = jnp.einsum("qhe,khe->hqk", d_attended, values_h, preferred_element_type=f32)
        delta = jnp.sum(probs * d_probs, axis=-1, keepdims=True)
        d_scores = (probs * (d_probs - delta)).astype(bf16)
        d_query_blk = (
            jnp.einsum("hqk,khe->qhe", d_scores, key_rot, preferred_element_type=f32) * scale
        )
        key_acc = (
            key_acc
            + jnp.einsum("hqk,qhe->khe", d_scores, q_blk, preferred_element_type=f32) * scale
        )
        return ((key_acc, value_acc), d_query_blk)

    empty = jnp.zeros((rows, heads, HEAD_DIM), f32)
    (d_key_rot, d_values), d_query_rot = lax.scan(backward_block, (empty, empty), jnp.arange(count))
    d_query_rot = d_query_rot.reshape(rows, heads, HEAD_DIM)
    d_values_b = d_values.reshape(rows, heads * HEAD_DIM).astype(bf16)
    d_query_n = rotate_back(d_query_rot, cosine, sine).reshape(rows, heads * HEAD_DIM)
    d_key_n = rotate_back(d_key_rot, cosine, sine).reshape(rows, heads * HEAD_DIM)
    grad_gq = jnp.sum(d_query_n * query_hat, axis=0)
    grad_gk = jnp.sum(d_key_n * key_hat, axis=0)
    d_query_hat = d_query_n * gq32
    d_key_hat = d_key_n * gk32
    query_inner, key_inner = lax.psum(
        (jnp.sum(d_query_hat * query_hat, axis=1), jnp.sum(d_key_hat * key_hat, axis=1)), "mp"
    )
    d_query_b = (query_factor * (d_query_hat - query_hat * (query_inner / width)[:, None])).astype(
        bf16
    )
    d_key_b = (key_factor * (d_key_hat - key_hat * (key_inner / width)[:, None])).astype(bf16)
    grad_qkvo = jnp.einsum(
        "xrd,xrc->xdc",
        jnp.stack([tokens, tokens, tokens, d_attn_b]),
        jnp.stack([d_query_b, d_key_b, d_values_b, attended_b]),
        preferred_element_type=f32,
    )
    (grad_qkvo_s,), sent = scatter_group([(grad_qkvo, 1)], ring, after=sent)
    grad_wq_s, grad_wk_s, grad_wv_s = grad_qkvo_s[0], grad_qkvo_s[1], grad_qkvo_s[2]
    grad_wo_s = grad_qkvo_s[3].T

    def spread(g):
        return jnp.pad(g.reshape(n_dp, -1), ((0, 0), (0, slab - g.shape[0] // n_dp))).reshape(-1)

    grad_gains = jnp.stack([spread(grad_gq), spread(grad_gk), grad_ag, grad_mg])
    (grad_gains_s,), sent = scatter_group([(grad_gains, 1)], ring, carry=jnp.float32, after=sent)
    grad_gq_s = grad_gains_s[0, :head_piece]
    grad_gk_s = grad_gains_s[1, :head_piece]
    grad_ag_s = grad_gains_s[2]
    grad_mg_s = grad_gains_s[3]
    input_part = jnp.einsum("rc,dc->rd", d_query_b, wq, preferred_element_type=f32)
    input_part = input_part + jnp.einsum("rc,dc->rd", d_key_b, wk, preferred_element_type=f32)
    input_part = input_part + jnp.einsum("rc,dc->rd", d_values_b, wv, preferred_element_type=f32)
    input_grad = d_hidden + input_total(input_part)
    return (
        layer_out,
        input_grad,
        grad_wq_s,
        grad_wk_s,
        grad_wv_s,
        grad_wo_s,
        grad_gq_s,
        grad_gk_s,
        grad_ag_s,
        grad_wg_s,
        grad_wu_s,
        grad_wd_s,
        grad_mg_s,
    )


def solution(mesh):
    placed = (
        P("dp", None),
        P("dp", None),
        P("dp"),
        P("dp", None),
        P("dp", "mp"),
        P("dp", "mp"),
        P("dp", "mp"),
        P("mp", "dp"),
        P(("mp", "dp")),
        P(("mp", "dp")),
        P("dp"),
        P("dp", "mp"),
        P("dp", "mp"),
        P("mp", "dp"),
        P("dp"),
    )
    ring = ring_order(mesh)
    return jax.shard_map(
        functools.partial(per_device, ring=ring),
        mesh=mesh,
        in_specs=placed,
        out_specs=(
            P("dp", None),
            P("dp", None),
            P("dp", "mp"),
            P("dp", "mp"),
            P("dp", "mp"),
            P("mp", "dp"),
            P(("mp", "dp")),
            P(("mp", "dp")),
            P("dp"),
            P("dp", "mp"),
            P("dp", "mp"),
            P("mp", "dp"),
            P("dp"),
        ),
        check_vma=False,
    )
```

```python
import functools

import jax
import jax.numpy as jnp
import numpy as np
from jax import lax
from jax.sharding import PartitionSpec as P

HEAD_DIM = 128


EPS = 1e-06
THETA = 500000.0


def rope_tables(rows, head_dim):
    half = head_dim // 2
    inverse = THETA ** (-(jnp.arange(half).astype(jnp.float32) * 2.0) / head_dim)
    angles = jnp.arange(rows).astype(jnp.float32)[:, None] * inverse[None, :]
    return (jnp.cos(angles)[:, None, :], jnp.sin(angles)[:, None, :])


def rotate(value, cosine, sine):
    half = value.shape[-1] // 2
    first, second = (value[..., :half], value[..., half:])
    return jnp.concatenate(
        [first * cosine - second * sine, second * cosine + first * sine], axis=-1
    )


def rotate_back(grad, cosine, sine):
    half = grad.shape[-1] // 2
    first, second = (grad[..., :half], grad[..., half:])
    return jnp.concatenate(
        [first * cosine + second * sine, second * cosine - first * sine], axis=-1
    )


def allowed_block(start, block, seg_row, length):
    query_pos = start + jnp.arange(block)
    key_pos = jnp.arange(seg_row.shape[0])
    same = seg_row[:, None] == seg_row[None, :]
    causal = key_pos[None, :] <= query_pos[:, None]
    inside = key_pos[None, :] < length
    return same & causal & inside | (key_pos[None, :] == query_pos[:, None])


def mp_allreduce(x, carry=jnp.bfloat16):
    m = lax.axis_size("mp")
    me = lax.axis_index("mp")
    core = me % 2
    chips = m // 2
    chip = me // 2
    half = x.shape[1] // 2
    pair = [(i, i ^ 1) for i in range(m)]
    mine = lax.dynamic_slice_in_dim(x, core * half, half, 1)
    other = lax.dynamic_slice_in_dim(x, (1 - core) * half, half, 1)
    part = mine + lax.ppermute(other, "mp", pair)
    if chips > 1:
        low = part.astype(carry)
        got = [low]
        for k in range(1, chips):
            perm = [(c * 2 + r, ((c + k) % chips) * 2 + r) for c in range(chips) for r in range(2)]
            got.append(lax.ppermute(low, "mp", perm))
        stack = jnp.stack(got)
        order = (chip - jnp.arange(chips)) % chips
        ordered = jnp.take(stack, order, axis=0).astype(jnp.float32)
        part = ordered[0]
        for k in range(1, chips):
            part = part + ordered[k]
    swapped = lax.ppermute(part, "mp", pair)
    full = jnp.zeros(x.shape, jnp.float32)
    full = lax.dynamic_update_slice_in_dim(full, part, core * half, 1)
    full = lax.dynamic_update_slice_in_dim(full, swapped, (1 - core) * half, 1)
    return full


def branch_total(partial_sum):
    return mp_allreduce(partial_sum)


def input_total(partial_sum):
    return mp_allreduce(partial_sum)


def norm_forward(total):
    factor = lax.rsqrt(jnp.mean(total * total, axis=1, keepdims=True) + EPS)
    return (total * factor, factor)


def norm_back(grad, normed, factor, gain):
    grad_gain = jnp.sum(grad * normed, axis=0)
    scaled = grad * gain
    inner = jnp.mean(scaled * normed, axis=1, keepdims=True)
    return (factor * (scaled - normed * inner), grad_gain)


def ring_order(mesh):
    column = [mesh.devices[i, 0] for i in range(mesh.devices.shape[0])]
    count = len(column)
    try:
        coords = [tuple(d.coords) for d in column]
    except AttributeError:
        return list(range(count))
    axes = [a for a in range(len(coords[0])) if len({c[a] for c in coords}) > 1]
    if len(axes) != 2:
        return list(range(count))
    sizes = {a: len({c[a] for c in coords}) for a in axes}
    even = [a for a in axes if sizes[a] % 2 == 0]
    if not even:
        return list(range(count))
    outer = min(even, key=lambda a: sizes[a])
    inner = [a for a in axes if a != outer][0]
    lo = {a: min(c[a] for c in coords) for a in axes}
    where = {(c[outer] - lo[outer], c[inner] - lo[inner]): i for i, c in enumerate(coords)}
    order = []
    for o in range(sizes[outer]):
        steps = range(sizes[inner]) if o % 2 == 0 else reversed(range(sizes[inner]))
        for k in steps:
            order.append(where[(o, k)])
    if sorted(order) != list(range(count)):
        return list(range(count))
    return order


def ring_steps(ring):
    n = len(ring)
    pos_of = [ring.index(d) for d in range(n)]
    mypos = jnp.asarray(pos_of, jnp.int32)[lax.axis_index("dp")]
    fwd = [(ring[p], ring[(p + 1) % n]) for p in range(n)]
    bwd = [(ring[p], ring[(p - 1) % n]) for p in range(n)]
    nf = n // 2
    return n, mypos, fwd, bwd, nf, n - 1 - nf


def gather_group(pieces, ring, after=None):
    locals_ = tuple(p.astype(jnp.bfloat16) for p, _ in pieces)
    if after is not None:
        locals_, _ = lax.optimization_barrier((locals_, after))
    n, mypos, fwd, bwd, nf, nb = ring_steps(ring)
    ring_arr = jnp.asarray(ring, jnp.int32)
    parts = {0: locals_}
    a = locals_
    for s in range(nf):
        a = lax.ppermute(a, "dp", fwd)
        parts[-(s + 1)] = a
    b = locals_
    for s in range(nb):
        b = lax.ppermute(b, "dp", bwd)
        parts[s + 1] = b
    out = []
    last = parts[-nf] if nf else locals_
    for i, (p, axis) in enumerate(pieces):
        shape = list(p.shape)
        width = shape[axis]
        shape[axis] *= n
        full = jnp.zeros(shape, jnp.bfloat16)
        for k in range(-nf, nb + 1):
            owner = ring_arr[(mypos + k) % n]
            full = lax.dynamic_update_slice_in_dim(full, parts[k][i], owner * width, axis)
        out.append(full)
    return out, last


def scatter_group(pieces, ring, carry=jnp.bfloat16):
    n, mypos, fwd, bwd, nf, nb = ring_steps(ring)
    ring_arr = jnp.asarray(ring, jnp.int32)
    widths = [g.shape[axis] // n for g, axis in pieces]

    def own(q):
        owner = ring_arr[q % n]
        return tuple(
            lax.dynamic_slice_in_dim(g, owner * w, w, axis).astype(jnp.float32)
            for (g, axis), w in zip(pieces, widths)
        )

    def send(vals, got, perm):
        if got is not None:
            vals = tuple(v + r.astype(jnp.float32) for v, r in zip(vals, got))
        return lax.ppermute(tuple(v.astype(carry) for v in vals), "dp", perm)

    got_f = None
    for s in range(nf):
        got_f = send(own(mypos + nf - s), got_f, fwd)
    got_b = None
    for s in range(nb):
        got_b = send(own(mypos - nb + s), got_b, bwd)
    total = own(mypos)
    total = tuple(t + r.astype(jnp.float32) for t, r in zip(total, got_f))
    if got_b is not None:
        total = tuple(t + r.astype(jnp.float32) for t, r in zip(total, got_b))
    return list(total)


def per_device(
    tokens,
    segment_ids,
    valid_lengths,
    cotangent,
    w_query,
    w_key,
    w_value,
    w_out,
    query_gain,
    key_gain,
    attn_gain,
    w_gate,
    w_up,
    w_down,
    mlp_gain,
    ring,
):
    f32 = jnp.float32
    bf16 = jnp.bfloat16
    rows, width = tokens.shape
    seg_row = segment_ids[0]
    length = valid_lengths[0]
    block = min(512, rows)
    count = rows // block
    scale = HEAD_DIM ** (-0.5)
    n_dp = len(ring)
    slab = attn_gain.shape[0]
    head_piece = query_gain.shape[0]

    def padded(g):
        return jnp.pad(g, (0, slab - g.shape[0]))

    gains = jnp.stack([padded(query_gain), padded(key_gain), attn_gain, mlp_gain])
    (qkvo, gains_full), seen = gather_group(
        [(jnp.stack([w_query, w_key, w_value, w_out.T]), 1), (gains, 1)], ring
    )
    wq, wk, wv, wo_t = qkvo[0], qkvo[1], qkvo[2], qkvo[3]
    gq = gains_full[0].reshape(n_dp, slab)[:, :head_piece].reshape(-1)
    gk = gains_full[1].reshape(n_dp, slab)[:, :head_piece].reshape(-1)
    ga = gains_full[2]
    gm = gains_full[3]
    (gud,), seen = gather_group([(jnp.stack([w_gate, w_up, w_down.T]), 1)], ring, after=seen)
    wg, wu, wd_t = gud[0], gud[1], gud[2]
    gq32 = gq.astype(f32)
    gk32 = gk.astype(f32)
    ga32 = ga.astype(f32)
    gm32 = gm.astype(f32)
    query = jnp.dot(tokens, wq, preferred_element_type=f32)
    keys = jnp.dot(tokens, wk, preferred_element_type=f32)
    values = jnp.dot(tokens, wv, preferred_element_type=f32).astype(bf16)
    query_sq, key_sq = lax.psum(
        (jnp.sum(query * query, axis=1), jnp.sum(keys * keys, axis=1)), "mp"
    )
    query_factor = lax.rsqrt(query_sq / width + EPS)[:, None]
    key_factor = lax.rsqrt(key_sq / width + EPS)[:, None]
    query_hat = query * query_factor
    key_hat = keys * key_factor
    heads = query.shape[1] // HEAD_DIM
    cosine, sine = rope_tables(rows, HEAD_DIM)
    query_rot = rotate((query_hat * gq32).reshape(rows, heads, HEAD_DIM), cosine, sine).astype(bf16)
    key_rot = rotate((key_hat * gk32).reshape(rows, heads, HEAD_DIM), cosine, sine).astype(bf16)
    values_h = values.reshape(rows, heads, HEAD_DIM)

    def block_scores(start):
        scores = jnp.einsum("qhe,khe->hqk", query_rot, key_rot, preferred_element_type=f32) * scale
        mask = allowed_block(start, block, seg_row, length)
        return (query_rot, jnp.where(mask[None], scores, -1e30))

    def forward_block(index):
        start = index * block
        q_blk, scores = block_scores(start)
        top = jnp.max(scores, axis=-1, keepdims=True)
        total = jnp.sum(jnp.exp(scores - top), axis=-1, keepdims=True)
        logsum = top + jnp.log(total)
        probs = jnp.exp(scores - logsum).astype(bf16)
        attended = jnp.einsum("hqk,khe->qhe", probs, values_h, preferred_element_type=f32)
        return (attended, logsum[..., 0])

    attended, logsums = lax.map(forward_block, jnp.arange(count))
    attended_b = attended.reshape(rows, heads * HEAD_DIM).astype(bf16)
    attn_partial = jnp.einsum("rc,dc->rd", attended_b, wo_t, preferred_element_type=f32)
    attn_total = branch_total(attn_partial)
    attn_hat, attn_factor = norm_forward(attn_total)
    hidden = tokens.astype(f32) + attn_hat * ga32
    hidden_b = hidden.astype(bf16)
    gate = jnp.dot(hidden_b, wg, preferred_element_type=f32)
    up = jnp.dot(hidden_b, wu, preferred_element_type=f32)
    active = jax.nn.silu(gate)
    mixed_b = (active * up).astype(bf16)
    mlp_partial = jnp.einsum("rf,df->rd", mixed_b, wd_t, preferred_element_type=f32)
    mlp_total = branch_total(mlp_partial)
    mlp_hat, mlp_factor = norm_forward(mlp_total)
    layer_out = (hidden + mlp_hat * gm32).astype(bf16)
    grad_out = cotangent.astype(f32)
    d_mlp, grad_mg = norm_back(grad_out, mlp_hat, mlp_factor, gm32)
    d_mlp_b = d_mlp.astype(bf16)
    grad_wd = jnp.einsum("rf,rd->fd", mixed_b, d_mlp_b, preferred_element_type=f32)
    (grad_wd_s,) = scatter_group([(grad_wd, 1)], ring)
    d_mixed = jnp.einsum("rd,df->rf", d_mlp_b, wd_t, preferred_element_type=f32)
    sigma = jax.nn.sigmoid(gate)
    d_gate = (d_mixed * up * sigma * (1.0 + gate * (1.0 - sigma))).astype(bf16)
    d_up = (d_mixed * active).astype(bf16)
    grad_gu = jnp.einsum(
        "rd,xrf->xdf", hidden_b, jnp.stack([d_gate, d_up]), preferred_element_type=f32
    )
    (grad_gu_s,) = scatter_group([(grad_gu, 1)], ring)
    grad_wg_s, grad_wu_s = grad_gu_s[0], grad_gu_s[1]
    hidden_partial = jnp.einsum("rf,df->rd", d_gate, wg, preferred_element_type=f32) + jnp.einsum(
        "rf,df->rd", d_up, wu, preferred_element_type=f32
    )
    d_hidden = grad_out + input_total(hidden_partial)
    d_attn, grad_ag = norm_back(d_hidden, attn_hat, attn_factor, ga32)
    d_attn_b = d_attn.astype(bf16)
    grad_wo = jnp.einsum("rc,rd->cd", attended_b, d_attn_b, preferred_element_type=f32)
    (grad_wo_s,) = scatter_group([(grad_wo, 1)], ring)
    d_attended = jnp.einsum("rd,dc->rc", d_attn_b, wo_t, preferred_element_type=f32).astype(bf16)
    d_attended = d_attended.reshape(rows, heads, HEAD_DIM)

    def backward_block(carry, index):
        key_acc, value_acc = carry
        start = index * block
        q_blk, scores = block_scores(start)
        logsum = lax.dynamic_index_in_dim(logsums, index, 0, keepdims=False)
        probs = jnp.exp(scores - logsum[..., None])
        value_acc = value_acc + jnp.einsum(
            "hqk,qhe->khe", probs.astype(bf16), d_attended, preferred_element_type=f32
        )
        d_probs = jnp.einsum("qhe,khe->hqk", d_attended, values_h, preferred_element_type=f32)
        delta = jnp.sum(probs * d_probs, axis=-1, keepdims=True)
        d_scores = (probs * (d_probs - delta)).astype(bf16)
        d_query_blk = (
            jnp.einsum("hqk,khe->qhe", d_scores, key_rot, preferred_element_type=f32) * scale
        )
        key_acc = (
            key_acc
            + jnp.einsum("hqk,qhe->khe", d_scores, q_blk, preferred_element_type=f32) * scale
        )
        return ((key_acc, value_acc), d_query_blk)

    empty = jnp.zeros((rows, heads, HEAD_DIM), f32)
    (d_key_rot, d_values), d_query_rot = lax.scan(backward_block, (empty, empty), jnp.arange(count))
    d_query_rot = d_query_rot.reshape(rows, heads, HEAD_DIM)
    d_values_b = d_values.reshape(rows, heads * HEAD_DIM).astype(bf16)
    d_query_n = rotate_back(d_query_rot, cosine, sine).reshape(rows, heads * HEAD_DIM)
    d_key_n = rotate_back(d_key_rot, cosine, sine).reshape(rows, heads * HEAD_DIM)
    grad_gq = jnp.sum(d_query_n * query_hat, axis=0)
    grad_gk = jnp.sum(d_key_n * key_hat, axis=0)
    d_query_hat = d_query_n * gq32
    d_key_hat = d_key_n * gk32
    query_inner, key_inner = lax.psum(
        (jnp.sum(d_query_hat * query_hat, axis=1), jnp.sum(d_key_hat * key_hat, axis=1)), "mp"
    )
    d_query_b = (query_factor * (d_query_hat - query_hat * (query_inner / width)[:, None])).astype(
        bf16
    )
    d_key_b = (key_factor * (d_key_hat - key_hat * (key_inner / width)[:, None])).astype(bf16)
    grad_qkv = jnp.einsum(
        "rd,xrc->xdc", tokens, jnp.stack([d_query_b, d_key_b, d_values_b]),
        preferred_element_type=f32,
    )
    (grad_qkv_s,) = scatter_group([(grad_qkv, 1)], ring)
    grad_wq_s, grad_wk_s, grad_wv_s = grad_qkv_s[0], grad_qkv_s[1], grad_qkv_s[2]

    def spread(g):
        return jnp.pad(g.reshape(n_dp, -1), ((0, 0), (0, slab - g.shape[0] // n_dp))).reshape(-1)

    grad_gains = jnp.stack([spread(grad_gq), spread(grad_gk), grad_ag, grad_mg])
    (grad_gains_s,) = scatter_group([(grad_gains, 1)], ring, carry=jnp.float32)
    grad_gq_s = grad_gains_s[0, :head_piece]
    grad_gk_s = grad_gains_s[1, :head_piece]
    grad_ag_s = grad_gains_s[2]
    grad_mg_s = grad_gains_s[3]
    input_part = jnp.einsum("rc,dc->rd", d_query_b, wq, preferred_element_type=f32)
    input_part = input_part + jnp.einsum("rc,dc->rd", d_key_b, wk, preferred_element_type=f32)
    input_part = input_part + jnp.einsum("rc,dc->rd", d_values_b, wv, preferred_element_type=f32)
    input_grad = d_hidden + input_total(input_part)
    return (
        layer_out,
        input_grad,
        grad_wq_s,
        grad_wk_s,
        grad_wv_s,
        grad_wo_s,
        grad_gq_s,
        grad_gk_s,
        grad_ag_s,
        grad_wg_s,
        grad_wu_s,
        grad_wd_s,
        grad_mg_s,
    )


def solution(mesh):
    placed = (
        P("dp", None),
        P("dp", None),
        P("dp"),
        P("dp", None),
        P("dp", "mp"),
        P("dp", "mp"),
        P("dp", "mp"),
        P("mp", "dp"),
        P(("mp", "dp")),
        P(("mp", "dp")),
        P("dp"),
        P("dp", "mp"),
        P("dp", "mp"),
        P("mp", "dp"),
        P("dp"),
    )
    ring = ring_order(mesh)
    return jax.shard_map(
        functools.partial(per_device, ring=ring),
        mesh=mesh,
        in_specs=placed,
        out_specs=(
            P("dp", None),
            P("dp", None),
            P("dp", "mp"),
            P("dp", "mp"),
            P("dp", "mp"),
            P("mp", "dp"),
            P(("mp", "dp")),
            P(("mp", "dp")),
            P("dp"),
            P("dp", "mp"),
            P("dp", "mp"),
            P("mp", "dp"),
            P("dp"),
        ),
        check_vma=False,
    )
```

```python
import functools

import jax
import jax.numpy as jnp
import numpy as np
from jax import lax
from jax.sharding import PartitionSpec as P

HEAD_DIM = 128


EPS = 1e-06
THETA = 500000.0


def rope_tables(rows, head_dim):
    half = head_dim // 2
    inverse = THETA ** (-(jnp.arange(half).astype(jnp.float32) * 2.0) / head_dim)
    angles = jnp.arange(rows).astype(jnp.float32)[:, None] * inverse[None, :]
    return (jnp.cos(angles)[:, None, :], jnp.sin(angles)[:, None, :])


def rotate(value, cosine, sine):
    half = value.shape[-1] // 2
    first, second = (value[..., :half], value[..., half:])
    return jnp.concatenate(
        [first * cosine - second * sine, second * cosine + first * sine], axis=-1
    )


def rotate_back(grad, cosine, sine):
    half = grad.shape[-1] // 2
    first, second = (grad[..., :half], grad[..., half:])
    return jnp.concatenate(
        [first * cosine + second * sine, second * cosine - first * sine], axis=-1
    )


def allowed_block(start, block, seg_row, length):
    query_pos = start + jnp.arange(block)
    key_pos = jnp.arange(seg_row.shape[0])
    same = seg_row[:, None] == seg_row[None, :]
    causal = key_pos[None, :] <= query_pos[:, None]
    inside = key_pos[None, :] < length
    return same & causal & inside | (key_pos[None, :] == query_pos[:, None])


def mp_allreduce(x, carry=jnp.bfloat16):
    m = lax.axis_size("mp")
    me = lax.axis_index("mp")
    core = me % 2
    chips = m // 2
    chip = me // 2
    half = x.shape[1] // 2
    pair = [(i, i ^ 1) for i in range(m)]
    mine = lax.dynamic_slice_in_dim(x, core * half, half, 1)
    other = lax.dynamic_slice_in_dim(x, (1 - core) * half, half, 1)
    part = mine + lax.ppermute(other, "mp", pair)
    if chips > 1:
        low = part.astype(carry)
        got = [low]
        for k in range(1, chips):
            perm = [(c * 2 + r, ((c + k) % chips) * 2 + r) for c in range(chips) for r in range(2)]
            got.append(lax.ppermute(low, "mp", perm))
        stack = jnp.stack(got)
        order = (chip - jnp.arange(chips)) % chips
        ordered = jnp.take(stack, order, axis=0).astype(jnp.float32)
        part = ordered[0]
        for k in range(1, chips):
            part = part + ordered[k]
    swapped = lax.ppermute(part, "mp", pair)
    full = jnp.zeros(x.shape, jnp.float32)
    full = lax.dynamic_update_slice_in_dim(full, part, core * half, 1)
    full = lax.dynamic_update_slice_in_dim(full, swapped, (1 - core) * half, 1)
    return full


def branch_total(partial_sum):
    return mp_allreduce(partial_sum)


def input_total(partial_sum):
    return mp_allreduce(partial_sum)


def norm_forward(total):
    factor = lax.rsqrt(jnp.mean(total * total, axis=1, keepdims=True) + EPS)
    return (total * factor, factor)


def norm_back(grad, normed, factor, gain):
    grad_gain = jnp.sum(grad * normed, axis=0)
    scaled = grad * gain
    inner = jnp.mean(scaled * normed, axis=1, keepdims=True)
    return (factor * (scaled - normed * inner), grad_gain)


def ring_order(mesh):
    column = [mesh.devices[i, 0] for i in range(mesh.devices.shape[0])]
    count = len(column)
    try:
        coords = [tuple(d.coords) for d in column]
    except AttributeError:
        return list(range(count))
    axes = [a for a in range(len(coords[0])) if len({c[a] for c in coords}) > 1]
    if len(axes) != 2:
        return list(range(count))
    sizes = {a: len({c[a] for c in coords}) for a in axes}
    even = [a for a in axes if sizes[a] % 2 == 0]
    if not even:
        return list(range(count))
    outer = min(even, key=lambda a: sizes[a])
    inner = [a for a in axes if a != outer][0]
    lo = {a: min(c[a] for c in coords) for a in axes}
    where = {(c[outer] - lo[outer], c[inner] - lo[inner]): i for i, c in enumerate(coords)}
    order = []
    for o in range(sizes[outer]):
        steps = range(sizes[inner]) if o % 2 == 0 else reversed(range(sizes[inner]))
        for k in steps:
            order.append(where[(o, k)])
    if sorted(order) != list(range(count)):
        return list(range(count))
    return order


def ring_steps(ring):
    n = len(ring)
    pos_of = [ring.index(d) for d in range(n)]
    mypos = jnp.asarray(pos_of, jnp.int32)[lax.axis_index("dp")]
    fwd = [(ring[p], ring[(p + 1) % n]) for p in range(n)]
    bwd = [(ring[p], ring[(p - 1) % n]) for p in range(n)]
    nf = n // 2
    return n, mypos, fwd, bwd, nf, n - 1 - nf


def gather_group(pieces, ring, after=None):
    locals_ = tuple(p.astype(jnp.bfloat16) for p, _ in pieces)
    if after is not None:
        locals_, _ = lax.optimization_barrier((locals_, after))
    n, mypos, fwd, bwd, nf, nb = ring_steps(ring)
    ring_arr = jnp.asarray(ring, jnp.int32)
    parts = {0: locals_}
    a = locals_
    b = locals_
    for s in range(nf):
        a = lax.ppermute(a, "dp", fwd)
        if s < nb:
            b = lax.ppermute(b, "dp", bwd)
            a, b = lax.optimization_barrier((a, b))
            parts[s + 1] = b
        parts[-(s + 1)] = a
    out = []
    last = (a, b)
    for i, (p, axis) in enumerate(pieces):
        shape = list(p.shape)
        width = shape[axis]
        shape[axis] *= n
        full = jnp.zeros(shape, jnp.bfloat16)
        for k in range(-nf, nb + 1):
            owner = ring_arr[(mypos + k) % n]
            full = lax.dynamic_update_slice_in_dim(full, parts[k][i], owner * width, axis)
        out.append(full)
    return out, last


def scatter_group(pieces, ring, carry=jnp.bfloat16, after=None):
    if after is not None:
        grads, _ = lax.optimization_barrier((tuple(g for g, _ in pieces), after))
        pieces = [(g, axis) for g, (_, axis) in zip(grads, pieces)]
    n, mypos, fwd, bwd, nf, nb = ring_steps(ring)
    ring_arr = jnp.asarray(ring, jnp.int32)
    widths = [g.shape[axis] // n for g, axis in pieces]

    def own(q):
        owner = ring_arr[q % n]
        return tuple(
            lax.dynamic_slice_in_dim(g, owner * w, w, axis).astype(jnp.float32)
            for (g, axis), w in zip(pieces, widths)
        )

    def send(vals, got, perm):
        if got is not None:
            vals = tuple(v + r.astype(jnp.float32) for v, r in zip(vals, got))
        return lax.ppermute(tuple(v.astype(carry) for v in vals), "dp", perm)

    got_f = None
    got_b = None
    for s in range(nf):
        got_f = send(own(mypos + nf - s), got_f, fwd)
        if s < nb:
            got_b = send(own(mypos - nb + s), got_b, bwd)
            got_f, got_b = lax.optimization_barrier((got_f, got_b))
    last = (got_f, got_b)
    total = own(mypos)
    total = tuple(t + r.astype(jnp.float32) for t, r in zip(total, got_f))
    if got_b is not None:
        total = tuple(t + r.astype(jnp.float32) for t, r in zip(total, got_b))
    return list(total), last


def per_device(
    tokens,
    segment_ids,
    valid_lengths,
    cotangent,
    w_query,
    w_key,
    w_value,
    w_out,
    query_gain,
    key_gain,
    attn_gain,
    w_gate,
    w_up,
    w_down,
    mlp_gain,
    ring,
):
    f32 = jnp.float32
    bf16 = jnp.bfloat16
    rows, width = tokens.shape
    seg_row = segment_ids[0]
    length = valid_lengths[0]
    block = min(512, rows)
    count = rows // block
    scale = HEAD_DIM ** (-0.5)
    n_dp = len(ring)
    slab = attn_gain.shape[0]
    head_piece = query_gain.shape[0]

    def padded(g):
        return jnp.pad(g, (0, slab - g.shape[0]))

    gains = jnp.stack([padded(query_gain), padded(key_gain), attn_gain, mlp_gain])
    (qkvo, gains_full), seen = gather_group(
        [(jnp.stack([w_query, w_key, w_value, w_out.T]), 1), (gains, 1)], ring
    )
    wq, wk, wv, wo_t = qkvo[0], qkvo[1], qkvo[2], qkvo[3]
    gq = gains_full[0].reshape(n_dp, slab)[:, :head_piece].reshape(-1)
    gk = gains_full[1].reshape(n_dp, slab)[:, :head_piece].reshape(-1)
    ga = gains_full[2]
    gm = gains_full[3]
    (gud,), seen = gather_group([(jnp.stack([w_gate, w_up, w_down.T]), 1)], ring, after=seen)
    wg, wu, wd_t = gud[0], gud[1], gud[2]
    gq32 = gq.astype(f32)
    gk32 = gk.astype(f32)
    ga32 = ga.astype(f32)
    gm32 = gm.astype(f32)
    query = jnp.dot(tokens, wq, preferred_element_type=f32)
    keys = jnp.dot(tokens, wk, preferred_element_type=f32)
    values = jnp.dot(tokens, wv, preferred_element_type=f32).astype(bf16)
    query_sq, key_sq = lax.psum(
        (jnp.sum(query * query, axis=1), jnp.sum(keys * keys, axis=1)), "mp"
    )
    query_factor = lax.rsqrt(query_sq / width + EPS)[:, None]
    key_factor = lax.rsqrt(key_sq / width + EPS)[:, None]
    query_hat = query * query_factor
    key_hat = keys * key_factor
    heads = query.shape[1] // HEAD_DIM
    cosine, sine = rope_tables(rows, HEAD_DIM)
    query_rot = rotate((query_hat * gq32).reshape(rows, heads, HEAD_DIM), cosine, sine).astype(bf16)
    key_rot = rotate((key_hat * gk32).reshape(rows, heads, HEAD_DIM), cosine, sine).astype(bf16)
    values_h = values.reshape(rows, heads, HEAD_DIM)

    def block_scores(start):
        scores = jnp.einsum("qhe,khe->hqk", query_rot, key_rot, preferred_element_type=f32) * scale
        mask = allowed_block(start, block, seg_row, length)
        return (query_rot, jnp.where(mask[None], scores, -1e30))

    def forward_block(index):
        start = index * block
        q_blk, scores = block_scores(start)
        top = jnp.max(scores, axis=-1, keepdims=True)
        total = jnp.sum(jnp.exp(scores - top), axis=-1, keepdims=True)
        logsum = top + jnp.log(total)
        probs = jnp.exp(scores - logsum).astype(bf16)
        attended = jnp.einsum("hqk,khe->qhe", probs, values_h, preferred_element_type=f32)
        return (attended, logsum[..., 0])

    attended, logsums = lax.map(forward_block, jnp.arange(count))
    attended_b = attended.reshape(rows, heads * HEAD_DIM).astype(bf16)
    attn_partial = jnp.einsum("rc,dc->rd", attended_b, wo_t, preferred_element_type=f32)
    attn_total = branch_total(attn_partial)
    attn_hat, attn_factor = norm_forward(attn_total)
    hidden = tokens.astype(f32) + attn_hat * ga32
    hidden_b = hidden.astype(bf16)
    gate = jnp.dot(hidden_b, wg, preferred_element_type=f32)
    up = jnp.dot(hidden_b, wu, preferred_element_type=f32)
    active = jax.nn.silu(gate)
    mixed_b = (active * up).astype(bf16)
    mlp_partial = jnp.einsum("rf,df->rd", mixed_b, wd_t, preferred_element_type=f32)
    mlp_total = branch_total(mlp_partial)
    mlp_hat, mlp_factor = norm_forward(mlp_total)
    layer_out = (hidden + mlp_hat * gm32).astype(bf16)
    grad_out = cotangent.astype(f32)
    d_mlp, grad_mg = norm_back(grad_out, mlp_hat, mlp_factor, gm32)
    d_mlp_b = d_mlp.astype(bf16)
    d_mixed = jnp.einsum("rd,df->rf", d_mlp_b, wd_t, preferred_element_type=f32)
    sigma = jax.nn.sigmoid(gate)
    d_gate = (d_mixed * up * sigma * (1.0 + gate * (1.0 - sigma))).astype(bf16)
    d_up = (d_mixed * active).astype(bf16)
    grad_gud = jnp.einsum(
        "xrd,xrf->xdf",
        jnp.stack([hidden_b, hidden_b, d_mlp_b]),
        jnp.stack([d_gate, d_up, mixed_b]),
        preferred_element_type=f32,
    )
    (grad_gud_s,), sent = scatter_group([(grad_gud, 1)], ring)
    grad_wg_s, grad_wu_s, grad_wd_s = grad_gud_s[0], grad_gud_s[1], grad_gud_s[2].T
    hidden_partial = jnp.einsum("rf,df->rd", d_gate, wg, preferred_element_type=f32) + jnp.einsum(
        "rf,df->rd", d_up, wu, preferred_element_type=f32
    )
    d_hidden = grad_out + input_total(hidden_partial)
    d_attn, grad_ag = norm_back(d_hidden, attn_hat, attn_factor, ga32)
    d_attn_b = d_attn.astype(bf16)
    d_attended = jnp.einsum("rd,dc->rc", d_attn_b, wo_t, preferred_element_type=f32).astype(bf16)
    d_attended = d_attended.reshape(rows, heads, HEAD_DIM)

    def backward_block(carry, index):
        key_acc, value_acc = carry
        start = index * block
        q_blk, scores = block_scores(start)
        logsum = lax.dynamic_index_in_dim(logsums, index, 0, keepdims=False)
        probs = jnp.exp(scores - logsum[..., None])
        value_acc = value_acc + jnp.einsum(
            "hqk,qhe->khe", probs.astype(bf16), d_attended, preferred_element_type=f32
        )
        d_probs = jnp.einsum("qhe,khe->hqk", d_attended, values_h, preferred_element_type=f32)
        delta = jnp.sum(probs * d_probs, axis=-1, keepdims=True)
        d_scores = (probs * (d_probs - delta)).astype(bf16)
        d_query_blk = (
            jnp.einsum("hqk,khe->qhe", d_scores, key_rot, preferred_element_type=f32) * scale
        )
        key_acc = (
            key_acc
            + jnp.einsum("hqk,qhe->khe", d_scores, q_blk, preferred_element_type=f32) * scale
        )
        return ((key_acc, value_acc), d_query_blk)

    empty = jnp.zeros((rows, heads, HEAD_DIM), f32)
    (d_key_rot, d_values), d_query_rot = lax.scan(backward_block, (empty, empty), jnp.arange(count))
    d_query_rot = d_query_rot.reshape(rows, heads, HEAD_DIM)
    d_values_b = d_values.reshape(rows, heads * HEAD_DIM).astype(bf16)
    d_query_n = rotate_back(d_query_rot, cosine, sine).reshape(rows, heads * HEAD_DIM)
    d_key_n = rotate_back(d_key_rot, cosine, sine).reshape(rows, heads * HEAD_DIM)
    grad_gq = jnp.sum(d_query_n * query_hat, axis=0)
    grad_gk = jnp.sum(d_key_n * key_hat, axis=0)
    d_query_hat = d_query_n * gq32
    d_key_hat = d_key_n * gk32
    query_inner, key_inner = lax.psum(
        (jnp.sum(d_query_hat * query_hat, axis=1), jnp.sum(d_key_hat * key_hat, axis=1)), "mp"
    )
    d_query_b = (query_factor * (d_query_hat - query_hat * (query_inner / width)[:, None])).astype(
        bf16
    )
    d_key_b = (key_factor * (d_key_hat - key_hat * (key_inner / width)[:, None])).astype(bf16)
    grad_qkvo = jnp.einsum(
        "xrd,xrc->xdc",
        jnp.stack([tokens, tokens, tokens, d_attn_b]),
        jnp.stack([d_query_b, d_key_b, d_values_b, attended_b]),
        preferred_element_type=f32,
    )
    (grad_qkvo_s,), sent = scatter_group([(grad_qkvo, 1)], ring, after=sent)
    grad_wq_s, grad_wk_s, grad_wv_s = grad_qkvo_s[0], grad_qkvo_s[1], grad_qkvo_s[2]
    grad_wo_s = grad_qkvo_s[3].T

    def spread(g):
        return jnp.pad(g.reshape(n_dp, -1), ((0, 0), (0, slab - g.shape[0] // n_dp))).reshape(-1)

    grad_gains = jnp.stack([spread(grad_gq), spread(grad_gk), grad_ag, grad_mg])
    (grad_gains_s,), sent = scatter_group([(grad_gains, 1)], ring, carry=jnp.float32, after=sent)
    grad_gq_s = grad_gains_s[0, :head_piece]
    grad_gk_s = grad_gains_s[1, :head_piece]
    grad_ag_s = grad_gains_s[2]
    grad_mg_s = grad_gains_s[3]
    input_part = jnp.einsum("rc,dc->rd", d_query_b, wq, preferred_element_type=f32)
    input_part = input_part + jnp.einsum("rc,dc->rd", d_key_b, wk, preferred_element_type=f32)
    input_part = input_part + jnp.einsum("rc,dc->rd", d_values_b, wv, preferred_element_type=f32)
    input_grad = d_hidden + input_total(input_part)
    return (
        layer_out,
        input_grad,
        grad_wq_s,
        grad_wk_s,
        grad_wv_s,
        grad_wo_s,
        grad_gq_s,
        grad_gk_s,
        grad_ag_s,
        grad_wg_s,
        grad_wu_s,
        grad_wd_s,
        grad_mg_s,
    )


def solution(mesh):
    placed = (
        P("dp", None),
        P("dp", None),
        P("dp"),
        P("dp", None),
        P("dp", "mp"),
        P("dp", "mp"),
        P("dp", "mp"),
        P("mp", "dp"),
        P(("mp", "dp")),
        P(("mp", "dp")),
        P("dp"),
        P("dp", "mp"),
        P("dp", "mp"),
        P("mp", "dp"),
        P("dp"),
    )
    ring = ring_order(mesh)
    return jax.shard_map(
        functools.partial(per_device, ring=ring),
        mesh=mesh,
        in_specs=placed,
        out_specs=(
            P("dp", None),
            P("dp", None),
            P("dp", "mp"),
            P("dp", "mp"),
            P("dp", "mp"),
            P("mp", "dp"),
            P(("mp", "dp")),
            P(("mp", "dp")),
            P("dp"),
            P("dp", "mp"),
            P("dp", "mp"),
            P("mp", "dp"),
            P("dp"),
        ),
        check_vma=False,
    )
```

```python
import functools

import jax
import jax.numpy as jnp
import numpy as np
from jax import lax
from jax.sharding import PartitionSpec as P

HEAD_DIM = 128


EPS = 1e-06
THETA = 500000.0


def rope_tables(rows, head_dim):
    half = head_dim // 2
    inverse = THETA ** (-(jnp.arange(half).astype(jnp.float32) * 2.0) / head_dim)
    angles = jnp.arange(rows).astype(jnp.float32)[:, None] * inverse[None, :]
    return (jnp.cos(angles)[:, None, :], jnp.sin(angles)[:, None, :])


def rotate(value, cosine, sine):
    half = value.shape[-1] // 2
    first, second = (value[..., :half], value[..., half:])
    return jnp.concatenate(
        [first * cosine - second * sine, second * cosine + first * sine], axis=-1
    )


def rotate_back(grad, cosine, sine):
    half = grad.shape[-1] // 2
    first, second = (grad[..., :half], grad[..., half:])
    return jnp.concatenate(
        [first * cosine + second * sine, second * cosine - first * sine], axis=-1
    )


def allowed_block(start, block, seg_row, length):
    query_pos = start + jnp.arange(block)
    key_pos = jnp.arange(seg_row.shape[0])
    same = seg_row[:, None] == seg_row[None, :]
    causal = key_pos[None, :] <= query_pos[:, None]
    inside = key_pos[None, :] < length
    return same & causal & inside | (key_pos[None, :] == query_pos[:, None])


def mp_allreduce(x, carry=jnp.bfloat16):
    m = lax.axis_size("mp")
    me = lax.axis_index("mp")
    core = me % 2
    chips = m // 2
    chip = me // 2
    half = x.shape[1] // 2
    pair = [(i, i ^ 1) for i in range(m)]
    mine = lax.dynamic_slice_in_dim(x, core * half, half, 1)
    other = lax.dynamic_slice_in_dim(x, (1 - core) * half, half, 1)
    part = mine + lax.ppermute(other, "mp", pair)
    if chips > 1:
        low = part.astype(carry)
        got = [low]
        for k in range(1, chips):
            perm = [(c * 2 + r, ((c + k) % chips) * 2 + r) for c in range(chips) for r in range(2)]
            got.append(lax.ppermute(low, "mp", perm))
        stack = jnp.stack(got)
        order = (chip - jnp.arange(chips)) % chips
        ordered = jnp.take(stack, order, axis=0).astype(jnp.float32)
        part = ordered[0]
        for k in range(1, chips):
            part = part + ordered[k]
    swapped = lax.ppermute(part, "mp", pair)
    full = jnp.zeros(x.shape, jnp.float32)
    full = lax.dynamic_update_slice_in_dim(full, part, core * half, 1)
    full = lax.dynamic_update_slice_in_dim(full, swapped, (1 - core) * half, 1)
    return full


def branch_total(partial_sum):
    return mp_allreduce(partial_sum)


def input_total(partial_sum):
    return mp_allreduce(partial_sum)


def norm_forward(total):
    factor = lax.rsqrt(jnp.mean(total * total, axis=1, keepdims=True) + EPS)
    return (total * factor, factor)


def norm_back(grad, normed, factor, gain):
    grad_gain = jnp.sum(grad * normed, axis=0)
    scaled = grad * gain
    inner = jnp.mean(scaled * normed, axis=1, keepdims=True)
    return (factor * (scaled - normed * inner), grad_gain)


def ring_order(mesh):
    column = [mesh.devices[i, 0] for i in range(mesh.devices.shape[0])]
    count = len(column)
    try:
        coords = [tuple(d.coords) for d in column]
    except AttributeError:
        return list(range(count))
    axes = [a for a in range(len(coords[0])) if len({c[a] for c in coords}) > 1]
    if len(axes) != 2:
        return list(range(count))
    sizes = {a: len({c[a] for c in coords}) for a in axes}
    even = [a for a in axes if sizes[a] % 2 == 0]
    if not even:
        return list(range(count))
    outer = min(even, key=lambda a: sizes[a])
    inner = [a for a in axes if a != outer][0]
    lo = {a: min(c[a] for c in coords) for a in axes}
    where = {(c[outer] - lo[outer], c[inner] - lo[inner]): i for i, c in enumerate(coords)}
    order = []
    for o in range(sizes[outer]):
        steps = range(sizes[inner]) if o % 2 == 0 else reversed(range(sizes[inner]))
        for k in steps:
            order.append(where[(o, k)])
    if sorted(order) != list(range(count)):
        return list(range(count))
    return order


def ring_steps(ring):
    n = len(ring)
    pos_of = [ring.index(d) for d in range(n)]
    mypos = jnp.asarray(pos_of, jnp.int32)[lax.axis_index("dp")]
    fwd = [(ring[p], ring[(p + 1) % n]) for p in range(n)]
    bwd = [(ring[p], ring[(p - 1) % n]) for p in range(n)]
    nf = n // 2
    return n, mypos, fwd, bwd, nf, n - 1 - nf


def gather_group(pieces, ring, after=None):
    locals_ = tuple(p.astype(jnp.bfloat16) for p, _ in pieces)
    if after is not None:
        locals_, _ = lax.optimization_barrier((locals_, after))
    n, mypos, fwd, bwd, nf, nb = ring_steps(ring)
    ring_arr = jnp.asarray(ring, jnp.int32)
    parts = {0: locals_}
    a = locals_
    b = locals_
    for s in range(nf):
        a = lax.ppermute(a, "dp", fwd)
        if s < nb:
            b = lax.ppermute(b, "dp", bwd)
            a, b = lax.optimization_barrier((a, b))
            parts[s + 1] = b
        parts[-(s + 1)] = a
    out = []
    last = (a, b)
    for i, (p, axis) in enumerate(pieces):
        shape = list(p.shape)
        width = shape[axis]
        shape[axis] *= n
        full = jnp.zeros(shape, jnp.bfloat16)
        arrival = [0]
        for s in range(nf):
            arrival.append(-(s + 1))
            if s < nb:
                arrival.append(s + 1)
        for k in arrival:
            owner = ring_arr[(mypos + k) % n]
            full = lax.dynamic_update_slice_in_dim(full, parts[k][i], owner * width, axis)
        out.append(full)
    return out, last


def scatter_group(pieces, ring, carry=jnp.bfloat16, after=None):
    if after is not None:
        arrays = tuple(p[1:] if isinstance(p[0], str) else (p[0],) for p in pieces)
        arrays, _ = lax.optimization_barrier((arrays, after))
        pieces = [
            ("prod",) + tuple(a) if isinstance(p[0], str) else (a[0], p[1]) for p, a in zip(pieces, arrays)
        ]
    n, mypos, fwd, bwd, nf, nb = ring_steps(ring)
    ring_arr = jnp.asarray(ring, jnp.int32)

    def chunk(piece, owner):
        if isinstance(piece[0], str):
            _, lhs, rhs = piece
            w = lhs.shape[2] // n
            part = lax.dynamic_slice_in_dim(lhs, owner * w, w, 2)
            return jnp.einsum("xrd,xrf->xdf", part, rhs, preferred_element_type=jnp.float32)
        g, axis = piece
        w = g.shape[axis] // n
        return lax.dynamic_slice_in_dim(g, owner * w, w, axis).astype(jnp.float32)

    def own(q):
        owner = ring_arr[q % n]
        return tuple(chunk(p, owner) for p in pieces)

    carries = carry if isinstance(carry, tuple) else (carry,) * len(pieces)

    def send(vals, got, perm):
        if got is not None:
            vals = tuple(v + r.astype(jnp.float32) for v, r in zip(vals, got))
        return lax.ppermute(tuple(v.astype(c) for v, c in zip(vals, carries)), "dp", perm)

    got_f = None
    got_b = None
    for s in range(nf):
        got_f = send(own(mypos + nf - s), got_f, fwd)
        if s < nb:
            got_b = send(own(mypos - nb + s), got_b, bwd)
            got_f, got_b = lax.optimization_barrier((got_f, got_b))
    last = (got_f, got_b)
    total = own(mypos)
    total = tuple(t + r.astype(jnp.float32) for t, r in zip(total, got_f))
    if got_b is not None:
        total = tuple(t + r.astype(jnp.float32) for t, r in zip(total, got_b))
    return list(total), last


def per_device(
    tokens,
    segment_ids,
    valid_lengths,
    cotangent,
    w_query,
    w_key,
    w_value,
    w_out,
    query_gain,
    key_gain,
    attn_gain,
    w_gate,
    w_up,
    w_down,
    mlp_gain,
    ring,
):
    f32 = jnp.float32
    bf16 = jnp.bfloat16
    rows, width = tokens.shape
    seg_row = segment_ids[0]
    length = valid_lengths[0]
    block = min(512, rows)
    count = rows // block
    scale = HEAD_DIM ** (-0.5)
    n_dp = len(ring)
    slab = attn_gain.shape[0]
    head_piece = query_gain.shape[0]

    def padded(g):
        return jnp.pad(g, (0, slab - g.shape[0]))

    gains = jnp.stack([padded(query_gain), padded(key_gain), attn_gain, mlp_gain])
    (qkvo, gains_full), seen = gather_group(
        [(jnp.stack([w_query, w_key, w_value, w_out.T]), 1), (gains, 1)], ring
    )
    wq, wk, wv, wo_t = qkvo[0], qkvo[1], qkvo[2], qkvo[3]
    gq = gains_full[0].reshape(n_dp, slab)[:, :head_piece].reshape(-1)
    gk = gains_full[1].reshape(n_dp, slab)[:, :head_piece].reshape(-1)
    ga = gains_full[2]
    gm = gains_full[3]
    (gud,), seen = gather_group([(jnp.stack([w_gate, w_up, w_down.T]), 1)], ring, after=seen)
    wg, wu, wd_t = gud[0], gud[1], gud[2]
    gq32 = gq.astype(f32)
    gk32 = gk.astype(f32)
    ga32 = ga.astype(f32)
    gm32 = gm.astype(f32)
    query = jnp.dot(tokens, wq, preferred_element_type=f32)
    keys = jnp.dot(tokens, wk, preferred_element_type=f32)
    values = jnp.dot(tokens, wv, preferred_element_type=f32).astype(bf16)
    query_sq, key_sq = lax.psum(
        (jnp.sum(query * query, axis=1), jnp.sum(keys * keys, axis=1)), "mp"
    )
    query_factor = lax.rsqrt(query_sq / width + EPS)[:, None]
    key_factor = lax.rsqrt(key_sq / width + EPS)[:, None]
    query_hat = query * query_factor
    key_hat = keys * key_factor
    heads = query.shape[1] // HEAD_DIM
    cosine, sine = rope_tables(rows, HEAD_DIM)
    query_rot = rotate((query_hat * gq32).reshape(rows, heads, HEAD_DIM), cosine, sine).astype(bf16)
    key_rot = rotate((key_hat * gk32).reshape(rows, heads, HEAD_DIM), cosine, sine).astype(bf16)
    values_h = values.reshape(rows, heads, HEAD_DIM)

    def block_scores(start):
        scores = jnp.einsum("qhe,khe->hqk", query_rot, key_rot, preferred_element_type=f32) * scale
        mask = allowed_block(start, block, seg_row, length)
        return (query_rot, jnp.where(mask[None], scores, -1e30))

    def forward_block(index):
        start = index * block
        q_blk, scores = block_scores(start)
        top = jnp.max(scores, axis=-1, keepdims=True)
        total = jnp.sum(jnp.exp(scores - top), axis=-1, keepdims=True)
        logsum = top + jnp.log(total)
        probs = jnp.exp(scores - logsum).astype(bf16)
        attended = jnp.einsum("hqk,khe->qhe", probs, values_h, preferred_element_type=f32)
        return (attended, logsum[..., 0])

    attended, logsums = lax.map(forward_block, jnp.arange(count))
    attended_b = attended.reshape(rows, heads * HEAD_DIM).astype(bf16)
    attn_partial = jnp.einsum("rc,dc->rd", attended_b, wo_t, preferred_element_type=f32)
    attn_total = branch_total(attn_partial)
    attn_hat, attn_factor = norm_forward(attn_total)
    hidden = tokens.astype(f32) + attn_hat * ga32
    hidden_b = hidden.astype(bf16)
    gate = jnp.dot(hidden_b, wg, preferred_element_type=f32)
    up = jnp.dot(hidden_b, wu, preferred_element_type=f32)
    active = jax.nn.silu(gate)
    mixed_b = (active * up).astype(bf16)
    mlp_partial = jnp.einsum("rf,df->rd", mixed_b, wd_t, preferred_element_type=f32)
    mlp_total = branch_total(mlp_partial)
    mlp_hat, mlp_factor = norm_forward(mlp_total)
    layer_out = (hidden + mlp_hat * gm32).astype(bf16)
    grad_out = cotangent.astype(f32)
    d_mlp, grad_mg = norm_back(grad_out, mlp_hat, mlp_factor, gm32)
    d_mlp_b = d_mlp.astype(bf16)
    d_mixed = jnp.einsum("rd,df->rf", d_mlp_b, wd_t, preferred_element_type=f32)
    sigma = jax.nn.sigmoid(gate)
    d_gate = (d_mixed * up * sigma * (1.0 + gate * (1.0 - sigma))).astype(bf16)
    d_up = (d_mixed * active).astype(bf16)
    grad_gud = (
        "prod",
        jnp.stack([hidden_b, hidden_b, d_mlp_b]),
        jnp.stack([d_gate, d_up, mixed_b]),
    )
    (grad_gud_s,), sent = scatter_group([grad_gud], ring)
    grad_wg_s, grad_wu_s, grad_wd_s = grad_gud_s[0], grad_gud_s[1], grad_gud_s[2].T
    hidden_partial = jnp.einsum("rf,df->rd", d_gate, wg, preferred_element_type=f32) + jnp.einsum(
        "rf,df->rd", d_up, wu, preferred_element_type=f32
    )
    d_hidden = grad_out + input_total(hidden_partial)
    d_attn, grad_ag = norm_back(d_hidden, attn_hat, attn_factor, ga32)
    d_attn_b = d_attn.astype(bf16)
    d_attended = jnp.einsum("rd,dc->rc", d_attn_b, wo_t, preferred_element_type=f32).astype(bf16)
    d_attended = d_attended.reshape(rows, heads, HEAD_DIM)

    def backward_block(carry, index):
        key_acc, value_acc = carry
        start = index * block
        q_blk, scores = block_scores(start)
        logsum = lax.dynamic_index_in_dim(logsums, index, 0, keepdims=False)
        probs = jnp.exp(scores - logsum[..., None])
        value_acc = value_acc + jnp.einsum(
            "hqk,qhe->khe", probs.astype(bf16), d_attended, preferred_element_type=f32
        )
        d_probs = jnp.einsum("qhe,khe->hqk", d_attended, values_h, preferred_element_type=f32)
        delta = jnp.sum(probs * d_probs, axis=-1, keepdims=True)
        d_scores = (probs * (d_probs - delta)).astype(bf16)
        d_query_blk = (
            jnp.einsum("hqk,khe->qhe", d_scores, key_rot, preferred_element_type=f32) * scale
        )
        key_acc = (
            key_acc
            + jnp.einsum("hqk,qhe->khe", d_scores, q_blk, preferred_element_type=f32) * scale
        )
        return ((key_acc, value_acc), d_query_blk)

    empty = jnp.zeros((rows, heads, HEAD_DIM), f32)
    (d_key_rot, d_values), d_query_rot = lax.scan(backward_block, (empty, empty), jnp.arange(count))
    d_query_rot = d_query_rot.reshape(rows, heads, HEAD_DIM)
    d_values_b = d_values.reshape(rows, heads * HEAD_DIM).astype(bf16)
    d_query_n = rotate_back(d_query_rot, cosine, sine).reshape(rows, heads * HEAD_DIM)
    d_key_n = rotate_back(d_key_rot, cosine, sine).reshape(rows, heads * HEAD_DIM)
    grad_gq = jnp.sum(d_query_n * query_hat, axis=0)
    grad_gk = jnp.sum(d_key_n * key_hat, axis=0)
    d_query_hat = d_query_n * gq32
    d_key_hat = d_key_n * gk32
    query_inner, key_inner = lax.psum(
        (jnp.sum(d_query_hat * query_hat, axis=1), jnp.sum(d_key_hat * key_hat, axis=1)), "mp"
    )
    d_query_b = (query_factor * (d_query_hat - query_hat * (query_inner / width)[:, None])).astype(
        bf16
    )
    d_key_b = (key_factor * (d_key_hat - key_hat * (key_inner / width)[:, None])).astype(bf16)
    grad_qkvo = (
        "prod",
        jnp.stack([tokens, tokens, tokens, d_attn_b]),
        jnp.stack([d_query_b, d_key_b, d_values_b, attended_b]),
    )

    def spread(g):
        return jnp.pad(g.reshape(n_dp, -1), ((0, 0), (0, slab - g.shape[0] // n_dp))).reshape(-1)

    grad_gains = jnp.stack([spread(grad_gq), spread(grad_gk), grad_ag, grad_mg])
    (grad_qkvo_s, grad_gains_s), sent = scatter_group(
        [grad_qkvo, (grad_gains, 1)], ring, carry=(jnp.bfloat16, jnp.float32), after=sent
    )
    grad_wq_s, grad_wk_s, grad_wv_s = grad_qkvo_s[0], grad_qkvo_s[1], grad_qkvo_s[2]
    grad_wo_s = grad_qkvo_s[3].T
    grad_gq_s = grad_gains_s[0, :head_piece]
    grad_gk_s = grad_gains_s[1, :head_piece]
    grad_ag_s = grad_gains_s[2]
    grad_mg_s = grad_gains_s[3]
    input_part = jnp.einsum("rc,dc->rd", d_query_b, wq, preferred_element_type=f32)
    input_part = input_part + jnp.einsum("rc,dc->rd", d_key_b, wk, preferred_element_type=f32)
    input_part = input_part + jnp.einsum("rc,dc->rd", d_values_b, wv, preferred_element_type=f32)
    input_grad = d_hidden + input_total(input_part)
    return (
        layer_out,
        input_grad,
        grad_wq_s,
        grad_wk_s,
        grad_wv_s,
        grad_wo_s,
        grad_gq_s,
        grad_gk_s,
        grad_ag_s,
        grad_wg_s,
        grad_wu_s,
        grad_wd_s,
        grad_mg_s,
    )


def solution(mesh):
    placed = (
        P("dp", None),
        P("dp", None),
        P("dp"),
        P("dp", None),
        P("dp", "mp"),
        P("dp", "mp"),
        P("dp", "mp"),
        P("mp", "dp"),
        P(("mp", "dp")),
        P(("mp", "dp")),
        P("dp"),
        P("dp", "mp"),
        P("dp", "mp"),
        P("mp", "dp"),
        P("dp"),
    )
    ring = ring_order(mesh)
    return jax.shard_map(
        functools.partial(per_device, ring=ring),
        mesh=mesh,
        in_specs=placed,
        out_specs=(
            P("dp", None),
            P("dp", None),
            P("dp", "mp"),
            P("dp", "mp"),
            P("dp", "mp"),
            P("mp", "dp"),
            P(("mp", "dp")),
            P(("mp", "dp")),
            P("dp"),
            P("dp", "mp"),
            P("dp", "mp"),
            P("mp", "dp"),
            P("dp"),
        ),
        check_vma=False,
    )
```

```python
import functools

import jax
import jax.numpy as jnp
import numpy as np
from jax import lax
from jax.sharding import PartitionSpec as P

HEAD_DIM = 128


EPS = 1e-06
THETA = 500000.0


def rope_tables(rows, head_dim):
    half = head_dim // 2
    inverse = THETA ** (-(jnp.arange(half).astype(jnp.float32) * 2.0) / head_dim)
    angles = jnp.arange(rows).astype(jnp.float32)[:, None] * inverse[None, :]
    return (jnp.cos(angles)[:, None, :], jnp.sin(angles)[:, None, :])


def rotate(value, cosine, sine):
    half = value.shape[-1] // 2
    first, second = (value[..., :half], value[..., half:])
    return jnp.concatenate(
        [first * cosine - second * sine, second * cosine + first * sine], axis=-1
    )


def rotate_back(grad, cosine, sine):
    half = grad.shape[-1] // 2
    first, second = (grad[..., :half], grad[..., half:])
    return jnp.concatenate(
        [first * cosine + second * sine, second * cosine - first * sine], axis=-1
    )


def allowed_block(start, block, seg_row, length):
    query_pos = start + jnp.arange(block)
    key_pos = jnp.arange(seg_row.shape[0])
    same = seg_row[:, None] == seg_row[None, :]
    causal = key_pos[None, :] <= query_pos[:, None]
    inside = key_pos[None, :] < length
    return same & causal & inside | (key_pos[None, :] == query_pos[:, None])


def mp_allreduce(x, carry=jnp.bfloat16):
    m = lax.axis_size("mp")
    me = lax.axis_index("mp")
    core = me % 2
    chips = m // 2
    chip = me // 2
    half = x.shape[1] // 2
    pair = [(i, i ^ 1) for i in range(m)]
    mine = lax.dynamic_slice_in_dim(x, core * half, half, 1)
    other = lax.dynamic_slice_in_dim(x, (1 - core) * half, half, 1)
    part = mine + lax.ppermute(other, "mp", pair)
    if chips == 2:
        low = part.astype(carry)
        got = lax.ppermute(low, "mp", [(i, i ^ 2) for i in range(m)])
        part = low.astype(jnp.float32) + got.astype(jnp.float32)
    elif chips > 2:
        low = part.astype(carry)
        got = [low]
        for k in range(1, chips):
            perm = [(c * 2 + r, ((c + k) % chips) * 2 + r) for c in range(chips) for r in range(2)]
            got.append(lax.ppermute(low, "mp", perm))
        stack = jnp.stack(got)
        order = (chip - jnp.arange(chips)) % chips
        ordered = jnp.take(stack, order, axis=0).astype(jnp.float32)
        part = ordered[0]
        for k in range(1, chips):
            part = part + ordered[k]
    swapped = lax.ppermute(part, "mp", pair)
    first = jnp.where(core == 0, part, swapped)
    second = jnp.where(core == 0, swapped, part)
    return jnp.concatenate([first, second], axis=1)


def branch_total(partial_sum):
    return mp_allreduce(partial_sum)


def input_total(partial_sum):
    return mp_allreduce(partial_sum)


def norm_forward(total):
    factor = lax.rsqrt(jnp.mean(total * total, axis=1, keepdims=True) + EPS)
    return (total * factor, factor)


def norm_back(grad, normed, factor, gain):
    grad_gain = jnp.sum(grad * normed, axis=0)
    scaled = grad * gain
    inner = jnp.mean(scaled * normed, axis=1, keepdims=True)
    return (factor * (scaled - normed * inner), grad_gain)


def ring_order(mesh):
    column = [mesh.devices[i, 0] for i in range(mesh.devices.shape[0])]
    count = len(column)
    try:
        coords = [tuple(d.coords) for d in column]
    except AttributeError:
        return list(range(count))
    axes = [a for a in range(len(coords[0])) if len({c[a] for c in coords}) > 1]
    if len(axes) != 2:
        return list(range(count))
    sizes = {a: len({c[a] for c in coords}) for a in axes}
    even = [a for a in axes if sizes[a] % 2 == 0]
    if not even:
        return list(range(count))
    outer = min(even, key=lambda a: sizes[a])
    inner = [a for a in axes if a != outer][0]
    lo = {a: min(c[a] for c in coords) for a in axes}
    where = {(c[outer] - lo[outer], c[inner] - lo[inner]): i for i, c in enumerate(coords)}
    order = []
    for o in range(sizes[outer]):
        steps = range(sizes[inner]) if o % 2 == 0 else reversed(range(sizes[inner]))
        for k in steps:
            order.append(where[(o, k)])
    if sorted(order) != list(range(count)):
        return list(range(count))
    return order


def ring_steps(ring):
    n = len(ring)
    pos_of = [ring.index(d) for d in range(n)]
    mypos = jnp.asarray(pos_of, jnp.int32)[lax.axis_index("dp")]
    fwd = [(ring[p], ring[(p + 1) % n]) for p in range(n)]
    bwd = [(ring[p], ring[(p - 1) % n]) for p in range(n)]
    nf = n // 2
    return n, mypos, fwd, bwd, nf, n - 1 - nf


def gather_group(pieces, ring, after=None):
    locals_ = tuple(p.astype(jnp.bfloat16) for p, _ in pieces)
    if after is not None:
        locals_, _ = lax.optimization_barrier((locals_, after))
    n, mypos, fwd, bwd, nf, nb = ring_steps(ring)
    ring_arr = jnp.asarray(ring, jnp.int32)
    parts = {0: locals_}
    a = locals_
    b = locals_
    for s in range(nf):
        a = lax.ppermute(a, "dp", fwd)
        if s < nb:
            b = lax.ppermute(b, "dp", bwd)
            a, b = lax.optimization_barrier((a, b))
            parts[s + 1] = b
        parts[-(s + 1)] = a
    out = []
    last = (a, b)
    for i, (p, axis) in enumerate(pieces):
        shape = list(p.shape)
        width = shape[axis]
        shape[axis] *= n
        full = jnp.zeros(shape, jnp.bfloat16)
        arrival = [0]
        for s in range(nf):
            arrival.append(-(s + 1))
            if s < nb:
                arrival.append(s + 1)
        for k in arrival:
            owner = ring_arr[(mypos + k) % n]
            full = lax.dynamic_update_slice_in_dim(full, parts[k][i], owner * width, axis)
        out.append(full)
    return out, last


def scatter_group(pieces, ring, carry=jnp.bfloat16, after=None):
    if after is not None:
        arrays = tuple(p[1:] if isinstance(p[0], str) else (p[0],) for p in pieces)
        arrays, _ = lax.optimization_barrier((arrays, after))
        pieces = [
            ("prod",) + tuple(a) if isinstance(p[0], str) else (a[0], p[1]) for p, a in zip(pieces, arrays)
        ]
    n, mypos, fwd, bwd, nf, nb = ring_steps(ring)
    ring_arr = jnp.asarray(ring, jnp.int32)

    def chunk(piece, owner):
        if isinstance(piece[0], str):
            _, lhs, rhs = piece
            w = lhs.shape[2] // n
            part = lax.dynamic_slice_in_dim(lhs, owner * w, w, 2)
            return jnp.einsum("xrd,xrf->xdf", part, rhs, preferred_element_type=jnp.float32)
        g, axis = piece
        w = g.shape[axis] // n
        return lax.dynamic_slice_in_dim(g, owner * w, w, axis).astype(jnp.float32)

    def own(q):
        owner = ring_arr[q % n]
        return tuple(chunk(p, owner) for p in pieces)

    carries = carry if isinstance(carry, tuple) else (carry,) * len(pieces)

    def send(vals, got, perm):
        if got is not None:
            vals = tuple(v + r.astype(jnp.float32) for v, r in zip(vals, got))
        return lax.ppermute(tuple(v.astype(c) for v, c in zip(vals, carries)), "dp", perm)

    got_f = None
    got_b = None
    for s in range(nf):
        got_f = send(own(mypos + nf - s), got_f, fwd)
        if s < nb:
            got_b = send(own(mypos - nb + s), got_b, bwd)
            got_f, got_b = lax.optimization_barrier((got_f, got_b))
    last = (got_f, got_b)
    total = own(mypos)
    total = tuple(t + r.astype(jnp.float32) for t, r in zip(total, got_f))
    if got_b is not None:
        total = tuple(t + r.astype(jnp.float32) for t, r in zip(total, got_b))
    return list(total), last


def per_device(
    tokens,
    segment_ids,
    valid_lengths,
    cotangent,
    w_query,
    w_key,
    w_value,
    w_out,
    query_gain,
    key_gain,
    attn_gain,
    w_gate,
    w_up,
    w_down,
    mlp_gain,
    ring,
):
    f32 = jnp.float32
    bf16 = jnp.bfloat16
    rows, width = tokens.shape
    seg_row = segment_ids[0]
    length = valid_lengths[0]
    block = min(512, rows)
    count = rows // block
    scale = HEAD_DIM ** (-0.5)
    n_dp = len(ring)
    slab = attn_gain.shape[0]
    head_piece = query_gain.shape[0]

    def padded(g):
        return jnp.pad(g, (0, slab - g.shape[0]))

    gains = jnp.stack([padded(query_gain), padded(key_gain), attn_gain, mlp_gain])
    (qkvo, gains_full), seen = gather_group(
        [(jnp.stack([w_query, w_key, w_value, w_out.T]), 1), (gains, 1)], ring
    )
    wq, wk, wv, wo_t = qkvo[0], qkvo[1], qkvo[2], qkvo[3]
    gq = gains_full[0].reshape(n_dp, slab)[:, :head_piece].reshape(-1)
    gk = gains_full[1].reshape(n_dp, slab)[:, :head_piece].reshape(-1)
    ga = gains_full[2]
    gm = gains_full[3]
    (gud,), seen = gather_group([(jnp.stack([w_gate, w_up, w_down.T]), 1)], ring, after=seen)
    wg, wu, wd_t = gud[0], gud[1], gud[2]
    gq32 = gq.astype(f32)
    gk32 = gk.astype(f32)
    ga32 = ga.astype(f32)
    gm32 = gm.astype(f32)
    query = jnp.dot(tokens, wq, preferred_element_type=f32)
    keys = jnp.dot(tokens, wk, preferred_element_type=f32)
    values = jnp.dot(tokens, wv, preferred_element_type=f32).astype(bf16)
    query_sq, key_sq = lax.psum(
        (jnp.sum(query * query, axis=1), jnp.sum(keys * keys, axis=1)), "mp"
    )
    query_factor = lax.rsqrt(query_sq / width + EPS)[:, None]
    key_factor = lax.rsqrt(key_sq / width + EPS)[:, None]
    query_hat = query * query_factor
    key_hat = keys * key_factor
    heads = query.shape[1] // HEAD_DIM
    cosine, sine = rope_tables(rows, HEAD_DIM)
    query_rot = rotate((query_hat * gq32).reshape(rows, heads, HEAD_DIM), cosine, sine).astype(bf16)
    key_rot = rotate((key_hat * gk32).reshape(rows, heads, HEAD_DIM), cosine, sine).astype(bf16)
    values_h = values.reshape(rows, heads, HEAD_DIM)

    def block_scores(start):
        scores = jnp.einsum("qhe,khe->hqk", query_rot, key_rot, preferred_element_type=f32) * scale
        mask = allowed_block(start, block, seg_row, length)
        return (query_rot, jnp.where(mask[None], scores, -1e30))

    def forward_block(index):
        start = index * block
        q_blk, scores = block_scores(start)
        top = jnp.max(scores, axis=-1, keepdims=True)
        total = jnp.sum(jnp.exp(scores - top), axis=-1, keepdims=True)
        logsum = top + jnp.log(total)
        probs = jnp.exp(scores - logsum).astype(bf16)
        attended = jnp.einsum("hqk,khe->qhe", probs, values_h, preferred_element_type=f32)
        return (attended, logsum[..., 0])

    attended, logsums = lax.map(forward_block, jnp.arange(count))
    attended_b = attended.reshape(rows, heads * HEAD_DIM).astype(bf16)
    attn_partial = jnp.einsum("rc,dc->rd", attended_b, wo_t, preferred_element_type=f32)
    attn_total = branch_total(attn_partial)
    attn_hat, attn_factor = norm_forward(attn_total)
    hidden = tokens.astype(f32) + attn_hat * ga32
    hidden_b = hidden.astype(bf16)
    gate = jnp.dot(hidden_b, wg, preferred_element_type=f32)
    up = jnp.dot(hidden_b, wu, preferred_element_type=f32)
    active = jax.nn.silu(gate)
    mixed_b = (active * up).astype(bf16)
    mlp_partial = jnp.einsum("rf,df->rd", mixed_b, wd_t, preferred_element_type=f32)
    mlp_total = branch_total(mlp_partial)
    mlp_hat, mlp_factor = norm_forward(mlp_total)
    layer_out = (hidden + mlp_hat * gm32).astype(bf16)
    grad_out = cotangent.astype(f32)
    d_mlp, grad_mg = norm_back(grad_out, mlp_hat, mlp_factor, gm32)
    d_mlp_b = d_mlp.astype(bf16)
    (grad_wd_t_s,), sent = scatter_group([("prod", d_mlp_b[None], mixed_b[None])], ring)
    grad_wd_s = grad_wd_t_s[0].T
    d_mixed = jnp.einsum("rd,df->rf", d_mlp_b, wd_t, preferred_element_type=f32)
    sigma = jax.nn.sigmoid(gate)
    d_gate = (d_mixed * up * sigma * (1.0 + gate * (1.0 - sigma))).astype(bf16)
    d_up = (d_mixed * active).astype(bf16)
    grad_gu = ("prod", jnp.stack([hidden_b, hidden_b]), jnp.stack([d_gate, d_up]))
    (grad_gu_s,), sent = scatter_group([grad_gu], ring, after=sent)
    grad_wg_s, grad_wu_s = grad_gu_s[0], grad_gu_s[1]
    hidden_partial = jnp.einsum("rf,df->rd", d_gate, wg, preferred_element_type=f32) + jnp.einsum(
        "rf,df->rd", d_up, wu, preferred_element_type=f32
    )
    d_hidden = grad_out + input_total(hidden_partial)
    d_attn, grad_ag = norm_back(d_hidden, attn_hat, attn_factor, ga32)
    d_attn_b = d_attn.astype(bf16)
    d_attended = jnp.einsum("rd,dc->rc", d_attn_b, wo_t, preferred_element_type=f32).astype(bf16)
    d_attended = d_attended.reshape(rows, heads, HEAD_DIM)

    def backward_block(carry, index):
        key_acc, value_acc = carry
        start = index * block
        q_blk, scores = block_scores(start)
        logsum = lax.dynamic_index_in_dim(logsums, index, 0, keepdims=False)
        probs = jnp.exp(scores - logsum[..., None])
        value_acc = value_acc + jnp.einsum(
            "hqk,qhe->khe", probs.astype(bf16), d_attended, preferred_element_type=f32
        )
        d_probs = jnp.einsum("qhe,khe->hqk", d_attended, values_h, preferred_element_type=f32)
        delta = jnp.sum(probs * d_probs, axis=-1, keepdims=True)
        d_scores = (probs * (d_probs - delta)).astype(bf16)
        d_query_blk = (
            jnp.einsum("hqk,khe->qhe", d_scores, key_rot, preferred_element_type=f32) * scale
        )
        key_acc = (
            key_acc
            + jnp.einsum("hqk,qhe->khe", d_scores, q_blk, preferred_element_type=f32) * scale
        )
        return ((key_acc, value_acc), d_query_blk)

    empty = jnp.zeros((rows, heads, HEAD_DIM), f32)
    (d_key_rot, d_values), d_query_rot = lax.scan(backward_block, (empty, empty), jnp.arange(count))
    d_query_rot = d_query_rot.reshape(rows, heads, HEAD_DIM)
    d_values_b = d_values.reshape(rows, heads * HEAD_DIM).astype(bf16)
    d_query_n = rotate_back(d_query_rot, cosine, sine).reshape(rows, heads * HEAD_DIM)
    d_key_n = rotate_back(d_key_rot, cosine, sine).reshape(rows, heads * HEAD_DIM)
    grad_gq = jnp.sum(d_query_n * query_hat, axis=0)
    grad_gk = jnp.sum(d_key_n * key_hat, axis=0)
    d_query_hat = d_query_n * gq32
    d_key_hat = d_key_n * gk32
    query_inner, key_inner = lax.psum(
        (jnp.sum(d_query_hat * query_hat, axis=1), jnp.sum(d_key_hat * key_hat, axis=1)), "mp"
    )
    d_query_b = (query_factor * (d_query_hat - query_hat * (query_inner / width)[:, None])).astype(
        bf16
    )
    d_key_b = (key_factor * (d_key_hat - key_hat * (key_inner / width)[:, None])).astype(bf16)
    grad_qkvo = (
        "prod",
        jnp.stack([tokens, tokens, tokens, d_attn_b]),
        jnp.stack([d_query_b, d_key_b, d_values_b, attended_b]),
    )

    def spread(g):
        return jnp.pad(g.reshape(n_dp, -1), ((0, 0), (0, slab - g.shape[0] // n_dp))).reshape(-1)

    grad_gains = jnp.stack([spread(grad_gq), spread(grad_gk), grad_ag, grad_mg])
    (grad_qkvo_s, grad_gains_s), sent = scatter_group(
        [grad_qkvo, (grad_gains, 1)], ring, carry=(jnp.bfloat16, jnp.float32), after=sent
    )
    grad_wq_s, grad_wk_s, grad_wv_s = grad_qkvo_s[0], grad_qkvo_s[1], grad_qkvo_s[2]
    grad_wo_s = grad_qkvo_s[3].T
    grad_gq_s = grad_gains_s[0, :head_piece]
    grad_gk_s = grad_gains_s[1, :head_piece]
    grad_ag_s = grad_gains_s[2]
    grad_mg_s = grad_gains_s[3]
    input_part = jnp.einsum("rc,dc->rd", d_query_b, wq, preferred_element_type=f32)
    input_part = input_part + jnp.einsum("rc,dc->rd", d_key_b, wk, preferred_element_type=f32)
    input_part = input_part + jnp.einsum("rc,dc->rd", d_values_b, wv, preferred_element_type=f32)
    input_grad = d_hidden + input_total(input_part)
    return (
        layer_out,
        input_grad,
        grad_wq_s,
        grad_wk_s,
        grad_wv_s,
        grad_wo_s,
        grad_gq_s,
        grad_gk_s,
        grad_ag_s,
        grad_wg_s,
        grad_wu_s,
        grad_wd_s,
        grad_mg_s,
    )


def solution(mesh):
    placed = (
        P("dp", None),
        P("dp", None),
        P("dp"),
        P("dp", None),
        P("dp", "mp"),
        P("dp", "mp"),
        P("dp", "mp"),
        P("mp", "dp"),
        P(("mp", "dp")),
        P(("mp", "dp")),
        P("dp"),
        P("dp", "mp"),
        P("dp", "mp"),
        P("mp", "dp"),
        P("dp"),
    )
    ring = ring_order(mesh)
    return jax.shard_map(
        functools.partial(per_device, ring=ring),
        mesh=mesh,
        in_specs=placed,
        out_specs=(
            P("dp", None),
            P("dp", None),
            P("dp", "mp"),
            P("dp", "mp"),
            P("dp", "mp"),
            P("mp", "dp"),
            P(("mp", "dp")),
            P(("mp", "dp")),
            P("dp"),
            P("dp", "mp"),
            P("dp", "mp"),
            P("mp", "dp"),
            P("dp"),
        ),
        check_vma=False,
    )
```

```python
import functools

import jax
import jax.numpy as jnp
import numpy as np
from jax import lax
from jax.sharding import PartitionSpec as P

HEAD_DIM = 128


EPS = 1e-06
THETA = 500000.0


def rope_tables(rows, head_dim):
    half = head_dim // 2
    inverse = THETA ** (-(jnp.arange(half).astype(jnp.float32) * 2.0) / head_dim)
    angles = jnp.arange(rows).astype(jnp.float32)[:, None] * inverse[None, :]
    return (jnp.cos(angles)[:, None, :], jnp.sin(angles)[:, None, :])


def rotate(value, cosine, sine):
    half = value.shape[-1] // 2
    first, second = (value[..., :half], value[..., half:])
    return jnp.concatenate(
        [first * cosine - second * sine, second * cosine + first * sine], axis=-1
    )


def rotate_back(grad, cosine, sine):
    half = grad.shape[-1] // 2
    first, second = (grad[..., :half], grad[..., half:])
    return jnp.concatenate(
        [first * cosine + second * sine, second * cosine - first * sine], axis=-1
    )


def allowed_block(start, block, seg_row, length):
    query_pos = start + jnp.arange(block)
    key_pos = jnp.arange(seg_row.shape[0])
    same = seg_row[:, None] == seg_row[None, :]
    causal = key_pos[None, :] <= query_pos[:, None]
    inside = key_pos[None, :] < length
    return same & causal & inside | (key_pos[None, :] == query_pos[:, None])


def mp_allreduce(x, carry=jnp.bfloat16):
    m = lax.axis_size("mp")
    me = lax.axis_index("mp")
    core = me % 2
    chips = m // 2
    chip = me // 2
    half = x.shape[1] // 2
    pair = [(i, i ^ 1) for i in range(m)]
    mine = lax.dynamic_slice_in_dim(x, core * half, half, 1)
    other = lax.dynamic_slice_in_dim(x, (1 - core) * half, half, 1)
    part = mine + lax.ppermute(other, "mp", pair)
    if chips == 2:
        low = part.astype(carry)
        got = lax.ppermute(low, "mp", [(i, i ^ 2) for i in range(m)])
        part = low.astype(jnp.float32) + got.astype(jnp.float32)
    elif chips > 2:
        low = part.astype(carry)
        got = [low]
        for k in range(1, chips):
            perm = [(c * 2 + r, ((c + k) % chips) * 2 + r) for c in range(chips) for r in range(2)]
            got.append(lax.ppermute(low, "mp", perm))
        stack = jnp.stack(got)
        order = (chip - jnp.arange(chips)) % chips
        ordered = jnp.take(stack, order, axis=0).astype(jnp.float32)
        part = ordered[0]
        for k in range(1, chips):
            part = part + ordered[k]
    swapped = lax.ppermute(part, "mp", pair)
    first = jnp.where(core == 0, part, swapped)
    second = jnp.where(core == 0, swapped, part)
    return jnp.concatenate([first, second], axis=1)


def branch_total(partial_sum):
    return mp_allreduce(partial_sum)


def input_total(partial_sum):
    return mp_allreduce(partial_sum)


def norm_forward(total):
    factor = lax.rsqrt(jnp.mean(total * total, axis=1, keepdims=True) + EPS)
    return (total * factor, factor)


def norm_back(grad, normed, factor, gain):
    grad_gain = jnp.sum(grad * normed, axis=0)
    scaled = grad * gain
    inner = jnp.mean(scaled * normed, axis=1, keepdims=True)
    return (factor * (scaled - normed * inner), grad_gain)


def ring_order(mesh):
    column = [mesh.devices[i, 0] for i in range(mesh.devices.shape[0])]
    count = len(column)
    try:
        coords = [tuple(d.coords) for d in column]
    except AttributeError:
        return list(range(count))
    axes = [a for a in range(len(coords[0])) if len({c[a] for c in coords}) > 1]
    if len(axes) != 2:
        return list(range(count))
    sizes = {a: len({c[a] for c in coords}) for a in axes}
    even = [a for a in axes if sizes[a] % 2 == 0]
    if not even:
        return list(range(count))
    outer = min(even, key=lambda a: sizes[a])
    inner = [a for a in axes if a != outer][0]
    lo = {a: min(c[a] for c in coords) for a in axes}
    where = {(c[outer] - lo[outer], c[inner] - lo[inner]): i for i, c in enumerate(coords)}
    order = []
    for o in range(sizes[outer]):
        steps = range(sizes[inner]) if o % 2 == 0 else reversed(range(sizes[inner]))
        for k in steps:
            order.append(where[(o, k)])
    if sorted(order) != list(range(count)):
        return list(range(count))
    return order


def ring_steps(ring):
    n = len(ring)
    pos_of = [ring.index(d) for d in range(n)]
    mypos = jnp.asarray(pos_of, jnp.int32)[lax.axis_index("dp")]
    fwd = [(ring[p], ring[(p + 1) % n]) for p in range(n)]
    bwd = [(ring[p], ring[(p - 1) % n]) for p in range(n)]
    nf = n // 2
    return n, mypos, fwd, bwd, nf, n - 1 - nf


def gather_group(pieces, ring, after=None):
    locals_ = tuple(p.astype(jnp.bfloat16) for p, _ in pieces)
    if after is not None:
        locals_, _ = lax.optimization_barrier((locals_, after))
    n, mypos, fwd, bwd, nf, nb = ring_steps(ring)
    ring_arr = jnp.asarray(ring, jnp.int32)
    parts = {0: locals_}
    a = locals_
    b = locals_
    for s in range(nf):
        a = lax.ppermute(a, "dp", fwd)
        if s < nb:
            b = lax.ppermute(b, "dp", bwd)
            a, b = lax.optimization_barrier((a, b))
            parts[s + 1] = b
        parts[-(s + 1)] = a
    out = []
    last = (a, b)
    for i, (p, axis) in enumerate(pieces):
        shape = list(p.shape)
        width = shape[axis]
        shape[axis] *= n
        full = jnp.zeros(shape, jnp.bfloat16)
        arrival = [0]
        for s in range(nf):
            arrival.append(-(s + 1))
            if s < nb:
                arrival.append(s + 1)
        for k in arrival:
            owner = ring_arr[(mypos + k) % n]
            full = lax.dynamic_update_slice_in_dim(full, parts[k][i], owner * width, axis)
        out.append(full)
    return out, last


def scatter_group(pieces, ring, carry=jnp.bfloat16, after=None):
    if after is not None:
        arrays = tuple(p[1:] if isinstance(p[0], str) else (p[0],) for p in pieces)
        arrays, _ = lax.optimization_barrier((arrays, after))
        pieces = [
            ("prod",) + tuple(a) if isinstance(p[0], str) else (a[0], p[1]) for p, a in zip(pieces, arrays)
        ]
    n, mypos, fwd, bwd, nf, nb = ring_steps(ring)
    ring_arr = jnp.asarray(ring, jnp.int32)

    def chunk(piece, owner):
        if isinstance(piece[0], str):
            _, lhs, rhs = piece
            w = lhs.shape[2] // n
            part = lax.dynamic_slice_in_dim(lhs, owner * w, w, 2)
            return jnp.einsum("xrd,xrf->xdf", part, rhs, preferred_element_type=jnp.float32)
        g, axis = piece
        w = g.shape[axis] // n
        return lax.dynamic_slice_in_dim(g, owner * w, w, axis).astype(jnp.float32)

    def own(q):
        owner = ring_arr[q % n]
        return tuple(chunk(p, owner) for p in pieces)

    carries = carry if isinstance(carry, tuple) else (carry,) * len(pieces)

    def send(vals, got, perm):
        if got is not None:
            vals = tuple(v + r.astype(jnp.float32) for v, r in zip(vals, got))
        return lax.ppermute(tuple(v.astype(c) for v, c in zip(vals, carries)), "dp", perm)

    got_f = None
    got_b = None
    for s in range(nf):
        got_f = send(own(mypos + nf - s), got_f, fwd)
        if s < nb:
            got_b = send(own(mypos - nb + s), got_b, bwd)
            got_f, got_b = lax.optimization_barrier((got_f, got_b))
    last = (got_f, got_b)
    total = own(mypos)
    total = tuple(t + r.astype(jnp.float32) for t, r in zip(total, got_f))
    if got_b is not None:
        total = tuple(t + r.astype(jnp.float32) for t, r in zip(total, got_b))
    return list(total), last


def per_device(
    tokens,
    segment_ids,
    valid_lengths,
    cotangent,
    w_query,
    w_key,
    w_value,
    w_out,
    query_gain,
    key_gain,
    attn_gain,
    w_gate,
    w_up,
    w_down,
    mlp_gain,
    ring,
):
    f32 = jnp.float32
    bf16 = jnp.bfloat16
    rows, width = tokens.shape
    seg_row = segment_ids[0]
    length = valid_lengths[0]
    block = min(512, rows)
    count = rows // block
    scale = HEAD_DIM ** (-0.5)
    n_dp = len(ring)
    slab = attn_gain.shape[0]
    head_piece = query_gain.shape[0]

    def padded(g):
        return jnp.pad(g, (0, slab - g.shape[0]))

    gains = jnp.stack([padded(query_gain), padded(key_gain), attn_gain, mlp_gain])
    (qkvo, gains_full), seen = gather_group(
        [(jnp.stack([w_query, w_key, w_value, w_out.T]), 1), (gains, 1)], ring
    )
    wq, wk, wv, wo_t = qkvo[0], qkvo[1], qkvo[2], qkvo[3]
    gq = gains_full[0].reshape(n_dp, slab)[:, :head_piece].reshape(-1)
    gk = gains_full[1].reshape(n_dp, slab)[:, :head_piece].reshape(-1)
    ga = gains_full[2]
    gm = gains_full[3]
    (gud,), seen = gather_group([(jnp.stack([w_gate, w_up, w_down.T]), 1)], ring, after=seen)
    wg, wu, wd_t = gud[0], gud[1], gud[2]
    gq32 = gq.astype(f32)
    gk32 = gk.astype(f32)
    ga32 = ga.astype(f32)
    gm32 = gm.astype(f32)
    query = jnp.dot(tokens, wq, preferred_element_type=f32)
    keys = jnp.dot(tokens, wk, preferred_element_type=f32)
    values = jnp.dot(tokens, wv, preferred_element_type=f32).astype(bf16)
    query_sq, key_sq = lax.psum(
        (jnp.sum(query * query, axis=1), jnp.sum(keys * keys, axis=1)), "mp"
    )
    query_factor = lax.rsqrt(query_sq / width + EPS)[:, None]
    key_factor = lax.rsqrt(key_sq / width + EPS)[:, None]
    query_hat = query * query_factor
    key_hat = keys * key_factor
    heads = query.shape[1] // HEAD_DIM
    cosine, sine = rope_tables(rows, HEAD_DIM)
    query_rot = rotate((query_hat * gq32).reshape(rows, heads, HEAD_DIM), cosine, sine).astype(bf16)
    key_rot = rotate((key_hat * gk32).reshape(rows, heads, HEAD_DIM), cosine, sine).astype(bf16)
    values_h = values.reshape(rows, heads, HEAD_DIM)

    def block_scores(start):
        scores = jnp.einsum("qhe,khe->hqk", query_rot, key_rot, preferred_element_type=f32) * scale
        mask = allowed_block(start, block, seg_row, length)
        return (query_rot, jnp.where(mask[None], scores, -1e30))

    def forward_block(index):
        start = index * block
        q_blk, scores = block_scores(start)
        top = jnp.max(scores, axis=-1, keepdims=True)
        total = jnp.sum(jnp.exp(scores - top), axis=-1, keepdims=True)
        logsum = top + jnp.log(total)
        probs = jnp.exp(scores - logsum).astype(bf16)
        attended = jnp.einsum("hqk,khe->qhe", probs, values_h, preferred_element_type=f32)
        return (attended, logsum[..., 0])

    attended, logsums = lax.map(forward_block, jnp.arange(count))
    attended_b = attended.reshape(rows, heads * HEAD_DIM).astype(bf16)
    attn_partial = jnp.einsum("rc,dc->rd", attended_b, wo_t, preferred_element_type=f32)
    attn_total = branch_total(attn_partial)
    attn_hat, attn_factor = norm_forward(attn_total)
    hidden = tokens.astype(f32) + attn_hat * ga32
    hidden_b = hidden.astype(bf16)
    gate = jnp.dot(hidden_b, wg, preferred_element_type=f32)
    up = jnp.dot(hidden_b, wu, preferred_element_type=f32)
    active = jax.nn.silu(gate)
    mixed_b = (active * up).astype(bf16)
    mlp_partial = jnp.einsum("rf,df->rd", mixed_b, wd_t, preferred_element_type=f32)
    mlp_total = branch_total(mlp_partial)
    mlp_hat, mlp_factor = norm_forward(mlp_total)
    layer_out = (hidden + mlp_hat * gm32).astype(bf16)
    grad_out = cotangent.astype(f32)
    d_mlp, grad_mg = norm_back(grad_out, mlp_hat, mlp_factor, gm32)
    d_mlp_b = d_mlp.astype(bf16)
    (grad_wd_t_s,), sent = scatter_group([("prod", d_mlp_b[None], mixed_b[None])], ring)
    grad_wd_s = grad_wd_t_s[0].T
    d_mixed = jnp.einsum("rd,df->rf", d_mlp_b, wd_t, preferred_element_type=f32)
    sigma = jax.nn.sigmoid(gate)
    d_gate = (d_mixed * up * sigma * (1.0 + gate * (1.0 - sigma))).astype(bf16)
    d_up = (d_mixed * active).astype(bf16)
    grad_gu = ("prod", jnp.stack([hidden_b, hidden_b]), jnp.stack([d_gate, d_up]))
    (grad_gu_s,), sent = scatter_group([grad_gu], ring)
    grad_wg_s, grad_wu_s = grad_gu_s[0], grad_gu_s[1]
    hidden_partial = jnp.einsum("rf,df->rd", d_gate, wg, preferred_element_type=f32) + jnp.einsum(
        "rf,df->rd", d_up, wu, preferred_element_type=f32
    )
    d_hidden = grad_out + input_total(hidden_partial)
    d_attn, grad_ag = norm_back(d_hidden, attn_hat, attn_factor, ga32)
    d_attn_b = d_attn.astype(bf16)
    d_attended = jnp.einsum("rd,dc->rc", d_attn_b, wo_t, preferred_element_type=f32).astype(bf16)
    d_attended = d_attended.reshape(rows, heads, HEAD_DIM)

    def backward_block(carry, index):
        key_acc, value_acc = carry
        start = index * block
        q_blk, scores = block_scores(start)
        logsum = lax.dynamic_index_in_dim(logsums, index, 0, keepdims=False)
        probs = jnp.exp(scores - logsum[..., None])
        value_acc = value_acc + jnp.einsum(
            "hqk,qhe->khe", probs.astype(bf16), d_attended, preferred_element_type=f32
        )
        d_probs = jnp.einsum("qhe,khe->hqk", d_attended, values_h, preferred_element_type=f32)
        delta = jnp.sum(probs * d_probs, axis=-1, keepdims=True)
        d_scores = (probs * (d_probs - delta)).astype(bf16)
        d_query_blk = (
            jnp.einsum("hqk,khe->qhe", d_scores, key_rot, preferred_element_type=f32) * scale
        )
        key_acc = (
            key_acc
            + jnp.einsum("hqk,qhe->khe", d_scores, q_blk, preferred_element_type=f32) * scale
        )
        return ((key_acc, value_acc), d_query_blk)

    empty = jnp.zeros((rows, heads, HEAD_DIM), f32)
    (d_key_rot, d_values), d_query_rot = lax.scan(backward_block, (empty, empty), jnp.arange(count))
    d_query_rot = d_query_rot.reshape(rows, heads, HEAD_DIM)
    d_values_b = d_values.reshape(rows, heads * HEAD_DIM).astype(bf16)
    d_query_n = rotate_back(d_query_rot, cosine, sine).reshape(rows, heads * HEAD_DIM)
    d_key_n = rotate_back(d_key_rot, cosine, sine).reshape(rows, heads * HEAD_DIM)
    grad_gq = jnp.sum(d_query_n * query_hat, axis=0)
    grad_gk = jnp.sum(d_key_n * key_hat, axis=0)
    d_query_hat = d_query_n * gq32
    d_key_hat = d_key_n * gk32
    query_inner, key_inner = lax.psum(
        (jnp.sum(d_query_hat * query_hat, axis=1), jnp.sum(d_key_hat * key_hat, axis=1)), "mp"
    )
    d_query_b = (query_factor * (d_query_hat - query_hat * (query_inner / width)[:, None])).astype(
        bf16
    )
    d_key_b = (key_factor * (d_key_hat - key_hat * (key_inner / width)[:, None])).astype(bf16)
    grad_qkvo = (
        "prod",
        jnp.stack([tokens, tokens, tokens, d_attn_b]),
        jnp.stack([d_query_b, d_key_b, d_values_b, attended_b]),
    )

    def spread(g):
        return jnp.pad(g.reshape(n_dp, -1), ((0, 0), (0, slab - g.shape[0] // n_dp))).reshape(-1)

    grad_gains = jnp.stack([spread(grad_gq), spread(grad_gk), grad_ag, grad_mg])
    (grad_qkvo_s, grad_gains_s), sent = scatter_group(
        [grad_qkvo, (grad_gains, 1)], ring, carry=(jnp.bfloat16, jnp.float32)
    )
    grad_wq_s, grad_wk_s, grad_wv_s = grad_qkvo_s[0], grad_qkvo_s[1], grad_qkvo_s[2]
    grad_wo_s = grad_qkvo_s[3].T
    grad_gq_s = grad_gains_s[0, :head_piece]
    grad_gk_s = grad_gains_s[1, :head_piece]
    grad_ag_s = grad_gains_s[2]
    grad_mg_s = grad_gains_s[3]
    input_part = jnp.einsum("rc,dc->rd", d_query_b, wq, preferred_element_type=f32)
    input_part = input_part + jnp.einsum("rc,dc->rd", d_key_b, wk, preferred_element_type=f32)
    input_part = input_part + jnp.einsum("rc,dc->rd", d_values_b, wv, preferred_element_type=f32)
    input_grad = d_hidden + input_total(input_part)
    return (
        layer_out,
        input_grad,
        grad_wq_s,
        grad_wk_s,
        grad_wv_s,
        grad_wo_s,
        grad_gq_s,
        grad_gk_s,
        grad_ag_s,
        grad_wg_s,
        grad_wu_s,
        grad_wd_s,
        grad_mg_s,
    )


def solution(mesh):
    placed = (
        P("dp", None),
        P("dp", None),
        P("dp"),
        P("dp", None),
        P("dp", "mp"),
        P("dp", "mp"),
        P("dp", "mp"),
        P("mp", "dp"),
        P(("mp", "dp")),
        P(("mp", "dp")),
        P("dp"),
        P("dp", "mp"),
        P("dp", "mp"),
        P("mp", "dp"),
        P("dp"),
    )
    ring = ring_order(mesh)
    return jax.shard_map(
        functools.partial(per_device, ring=ring),
        mesh=mesh,
        in_specs=placed,
        out_specs=(
            P("dp", None),
            P("dp", None),
            P("dp", "mp"),
            P("dp", "mp"),
            P("dp", "mp"),
            P("mp", "dp"),
            P(("mp", "dp")),
            P(("mp", "dp")),
            P("dp"),
            P("dp", "mp"),
            P("dp", "mp"),
            P("mp", "dp"),
            P("dp"),
        ),
        check_vma=False,
    )
```

```python
import functools

import jax
import jax.numpy as jnp
import numpy as np
from jax import lax
from jax.sharding import PartitionSpec as P

HEAD_DIM = 128


EPS = 1e-06
THETA = 500000.0


def rope_tables(rows, head_dim):
    half = head_dim // 2
    inverse = THETA ** (-(jnp.arange(half).astype(jnp.float32) * 2.0) / head_dim)
    angles = jnp.arange(rows).astype(jnp.float32)[:, None] * inverse[None, :]
    return (jnp.cos(angles)[:, None, :], jnp.sin(angles)[:, None, :])


def rotate(value, cosine, sine):
    half = value.shape[-1] // 2
    first, second = (value[..., :half], value[..., half:])
    return jnp.concatenate(
        [first * cosine - second * sine, second * cosine + first * sine], axis=-1
    )


def rotate_back(grad, cosine, sine):
    half = grad.shape[-1] // 2
    first, second = (grad[..., :half], grad[..., half:])
    return jnp.concatenate(
        [first * cosine + second * sine, second * cosine - first * sine], axis=-1
    )


def allowed_block(start, block, seg_row, length):
    query_pos = start + jnp.arange(block)
    key_pos = jnp.arange(seg_row.shape[0])
    same = seg_row[:, None] == seg_row[None, :]
    causal = key_pos[None, :] <= query_pos[:, None]
    inside = key_pos[None, :] < length
    return same & causal & inside | (key_pos[None, :] == query_pos[:, None])


def mp_allreduce(x, carry=jnp.bfloat16):
    m = lax.axis_size("mp")
    me = lax.axis_index("mp")
    core = me % 2
    chips = m // 2
    chip = me // 2
    half = x.shape[1] // 2
    pair = [(i, i ^ 1) for i in range(m)]
    mine = lax.dynamic_slice_in_dim(x, core * half, half, 1)
    other = lax.dynamic_slice_in_dim(x, (1 - core) * half, half, 1)
    part = mine + lax.ppermute(other, "mp", pair)
    if chips == 2:
        low = part.astype(carry)
        got = lax.ppermute(low, "mp", [(i, i ^ 2) for i in range(m)])
        part = low.astype(jnp.float32) + got.astype(jnp.float32)
    elif chips > 2:
        low = part.astype(carry)
        got = [low]
        for k in range(1, chips):
            perm = [(c * 2 + r, ((c + k) % chips) * 2 + r) for c in range(chips) for r in range(2)]
            got.append(lax.ppermute(low, "mp", perm))
        stack = jnp.stack(got)
        order = (chip - jnp.arange(chips)) % chips
        ordered = jnp.take(stack, order, axis=0).astype(jnp.float32)
        part = ordered[0]
        for k in range(1, chips):
            part = part + ordered[k]
    swapped = lax.ppermute(part, "mp", pair)
    first = jnp.where(core == 0, part, swapped)
    second = jnp.where(core == 0, swapped, part)
    return jnp.concatenate([first, second], axis=1)


def small_psum(parts):
    stacked = jnp.stack(parts)
    m = lax.axis_size("mp")
    if m != 4:
        total = lax.psum(stacked, "mp")
    else:
        total = stacked + lax.ppermute(stacked, "mp", [(i, i ^ 1) for i in range(m)])
        total = total + lax.ppermute(total, "mp", [(i, i ^ 2) for i in range(m)])
    return tuple(total[i] for i in range(len(parts)))


def branch_total(partial_sum):
    return mp_allreduce(partial_sum)


def input_total(partial_sum):
    return mp_allreduce(partial_sum)


def norm_forward(total):
    factor = lax.rsqrt(jnp.mean(total * total, axis=1, keepdims=True) + EPS)
    return (total * factor, factor)


def norm_back(grad, normed, factor, gain):
    grad_gain = jnp.sum(grad * normed, axis=0)
    scaled = grad * gain
    inner = jnp.mean(scaled * normed, axis=1, keepdims=True)
    return (factor * (scaled - normed * inner), grad_gain)


def ring_order(mesh):
    column = [mesh.devices[i, 0] for i in range(mesh.devices.shape[0])]
    count = len(column)
    try:
        coords = [tuple(d.coords) for d in column]
    except AttributeError:
        return list(range(count))
    axes = [a for a in range(len(coords[0])) if len({c[a] for c in coords}) > 1]
    if len(axes) != 2:
        return list(range(count))
    sizes = {a: len({c[a] for c in coords}) for a in axes}
    even = [a for a in axes if sizes[a] % 2 == 0]
    if not even:
        return list(range(count))
    outer = min(even, key=lambda a: sizes[a])
    inner = [a for a in axes if a != outer][0]
    lo = {a: min(c[a] for c in coords) for a in axes}
    where = {(c[outer] - lo[outer], c[inner] - lo[inner]): i for i, c in enumerate(coords)}
    order = []
    for o in range(sizes[outer]):
        steps = range(sizes[inner]) if o % 2 == 0 else reversed(range(sizes[inner]))
        for k in steps:
            order.append(where[(o, k)])
    if sorted(order) != list(range(count)):
        return list(range(count))
    return order


def ring_steps(ring):
    n = len(ring)
    pos_of = [ring.index(d) for d in range(n)]
    mypos = jnp.asarray(pos_of, jnp.int32)[lax.axis_index("dp")]
    fwd = [(ring[p], ring[(p + 1) % n]) for p in range(n)]
    bwd = [(ring[p], ring[(p - 1) % n]) for p in range(n)]
    nf = n // 2
    return n, mypos, fwd, bwd, nf, n - 1 - nf


def gather_group(pieces, ring, after=None):
    locals_ = tuple(p.astype(jnp.bfloat16) for p, _ in pieces)
    if after is not None:
        locals_, _ = lax.optimization_barrier((locals_, after))
    n, mypos, fwd, bwd, nf, nb = ring_steps(ring)
    ring_arr = jnp.asarray(ring, jnp.int32)
    parts = {0: locals_}
    a = locals_
    b = locals_
    for s in range(nf):
        a = lax.ppermute(a, "dp", fwd)
        if s < nb:
            b = lax.ppermute(b, "dp", bwd)
            a, b = lax.optimization_barrier((a, b))
            parts[s + 1] = b
        parts[-(s + 1)] = a
    out = []
    last = (a, b)
    for i, (p, axis) in enumerate(pieces):
        shape = list(p.shape)
        width = shape[axis]
        shape[axis] *= n
        full = jnp.zeros(shape, jnp.bfloat16)
        arrival = [0]
        for s in range(nf):
            arrival.append(-(s + 1))
            if s < nb:
                arrival.append(s + 1)
        for k in arrival:
            owner = ring_arr[(mypos + k) % n]
            full = lax.dynamic_update_slice_in_dim(full, parts[k][i], owner * width, axis)
        out.append(full)
    return out, last


def scatter_group(pieces, ring, carry=jnp.bfloat16, after=None):
    if after is not None:
        arrays = tuple(p[1:] if isinstance(p[0], str) else (p[0],) for p in pieces)
        arrays, _ = lax.optimization_barrier((arrays, after))
        pieces = [
            ("prod",) + tuple(a) if isinstance(p[0], str) else (a[0], p[1]) for p, a in zip(pieces, arrays)
        ]
    n, mypos, fwd, bwd, nf, nb = ring_steps(ring)
    ring_arr = jnp.asarray(ring, jnp.int32)

    def chunk(piece, owner):
        if isinstance(piece[0], str):
            _, lhs, rhs = piece
            w = lhs.shape[2] // n
            part = lax.dynamic_slice_in_dim(lhs, owner * w, w, 2)
            return jnp.einsum("xrd,xrf->xdf", part, rhs, preferred_element_type=jnp.float32)
        g, axis = piece
        w = g.shape[axis] // n
        return lax.dynamic_slice_in_dim(g, owner * w, w, axis).astype(jnp.float32)

    def own(q):
        owner = ring_arr[q % n]
        return tuple(chunk(p, owner) for p in pieces)

    carries = carry if isinstance(carry, tuple) else (carry,) * len(pieces)

    def send(vals, got, perm):
        if got is not None:
            vals = tuple(v + r.astype(jnp.float32) for v, r in zip(vals, got))
        return lax.ppermute(tuple(v.astype(c) for v, c in zip(vals, carries)), "dp", perm)

    got_f = None
    got_b = None
    for s in range(nf):
        got_f = send(own(mypos + nf - s), got_f, fwd)
        if s < nb:
            got_b = send(own(mypos - nb + s), got_b, bwd)
            got_f, got_b = lax.optimization_barrier((got_f, got_b))
    last = (got_f, got_b)
    total = own(mypos)
    total = tuple(t + r.astype(jnp.float32) for t, r in zip(total, got_f))
    if got_b is not None:
        total = tuple(t + r.astype(jnp.float32) for t, r in zip(total, got_b))
    return list(total), last


def per_device(
    tokens,
    segment_ids,
    valid_lengths,
    cotangent,
    w_query,
    w_key,
    w_value,
    w_out,
    query_gain,
    key_gain,
    attn_gain,
    w_gate,
    w_up,
    w_down,
    mlp_gain,
    ring,
):
    f32 = jnp.float32
    bf16 = jnp.bfloat16
    rows, width = tokens.shape
    seg_row = segment_ids[0]
    length = valid_lengths[0]
    block = min(512, rows)
    count = rows // block
    scale = HEAD_DIM ** (-0.5)
    n_dp = len(ring)
    slab = attn_gain.shape[0]
    head_piece = query_gain.shape[0]

    def padded(g):
        return jnp.pad(g, (0, slab - g.shape[0]))

    gains = jnp.stack([padded(query_gain), padded(key_gain), attn_gain, mlp_gain])
    (qkvo, gains_full), seen = gather_group(
        [(jnp.stack([w_query, w_key, w_value, w_out.T]), 1), (gains, 1)], ring
    )
    wq, wk, wv, wo_t = qkvo[0], qkvo[1], qkvo[2], qkvo[3]
    gq = gains_full[0].reshape(n_dp, slab)[:, :head_piece].reshape(-1)
    gk = gains_full[1].reshape(n_dp, slab)[:, :head_piece].reshape(-1)
    ga = gains_full[2]
    gm = gains_full[3]
    (gud,), seen = gather_group([(jnp.stack([w_gate, w_up, w_down.T]), 1)], ring, after=seen)
    wg, wu, wd_t = gud[0], gud[1], gud[2]
    gq32 = gq.astype(f32)
    gk32 = gk.astype(f32)
    ga32 = ga.astype(f32)
    gm32 = gm.astype(f32)
    query = jnp.dot(tokens, wq, preferred_element_type=f32)
    keys = jnp.dot(tokens, wk, preferred_element_type=f32)
    values = jnp.dot(tokens, wv, preferred_element_type=f32).astype(bf16)
    query_sq, key_sq = small_psum((jnp.sum(query * query, axis=1), jnp.sum(keys * keys, axis=1)))
    query_factor = lax.rsqrt(query_sq / width + EPS)[:, None]
    key_factor = lax.rsqrt(key_sq / width + EPS)[:, None]
    query_hat = query * query_factor
    key_hat = keys * key_factor
    heads = query.shape[1] // HEAD_DIM
    cosine, sine = rope_tables(rows, HEAD_DIM)
    query_rot = rotate((query_hat * gq32).reshape(rows, heads, HEAD_DIM), cosine, sine).astype(bf16)
    key_rot = rotate((key_hat * gk32).reshape(rows, heads, HEAD_DIM), cosine, sine).astype(bf16)
    values_h = values.reshape(rows, heads, HEAD_DIM)

    def block_scores(start):
        scores = jnp.einsum("qhe,khe->hqk", query_rot, key_rot, preferred_element_type=f32) * scale
        mask = allowed_block(start, block, seg_row, length)
        return (query_rot, jnp.where(mask[None], scores, -1e30))

    def forward_block(index):
        start = index * block
        q_blk, scores = block_scores(start)
        top = jnp.max(scores, axis=-1, keepdims=True)
        total = jnp.sum(jnp.exp(scores - top), axis=-1, keepdims=True)
        logsum = top + jnp.log(total)
        probs = jnp.exp(scores - logsum).astype(bf16)
        attended = jnp.einsum("hqk,khe->qhe", probs, values_h, preferred_element_type=f32)
        return (attended, logsum[..., 0])

    attended, logsums = lax.map(forward_block, jnp.arange(count))
    attended_b = attended.reshape(rows, heads * HEAD_DIM).astype(bf16)
    attn_partial = jnp.einsum("rc,dc->rd", attended_b, wo_t, preferred_element_type=f32)
    attn_total = branch_total(attn_partial)
    attn_hat, attn_factor = norm_forward(attn_total)
    hidden = tokens.astype(f32) + attn_hat * ga32
    hidden_b = hidden.astype(bf16)
    gate = jnp.dot(hidden_b, wg, preferred_element_type=f32)
    up = jnp.dot(hidden_b, wu, preferred_element_type=f32)
    active = jax.nn.silu(gate)
    mixed_b = (active * up).astype(bf16)
    mlp_partial = jnp.einsum("rf,df->rd", mixed_b, wd_t, preferred_element_type=f32)
    mlp_total = branch_total(mlp_partial)
    mlp_hat, mlp_factor = norm_forward(mlp_total)
    layer_out = (hidden + mlp_hat * gm32).astype(bf16)
    grad_out = cotangent.astype(f32)
    d_mlp, grad_mg = norm_back(grad_out, mlp_hat, mlp_factor, gm32)
    d_mlp_b = d_mlp.astype(bf16)
    (grad_wd_t_s,), sent = scatter_group([("prod", d_mlp_b[None], mixed_b[None])], ring)
    grad_wd_s = grad_wd_t_s[0].T
    d_mixed = jnp.einsum("rd,df->rf", d_mlp_b, wd_t, preferred_element_type=f32)
    sigma = jax.nn.sigmoid(gate)
    d_gate = (d_mixed * up * sigma * (1.0 + gate * (1.0 - sigma))).astype(bf16)
    d_up = (d_mixed * active).astype(bf16)
    grad_gu = ("prod", jnp.stack([hidden_b, hidden_b]), jnp.stack([d_gate, d_up]))
    (grad_gu_s,), sent = scatter_group([grad_gu], ring, after=sent)
    grad_wg_s, grad_wu_s = grad_gu_s[0], grad_gu_s[1]
    hidden_partial = jnp.einsum("rf,df->rd", d_gate, wg, preferred_element_type=f32) + jnp.einsum(
        "rf,df->rd", d_up, wu, preferred_element_type=f32
    )
    d_hidden = grad_out + input_total(hidden_partial)
    d_attn, grad_ag = norm_back(d_hidden, attn_hat, attn_factor, ga32)
    d_attn_b = d_attn.astype(bf16)
    d_attended = jnp.einsum("rd,dc->rc", d_attn_b, wo_t, preferred_element_type=f32).astype(bf16)
    d_attended = d_attended.reshape(rows, heads, HEAD_DIM)

    def backward_block(carry, index):
        key_acc, value_acc = carry
        start = index * block
        q_blk, scores = block_scores(start)
        logsum = lax.dynamic_index_in_dim(logsums, index, 0, keepdims=False)
        probs = jnp.exp(scores - logsum[..., None])
        value_acc = value_acc + jnp.einsum(
            "hqk,qhe->khe", probs.astype(bf16), d_attended, preferred_element_type=f32
        )
        d_probs = jnp.einsum("qhe,khe->hqk", d_attended, values_h, preferred_element_type=f32)
        delta = jnp.sum(probs * d_probs, axis=-1, keepdims=True)
        d_scores = (probs * (d_probs - delta)).astype(bf16)
        d_query_blk = (
            jnp.einsum("hqk,khe->qhe", d_scores, key_rot, preferred_element_type=f32) * scale
        )
        key_acc = (
            key_acc
            + jnp.einsum("hqk,qhe->khe", d_scores, q_blk, preferred_element_type=f32) * scale
        )
        return ((key_acc, value_acc), d_query_blk)

    empty = jnp.zeros((rows, heads, HEAD_DIM), f32)
    (d_key_rot, d_values), d_query_rot = lax.scan(backward_block, (empty, empty), jnp.arange(count))
    d_query_rot = d_query_rot.reshape(rows, heads, HEAD_DIM)
    d_values_b = d_values.reshape(rows, heads * HEAD_DIM).astype(bf16)
    d_query_n = rotate_back(d_query_rot, cosine, sine).reshape(rows, heads * HEAD_DIM)
    d_key_n = rotate_back(d_key_rot, cosine, sine).reshape(rows, heads * HEAD_DIM)
    grad_gq = jnp.sum(d_query_n * query_hat, axis=0)
    grad_gk = jnp.sum(d_key_n * key_hat, axis=0)
    d_query_hat = d_query_n * gq32
    d_key_hat = d_key_n * gk32
    query_inner, key_inner = small_psum(
        (jnp.sum(d_query_hat * query_hat, axis=1), jnp.sum(d_key_hat * key_hat, axis=1))
    )
    d_query_b = (query_factor * (d_query_hat - query_hat * (query_inner / width)[:, None])).astype(
        bf16
    )
    d_key_b = (key_factor * (d_key_hat - key_hat * (key_inner / width)[:, None])).astype(bf16)
    grad_qkvo = (
        "prod",
        jnp.stack([tokens, tokens, tokens, d_attn_b]),
        jnp.stack([d_query_b, d_key_b, d_values_b, attended_b]),
    )

    def spread(g):
        return jnp.pad(g.reshape(n_dp, -1), ((0, 0), (0, slab - g.shape[0] // n_dp))).reshape(-1)

    grad_gains = jnp.stack([spread(grad_gq), spread(grad_gk), grad_ag, grad_mg])
    (grad_qkvo_s, grad_gains_s), sent = scatter_group(
        [grad_qkvo, (grad_gains, 1)], ring, carry=(jnp.bfloat16, jnp.float32), after=sent
    )
    grad_wq_s, grad_wk_s, grad_wv_s = grad_qkvo_s[0], grad_qkvo_s[1], grad_qkvo_s[2]
    grad_wo_s = grad_qkvo_s[3].T
    grad_gq_s = grad_gains_s[0, :head_piece]
    grad_gk_s = grad_gains_s[1, :head_piece]
    grad_ag_s = grad_gains_s[2]
    grad_mg_s = grad_gains_s[3]
    input_part = jnp.einsum("rc,dc->rd", d_query_b, wq, preferred_element_type=f32)
    input_part = input_part + jnp.einsum("rc,dc->rd", d_key_b, wk, preferred_element_type=f32)
    input_part = input_part + jnp.einsum("rc,dc->rd", d_values_b, wv, preferred_element_type=f32)
    input_grad = d_hidden + input_total(input_part)
    return (
        layer_out,
        input_grad,
        grad_wq_s,
        grad_wk_s,
        grad_wv_s,
        grad_wo_s,
        grad_gq_s,
        grad_gk_s,
        grad_ag_s,
        grad_wg_s,
        grad_wu_s,
        grad_wd_s,
        grad_mg_s,
    )


def solution(mesh):
    placed = (
        P("dp", None),
        P("dp", None),
        P("dp"),
        P("dp", None),
        P("dp", "mp"),
        P("dp", "mp"),
        P("dp", "mp"),
        P("mp", "dp"),
        P(("mp", "dp")),
        P(("mp", "dp")),
        P("dp"),
        P("dp", "mp"),
        P("dp", "mp"),
        P("mp", "dp"),
        P("dp"),
    )
    ring = ring_order(mesh)
    return jax.shard_map(
        functools.partial(per_device, ring=ring),
        mesh=mesh,
        in_specs=placed,
        out_specs=(
            P("dp", None),
            P("dp", None),
            P("dp", "mp"),
            P("dp", "mp"),
            P("dp", "mp"),
            P("mp", "dp"),
            P(("mp", "dp")),
            P(("mp", "dp")),
            P("dp"),
            P("dp", "mp"),
            P("dp", "mp"),
            P("mp", "dp"),
            P("dp"),
        ),
        check_vma=False,
    )
```

```python
import functools

import jax
import jax.numpy as jnp
import numpy as np
from jax import lax
from jax.sharding import PartitionSpec as P

HEAD_DIM = 128


EPS = 1e-06
THETA = 500000.0


def rope_tables(rows, head_dim):
    half = head_dim // 2
    inverse = THETA ** (-(jnp.arange(half).astype(jnp.float32) * 2.0) / head_dim)
    angles = jnp.arange(rows).astype(jnp.float32)[:, None] * inverse[None, :]
    return (jnp.cos(angles)[:, None, :], jnp.sin(angles)[:, None, :])


def rotate(value, cosine, sine):
    half = value.shape[-1] // 2
    first, second = (value[..., :half], value[..., half:])
    return jnp.concatenate(
        [first * cosine - second * sine, second * cosine + first * sine], axis=-1
    )


def rotate_back(grad, cosine, sine):
    half = grad.shape[-1] // 2
    first, second = (grad[..., :half], grad[..., half:])
    return jnp.concatenate(
        [first * cosine + second * sine, second * cosine - first * sine], axis=-1
    )


def allowed_block(start, block, seg_row, length):
    query_pos = start + jnp.arange(block)
    key_pos = jnp.arange(seg_row.shape[0])
    same = seg_row[:, None] == seg_row[None, :]
    causal = key_pos[None, :] <= query_pos[:, None]
    inside = key_pos[None, :] < length
    return same & causal & inside | (key_pos[None, :] == query_pos[:, None])


def mp_allreduce(x, carry=jnp.bfloat16):
    m = lax.axis_size("mp")
    me = lax.axis_index("mp")
    core = me % 2
    chips = m // 2
    chip = me // 2
    half = x.shape[1] // 2
    pair = [(i, i ^ 1) for i in range(m)]
    mine = lax.dynamic_slice_in_dim(x, core * half, half, 1)
    other = lax.dynamic_slice_in_dim(x, (1 - core) * half, half, 1)
    part = mine + lax.ppermute(other, "mp", pair)
    if chips == 2:
        low = part.astype(carry)
        got = lax.ppermute(low, "mp", [(i, i ^ 2) for i in range(m)])
        part = low.astype(jnp.float32) + got.astype(jnp.float32)
    elif chips > 2:
        low = part.astype(carry)
        got = [low]
        for k in range(1, chips):
            perm = [(c * 2 + r, ((c + k) % chips) * 2 + r) for c in range(chips) for r in range(2)]
            got.append(lax.ppermute(low, "mp", perm))
        stack = jnp.stack(got)
        order = (chip - jnp.arange(chips)) % chips
        ordered = jnp.take(stack, order, axis=0).astype(jnp.float32)
        part = ordered[0]
        for k in range(1, chips):
            part = part + ordered[k]
    swapped = lax.ppermute(part, "mp", pair)
    first = jnp.where(core == 0, part, swapped)
    second = jnp.where(core == 0, swapped, part)
    return jnp.concatenate([first, second], axis=1)


def branch_total(partial_sum):
    return mp_allreduce(partial_sum)


def input_total(partial_sum):
    return mp_allreduce(partial_sum)


def norm_forward(total):
    factor = lax.rsqrt(jnp.mean(total * total, axis=1, keepdims=True) + EPS)
    return (total * factor, factor)


def norm_back(grad, normed, factor, gain):
    grad_gain = jnp.sum(grad * normed, axis=0)
    scaled = grad * gain
    inner = jnp.mean(scaled * normed, axis=1, keepdims=True)
    return (factor * (scaled - normed * inner), grad_gain)


def ring_order(mesh):
    column = [mesh.devices[i, 0] for i in range(mesh.devices.shape[0])]
    count = len(column)
    try:
        coords = [tuple(d.coords) for d in column]
    except AttributeError:
        return list(range(count))
    axes = [a for a in range(len(coords[0])) if len({c[a] for c in coords}) > 1]
    if len(axes) != 2:
        return list(range(count))
    sizes = {a: len({c[a] for c in coords}) for a in axes}
    even = [a for a in axes if sizes[a] % 2 == 0]
    if not even:
        return list(range(count))
    outer = min(even, key=lambda a: sizes[a])
    inner = [a for a in axes if a != outer][0]
    lo = {a: min(c[a] for c in coords) for a in axes}
    where = {(c[outer] - lo[outer], c[inner] - lo[inner]): i for i, c in enumerate(coords)}
    order = []
    for o in range(sizes[outer]):
        steps = range(sizes[inner]) if o % 2 == 0 else reversed(range(sizes[inner]))
        for k in steps:
            order.append(where[(o, k)])
    if sorted(order) != list(range(count)):
        return list(range(count))
    return order


def ring_steps(ring):
    n = len(ring)
    pos_of = [ring.index(d) for d in range(n)]
    mypos = jnp.asarray(pos_of, jnp.int32)[lax.axis_index("dp")]
    fwd = [(ring[p], ring[(p + 1) % n]) for p in range(n)]
    bwd = [(ring[p], ring[(p - 1) % n]) for p in range(n)]
    nf = n // 2
    return n, mypos, fwd, bwd, nf, n - 1 - nf


def split_axis(ndim, axis):
    return ndim - 1 if axis != ndim - 1 else 0


def halves(values, axes, which):
    out = []
    for x, ax in zip(values, axes):
        h = x.shape[ax] // 2
        out.append(lax.slice_in_dim(x, which * h, (which + 1) * h, axis=ax))
    return tuple(out)


def joined(first, second, axes):
    return tuple(jnp.concatenate([x, y], axis=ax) for x, y, ax in zip(first, second, axes))


def gather_group(pieces, ring, after=None):
    locals_ = tuple(p.astype(jnp.bfloat16) for p, _ in pieces)
    if after is not None:
        locals_, _ = lax.optimization_barrier((locals_, after))
    n, mypos, fwd, bwd, nf, nb = ring_steps(ring)
    ring_arr = jnp.asarray(ring, jnp.int32)
    axes = [split_axis(p.ndim, axis) for p, axis in pieces]
    parts = {0: locals_}
    a = locals_
    b = locals_
    if n % 2 == 0:
        for s in range(nf - 1):
            a = lax.ppermute(a, "dp", fwd)
            b = lax.ppermute(b, "dp", bwd)
            a, b = lax.optimization_barrier((a, b))
            parts[-(s + 1)] = a
            parts[s + 1] = b
        ha = lax.ppermute(halves(a, axes, 0), "dp", fwd)
        hb = lax.ppermute(halves(b, axes, 1), "dp", bwd)
        ha, hb = lax.optimization_barrier((ha, hb))
        parts[-nf] = (ha, hb)
        last = (ha, hb)
        arrival = [0]
        for s in range(nf - 1):
            arrival += [-(s + 1), s + 1]
        arrival.append(-nf)
    else:
        for s in range(nf):
            a = lax.ppermute(a, "dp", fwd)
            if s < nb:
                b = lax.ppermute(b, "dp", bwd)
                a, b = lax.optimization_barrier((a, b))
                parts[s + 1] = b
            parts[-(s + 1)] = a
        last = (a, b)
        arrival = [0]
        for s in range(nf):
            arrival.append(-(s + 1))
            if s < nb:
                arrival.append(s + 1)
    out = []
    for i, (p, axis) in enumerate(pieces):
        shape = list(p.shape)
        width = shape[axis]
        shape[axis] *= n
        full = jnp.zeros(shape, jnp.bfloat16)
        for k in arrival:
            owner = ring_arr[(mypos + k) % n]
            if n % 2 == 0 and k == -nf:
                first, second = parts[k][0][i], parts[k][1][i]
                start = [0] * p.ndim
                start[axis] = owner * width
                full = lax.dynamic_update_slice(full, first, start)
                start[axes[i]] = first.shape[axes[i]]
                full = lax.dynamic_update_slice(full, second, start)
            else:
                full = lax.dynamic_update_slice_in_dim(full, parts[k][i], owner * width, axis)
        out.append(full)
    return out, last


def scatter_group(pieces, ring, carry=jnp.bfloat16, after=None):
    if after is not None:
        arrays = tuple(p[1:] if isinstance(p[0], str) else (p[0],) for p in pieces)
        arrays, _ = lax.optimization_barrier((arrays, after))
        pieces = [
            ("prod",) + tuple(a) if isinstance(p[0], str) else (a[0], p[1]) for p, a in zip(pieces, arrays)
        ]
    n, mypos, fwd, bwd, nf, nb = ring_steps(ring)
    ring_arr = jnp.asarray(ring, jnp.int32)

    def chunk(piece, owner):
        if isinstance(piece[0], str):
            _, lhs, rhs = piece
            w = lhs.shape[2] // n
            part = lax.dynamic_slice_in_dim(lhs, owner * w, w, 2)
            return jnp.einsum("xrd,xrf->xdf", part, rhs, preferred_element_type=jnp.float32)
        g, axis = piece
        w = g.shape[axis] // n
        return lax.dynamic_slice_in_dim(g, owner * w, w, axis).astype(jnp.float32)

    def own(q):
        owner = ring_arr[q % n]
        return tuple(chunk(p, owner) for p in pieces)

    axes = [2 if isinstance(p[0], str) else split_axis(p[0].ndim, p[1]) for p in pieces]
    carries = carry if isinstance(carry, tuple) else (carry,) * len(pieces)

    def cast(vals):
        return tuple(v.astype(c) for v, c in zip(vals, carries))

    def wide(vals):
        return tuple(v.astype(jnp.float32) for v in vals)

    def plus(x, y):
        return tuple(u + v for u, v in zip(x, y))

    if n % 2 == 0:
        opposite = own(mypos + nf)
        got_f = lax.ppermute(cast(halves(opposite, axes, 0)), "dp", fwd)
        got_b = lax.ppermute(cast(halves(opposite, axes, 1)), "dp", bwd)
        got_f, got_b = lax.optimization_barrier((got_f, got_b))
        for s in range(1, nf):
            vf = own(mypos + nf - s)
            vb = own(mypos - nf + s)
            if s == 1:
                vf = joined(plus(halves(vf, axes, 0), wide(got_f)), halves(vf, axes, 1), axes)
                vb = joined(halves(vb, axes, 0), plus(halves(vb, axes, 1), wide(got_b)), axes)
            else:
                vf = plus(vf, wide(got_f))
                vb = plus(vb, wide(got_b))
            got_f = lax.ppermute(cast(vf), "dp", fwd)
            got_b = lax.ppermute(cast(vb), "dp", bwd)
            got_f, got_b = lax.optimization_barrier((got_f, got_b))
        last = (got_f, got_b)
        total = own(mypos)
        if nf == 1:
            total = plus(total, joined(wide(got_f), wide(got_b), axes))
        else:
            total = plus(plus(total, wide(got_f)), wide(got_b))
        return list(total), last

    def send(vals, got, perm):
        if got is not None:
            vals = plus(vals, wide(got))
        return lax.ppermute(cast(vals), "dp", perm)

    got_f = None
    got_b = None
    for s in range(nf):
        got_f = send(own(mypos + nf - s), got_f, fwd)
        if s < nb:
            got_b = send(own(mypos - nb + s), got_b, bwd)
            got_f, got_b = lax.optimization_barrier((got_f, got_b))
    last = (got_f, got_b)
    total = own(mypos)
    total = plus(total, wide(got_f))
    if got_b is not None:
        total = plus(total, wide(got_b))
    return list(total), last


def per_device(
    tokens,
    segment_ids,
    valid_lengths,
    cotangent,
    w_query,
    w_key,
    w_value,
    w_out,
    query_gain,
    key_gain,
    attn_gain,
    w_gate,
    w_up,
    w_down,
    mlp_gain,
    ring,
):
    f32 = jnp.float32
    bf16 = jnp.bfloat16
    rows, width = tokens.shape
    seg_row = segment_ids[0]
    length = valid_lengths[0]
    block = min(512, rows)
    count = rows // block
    scale = HEAD_DIM ** (-0.5)
    n_dp = len(ring)
    slab = attn_gain.shape[0]
    head_piece = query_gain.shape[0]

    def padded(g):
        return jnp.pad(g, (0, slab - g.shape[0]))

    gains = jnp.stack([padded(query_gain), padded(key_gain), attn_gain, mlp_gain])
    (qkvo, gains_full), seen = gather_group(
        [(jnp.stack([w_query, w_key, w_value, w_out.T]), 1), (gains, 1)], ring
    )
    wq, wk, wv, wo_t = qkvo[0], qkvo[1], qkvo[2], qkvo[3]
    gq = gains_full[0].reshape(n_dp, slab)[:, :head_piece].reshape(-1)
    gk = gains_full[1].reshape(n_dp, slab)[:, :head_piece].reshape(-1)
    ga = gains_full[2]
    gm = gains_full[3]
    (gud,), seen = gather_group([(jnp.stack([w_gate, w_up, w_down.T]), 1)], ring, after=seen)
    wg, wu, wd_t = gud[0], gud[1], gud[2]
    gq32 = gq.astype(f32)
    gk32 = gk.astype(f32)
    ga32 = ga.astype(f32)
    gm32 = gm.astype(f32)
    query = jnp.dot(tokens, wq, preferred_element_type=f32)
    keys = jnp.dot(tokens, wk, preferred_element_type=f32)
    values = jnp.dot(tokens, wv, preferred_element_type=f32).astype(bf16)
    query_sq, key_sq = lax.psum(
        (jnp.sum(query * query, axis=1), jnp.sum(keys * keys, axis=1)), "mp"
    )
    query_factor = lax.rsqrt(query_sq / width + EPS)[:, None]
    key_factor = lax.rsqrt(key_sq / width + EPS)[:, None]
    query_hat = query * query_factor
    key_hat = keys * key_factor
    heads = query.shape[1] // HEAD_DIM
    cosine, sine = rope_tables(rows, HEAD_DIM)
    query_rot = rotate((query_hat * gq32).reshape(rows, heads, HEAD_DIM), cosine, sine).astype(bf16)
    key_rot = rotate((key_hat * gk32).reshape(rows, heads, HEAD_DIM), cosine, sine).astype(bf16)
    values_h = values.reshape(rows, heads, HEAD_DIM)

    def block_scores(start):
        scores = jnp.einsum("qhe,khe->hqk", query_rot, key_rot, preferred_element_type=f32) * scale
        mask = allowed_block(start, block, seg_row, length)
        return (query_rot, jnp.where(mask[None], scores, -1e30))

    def forward_block(index):
        start = index * block
        q_blk, scores = block_scores(start)
        top = jnp.max(scores, axis=-1, keepdims=True)
        total = jnp.sum(jnp.exp(scores - top), axis=-1, keepdims=True)
        logsum = top + jnp.log(total)
        probs = jnp.exp(scores - logsum).astype(bf16)
        attended = jnp.einsum("hqk,khe->qhe", probs, values_h, preferred_element_type=f32)
        return (attended, logsum[..., 0])

    attended, logsums = lax.map(forward_block, jnp.arange(count))
    attended_b = attended.reshape(rows, heads * HEAD_DIM).astype(bf16)
    attn_partial = jnp.einsum("rc,dc->rd", attended_b, wo_t, preferred_element_type=f32)
    attn_total = branch_total(attn_partial)
    attn_hat, attn_factor = norm_forward(attn_total)
    hidden = tokens.astype(f32) + attn_hat * ga32
    hidden_b = hidden.astype(bf16)
    gate = jnp.dot(hidden_b, wg, preferred_element_type=f32)
    up = jnp.dot(hidden_b, wu, preferred_element_type=f32)
    active = jax.nn.silu(gate)
    mixed_b = (active * up).astype(bf16)
    mlp_partial = jnp.einsum("rf,df->rd", mixed_b, wd_t, preferred_element_type=f32)
    mlp_total = branch_total(mlp_partial)
    mlp_hat, mlp_factor = norm_forward(mlp_total)
    layer_out = (hidden + mlp_hat * gm32).astype(bf16)
    grad_out = cotangent.astype(f32)
    d_mlp, grad_mg = norm_back(grad_out, mlp_hat, mlp_factor, gm32)
    d_mlp_b = d_mlp.astype(bf16)
    (grad_wd_t_s,), sent = scatter_group([("prod", d_mlp_b[None], mixed_b[None])], ring)
    grad_wd_s = grad_wd_t_s[0].T
    d_mixed = jnp.einsum("rd,df->rf", d_mlp_b, wd_t, preferred_element_type=f32)
    sigma = jax.nn.sigmoid(gate)
    d_gate = (d_mixed * up * sigma * (1.0 + gate * (1.0 - sigma))).astype(bf16)
    d_up = (d_mixed * active).astype(bf16)
    grad_gu = ("prod", jnp.stack([hidden_b, hidden_b]), jnp.stack([d_gate, d_up]))
    (grad_gu_s,), sent = scatter_group([grad_gu], ring, after=sent)
    grad_wg_s, grad_wu_s = grad_gu_s[0], grad_gu_s[1]
    hidden_partial = jnp.einsum("rf,df->rd", d_gate, wg, preferred_element_type=f32) + jnp.einsum(
        "rf,df->rd", d_up, wu, preferred_element_type=f32
    )
    d_hidden = grad_out + input_total(hidden_partial)
    d_attn, grad_ag = norm_back(d_hidden, attn_hat, attn_factor, ga32)
    d_attn_b = d_attn.astype(bf16)
    d_attended = jnp.einsum("rd,dc->rc", d_attn_b, wo_t, preferred_element_type=f32).astype(bf16)
    d_attended = d_attended.reshape(rows, heads, HEAD_DIM)

    def backward_block(carry, index):
        key_acc, value_acc = carry
        start = index * block
        q_blk, scores = block_scores(start)
        logsum = lax.dynamic_index_in_dim(logsums, index, 0, keepdims=False)
        probs = jnp.exp(scores - logsum[..., None])
        value_acc = value_acc + jnp.einsum(
            "hqk,qhe->khe", probs.astype(bf16), d_attended, preferred_element_type=f32
        )
        d_probs = jnp.einsum("qhe,khe->hqk", d_attended, values_h, preferred_element_type=f32)
        delta = jnp.sum(probs * d_probs, axis=-1, keepdims=True)
        d_scores = (probs * (d_probs - delta)).astype(bf16)
        d_query_blk = (
            jnp.einsum("hqk,khe->qhe", d_scores, key_rot, preferred_element_type=f32) * scale
        )
        key_acc = (
            key_acc
            + jnp.einsum("hqk,qhe->khe", d_scores, q_blk, preferred_element_type=f32) * scale
        )
        return ((key_acc, value_acc), d_query_blk)

    empty = jnp.zeros((rows, heads, HEAD_DIM), f32)
    (d_key_rot, d_values), d_query_rot = lax.scan(backward_block, (empty, empty), jnp.arange(count))
    d_query_rot = d_query_rot.reshape(rows, heads, HEAD_DIM)
    d_values_b = d_values.reshape(rows, heads * HEAD_DIM).astype(bf16)
    d_query_n = rotate_back(d_query_rot, cosine, sine).reshape(rows, heads * HEAD_DIM)
    d_key_n = rotate_back(d_key_rot, cosine, sine).reshape(rows, heads * HEAD_DIM)
    grad_gq = jnp.sum(d_query_n * query_hat, axis=0)
    grad_gk = jnp.sum(d_key_n * key_hat, axis=0)
    d_query_hat = d_query_n * gq32
    d_key_hat = d_key_n * gk32
    query_inner, key_inner = lax.psum(
        (jnp.sum(d_query_hat * query_hat, axis=1), jnp.sum(d_key_hat * key_hat, axis=1)), "mp"
    )
    d_query_b = (query_factor * (d_query_hat - query_hat * (query_inner / width)[:, None])).astype(
        bf16
    )
    d_key_b = (key_factor * (d_key_hat - key_hat * (key_inner / width)[:, None])).astype(bf16)
    grad_qkvo = (
        "prod",
        jnp.stack([tokens, tokens, tokens, d_attn_b]),
        jnp.stack([d_query_b, d_key_b, d_values_b, attended_b]),
    )

    def spread(g):
        return jnp.pad(g.reshape(n_dp, -1), ((0, 0), (0, slab - g.shape[0] // n_dp))).reshape(-1)

    grad_gains = jnp.stack([spread(grad_gq), spread(grad_gk), grad_ag, grad_mg])
    (grad_qkvo_s, grad_gains_s), sent = scatter_group(
        [grad_qkvo, (grad_gains, 1)], ring, carry=(jnp.bfloat16, jnp.float32), after=sent
    )
    grad_wq_s, grad_wk_s, grad_wv_s = grad_qkvo_s[0], grad_qkvo_s[1], grad_qkvo_s[2]
    grad_wo_s = grad_qkvo_s[3].T
    grad_gq_s = grad_gains_s[0, :head_piece]
    grad_gk_s = grad_gains_s[1, :head_piece]
    grad_ag_s = grad_gains_s[2]
    grad_mg_s = grad_gains_s[3]
    input_part = jnp.einsum("rc,dc->rd", d_query_b, wq, preferred_element_type=f32)
    input_part = input_part + jnp.einsum("rc,dc->rd", d_key_b, wk, preferred_element_type=f32)
    input_part = input_part + jnp.einsum("rc,dc->rd", d_values_b, wv, preferred_element_type=f32)
    input_grad = d_hidden + input_total(input_part)
    return (
        layer_out,
        input_grad,
        grad_wq_s,
        grad_wk_s,
        grad_wv_s,
        grad_wo_s,
        grad_gq_s,
        grad_gk_s,
        grad_ag_s,
        grad_wg_s,
        grad_wu_s,
        grad_wd_s,
        grad_mg_s,
    )


def solution(mesh):
    placed = (
        P("dp", None),
        P("dp", None),
        P("dp"),
        P("dp", None),
        P("dp", "mp"),
        P("dp", "mp"),
        P("dp", "mp"),
        P("mp", "dp"),
        P(("mp", "dp")),
        P(("mp", "dp")),
        P("dp"),
        P("dp", "mp"),
        P("dp", "mp"),
        P("mp", "dp"),
        P("dp"),
    )
    ring = ring_order(mesh)
    return jax.shard_map(
        functools.partial(per_device, ring=ring),
        mesh=mesh,
        in_specs=placed,
        out_specs=(
            P("dp", None),
            P("dp", None),
            P("dp", "mp"),
            P("dp", "mp"),
            P("dp", "mp"),
            P("mp", "dp"),
            P(("mp", "dp")),
            P(("mp", "dp")),
            P("dp"),
            P("dp", "mp"),
            P("dp", "mp"),
            P("mp", "dp"),
            P("dp"),
        ),
        check_vma=False,
    )
```

```python
import functools

import jax
import jax.numpy as jnp
import numpy as np
from jax import lax
from jax.sharding import PartitionSpec as P

HEAD_DIM = 128


EPS = 1e-06
THETA = 500000.0


def rope_tables(rows, head_dim):
    half = head_dim // 2
    inverse = THETA ** (-(jnp.arange(half).astype(jnp.float32) * 2.0) / head_dim)
    angles = jnp.arange(rows).astype(jnp.float32)[:, None] * inverse[None, :]
    return (jnp.cos(angles)[:, None, :], jnp.sin(angles)[:, None, :])


def rotate(value, cosine, sine):
    half = value.shape[-1] // 2
    first, second = (value[..., :half], value[..., half:])
    return jnp.concatenate(
        [first * cosine - second * sine, second * cosine + first * sine], axis=-1
    )


def rotate_back(grad, cosine, sine):
    half = grad.shape[-1] // 2
    first, second = (grad[..., :half], grad[..., half:])
    return jnp.concatenate(
        [first * cosine + second * sine, second * cosine - first * sine], axis=-1
    )


def allowed_block(start, block, seg_row, length):
    query_pos = start + jnp.arange(block)
    key_pos = jnp.arange(seg_row.shape[0])
    same = seg_row[:, None] == seg_row[None, :]
    causal = key_pos[None, :] <= query_pos[:, None]
    inside = key_pos[None, :] < length
    return same & causal & inside | (key_pos[None, :] == query_pos[:, None])


def mp_allreduce(x, carry=jnp.bfloat16):
    m = lax.axis_size("mp")
    me = lax.axis_index("mp")
    core = me % 2
    chips = m // 2
    chip = me // 2
    half = x.shape[1] // 2
    pair = [(i, i ^ 1) for i in range(m)]
    mine = lax.dynamic_slice_in_dim(x, core * half, half, 1)
    other = lax.dynamic_slice_in_dim(x, (1 - core) * half, half, 1)
    part = mine + lax.ppermute(other, "mp", pair)
    if chips == 2:
        low = part.astype(carry)
        got = lax.ppermute(low, "mp", [(i, i ^ 2) for i in range(m)])
        part = low.astype(jnp.float32) + got.astype(jnp.float32)
    elif chips > 2:
        low = part.astype(carry)
        got = [low]
        for k in range(1, chips):
            perm = [(c * 2 + r, ((c + k) % chips) * 2 + r) for c in range(chips) for r in range(2)]
            got.append(lax.ppermute(low, "mp", perm))
        stack = jnp.stack(got)
        order = (chip - jnp.arange(chips)) % chips
        ordered = jnp.take(stack, order, axis=0).astype(jnp.float32)
        part = ordered[0]
        for k in range(1, chips):
            part = part + ordered[k]
    swapped = lax.ppermute(part, "mp", pair)
    first = jnp.where(core == 0, part, swapped)
    second = jnp.where(core == 0, swapped, part)
    return jnp.concatenate([first, second], axis=1)


def branch_total(partial_sum):
    return mp_allreduce(partial_sum)


def input_total(partial_sum):
    return mp_allreduce(partial_sum)


def norm_forward(total):
    factor = lax.rsqrt(jnp.mean(total * total, axis=1, keepdims=True) + EPS)
    return (total * factor, factor)


def norm_back(grad, normed, factor, gain):
    grad_gain = jnp.sum(grad * normed, axis=0)
    scaled = grad * gain
    inner = jnp.mean(scaled * normed, axis=1, keepdims=True)
    return (factor * (scaled - normed * inner), grad_gain)


def ring_order(mesh):
    column = [mesh.devices[i, 0] for i in range(mesh.devices.shape[0])]
    count = len(column)
    try:
        coords = [tuple(d.coords) for d in column]
    except AttributeError:
        return list(range(count))
    axes = [a for a in range(len(coords[0])) if len({c[a] for c in coords}) > 1]
    if len(axes) != 2:
        return list(range(count))
    sizes = {a: len({c[a] for c in coords}) for a in axes}
    even = [a for a in axes if sizes[a] % 2 == 0]
    if not even:
        return list(range(count))
    outer = min(even, key=lambda a: sizes[a])
    inner = [a for a in axes if a != outer][0]
    lo = {a: min(c[a] for c in coords) for a in axes}
    where = {(c[outer] - lo[outer], c[inner] - lo[inner]): i for i, c in enumerate(coords)}
    order = []
    for o in range(sizes[outer]):
        steps = range(sizes[inner]) if o % 2 == 0 else reversed(range(sizes[inner]))
        for k in steps:
            order.append(where[(o, k)])
    if sorted(order) != list(range(count)):
        return list(range(count))
    return order


def ring_steps(ring):
    n = len(ring)
    pos_of = [ring.index(d) for d in range(n)]
    mypos = jnp.asarray(pos_of, jnp.int32)[lax.axis_index("dp")]
    fwd = [(ring[p], ring[(p + 1) % n]) for p in range(n)]
    bwd = [(ring[p], ring[(p - 1) % n]) for p in range(n)]
    nf = n // 2
    return n, mypos, fwd, bwd, nf, n - 1 - nf


def split_axis(ndim, axis):
    return ndim - 1 if axis != ndim - 1 else 0


def halves(values, axes, which):
    out = []
    for x, ax in zip(values, axes):
        h = x.shape[ax] // 2
        out.append(lax.slice_in_dim(x, which * h, (which + 1) * h, axis=ax))
    return tuple(out)


def joined(first, second, axes):
    return tuple(jnp.concatenate([x, y], axis=ax) for x, y, ax in zip(first, second, axes))


def gather_group(pieces, ring, after=None):
    locals_ = tuple(p.astype(jnp.bfloat16) for p, _ in pieces)
    if after is not None:
        locals_, _ = lax.optimization_barrier((locals_, after))
    n, mypos, fwd, bwd, nf, nb = ring_steps(ring)
    ring_arr = jnp.asarray(ring, jnp.int32)
    axes = [split_axis(p.ndim, axis) for p, axis in pieces]
    parts = {0: locals_}
    a = locals_
    b = locals_
    if n % 2 == 0:
        for s in range(nf - 1):
            a = lax.ppermute(a, "dp", fwd)
            b = lax.ppermute(b, "dp", bwd)
            a, b = lax.optimization_barrier((a, b))
            parts[-(s + 1)] = a
            parts[s + 1] = b
        ha = lax.ppermute(halves(a, axes, 0), "dp", fwd)
        hb = lax.ppermute(halves(b, axes, 1), "dp", bwd)
        ha, hb = lax.optimization_barrier((ha, hb))
        parts[-nf] = (ha, hb)
        last = (ha, hb)
        arrival = [0]
        for s in range(nf - 1):
            arrival += [-(s + 1), s + 1]
        arrival.append(-nf)
    else:
        for s in range(nf):
            a = lax.ppermute(a, "dp", fwd)
            if s < nb:
                b = lax.ppermute(b, "dp", bwd)
                a, b = lax.optimization_barrier((a, b))
                parts[s + 1] = b
            parts[-(s + 1)] = a
        last = (a, b)
        arrival = [0]
        for s in range(nf):
            arrival.append(-(s + 1))
            if s < nb:
                arrival.append(s + 1)
    out = []
    for i, (p, axis) in enumerate(pieces):
        shape = list(p.shape)
        width = shape[axis]
        shape[axis] *= n
        first_in = parts[arrival[1]] if len(arrival) > 1 else parts[0]
        first_in = first_in[0] if isinstance(first_in[0], tuple) else first_in
        seed = first_in[i].reshape(-1)[:1] * 0
        full = jnp.broadcast_to(seed.reshape((1,) * p.ndim), shape)
        for k in arrival:
            owner = ring_arr[(mypos + k) % n]
            if n % 2 == 0 and k == -nf:
                first, second = parts[k][0][i], parts[k][1][i]
                start = [0] * p.ndim
                start[axis] = owner * width
                full = lax.dynamic_update_slice(full, first, start)
                start[axes[i]] = first.shape[axes[i]]
                full = lax.dynamic_update_slice(full, second, start)
            else:
                full = lax.dynamic_update_slice_in_dim(full, parts[k][i], owner * width, axis)
        out.append(full)
    return out, last


def scatter_group(pieces, ring, carry=jnp.bfloat16, after=None, taps=None):
    if after is not None:
        arrays = tuple(p[1:] if isinstance(p[0], str) else (p[0],) for p in pieces)
        arrays, _ = lax.optimization_barrier((arrays, after))
        pieces = [
            ("prod",) + tuple(a) if isinstance(p[0], str) else (a[0], p[1]) for p, a in zip(pieces, arrays)
        ]
    n, mypos, fwd, bwd, nf, nb = ring_steps(ring)
    ring_arr = jnp.asarray(ring, jnp.int32)

    def chunk(piece, owner):
        if isinstance(piece[0], str):
            _, lhs, rhs = piece
            w = lhs.shape[2] // n
            part = lax.dynamic_slice_in_dim(lhs, owner * w, w, 2)
            return jnp.einsum("xrd,xrf->xdf", part, rhs, preferred_element_type=jnp.float32)
        g, axis = piece
        w = g.shape[axis] // n
        return lax.dynamic_slice_in_dim(g, owner * w, w, axis).astype(jnp.float32)

    def own(q):
        owner = ring_arr[q % n]
        return tuple(chunk(p, owner) for p in pieces)

    axes = [2 if isinstance(p[0], str) else split_axis(p[0].ndim, p[1]) for p in pieces]
    carries = carry if isinstance(carry, tuple) else (carry,) * len(pieces)

    def cast(vals):
        return tuple(v.astype(c) for v, c in zip(vals, carries))

    def wide(vals):
        return tuple(v.astype(jnp.float32) for v in vals)

    def plus(x, y):
        return tuple(u + v for u, v in zip(x, y))

    if n % 2 == 0:
        opposite = own(mypos + nf)
        got_f = lax.ppermute(cast(halves(opposite, axes, 0)), "dp", fwd)
        got_b = lax.ppermute(cast(halves(opposite, axes, 1)), "dp", bwd)
        got_f, got_b = lax.optimization_barrier((got_f, got_b))
        for s in range(1, nf):
            vf = own(mypos + nf - s)
            vb = own(mypos - nf + s)
            if s == 1:
                vf = joined(plus(halves(vf, axes, 0), wide(got_f)), halves(vf, axes, 1), axes)
                vb = joined(halves(vb, axes, 0), plus(halves(vb, axes, 1), wide(got_b)), axes)
            else:
                vf = plus(vf, wide(got_f))
                vb = plus(vb, wide(got_b))
            if taps is not None:
                taps.append((vf, vb))
            got_f = lax.ppermute(cast(vf), "dp", fwd)
            got_b = lax.ppermute(cast(vb), "dp", bwd)
            got_f, got_b = lax.optimization_barrier((got_f, got_b))
        last = (got_f, got_b)
        total = own(mypos)
        if nf == 1:
            total = plus(total, joined(wide(got_f), wide(got_b), axes))
        else:
            total = plus(plus(total, wide(got_f)), wide(got_b))
        return list(total), last

    def send(vals, got, perm):
        if got is not None:
            vals = plus(vals, wide(got))
        return lax.ppermute(cast(vals), "dp", perm)

    got_f = None
    got_b = None
    for s in range(nf):
        got_f = send(own(mypos + nf - s), got_f, fwd)
        if s < nb:
            got_b = send(own(mypos - nb + s), got_b, bwd)
            got_f, got_b = lax.optimization_barrier((got_f, got_b))
    last = (got_f, got_b)
    total = own(mypos)
    total = plus(total, wide(got_f))
    if got_b is not None:
        total = plus(total, wide(got_b))
    return list(total), last


def per_device(
    tokens,
    segment_ids,
    valid_lengths,
    cotangent,
    w_query,
    w_key,
    w_value,
    w_out,
    query_gain,
    key_gain,
    attn_gain,
    w_gate,
    w_up,
    w_down,
    mlp_gain,
    ring,
):
    f32 = jnp.float32
    bf16 = jnp.bfloat16
    rows, width = tokens.shape
    seg_row = segment_ids[0]
    length = valid_lengths[0]
    block = min(512, rows)
    count = rows // block
    scale = HEAD_DIM ** (-0.5)
    n_dp = len(ring)
    slab = attn_gain.shape[0]
    head_piece = query_gain.shape[0]

    def padded(g):
        return jnp.pad(g, (0, slab - g.shape[0]))

    gains = jnp.stack([padded(query_gain), padded(key_gain), attn_gain, mlp_gain])
    (qkvo, gains_full), seen = gather_group(
        [(jnp.stack([w_query, w_key, w_value, w_out.T]), 1), (gains, 1)], ring
    )
    wq, wk, wv, wo_t = qkvo[0], qkvo[1], qkvo[2], qkvo[3]
    gq = gains_full[0].reshape(n_dp, slab)[:, :head_piece].reshape(-1)
    gk = gains_full[1].reshape(n_dp, slab)[:, :head_piece].reshape(-1)
    ga = gains_full[2]
    gm = gains_full[3]
    (gud,), seen = gather_group([(jnp.stack([w_gate, w_up, w_down.T]), 1)], ring, after=seen)
    wg, wu, wd_t = gud[0], gud[1], gud[2]
    gq32 = gq.astype(f32)
    gk32 = gk.astype(f32)
    ga32 = ga.astype(f32)
    gm32 = gm.astype(f32)
    query = jnp.dot(tokens, wq, preferred_element_type=f32)
    keys = jnp.dot(tokens, wk, preferred_element_type=f32)
    values = jnp.dot(tokens, wv, preferred_element_type=f32).astype(bf16)
    query_sq, key_sq = lax.psum(
        (jnp.sum(query * query, axis=1), jnp.sum(keys * keys, axis=1)), "mp"
    )
    query_factor = lax.rsqrt(query_sq / width + EPS)[:, None]
    key_factor = lax.rsqrt(key_sq / width + EPS)[:, None]
    query_hat = query * query_factor
    key_hat = keys * key_factor
    heads = query.shape[1] // HEAD_DIM
    cosine, sine = rope_tables(rows, HEAD_DIM)
    query_rot = rotate((query_hat * gq32).reshape(rows, heads, HEAD_DIM), cosine, sine).astype(bf16)
    key_rot = rotate((key_hat * gk32).reshape(rows, heads, HEAD_DIM), cosine, sine).astype(bf16)
    values_h = values.reshape(rows, heads, HEAD_DIM)

    def block_scores(start):
        scores = jnp.einsum("qhe,khe->hqk", query_rot, key_rot, preferred_element_type=f32) * scale
        mask = allowed_block(start, block, seg_row, length)
        return (query_rot, jnp.where(mask[None], scores, -1e30))

    def forward_block(index):
        start = index * block
        q_blk, scores = block_scores(start)
        top = jnp.max(scores, axis=-1, keepdims=True)
        total = jnp.sum(jnp.exp(scores - top), axis=-1, keepdims=True)
        logsum = top + jnp.log(total)
        probs = jnp.exp(scores - logsum).astype(bf16)
        attended = jnp.einsum("hqk,khe->qhe", probs, values_h, preferred_element_type=f32)
        return (attended, logsum[..., 0])

    attended, logsums = lax.map(forward_block, jnp.arange(count))
    attended_b = attended.reshape(rows, heads * HEAD_DIM).astype(bf16)
    attn_partial = jnp.einsum("rc,dc->rd", attended_b, wo_t, preferred_element_type=f32)
    attn_total = branch_total(attn_partial)
    attn_hat, attn_factor = norm_forward(attn_total)
    hidden = tokens.astype(f32) + attn_hat * ga32
    hidden_b = hidden.astype(bf16)
    gate = jnp.dot(hidden_b, wg, preferred_element_type=f32)
    up = jnp.dot(hidden_b, wu, preferred_element_type=f32)
    active = jax.nn.silu(gate)
    mixed_b = (active * up).astype(bf16)
    mlp_partial = jnp.einsum("rf,df->rd", mixed_b, wd_t, preferred_element_type=f32)
    mlp_total = branch_total(mlp_partial)
    mlp_hat, mlp_factor = norm_forward(mlp_total)
    layer_out = (hidden + mlp_hat * gm32).astype(bf16)
    grad_out = cotangent.astype(f32)
    d_mlp, grad_mg = norm_back(grad_out, mlp_hat, mlp_factor, gm32)
    d_mlp_b = d_mlp.astype(bf16)
    (grad_wd_t_s,), sent = scatter_group([("prod", d_mlp_b[None], mixed_b[None])], ring)
    grad_wd_s = grad_wd_t_s[0].T
    d_mixed = jnp.einsum("rd,df->rf", d_mlp_b, wd_t, preferred_element_type=f32)
    sigma = jax.nn.sigmoid(gate)
    d_gate = (d_mixed * up * sigma * (1.0 + gate * (1.0 - sigma))).astype(bf16)
    d_up = (d_mixed * active).astype(bf16)
    grad_gu = ("prod", jnp.stack([hidden_b, hidden_b]), jnp.stack([d_gate, d_up]))
    gu_taps = []
    (grad_gu_s,), sent = scatter_group([grad_gu], ring, after=sent, taps=gu_taps)
    grad_wg_s, grad_wu_s = grad_gu_s[0], grad_gu_s[1]
    hidden_partial = jnp.einsum("rf,df->rd", d_gate, wg, preferred_element_type=f32) + jnp.einsum(
        "rf,df->rd", d_up, wu, preferred_element_type=f32
    )
    d_hidden = grad_out + input_total(hidden_partial)
    d_attn, grad_ag = norm_back(d_hidden, attn_hat, attn_factor, ga32)
    d_attn_b = d_attn.astype(bf16)
    if gu_taps:
        d_attn_b, _ = lax.optimization_barrier((d_attn_b, gu_taps[0]))
    d_attended = jnp.einsum("rd,dc->rc", d_attn_b, wo_t, preferred_element_type=f32).astype(bf16)
    d_attended = d_attended.reshape(rows, heads, HEAD_DIM)

    def backward_block(carry, index):
        key_acc, value_acc = carry
        start = index * block
        q_blk, scores = block_scores(start)
        logsum = lax.dynamic_index_in_dim(logsums, index, 0, keepdims=False)
        probs = jnp.exp(scores - logsum[..., None])
        value_acc = value_acc + jnp.einsum(
            "hqk,qhe->khe", probs.astype(bf16), d_attended, preferred_element_type=f32
        )
        d_probs = jnp.einsum("qhe,khe->hqk", d_attended, values_h, preferred_element_type=f32)
        delta = jnp.sum(probs * d_probs, axis=-1, keepdims=True)
        d_scores = (probs * (d_probs - delta)).astype(bf16)
        d_query_blk = (
            jnp.einsum("hqk,khe->qhe", d_scores, key_rot, preferred_element_type=f32) * scale
        )
        key_acc = (
            key_acc
            + jnp.einsum("hqk,qhe->khe", d_scores, q_blk, preferred_element_type=f32) * scale
        )
        return ((key_acc, value_acc), d_query_blk)

    empty = jnp.zeros((rows, heads, HEAD_DIM), f32)
    (d_key_rot, d_values), d_query_rot = lax.scan(backward_block, (empty, empty), jnp.arange(count))
    d_query_rot = d_query_rot.reshape(rows, heads, HEAD_DIM)
    d_values_b = d_values.reshape(rows, heads * HEAD_DIM).astype(bf16)
    d_query_n = rotate_back(d_query_rot, cosine, sine).reshape(rows, heads * HEAD_DIM)
    d_key_n = rotate_back(d_key_rot, cosine, sine).reshape(rows, heads * HEAD_DIM)
    grad_gq = jnp.sum(d_query_n * query_hat, axis=0)
    grad_gk = jnp.sum(d_key_n * key_hat, axis=0)
    d_query_hat = d_query_n * gq32
    d_key_hat = d_key_n * gk32
    query_inner, key_inner = lax.psum(
        (jnp.sum(d_query_hat * query_hat, axis=1), jnp.sum(d_key_hat * key_hat, axis=1)), "mp"
    )
    d_query_b = (query_factor * (d_query_hat - query_hat * (query_inner / width)[:, None])).astype(
        bf16
    )
    d_key_b = (key_factor * (d_key_hat - key_hat * (key_inner / width)[:, None])).astype(bf16)
    grad_qkvo = (
        "prod",
        jnp.stack([tokens, tokens, tokens, d_attn_b]),
        jnp.stack([d_query_b, d_key_b, d_values_b, attended_b]),
    )

    def spread(g):
        return jnp.pad(g.reshape(n_dp, -1), ((0, 0), (0, slab - g.shape[0] // n_dp))).reshape(-1)

    grad_gains = jnp.stack([spread(grad_gq), spread(grad_gk), grad_ag, grad_mg])
    (grad_qkvo_s, grad_gains_s), sent = scatter_group(
        [grad_qkvo, (grad_gains, 1)], ring, carry=(jnp.bfloat16, jnp.float32), after=sent
    )
    grad_wq_s, grad_wk_s, grad_wv_s = grad_qkvo_s[0], grad_qkvo_s[1], grad_qkvo_s[2]
    grad_wo_s = grad_qkvo_s[3].T
    grad_gq_s = grad_gains_s[0, :head_piece]
    grad_gk_s = grad_gains_s[1, :head_piece]
    grad_ag_s = grad_gains_s[2]
    grad_mg_s = grad_gains_s[3]
    input_part = jnp.einsum("rc,dc->rd", d_query_b, wq, preferred_element_type=f32)
    input_part = input_part + jnp.einsum("rc,dc->rd", d_key_b, wk, preferred_element_type=f32)
    input_part = input_part + jnp.einsum("rc,dc->rd", d_values_b, wv, preferred_element_type=f32)
    input_grad = d_hidden + input_total(input_part)
    return (
        layer_out,
        input_grad,
        grad_wq_s,
        grad_wk_s,
        grad_wv_s,
        grad_wo_s,
        grad_gq_s,
        grad_gk_s,
        grad_ag_s,
        grad_wg_s,
        grad_wu_s,
        grad_wd_s,
        grad_mg_s,
    )


def solution(mesh):
    placed = (
        P("dp", None),
        P("dp", None),
        P("dp"),
        P("dp", None),
        P("dp", "mp"),
        P("dp", "mp"),
        P("dp", "mp"),
        P("mp", "dp"),
        P(("mp", "dp")),
        P(("mp", "dp")),
        P("dp"),
        P("dp", "mp"),
        P("dp", "mp"),
        P("mp", "dp"),
        P("dp"),
    )
    ring = ring_order(mesh)
    return jax.shard_map(
        functools.partial(per_device, ring=ring),
        mesh=mesh,
        in_specs=placed,
        out_specs=(
            P("dp", None),
            P("dp", None),
            P("dp", "mp"),
            P("dp", "mp"),
            P("dp", "mp"),
            P("mp", "dp"),
            P(("mp", "dp")),
            P(("mp", "dp")),
            P("dp"),
            P("dp", "mp"),
            P("dp", "mp"),
            P("mp", "dp"),
            P("dp"),
        ),
        check_vma=False,
    )
```

```python
import functools

import jax
import jax.numpy as jnp
import numpy as np
from jax import lax
from jax.sharding import PartitionSpec as P

HEAD_DIM = 128


EPS = 1e-06
THETA = 500000.0


def rope_tables(rows, head_dim):
    half = head_dim // 2
    inverse = THETA ** (-(jnp.arange(half).astype(jnp.float32) * 2.0) / head_dim)
    angles = jnp.arange(rows).astype(jnp.float32)[:, None] * inverse[None, :]
    return (jnp.cos(angles)[:, None, :], jnp.sin(angles)[:, None, :])


def rotate(value, cosine, sine):
    half = value.shape[-1] // 2
    first, second = (value[..., :half], value[..., half:])
    return jnp.concatenate(
        [first * cosine - second * sine, second * cosine + first * sine], axis=-1
    )


def rotate_back(grad, cosine, sine):
    half = grad.shape[-1] // 2
    first, second = (grad[..., :half], grad[..., half:])
    return jnp.concatenate(
        [first * cosine + second * sine, second * cosine - first * sine], axis=-1
    )


def allowed_block(start, block, seg_row, length):
    query_pos = start + jnp.arange(block)
    key_pos = jnp.arange(seg_row.shape[0])
    same = seg_row[:, None] == seg_row[None, :]
    causal = key_pos[None, :] <= query_pos[:, None]
    inside = key_pos[None, :] < length
    return same & causal & inside | (key_pos[None, :] == query_pos[:, None])


def mp_allreduce(x, carry=jnp.bfloat16):
    m = lax.axis_size("mp")
    me = lax.axis_index("mp")
    core = me % 2
    chips = m // 2
    chip = me // 2
    half = x.shape[1] // 2
    pair = [(i, i ^ 1) for i in range(m)]
    mine = lax.dynamic_slice_in_dim(x, core * half, half, 1)
    other = lax.dynamic_slice_in_dim(x, (1 - core) * half, half, 1)
    part = mine + lax.ppermute(other, "mp", pair)
    if chips == 2:
        low = part.astype(carry)
        got = lax.ppermute(low, "mp", [(i, i ^ 2) for i in range(m)])
        part = low.astype(jnp.float32) + got.astype(jnp.float32)
    elif chips > 2:
        low = part.astype(carry)
        got = [low]
        for k in range(1, chips):
            perm = [(c * 2 + r, ((c + k) % chips) * 2 + r) for c in range(chips) for r in range(2)]
            got.append(lax.ppermute(low, "mp", perm))
        stack = jnp.stack(got)
        order = (chip - jnp.arange(chips)) % chips
        ordered = jnp.take(stack, order, axis=0).astype(jnp.float32)
        part = ordered[0]
        for k in range(1, chips):
            part = part + ordered[k]
    swapped = lax.ppermute(part, "mp", pair)
    first = jnp.where(core == 0, part, swapped)
    second = jnp.where(core == 0, swapped, part)
    return jnp.concatenate([first, second], axis=1)


def branch_total(partial_sum):
    return mp_allreduce(partial_sum)


def input_total(partial_sum):
    return mp_allreduce(partial_sum)


def norm_forward(total):
    factor = lax.rsqrt(jnp.mean(total * total, axis=1, keepdims=True) + EPS)
    return (total * factor, factor)


def norm_back(grad, normed, factor, gain):
    grad_gain = jnp.sum(grad * normed, axis=0)
    scaled = grad * gain
    inner = jnp.mean(scaled * normed, axis=1, keepdims=True)
    return (factor * (scaled - normed * inner), grad_gain)


def ring_order(mesh):
    column = [mesh.devices[i, 0] for i in range(mesh.devices.shape[0])]
    count = len(column)
    try:
        coords = [tuple(d.coords) for d in column]
    except AttributeError:
        return list(range(count))
    axes = [a for a in range(len(coords[0])) if len({c[a] for c in coords}) > 1]
    if len(axes) != 2:
        return list(range(count))
    sizes = {a: len({c[a] for c in coords}) for a in axes}
    even = [a for a in axes if sizes[a] % 2 == 0]
    if not even:
        return list(range(count))
    outer = min(even, key=lambda a: sizes[a])
    inner = [a for a in axes if a != outer][0]
    lo = {a: min(c[a] for c in coords) for a in axes}
    where = {(c[outer] - lo[outer], c[inner] - lo[inner]): i for i, c in enumerate(coords)}
    order = []
    for o in range(sizes[outer]):
        steps = range(sizes[inner]) if o % 2 == 0 else reversed(range(sizes[inner]))
        for k in steps:
            order.append(where[(o, k)])
    if sorted(order) != list(range(count)):
        return list(range(count))
    return order


def ring_steps(ring):
    n = len(ring)
    pos_of = [ring.index(d) for d in range(n)]
    mypos = jnp.asarray(pos_of, jnp.int32)[lax.axis_index("dp")]
    fwd = [(ring[p], ring[(p + 1) % n]) for p in range(n)]
    bwd = [(ring[p], ring[(p - 1) % n]) for p in range(n)]
    nf = n // 2
    return n, mypos, fwd, bwd, nf, n - 1 - nf


def split_axis(ndim, axis):
    return ndim - 1 if axis != ndim - 1 else 0


def halves(values, axes, which):
    out = []
    for x, ax in zip(values, axes):
        h = x.shape[ax] // 2
        out.append(lax.slice_in_dim(x, which * h, (which + 1) * h, axis=ax))
    return tuple(out)


def joined(first, second, axes):
    return tuple(jnp.concatenate([x, y], axis=ax) for x, y, ax in zip(first, second, axes))


def gather_group(pieces, ring, after=None):
    locals_ = tuple(p.astype(jnp.bfloat16) for p, _ in pieces)
    if after is not None:
        locals_, _ = lax.optimization_barrier((locals_, after))
    n, mypos, fwd, bwd, nf, nb = ring_steps(ring)
    ring_arr = jnp.asarray(ring, jnp.int32)
    axes = [split_axis(p.ndim, axis) for p, axis in pieces]
    parts = {0: locals_}
    a = locals_
    b = locals_
    if n % 2 == 0:
        for s in range(nf - 1):
            a = lax.ppermute(a, "dp", fwd)
            b = lax.ppermute(b, "dp", bwd)
            a, b = lax.optimization_barrier((a, b))
            parts[-(s + 1)] = a
            parts[s + 1] = b
        ha = lax.ppermute(halves(a, axes, 0), "dp", fwd)
        hb = lax.ppermute(halves(b, axes, 1), "dp", bwd)
        ha, hb = lax.optimization_barrier((ha, hb))
        parts[-nf] = (ha, hb)
        last = (ha, hb)
        arrival = [0]
        for s in range(nf - 1):
            arrival += [-(s + 1), s + 1]
        arrival.append(-nf)
    else:
        for s in range(nf):
            a = lax.ppermute(a, "dp", fwd)
            if s < nb:
                b = lax.ppermute(b, "dp", bwd)
                a, b = lax.optimization_barrier((a, b))
                parts[s + 1] = b
            parts[-(s + 1)] = a
        last = (a, b)
        arrival = [0]
        for s in range(nf):
            arrival.append(-(s + 1))
            if s < nb:
                arrival.append(s + 1)
    out = []
    for i, (p, axis) in enumerate(pieces):
        shape = list(p.shape)
        width = shape[axis]
        shape[axis] *= n
        first_in = parts[arrival[1]] if len(arrival) > 1 else parts[0]
        first_in = first_in[0] if isinstance(first_in[0], tuple) else first_in
        seed = first_in[i].reshape(-1)[:1] * 0
        full = jnp.broadcast_to(seed.reshape((1,) * p.ndim), shape)
        for k in arrival:
            owner = ring_arr[(mypos + k) % n]
            if n % 2 == 0 and k == -nf:
                first, second = parts[k][0][i], parts[k][1][i]
                start = [0] * p.ndim
                start[axis] = owner * width
                full = lax.dynamic_update_slice(full, first, start)
                start[axes[i]] = first.shape[axes[i]]
                full = lax.dynamic_update_slice(full, second, start)
            else:
                full = lax.dynamic_update_slice_in_dim(full, parts[k][i], owner * width, axis)
        out.append(full)
    return out, last


def scatter_group(pieces, ring, carry=jnp.bfloat16, after=None, taps=None):
    if after is not None:
        arrays = tuple(p[1:] if isinstance(p[0], str) else (p[0],) for p in pieces)
        arrays, _ = lax.optimization_barrier((arrays, after))
        pieces = [
            ("prod",) + tuple(a) if isinstance(p[0], str) else (a[0], p[1]) for p, a in zip(pieces, arrays)
        ]
    n, mypos, fwd, bwd, nf, nb = ring_steps(ring)
    ring_arr = jnp.asarray(ring, jnp.int32)

    def chunk(piece, owner):
        if isinstance(piece[0], str):
            _, lhs, rhs = piece
            w = lhs.shape[2] // n
            part = lax.dynamic_slice_in_dim(lhs, owner * w, w, 2)
            return jnp.einsum("xrd,xrf->xdf", part, rhs, preferred_element_type=jnp.float32)
        g, axis = piece
        w = g.shape[axis] // n
        return lax.dynamic_slice_in_dim(g, owner * w, w, axis).astype(jnp.float32)

    def own(q):
        owner = ring_arr[q % n]
        return tuple(chunk(p, owner) for p in pieces)

    axes = [2 if isinstance(p[0], str) else split_axis(p[0].ndim, p[1]) for p in pieces]
    carries = carry if isinstance(carry, tuple) else (carry,) * len(pieces)

    def cast(vals):
        return tuple(v.astype(c) for v, c in zip(vals, carries))

    def wide(vals):
        return tuple(v.astype(jnp.float32) for v in vals)

    def plus(x, y):
        return tuple(u + v for u, v in zip(x, y))

    if n % 2 == 0:
        opposite = own(mypos + nf)
        got_f = lax.ppermute(cast(halves(opposite, axes, 0)), "dp", fwd)
        got_b = lax.ppermute(cast(halves(opposite, axes, 1)), "dp", bwd)
        got_f, got_b = lax.optimization_barrier((got_f, got_b))
        for s in range(1, nf):
            vf = own(mypos + nf - s)
            vb = own(mypos - nf + s)
            if s == 1:
                vf = joined(plus(halves(vf, axes, 0), wide(got_f)), halves(vf, axes, 1), axes)
                vb = joined(halves(vb, axes, 0), plus(halves(vb, axes, 1), wide(got_b)), axes)
            else:
                vf = plus(vf, wide(got_f))
                vb = plus(vb, wide(got_b))
            vf = cast(vf)
            vb = cast(vb)
            if taps is not None:
                taps.append((vf, vb))
            got_f = lax.ppermute(vf, "dp", fwd)
            got_b = lax.ppermute(vb, "dp", bwd)
            got_f, got_b = lax.optimization_barrier((got_f, got_b))
        last = (got_f, got_b)
        total = own(mypos)
        if nf == 1:
            total = plus(total, joined(wide(got_f), wide(got_b), axes))
        else:
            total = plus(plus(total, wide(got_f)), wide(got_b))
        return list(total), last

    def send(vals, got, perm):
        if got is not None:
            vals = plus(vals, wide(got))
        return lax.ppermute(cast(vals), "dp", perm)

    got_f = None
    got_b = None
    for s in range(nf):
        got_f = send(own(mypos + nf - s), got_f, fwd)
        if s < nb:
            got_b = send(own(mypos - nb + s), got_b, bwd)
            got_f, got_b = lax.optimization_barrier((got_f, got_b))
    last = (got_f, got_b)
    total = own(mypos)
    total = plus(total, wide(got_f))
    if got_b is not None:
        total = plus(total, wide(got_b))
    return list(total), last


def per_device(
    tokens,
    segment_ids,
    valid_lengths,
    cotangent,
    w_query,
    w_key,
    w_value,
    w_out,
    query_gain,
    key_gain,
    attn_gain,
    w_gate,
    w_up,
    w_down,
    mlp_gain,
    ring,
):
    f32 = jnp.float32
    bf16 = jnp.bfloat16
    rows, width = tokens.shape
    seg_row = segment_ids[0]
    length = valid_lengths[0]
    block = min(512, rows)
    count = rows // block
    scale = HEAD_DIM ** (-0.5)
    n_dp = len(ring)
    slab = attn_gain.shape[0]
    head_piece = query_gain.shape[0]

    def padded(g):
        return jnp.pad(g, (0, slab - g.shape[0]))

    gains = jnp.stack([padded(query_gain), padded(key_gain), attn_gain, mlp_gain])
    (qkvo, gains_full), seen = gather_group(
        [(jnp.stack([w_query, w_key, w_value, w_out.T]), 1), (gains, 1)], ring
    )
    wq, wk, wv, wo_t = qkvo[0], qkvo[1], qkvo[2], qkvo[3]
    gq = gains_full[0].reshape(n_dp, slab)[:, :head_piece].reshape(-1)
    gk = gains_full[1].reshape(n_dp, slab)[:, :head_piece].reshape(-1)
    ga = gains_full[2]
    gm = gains_full[3]
    (gud,), seen = gather_group([(jnp.stack([w_gate, w_up, w_down.T]), 1)], ring, after=seen)
    wg, wu, wd_t = gud[0], gud[1], gud[2]
    gq32 = gq.astype(f32)
    gk32 = gk.astype(f32)
    ga32 = ga.astype(f32)
    gm32 = gm.astype(f32)
    query = jnp.dot(tokens, wq, preferred_element_type=f32)
    keys = jnp.dot(tokens, wk, preferred_element_type=f32)
    values = jnp.dot(tokens, wv, preferred_element_type=f32).astype(bf16)
    query_sq, key_sq = lax.psum(
        (jnp.sum(query * query, axis=1), jnp.sum(keys * keys, axis=1)), "mp"
    )
    query_factor = lax.rsqrt(query_sq / width + EPS)[:, None]
    key_factor = lax.rsqrt(key_sq / width + EPS)[:, None]
    query_hat = query * query_factor
    key_hat = keys * key_factor
    heads = query.shape[1] // HEAD_DIM
    cosine, sine = rope_tables(rows, HEAD_DIM)
    query_rot = rotate((query_hat * gq32).reshape(rows, heads, HEAD_DIM), cosine, sine).astype(bf16)
    key_rot = rotate((key_hat * gk32).reshape(rows, heads, HEAD_DIM), cosine, sine).astype(bf16)
    values_h = values.reshape(rows, heads, HEAD_DIM)

    def block_scores(start):
        scores = jnp.einsum("qhe,khe->hqk", query_rot, key_rot, preferred_element_type=f32) * scale
        mask = allowed_block(start, block, seg_row, length)
        return (query_rot, jnp.where(mask[None], scores, -1e30))

    def forward_block(index):
        start = index * block
        q_blk, scores = block_scores(start)
        top = jnp.max(scores, axis=-1, keepdims=True)
        total = jnp.sum(jnp.exp(scores - top), axis=-1, keepdims=True)
        logsum = top + jnp.log(total)
        probs = jnp.exp(scores - logsum).astype(bf16)
        attended = jnp.einsum("hqk,khe->qhe", probs, values_h, preferred_element_type=f32)
        return (attended, logsum[..., 0])

    attended, logsums = lax.map(forward_block, jnp.arange(count))
    attended_b = attended.reshape(rows, heads * HEAD_DIM).astype(bf16)
    attn_partial = jnp.einsum("rc,dc->rd", attended_b, wo_t, preferred_element_type=f32)
    attn_total = branch_total(attn_partial)
    attn_hat, attn_factor = norm_forward(attn_total)
    hidden = tokens.astype(f32) + attn_hat * ga32
    hidden_b = hidden.astype(bf16)
    gate = jnp.dot(hidden_b, wg, preferred_element_type=f32)
    up = jnp.dot(hidden_b, wu, preferred_element_type=f32)
    active = jax.nn.silu(gate)
    mixed_b = (active * up).astype(bf16)
    mlp_partial = jnp.einsum("rf,df->rd", mixed_b, wd_t, preferred_element_type=f32)
    mlp_total = branch_total(mlp_partial)
    mlp_hat, mlp_factor = norm_forward(mlp_total)
    layer_out = (hidden + mlp_hat * gm32).astype(bf16)
    grad_out = cotangent.astype(f32)
    d_mlp, grad_mg = norm_back(grad_out, mlp_hat, mlp_factor, gm32)
    d_mlp_b = d_mlp.astype(bf16)
    (grad_wd_t_s,), sent = scatter_group([("prod", d_mlp_b[None], mixed_b[None])], ring)
    grad_wd_s = grad_wd_t_s[0].T
    d_mixed = jnp.einsum("rd,df->rf", d_mlp_b, wd_t, preferred_element_type=f32)
    sigma = jax.nn.sigmoid(gate)
    d_gate = (d_mixed * up * sigma * (1.0 + gate * (1.0 - sigma))).astype(bf16)
    d_up = (d_mixed * active).astype(bf16)
    grad_gu = ("prod", jnp.stack([hidden_b, hidden_b]), jnp.stack([d_gate, d_up]))
    gu_taps = []
    (grad_gu_s,), sent = scatter_group([grad_gu], ring, after=sent, taps=gu_taps)
    grad_wg_s, grad_wu_s = grad_gu_s[0], grad_gu_s[1]
    hidden_partial = jnp.einsum("rf,df->rd", d_gate, wg, preferred_element_type=f32) + jnp.einsum(
        "rf,df->rd", d_up, wu, preferred_element_type=f32
    )
    d_hidden = grad_out + input_total(hidden_partial)
    d_attn, grad_ag = norm_back(d_hidden, attn_hat, attn_factor, ga32)
    d_attn_b = d_attn.astype(bf16)
    if gu_taps:
        d_attn_b, _ = lax.optimization_barrier((d_attn_b, gu_taps[0]))
    d_attended = jnp.einsum("rd,dc->rc", d_attn_b, wo_t, preferred_element_type=f32).astype(bf16)
    d_attended = d_attended.reshape(rows, heads, HEAD_DIM)

    def backward_block(carry, index):
        key_acc, value_acc = carry
        start = index * block
        q_blk, scores = block_scores(start)
        logsum = lax.dynamic_index_in_dim(logsums, index, 0, keepdims=False)
        probs = jnp.exp(scores - logsum[..., None])
        value_acc = value_acc + jnp.einsum(
            "hqk,qhe->khe", probs.astype(bf16), d_attended, preferred_element_type=f32
        )
        d_probs = jnp.einsum("qhe,khe->hqk", d_attended, values_h, preferred_element_type=f32)
        delta = jnp.sum(probs * d_probs, axis=-1, keepdims=True)
        d_scores = (probs * (d_probs - delta)).astype(bf16)
        d_query_blk = (
            jnp.einsum("hqk,khe->qhe", d_scores, key_rot, preferred_element_type=f32) * scale
        )
        key_acc = (
            key_acc
            + jnp.einsum("hqk,qhe->khe", d_scores, q_blk, preferred_element_type=f32) * scale
        )
        return ((key_acc, value_acc), d_query_blk)

    empty = jnp.zeros((rows, heads, HEAD_DIM), f32)
    (d_key_rot, d_values), d_query_rot = lax.scan(backward_block, (empty, empty), jnp.arange(count))
    d_query_rot = d_query_rot.reshape(rows, heads, HEAD_DIM)
    d_values_b = d_values.reshape(rows, heads * HEAD_DIM).astype(bf16)
    d_query_n = rotate_back(d_query_rot, cosine, sine).reshape(rows, heads * HEAD_DIM)
    d_key_n = rotate_back(d_key_rot, cosine, sine).reshape(rows, heads * HEAD_DIM)
    grad_gq = jnp.sum(d_query_n * query_hat, axis=0)
    grad_gk = jnp.sum(d_key_n * key_hat, axis=0)
    d_query_hat = d_query_n * gq32
    d_key_hat = d_key_n * gk32
    query_inner, key_inner = lax.psum(
        (jnp.sum(d_query_hat * query_hat, axis=1), jnp.sum(d_key_hat * key_hat, axis=1)), "mp"
    )
    d_query_b = (query_factor * (d_query_hat - query_hat * (query_inner / width)[:, None])).astype(
        bf16
    )
    d_key_b = (key_factor * (d_key_hat - key_hat * (key_inner / width)[:, None])).astype(bf16)
    grad_qkvo = (
        "prod",
        jnp.stack([tokens, tokens, tokens, d_attn_b]),
        jnp.stack([d_query_b, d_key_b, d_values_b, attended_b]),
    )

    def spread(g):
        return jnp.pad(g.reshape(n_dp, -1), ((0, 0), (0, slab - g.shape[0] // n_dp))).reshape(-1)

    grad_gains = jnp.stack([spread(grad_gq), spread(grad_gk), grad_ag, grad_mg])
    (grad_qkvo_s, grad_gains_s), sent = scatter_group(
        [grad_qkvo, (grad_gains, 1)], ring, carry=(jnp.bfloat16, jnp.float32), after=sent
    )
    grad_wq_s, grad_wk_s, grad_wv_s = grad_qkvo_s[0], grad_qkvo_s[1], grad_qkvo_s[2]
    grad_wo_s = grad_qkvo_s[3].T
    grad_gq_s = grad_gains_s[0, :head_piece]
    grad_gk_s = grad_gains_s[1, :head_piece]
    grad_ag_s = grad_gains_s[2]
    grad_mg_s = grad_gains_s[3]
    input_part = jnp.einsum("rc,dc->rd", d_query_b, wq, preferred_element_type=f32)
    input_part = input_part + jnp.einsum("rc,dc->rd", d_key_b, wk, preferred_element_type=f32)
    input_part = input_part + jnp.einsum("rc,dc->rd", d_values_b, wv, preferred_element_type=f32)
    input_grad = d_hidden + input_total(input_part)
    return (
        layer_out,
        input_grad,
        grad_wq_s,
        grad_wk_s,
        grad_wv_s,
        grad_wo_s,
        grad_gq_s,
        grad_gk_s,
        grad_ag_s,
        grad_wg_s,
        grad_wu_s,
        grad_wd_s,
        grad_mg_s,
    )


def solution(mesh):
    placed = (
        P("dp", None),
        P("dp", None),
        P("dp"),
        P("dp", None),
        P("dp", "mp"),
        P("dp", "mp"),
        P("dp", "mp"),
        P("mp", "dp"),
        P(("mp", "dp")),
        P(("mp", "dp")),
        P("dp"),
        P("dp", "mp"),
        P("dp", "mp"),
        P("mp", "dp"),
        P("dp"),
    )
    ring = ring_order(mesh)
    return jax.shard_map(
        functools.partial(per_device, ring=ring),
        mesh=mesh,
        in_specs=placed,
        out_specs=(
            P("dp", None),
            P("dp", None),
            P("dp", "mp"),
            P("dp", "mp"),
            P("dp", "mp"),
            P("mp", "dp"),
            P(("mp", "dp")),
            P(("mp", "dp")),
            P("dp"),
            P("dp", "mp"),
            P("dp", "mp"),
            P("mp", "dp"),
            P("dp"),
        ),
        check_vma=False,
    )
```

```python
import functools

import jax
import jax.numpy as jnp
import numpy as np
from jax import lax
from jax.sharding import PartitionSpec as P

HEAD_DIM = 128


EPS = 1e-06
THETA = 500000.0


def rope_tables(rows, head_dim):
    half = head_dim // 2
    inverse = THETA ** (-(jnp.arange(half).astype(jnp.float32) * 2.0) / head_dim)
    angles = jnp.arange(rows).astype(jnp.float32)[:, None] * inverse[None, :]
    return (jnp.cos(angles)[:, None, :], jnp.sin(angles)[:, None, :])


def rotate(value, cosine, sine):
    half = value.shape[-1] // 2
    first, second = (value[..., :half], value[..., half:])
    return jnp.concatenate(
        [first * cosine - second * sine, second * cosine + first * sine], axis=-1
    )


def rotate_back(grad, cosine, sine):
    half = grad.shape[-1] // 2
    first, second = (grad[..., :half], grad[..., half:])
    return jnp.concatenate(
        [first * cosine + second * sine, second * cosine - first * sine], axis=-1
    )


def allowed_block(start, block, seg_row, length):
    query_pos = start + jnp.arange(block)
    key_pos = jnp.arange(seg_row.shape[0])
    same = seg_row[:, None] == seg_row[None, :]
    causal = key_pos[None, :] <= query_pos[:, None]
    inside = key_pos[None, :] < length
    return same & causal & inside | (key_pos[None, :] == query_pos[:, None])


def mp_allreduce(x, carry=jnp.bfloat16):
    m = lax.axis_size("mp")
    me = lax.axis_index("mp")
    core = me % 2
    chips = m // 2
    chip = me // 2
    half = x.shape[1] // 2
    pair = [(i, i ^ 1) for i in range(m)]
    mine = lax.dynamic_slice_in_dim(x, core * half, half, 1)
    other = lax.dynamic_slice_in_dim(x, (1 - core) * half, half, 1)
    part = mine + lax.ppermute(other, "mp", pair)
    if chips == 2:
        low = part.astype(carry)
        got = lax.ppermute(low, "mp", [(i, i ^ 2) for i in range(m)])
        part = low.astype(jnp.float32) + got.astype(jnp.float32)
    elif chips > 2:
        low = part.astype(carry)
        got = [low]
        for k in range(1, chips):
            perm = [(c * 2 + r, ((c + k) % chips) * 2 + r) for c in range(chips) for r in range(2)]
            got.append(lax.ppermute(low, "mp", perm))
        stack = jnp.stack(got)
        order = (chip - jnp.arange(chips)) % chips
        ordered = jnp.take(stack, order, axis=0).astype(jnp.float32)
        part = ordered[0]
        for k in range(1, chips):
            part = part + ordered[k]
    swapped = lax.ppermute(part, "mp", pair)
    first = jnp.where(core == 0, part, swapped)
    second = jnp.where(core == 0, swapped, part)
    return jnp.concatenate([first, second], axis=1)


def branch_total(partial_sum):
    return mp_allreduce(partial_sum)


def input_total(partial_sum):
    return mp_allreduce(partial_sum)


def norm_forward(total):
    factor = lax.rsqrt(jnp.mean(total * total, axis=1, keepdims=True) + EPS)
    return (total * factor, factor)


def norm_back(grad, normed, factor, gain):
    grad_gain = jnp.sum(grad * normed, axis=0)
    scaled = grad * gain
    inner = jnp.mean(scaled * normed, axis=1, keepdims=True)
    return (factor * (scaled - normed * inner), grad_gain)


def ring_order(mesh):
    column = [mesh.devices[i, 0] for i in range(mesh.devices.shape[0])]
    count = len(column)
    try:
        coords = [tuple(d.coords) for d in column]
    except AttributeError:
        return list(range(count))
    axes = [a for a in range(len(coords[0])) if len({c[a] for c in coords}) > 1]
    if len(axes) != 2:
        return list(range(count))
    sizes = {a: len({c[a] for c in coords}) for a in axes}
    even = [a for a in axes if sizes[a] % 2 == 0]
    if not even:
        return list(range(count))
    outer = min(even, key=lambda a: sizes[a])
    inner = [a for a in axes if a != outer][0]
    lo = {a: min(c[a] for c in coords) for a in axes}
    where = {(c[outer] - lo[outer], c[inner] - lo[inner]): i for i, c in enumerate(coords)}
    order = []
    for o in range(sizes[outer]):
        steps = range(sizes[inner]) if o % 2 == 0 else reversed(range(sizes[inner]))
        for k in steps:
            order.append(where[(o, k)])
    if sorted(order) != list(range(count)):
        return list(range(count))
    return order


def ring_steps(ring):
    n = len(ring)
    pos_of = [ring.index(d) for d in range(n)]
    mypos = jnp.asarray(pos_of, jnp.int32)[lax.axis_index("dp")]
    fwd = [(ring[p], ring[(p + 1) % n]) for p in range(n)]
    bwd = [(ring[p], ring[(p - 1) % n]) for p in range(n)]
    nf = n // 2
    return n, mypos, fwd, bwd, nf, n - 1 - nf


def split_axis(ndim, axis):
    return ndim - 1 if axis != ndim - 1 else 0


def halves(values, axes, which):
    out = []
    for x, ax in zip(values, axes):
        h = x.shape[ax] // 2
        out.append(lax.slice_in_dim(x, which * h, (which + 1) * h, axis=ax))
    return tuple(out)


def joined(first, second, axes):
    return tuple(jnp.concatenate([x, y], axis=ax) for x, y, ax in zip(first, second, axes))


def gather_group(pieces, ring, after=None):
    locals_ = tuple(p.astype(jnp.bfloat16) for p, _ in pieces)
    if after is not None:
        locals_, _ = lax.optimization_barrier((locals_, after))
    n, mypos, fwd, bwd, nf, nb = ring_steps(ring)
    ring_arr = jnp.asarray(ring, jnp.int32)
    axes = [split_axis(p.ndim, axis) for p, axis in pieces]
    parts = {0: locals_}
    a = locals_
    b = locals_
    if n % 2 == 0:
        for s in range(nf - 1):
            a = lax.ppermute(a, "dp", fwd)
            b = lax.ppermute(b, "dp", bwd)
            a, b = lax.optimization_barrier((a, b))
            parts[-(s + 1)] = a
            parts[s + 1] = b
        ha = lax.ppermute(halves(a, axes, 0), "dp", fwd)
        hb = lax.ppermute(halves(b, axes, 1), "dp", bwd)
        ha, hb = lax.optimization_barrier((ha, hb))
        parts[-nf] = (ha, hb)
        last = (ha, hb)
        arrival = [0]
        for s in range(nf - 1):
            arrival += [-(s + 1), s + 1]
        arrival.append(-nf)
    else:
        for s in range(nf):
            a = lax.ppermute(a, "dp", fwd)
            if s < nb:
                b = lax.ppermute(b, "dp", bwd)
                a, b = lax.optimization_barrier((a, b))
                parts[s + 1] = b
            parts[-(s + 1)] = a
        last = (a, b)
        arrival = [0]
        for s in range(nf):
            arrival.append(-(s + 1))
            if s < nb:
                arrival.append(s + 1)
    out = []
    for i, (p, axis) in enumerate(pieces):
        shape = list(p.shape)
        width = shape[axis]
        shape[axis] *= n
        first_in = parts[arrival[1]] if len(arrival) > 1 else parts[0]
        first_in = first_in[0] if isinstance(first_in[0], tuple) else first_in
        seed = first_in[i].reshape(-1)[:1] * 0
        full = jnp.broadcast_to(seed.reshape((1,) * p.ndim), shape)
        for k in arrival:
            owner = ring_arr[(mypos + k) % n]
            if n % 2 == 0 and k == -nf:
                first, second = parts[k][0][i], parts[k][1][i]
                start = [0] * p.ndim
                start[axis] = owner * width
                full = lax.dynamic_update_slice(full, first, start)
                start[axes[i]] = first.shape[axes[i]]
                full = lax.dynamic_update_slice(full, second, start)
            else:
                full = lax.dynamic_update_slice_in_dim(full, parts[k][i], owner * width, axis)
        out.append(full)
    return out, last


def scatter_group(pieces, ring, carry=jnp.bfloat16, after=None, taps=None):
    if after is not None:
        arrays = tuple(p[1:] if isinstance(p[0], str) else (p[0],) for p in pieces)
        arrays, _ = lax.optimization_barrier((arrays, after))
        pieces = [
            ("prod",) + tuple(a) if isinstance(p[0], str) else (a[0], p[1]) for p, a in zip(pieces, arrays)
        ]
    n, mypos, fwd, bwd, nf, nb = ring_steps(ring)
    ring_arr = jnp.asarray(ring, jnp.int32)

    def chunk(piece, owner):
        if isinstance(piece[0], str):
            _, lhs, rhs = piece
            w = lhs.shape[2] // n
            part = lax.dynamic_slice_in_dim(lhs, owner * w, w, 2)
            return jnp.einsum("xrd,xrf->xdf", part, rhs, preferred_element_type=jnp.float32)
        g, axis = piece
        w = g.shape[axis] // n
        return lax.dynamic_slice_in_dim(g, owner * w, w, axis).astype(jnp.float32)

    def own(q):
        owner = ring_arr[q % n]
        return tuple(chunk(p, owner) for p in pieces)

    axes = [2 if isinstance(p[0], str) else split_axis(p[0].ndim, p[1]) for p in pieces]
    carries = carry if isinstance(carry, tuple) else (carry,) * len(pieces)

    def cast(vals):
        return tuple(v.astype(c) for v, c in zip(vals, carries))

    def wide(vals):
        return tuple(v.astype(jnp.float32) for v in vals)

    def plus(x, y):
        return tuple(u + v for u, v in zip(x, y))

    if n % 2 == 0:
        opposite = own(mypos + nf)
        got_f = lax.ppermute(cast(halves(opposite, axes, 0)), "dp", fwd)
        got_b = lax.ppermute(cast(halves(opposite, axes, 1)), "dp", bwd)
        got_f, got_b = lax.optimization_barrier((got_f, got_b))
        for s in range(1, nf):
            vf = own(mypos + nf - s)
            vb = own(mypos - nf + s)
            if s == 1:
                vf = joined(plus(halves(vf, axes, 0), wide(got_f)), halves(vf, axes, 1), axes)
                vb = joined(halves(vb, axes, 0), plus(halves(vb, axes, 1), wide(got_b)), axes)
            else:
                vf = plus(vf, wide(got_f))
                vb = plus(vb, wide(got_b))
            vf = cast(vf)
            vb = cast(vb)
            if taps is not None:
                taps.append((vf, vb))
            got_f = lax.ppermute(vf, "dp", fwd)
            got_b = lax.ppermute(vb, "dp", bwd)
            got_f, got_b = lax.optimization_barrier((got_f, got_b))
        last = (got_f, got_b)
        total = own(mypos)
        if nf == 1:
            total = plus(total, joined(wide(got_f), wide(got_b), axes))
        else:
            total = plus(plus(total, wide(got_f)), wide(got_b))
        return list(total), last

    def send(vals, got, perm):
        if got is not None:
            vals = plus(vals, wide(got))
        return lax.ppermute(cast(vals), "dp", perm)

    got_f = None
    got_b = None
    for s in range(nf):
        got_f = send(own(mypos + nf - s), got_f, fwd)
        if s < nb:
            got_b = send(own(mypos - nb + s), got_b, bwd)
            got_f, got_b = lax.optimization_barrier((got_f, got_b))
    last = (got_f, got_b)
    total = own(mypos)
    total = plus(total, wide(got_f))
    if got_b is not None:
        total = plus(total, wide(got_b))
    return list(total), last


def per_device(
    tokens,
    segment_ids,
    valid_lengths,
    cotangent,
    w_query,
    w_key,
    w_value,
    w_out,
    query_gain,
    key_gain,
    attn_gain,
    w_gate,
    w_up,
    w_down,
    mlp_gain,
    ring,
):
    f32 = jnp.float32
    bf16 = jnp.bfloat16
    rows, width = tokens.shape
    seg_row = segment_ids[0]
    length = valid_lengths[0]
    block = min(512, rows)
    count = rows // block
    scale = HEAD_DIM ** (-0.5)
    n_dp = len(ring)
    slab = attn_gain.shape[0]
    head_piece = query_gain.shape[0]

    def padded(g):
        return jnp.pad(g, (0, slab - g.shape[0]))

    gains = jnp.stack([padded(query_gain), padded(key_gain), attn_gain, mlp_gain])
    (qkvo, gains_full), seen = gather_group(
        [(jnp.stack([w_query, w_key, w_value, w_out.T]), 1), (gains, 1)], ring
    )
    wq, wk, wv, wo_t = qkvo[0], qkvo[1], qkvo[2], qkvo[3]
    gq = gains_full[0].reshape(n_dp, slab)[:, :head_piece].reshape(-1)
    gk = gains_full[1].reshape(n_dp, slab)[:, :head_piece].reshape(-1)
    ga = gains_full[2]
    gm = gains_full[3]
    (gu,), seen = gather_group([(jnp.stack([w_gate, w_up]), 1)], ring, after=seen)
    wg, wu = gu[0], gu[1]
    (wd_t,), seen = gather_group([(w_down.T, 0)], ring, after=seen)
    gq32 = gq.astype(f32)
    gk32 = gk.astype(f32)
    ga32 = ga.astype(f32)
    gm32 = gm.astype(f32)
    query = jnp.dot(tokens, wq, preferred_element_type=f32)
    keys = jnp.dot(tokens, wk, preferred_element_type=f32)
    values = jnp.dot(tokens, wv, preferred_element_type=f32).astype(bf16)
    query_sq, key_sq = lax.psum(
        (jnp.sum(query * query, axis=1), jnp.sum(keys * keys, axis=1)), "mp"
    )
    query_factor = lax.rsqrt(query_sq / width + EPS)[:, None]
    key_factor = lax.rsqrt(key_sq / width + EPS)[:, None]
    query_hat = query * query_factor
    key_hat = keys * key_factor
    heads = query.shape[1] // HEAD_DIM
    cosine, sine = rope_tables(rows, HEAD_DIM)
    query_rot = rotate((query_hat * gq32).reshape(rows, heads, HEAD_DIM), cosine, sine).astype(bf16)
    key_rot = rotate((key_hat * gk32).reshape(rows, heads, HEAD_DIM), cosine, sine).astype(bf16)
    values_h = values.reshape(rows, heads, HEAD_DIM)

    def block_scores(start):
        scores = jnp.einsum("qhe,khe->hqk", query_rot, key_rot, preferred_element_type=f32) * scale
        mask = allowed_block(start, block, seg_row, length)
        return (query_rot, jnp.where(mask[None], scores, -1e30))

    def forward_block(index):
        start = index * block
        q_blk, scores = block_scores(start)
        top = jnp.max(scores, axis=-1, keepdims=True)
        total = jnp.sum(jnp.exp(scores - top), axis=-1, keepdims=True)
        logsum = top + jnp.log(total)
        probs = jnp.exp(scores - logsum).astype(bf16)
        attended = jnp.einsum("hqk,khe->qhe", probs, values_h, preferred_element_type=f32)
        return (attended, logsum[..., 0])

    attended, logsums = lax.map(forward_block, jnp.arange(count))
    attended_b = attended.reshape(rows, heads * HEAD_DIM).astype(bf16)
    attn_partial = jnp.einsum("rc,dc->rd", attended_b, wo_t, preferred_element_type=f32)
    attn_total = branch_total(attn_partial)
    attn_hat, attn_factor = norm_forward(attn_total)
    hidden = tokens.astype(f32) + attn_hat * ga32
    hidden_b = hidden.astype(bf16)
    gate = jnp.dot(hidden_b, wg, preferred_element_type=f32)
    up = jnp.dot(hidden_b, wu, preferred_element_type=f32)
    active = jax.nn.silu(gate)
    mixed_b = (active * up).astype(bf16)
    mlp_partial = jnp.einsum("rf,df->rd", mixed_b, wd_t, preferred_element_type=f32)
    mlp_total = branch_total(mlp_partial)
    mlp_hat, mlp_factor = norm_forward(mlp_total)
    layer_out = (hidden + mlp_hat * gm32).astype(bf16)
    grad_out = cotangent.astype(f32)
    d_mlp, grad_mg = norm_back(grad_out, mlp_hat, mlp_factor, gm32)
    d_mlp_b = d_mlp.astype(bf16)
    (grad_wd_t_s,), sent = scatter_group([("prod", d_mlp_b[None], mixed_b[None])], ring)
    grad_wd_s = grad_wd_t_s[0].T
    d_mixed = jnp.einsum("rd,df->rf", d_mlp_b, wd_t, preferred_element_type=f32)
    sigma = jax.nn.sigmoid(gate)
    d_gate = (d_mixed * up * sigma * (1.0 + gate * (1.0 - sigma))).astype(bf16)
    d_up = (d_mixed * active).astype(bf16)
    grad_gu = ("prod", jnp.stack([hidden_b, hidden_b]), jnp.stack([d_gate, d_up]))
    gu_taps = []
    (grad_gu_s,), sent = scatter_group([grad_gu], ring, after=sent, taps=gu_taps)
    grad_wg_s, grad_wu_s = grad_gu_s[0], grad_gu_s[1]
    hidden_partial = jnp.einsum("rf,df->rd", d_gate, wg, preferred_element_type=f32) + jnp.einsum(
        "rf,df->rd", d_up, wu, preferred_element_type=f32
    )
    d_hidden = grad_out + input_total(hidden_partial)
    d_attn, grad_ag = norm_back(d_hidden, attn_hat, attn_factor, ga32)
    d_attn_b = d_attn.astype(bf16)
    if gu_taps:
        d_attn_b, _ = lax.optimization_barrier((d_attn_b, gu_taps[0]))
    d_attended = jnp.einsum("rd,dc->rc", d_attn_b, wo_t, preferred_element_type=f32).astype(bf16)
    d_attended = d_attended.reshape(rows, heads, HEAD_DIM)

    def backward_block(carry, index):
        key_acc, value_acc = carry
        start = index * block
        q_blk, scores = block_scores(start)
        logsum = lax.dynamic_index_in_dim(logsums, index, 0, keepdims=False)
        probs = jnp.exp(scores - logsum[..., None])
        value_acc = value_acc + jnp.einsum(
            "hqk,qhe->khe", probs.astype(bf16), d_attended, preferred_element_type=f32
        )
        d_probs = jnp.einsum("qhe,khe->hqk", d_attended, values_h, preferred_element_type=f32)
        delta = jnp.sum(probs * d_probs, axis=-1, keepdims=True)
        d_scores = (probs * (d_probs - delta)).astype(bf16)
        d_query_blk = (
            jnp.einsum("hqk,khe->qhe", d_scores, key_rot, preferred_element_type=f32) * scale
        )
        key_acc = (
            key_acc
            + jnp.einsum("hqk,qhe->khe", d_scores, q_blk, preferred_element_type=f32) * scale
        )
        return ((key_acc, value_acc), d_query_blk)

    empty = jnp.zeros((rows, heads, HEAD_DIM), f32)
    (d_key_rot, d_values), d_query_rot = lax.scan(backward_block, (empty, empty), jnp.arange(count))
    d_query_rot = d_query_rot.reshape(rows, heads, HEAD_DIM)
    d_values_b = d_values.reshape(rows, heads * HEAD_DIM).astype(bf16)
    d_query_n = rotate_back(d_query_rot, cosine, sine).reshape(rows, heads * HEAD_DIM)
    d_key_n = rotate_back(d_key_rot, cosine, sine).reshape(rows, heads * HEAD_DIM)
    grad_gq = jnp.sum(d_query_n * query_hat, axis=0)
    grad_gk = jnp.sum(d_key_n * key_hat, axis=0)
    d_query_hat = d_query_n * gq32
    d_key_hat = d_key_n * gk32
    query_inner, key_inner = lax.psum(
        (jnp.sum(d_query_hat * query_hat, axis=1), jnp.sum(d_key_hat * key_hat, axis=1)), "mp"
    )
    d_query_b = (query_factor * (d_query_hat - query_hat * (query_inner / width)[:, None])).astype(
        bf16
    )
    d_key_b = (key_factor * (d_key_hat - key_hat * (key_inner / width)[:, None])).astype(bf16)
    grad_qkvo = (
        "prod",
        jnp.stack([tokens, tokens, tokens, d_attn_b]),
        jnp.stack([d_query_b, d_key_b, d_values_b, attended_b]),
    )

    def spread(g):
        return jnp.pad(g.reshape(n_dp, -1), ((0, 0), (0, slab - g.shape[0] // n_dp))).reshape(-1)

    grad_gains = jnp.stack([spread(grad_gq), spread(grad_gk), grad_ag, grad_mg])
    (grad_qkvo_s, grad_gains_s), sent = scatter_group(
        [grad_qkvo, (grad_gains, 1)], ring, carry=(jnp.bfloat16, jnp.float32), after=sent
    )
    grad_wq_s, grad_wk_s, grad_wv_s = grad_qkvo_s[0], grad_qkvo_s[1], grad_qkvo_s[2]
    grad_wo_s = grad_qkvo_s[3].T
    grad_gq_s = grad_gains_s[0, :head_piece]
    grad_gk_s = grad_gains_s[1, :head_piece]
    grad_ag_s = grad_gains_s[2]
    grad_mg_s = grad_gains_s[3]
    input_part = jnp.einsum("rc,dc->rd", d_query_b, wq, preferred_element_type=f32)
    input_part = input_part + jnp.einsum("rc,dc->rd", d_key_b, wk, preferred_element_type=f32)
    input_part = input_part + jnp.einsum("rc,dc->rd", d_values_b, wv, preferred_element_type=f32)
    input_grad = d_hidden + input_total(input_part)
    return (
        layer_out,
        input_grad,
        grad_wq_s,
        grad_wk_s,
        grad_wv_s,
        grad_wo_s,
        grad_gq_s,
        grad_gk_s,
        grad_ag_s,
        grad_wg_s,
        grad_wu_s,
        grad_wd_s,
        grad_mg_s,
    )


def solution(mesh):
    placed = (
        P("dp", None),
        P("dp", None),
        P("dp"),
        P("dp", None),
        P("dp", "mp"),
        P("dp", "mp"),
        P("dp", "mp"),
        P("mp", "dp"),
        P(("mp", "dp")),
        P(("mp", "dp")),
        P("dp"),
        P("dp", "mp"),
        P("dp", "mp"),
        P("mp", "dp"),
        P("dp"),
    )
    ring = ring_order(mesh)
    return jax.shard_map(
        functools.partial(per_device, ring=ring),
        mesh=mesh,
        in_specs=placed,
        out_specs=(
            P("dp", None),
            P("dp", None),
            P("dp", "mp"),
            P("dp", "mp"),
            P("dp", "mp"),
            P("mp", "dp"),
            P(("mp", "dp")),
            P(("mp", "dp")),
            P("dp"),
            P("dp", "mp"),
            P("dp", "mp"),
            P("mp", "dp"),
            P("dp"),
        ),
        check_vma=False,
    )
```

```python
import functools

import jax
import jax.numpy as jnp
import numpy as np
from jax import lax
from jax.sharding import PartitionSpec as P

HEAD_DIM = 128


EPS = 1e-06
THETA = 500000.0


def rope_tables(rows, head_dim):
    half = head_dim // 2
    inverse = THETA ** (-(jnp.arange(half).astype(jnp.float32) * 2.0) / head_dim)
    angles = jnp.arange(rows).astype(jnp.float32)[:, None] * inverse[None, :]
    return (jnp.cos(angles)[:, None, :], jnp.sin(angles)[:, None, :])


def rotate(value, cosine, sine):
    half = value.shape[-1] // 2
    first, second = (value[..., :half], value[..., half:])
    return jnp.concatenate(
        [first * cosine - second * sine, second * cosine + first * sine], axis=-1
    )


def rotate_back(grad, cosine, sine):
    half = grad.shape[-1] // 2
    first, second = (grad[..., :half], grad[..., half:])
    return jnp.concatenate(
        [first * cosine + second * sine, second * cosine - first * sine], axis=-1
    )


def allowed_block(start, block, seg_row, length):
    query_pos = start + jnp.arange(block)
    key_pos = jnp.arange(seg_row.shape[0])
    same = seg_row[:, None] == seg_row[None, :]
    causal = key_pos[None, :] <= query_pos[:, None]
    inside = key_pos[None, :] < length
    return same & causal & inside | (key_pos[None, :] == query_pos[:, None])


def mp_allreduce(x, carry=jnp.bfloat16):
    m = lax.axis_size("mp")
    me = lax.axis_index("mp")
    core = me % 2
    chips = m // 2
    chip = me // 2
    half = x.shape[1] // 2
    pair = [(i, i ^ 1) for i in range(m)]
    mine = lax.dynamic_slice_in_dim(x, core * half, half, 1)
    other = lax.dynamic_slice_in_dim(x, (1 - core) * half, half, 1)
    part = mine + lax.ppermute(other, "mp", pair)
    if chips == 2:
        low = part.astype(carry)
        got = lax.ppermute(low, "mp", [(i, i ^ 2) for i in range(m)])
        part = low.astype(jnp.float32) + got.astype(jnp.float32)
    elif chips > 2:
        low = part.astype(carry)
        got = [low]
        for k in range(1, chips):
            perm = [(c * 2 + r, ((c + k) % chips) * 2 + r) for c in range(chips) for r in range(2)]
            got.append(lax.ppermute(low, "mp", perm))
        stack = jnp.stack(got)
        order = (chip - jnp.arange(chips)) % chips
        ordered = jnp.take(stack, order, axis=0).astype(jnp.float32)
        part = ordered[0]
        for k in range(1, chips):
            part = part + ordered[k]
    swapped = lax.ppermute(part, "mp", pair)
    first = jnp.where(core == 0, part, swapped)
    second = jnp.where(core == 0, swapped, part)
    return jnp.concatenate([first, second], axis=1)


def branch_total(partial_sum):
    return mp_allreduce(partial_sum)


def input_total(partial_sum):
    return mp_allreduce(partial_sum)


def norm_forward(total):
    factor = lax.rsqrt(jnp.mean(total * total, axis=1, keepdims=True) + EPS)
    return (total * factor, factor)


def norm_back(grad, normed, factor, gain):
    grad_gain = jnp.sum(grad * normed, axis=0)
    scaled = grad * gain
    inner = jnp.mean(scaled * normed, axis=1, keepdims=True)
    return (factor * (scaled - normed * inner), grad_gain)


def ring_order(mesh):
    column = [mesh.devices[i, 0] for i in range(mesh.devices.shape[0])]
    count = len(column)
    try:
        coords = [tuple(d.coords) for d in column]
    except AttributeError:
        return list(range(count))
    axes = [a for a in range(len(coords[0])) if len({c[a] for c in coords}) > 1]
    if len(axes) != 2:
        return list(range(count))
    sizes = {a: len({c[a] for c in coords}) for a in axes}
    even = [a for a in axes if sizes[a] % 2 == 0]
    if not even:
        return list(range(count))
    outer = min(even, key=lambda a: sizes[a])
    inner = [a for a in axes if a != outer][0]
    lo = {a: min(c[a] for c in coords) for a in axes}
    where = {(c[outer] - lo[outer], c[inner] - lo[inner]): i for i, c in enumerate(coords)}
    order = []
    for o in range(sizes[outer]):
        steps = range(sizes[inner]) if o % 2 == 0 else reversed(range(sizes[inner]))
        for k in steps:
            order.append(where[(o, k)])
    if sorted(order) != list(range(count)):
        return list(range(count))
    return order


def ring_steps(ring):
    n = len(ring)
    pos_of = [ring.index(d) for d in range(n)]
    mypos = jnp.asarray(pos_of, jnp.int32)[lax.axis_index("dp")]
    fwd = [(ring[p], ring[(p + 1) % n]) for p in range(n)]
    bwd = [(ring[p], ring[(p - 1) % n]) for p in range(n)]
    nf = n // 2
    return n, mypos, fwd, bwd, nf, n - 1 - nf


def split_axis(ndim, axis):
    return ndim - 1 if axis != ndim - 1 else 0


def halves(values, axes, which):
    out = []
    for x, ax in zip(values, axes):
        h = x.shape[ax] // 2
        out.append(lax.slice_in_dim(x, which * h, (which + 1) * h, axis=ax))
    return tuple(out)


def joined(first, second, axes):
    return tuple(jnp.concatenate([x, y], axis=ax) for x, y, ax in zip(first, second, axes))


def gather_group(pieces, ring, after=None):
    locals_ = tuple(p.astype(jnp.bfloat16) for p, _ in pieces)
    if after is not None:
        locals_, _ = lax.optimization_barrier((locals_, after))
    n, mypos, fwd, bwd, nf, nb = ring_steps(ring)
    ring_arr = jnp.asarray(ring, jnp.int32)
    axes = [split_axis(p.ndim, axis) for p, axis in pieces]
    parts = {0: locals_}
    a = locals_
    b = locals_
    if n % 2 == 0:
        for s in range(nf - 1):
            a = lax.ppermute(a, "dp", fwd)
            b = lax.ppermute(b, "dp", bwd)
            a, b = lax.optimization_barrier((a, b))
            parts[-(s + 1)] = a
            parts[s + 1] = b
        ha = lax.ppermute(halves(a, axes, 0), "dp", fwd)
        hb = lax.ppermute(halves(b, axes, 1), "dp", bwd)
        ha, hb = lax.optimization_barrier((ha, hb))
        parts[-nf] = (ha, hb)
        last = (ha, hb)
        arrival = [0]
        for s in range(nf - 1):
            arrival += [-(s + 1), s + 1]
        arrival.append(-nf)
    else:
        for s in range(nf):
            a = lax.ppermute(a, "dp", fwd)
            if s < nb:
                b = lax.ppermute(b, "dp", bwd)
                a, b = lax.optimization_barrier((a, b))
                parts[s + 1] = b
            parts[-(s + 1)] = a
        last = (a, b)
        arrival = [0]
        for s in range(nf):
            arrival.append(-(s + 1))
            if s < nb:
                arrival.append(s + 1)
    out = []
    for i, (p, axis) in enumerate(pieces):
        shape = list(p.shape)
        width = shape[axis]
        shape[axis] *= n
        first_in = parts[arrival[1]] if len(arrival) > 1 else parts[0]
        first_in = first_in[0] if isinstance(first_in[0], tuple) else first_in
        seed = first_in[i].reshape(-1)[:1] * 0
        full = jnp.broadcast_to(seed.reshape((1,) * p.ndim), shape)
        for k in arrival:
            owner = ring_arr[(mypos + k) % n]
            if n % 2 == 0 and k == -nf:
                first, second = parts[k][0][i], parts[k][1][i]
                start = [0] * p.ndim
                start[axis] = owner * width
                full = lax.dynamic_update_slice(full, first, start)
                start[axes[i]] = first.shape[axes[i]]
                full = lax.dynamic_update_slice(full, second, start)
            else:
                full = lax.dynamic_update_slice_in_dim(full, parts[k][i], owner * width, axis)
        out.append(full)
    return out, last


def scatter_group(pieces, ring, carry=jnp.bfloat16, after=None, taps=None):
    if after is not None:
        arrays = tuple(p[1:] if isinstance(p[0], str) else (p[0],) for p in pieces)
        arrays, _ = lax.optimization_barrier((arrays, after))
        pieces = [
            ("prod",) + tuple(a) if isinstance(p[0], str) else (a[0], p[1]) for p, a in zip(pieces, arrays)
        ]
    n, mypos, fwd, bwd, nf, nb = ring_steps(ring)
    ring_arr = jnp.asarray(ring, jnp.int32)

    def chunk(piece, owner):
        if isinstance(piece[0], str):
            _, lhs, rhs = piece
            w = lhs.shape[2] // n
            part = lax.dynamic_slice_in_dim(lhs, owner * w, w, 2)
            return jnp.einsum("xrd,xrf->xdf", part, rhs, preferred_element_type=jnp.float32)
        g, axis = piece
        w = g.shape[axis] // n
        return lax.dynamic_slice_in_dim(g, owner * w, w, axis).astype(jnp.float32)

    def own(q):
        owner = ring_arr[q % n]
        return tuple(chunk(p, owner) for p in pieces)

    axes = [2 if isinstance(p[0], str) else split_axis(p[0].ndim, p[1]) for p in pieces]
    carries = carry if isinstance(carry, tuple) else (carry,) * len(pieces)

    def cast(vals):
        return tuple(v.astype(c) for v, c in zip(vals, carries))

    def wide(vals):
        return tuple(v.astype(jnp.float32) for v in vals)

    def plus(x, y):
        return tuple(u + v for u, v in zip(x, y))

    if n % 2 == 0:
        opposite = own(mypos + nf)
        got_f = lax.ppermute(cast(halves(opposite, axes, 0)), "dp", fwd)
        got_b = lax.ppermute(cast(halves(opposite, axes, 1)), "dp", bwd)
        got_f, got_b = lax.optimization_barrier((got_f, got_b))
        for s in range(1, nf):
            vf = own(mypos + nf - s)
            vb = own(mypos - nf + s)
            if s == 1:
                vf = joined(plus(halves(vf, axes, 0), wide(got_f)), halves(vf, axes, 1), axes)
                vb = joined(halves(vb, axes, 0), plus(halves(vb, axes, 1), wide(got_b)), axes)
            else:
                vf = plus(vf, wide(got_f))
                vb = plus(vb, wide(got_b))
            vf = cast(vf)
            vb = cast(vb)
            if taps is not None:
                taps.append((vf, vb))
            got_f = lax.ppermute(vf, "dp", fwd)
            got_b = lax.ppermute(vb, "dp", bwd)
            got_f, got_b = lax.optimization_barrier((got_f, got_b))
        last = (got_f, got_b)
        total = own(mypos)
        if nf == 1:
            total = plus(total, joined(wide(got_f), wide(got_b), axes))
        else:
            total = plus(plus(total, wide(got_f)), wide(got_b))
        return list(total), last

    def send(vals, got, perm):
        if got is not None:
            vals = plus(vals, wide(got))
        return lax.ppermute(cast(vals), "dp", perm)

    got_f = None
    got_b = None
    for s in range(nf):
        got_f = send(own(mypos + nf - s), got_f, fwd)
        if s < nb:
            got_b = send(own(mypos - nb + s), got_b, bwd)
            got_f, got_b = lax.optimization_barrier((got_f, got_b))
    last = (got_f, got_b)
    total = own(mypos)
    total = plus(total, wide(got_f))
    if got_b is not None:
        total = plus(total, wide(got_b))
    return list(total), last


def per_device(
    tokens,
    segment_ids,
    valid_lengths,
    cotangent,
    w_query,
    w_key,
    w_value,
    w_out,
    query_gain,
    key_gain,
    attn_gain,
    w_gate,
    w_up,
    w_down,
    mlp_gain,
    ring,
):
    f32 = jnp.float32
    bf16 = jnp.bfloat16
    rows, width = tokens.shape
    seg_row = segment_ids[0]
    length = valid_lengths[0]
    block = min(512, rows)
    count = rows // block
    scale = HEAD_DIM ** (-0.5)
    n_dp = len(ring)
    slab = attn_gain.shape[0]
    head_piece = query_gain.shape[0]

    def padded(g):
        return jnp.pad(g, (0, slab - g.shape[0]))

    gains = jnp.stack([padded(query_gain), padded(key_gain), attn_gain, mlp_gain])
    (qkvo, gains_full), seen = gather_group(
        [(jnp.stack([w_query, w_key, w_value, w_out.T]), 1), (gains, 1)], ring
    )
    wq, wk, wv, wo_t = qkvo[0], qkvo[1], qkvo[2], qkvo[3]
    gq = gains_full[0].reshape(n_dp, slab)[:, :head_piece].reshape(-1)
    gk = gains_full[1].reshape(n_dp, slab)[:, :head_piece].reshape(-1)
    ga = gains_full[2]
    gm = gains_full[3]
    (gu,), seen = gather_group([(jnp.stack([w_gate, w_up]), 1)], ring, after=seen)
    wg, wu = gu[0], gu[1]
    (wd_t,), seen = gather_group([(w_down.T, 0)], ring, after=seen)
    gq32 = gq.astype(f32)
    gk32 = gk.astype(f32)
    ga32 = ga.astype(f32)
    gm32 = gm.astype(f32)
    query = jnp.dot(tokens, wq, preferred_element_type=f32)
    keys = jnp.dot(tokens, wk, preferred_element_type=f32)
    values = jnp.dot(tokens, wv, preferred_element_type=f32).astype(bf16)
    query_sq, key_sq = lax.psum(
        (jnp.sum(query * query, axis=1), jnp.sum(keys * keys, axis=1)), "mp"
    )
    query_factor = lax.rsqrt(query_sq / width + EPS)[:, None]
    key_factor = lax.rsqrt(key_sq / width + EPS)[:, None]
    query_hat = query * query_factor
    key_hat = keys * key_factor
    heads = query.shape[1] // HEAD_DIM
    cosine, sine = rope_tables(rows, HEAD_DIM)
    query_rot = rotate((query_hat * gq32).reshape(rows, heads, HEAD_DIM), cosine, sine).astype(bf16)
    key_rot = rotate((key_hat * gk32).reshape(rows, heads, HEAD_DIM), cosine, sine).astype(bf16)
    values_h = values.reshape(rows, heads, HEAD_DIM)

    def block_scores(start):
        scores = jnp.einsum("qhe,khe->hqk", query_rot, key_rot, preferred_element_type=f32) * scale
        mask = allowed_block(start, block, seg_row, length)
        return (query_rot, jnp.where(mask[None], scores, -1e30))

    def forward_block(index):
        start = index * block
        q_blk, scores = block_scores(start)
        top = jnp.max(scores, axis=-1, keepdims=True)
        total = jnp.sum(jnp.exp(scores - top), axis=-1, keepdims=True)
        logsum = top + jnp.log(total)
        probs = jnp.exp(scores - logsum).astype(bf16)
        attended = jnp.einsum("hqk,khe->qhe", probs, values_h, preferred_element_type=f32)
        return (attended, logsum[..., 0])

    attended, logsums = lax.map(forward_block, jnp.arange(count))
    attended_b = attended.reshape(rows, heads * HEAD_DIM).astype(bf16)
    attn_partial = jnp.einsum("rc,dc->rd", attended_b, wo_t, preferred_element_type=f32)
    attn_total = branch_total(attn_partial)
    attn_hat, attn_factor = norm_forward(attn_total)
    hidden = tokens.astype(f32) + attn_hat * ga32
    hidden_b = hidden.astype(bf16)
    gate = jnp.dot(hidden_b, wg, preferred_element_type=f32)
    up = jnp.dot(hidden_b, wu, preferred_element_type=f32)
    active = jax.nn.silu(gate)
    mixed_b = (active * up).astype(bf16)
    split = rows // 2 if rows % 16 == 0 else rows
    mlp_total = jnp.concatenate(
        [
            branch_total(
                jnp.einsum("rf,df->rd", mixed_b[i : i + split], wd_t, preferred_element_type=f32)
            )
            for i in range(0, rows, split)
        ],
        axis=0,
    )
    mlp_hat, mlp_factor = norm_forward(mlp_total)
    layer_out = (hidden + mlp_hat * gm32).astype(bf16)
    grad_out = cotangent.astype(f32)
    d_mlp, grad_mg = norm_back(grad_out, mlp_hat, mlp_factor, gm32)
    d_mlp_b = d_mlp.astype(bf16)
    (grad_wd_t_s,), sent = scatter_group([("prod", d_mlp_b[None], mixed_b[None])], ring)
    grad_wd_s = grad_wd_t_s[0].T
    d_mixed = jnp.einsum("rd,df->rf", d_mlp_b, wd_t, preferred_element_type=f32)
    sigma = jax.nn.sigmoid(gate)
    d_gate = (d_mixed * up * sigma * (1.0 + gate * (1.0 - sigma))).astype(bf16)
    d_up = (d_mixed * active).astype(bf16)
    grad_gu = ("prod", jnp.stack([hidden_b, hidden_b]), jnp.stack([d_gate, d_up]))
    gu_taps = []
    (grad_gu_s,), sent = scatter_group([grad_gu], ring, after=sent, taps=gu_taps)
    grad_wg_s, grad_wu_s = grad_gu_s[0], grad_gu_s[1]
    hidden_partial = jnp.einsum("rf,df->rd", d_gate, wg, preferred_element_type=f32) + jnp.einsum(
        "rf,df->rd", d_up, wu, preferred_element_type=f32
    )
    d_hidden = grad_out + input_total(hidden_partial)
    d_attn, grad_ag = norm_back(d_hidden, attn_hat, attn_factor, ga32)
    d_attn_b = d_attn.astype(bf16)
    if gu_taps:
        d_attn_b, _ = lax.optimization_barrier((d_attn_b, gu_taps[0]))
    d_attended = jnp.einsum("rd,dc->rc", d_attn_b, wo_t, preferred_element_type=f32).astype(bf16)
    d_attended = d_attended.reshape(rows, heads, HEAD_DIM)

    def backward_block(carry, index):
        key_acc, value_acc = carry
        start = index * block
        q_blk, scores = block_scores(start)
        logsum = lax.dynamic_index_in_dim(logsums, index, 0, keepdims=False)
        probs = jnp.exp(scores - logsum[..., None])
        value_acc = value_acc + jnp.einsum(
            "hqk,qhe->khe", probs.astype(bf16), d_attended, preferred_element_type=f32
        )
        d_probs = jnp.einsum("qhe,khe->hqk", d_attended, values_h, preferred_element_type=f32)
        delta = jnp.sum(probs * d_probs, axis=-1, keepdims=True)
        d_scores = (probs * (d_probs - delta)).astype(bf16)
        d_query_blk = (
            jnp.einsum("hqk,khe->qhe", d_scores, key_rot, preferred_element_type=f32) * scale
        )
        key_acc = (
            key_acc
            + jnp.einsum("hqk,qhe->khe", d_scores, q_blk, preferred_element_type=f32) * scale
        )
        return ((key_acc, value_acc), d_query_blk)

    empty = jnp.zeros((rows, heads, HEAD_DIM), f32)
    (d_key_rot, d_values), d_query_rot = lax.scan(backward_block, (empty, empty), jnp.arange(count))
    d_query_rot = d_query_rot.reshape(rows, heads, HEAD_DIM)
    d_values_b = d_values.reshape(rows, heads * HEAD_DIM).astype(bf16)
    d_query_n = rotate_back(d_query_rot, cosine, sine).reshape(rows, heads * HEAD_DIM)
    d_key_n = rotate_back(d_key_rot, cosine, sine).reshape(rows, heads * HEAD_DIM)
    grad_gq = jnp.sum(d_query_n * query_hat, axis=0)
    grad_gk = jnp.sum(d_key_n * key_hat, axis=0)
    d_query_hat = d_query_n * gq32
    d_key_hat = d_key_n * gk32
    query_inner, key_inner = lax.psum(
        (jnp.sum(d_query_hat * query_hat, axis=1), jnp.sum(d_key_hat * key_hat, axis=1)), "mp"
    )
    d_query_b = (query_factor * (d_query_hat - query_hat * (query_inner / width)[:, None])).astype(
        bf16
    )
    d_key_b = (key_factor * (d_key_hat - key_hat * (key_inner / width)[:, None])).astype(bf16)
    grad_qkvo = (
        "prod",
        jnp.stack([tokens, tokens, tokens, d_attn_b]),
        jnp.stack([d_query_b, d_key_b, d_values_b, attended_b]),
    )

    def spread(g):
        return jnp.pad(g.reshape(n_dp, -1), ((0, 0), (0, slab - g.shape[0] // n_dp))).reshape(-1)

    grad_gains = jnp.stack([spread(grad_gq), spread(grad_gk), grad_ag, grad_mg])
    (grad_qkvo_s, grad_gains_s), sent = scatter_group(
        [grad_qkvo, (grad_gains, 1)], ring, carry=(jnp.bfloat16, jnp.float32), after=sent
    )
    grad_wq_s, grad_wk_s, grad_wv_s = grad_qkvo_s[0], grad_qkvo_s[1], grad_qkvo_s[2]
    grad_wo_s = grad_qkvo_s[3].T
    grad_gq_s = grad_gains_s[0, :head_piece]
    grad_gk_s = grad_gains_s[1, :head_piece]
    grad_ag_s = grad_gains_s[2]
    grad_mg_s = grad_gains_s[3]
    input_part = jnp.einsum("rc,dc->rd", d_query_b, wq, preferred_element_type=f32)
    input_part = input_part + jnp.einsum("rc,dc->rd", d_key_b, wk, preferred_element_type=f32)
    input_part = input_part + jnp.einsum("rc,dc->rd", d_values_b, wv, preferred_element_type=f32)
    input_grad = d_hidden + input_total(input_part)
    return (
        layer_out,
        input_grad,
        grad_wq_s,
        grad_wk_s,
        grad_wv_s,
        grad_wo_s,
        grad_gq_s,
        grad_gk_s,
        grad_ag_s,
        grad_wg_s,
        grad_wu_s,
        grad_wd_s,
        grad_mg_s,
    )


def solution(mesh):
    placed = (
        P("dp", None),
        P("dp", None),
        P("dp"),
        P("dp", None),
        P("dp", "mp"),
        P("dp", "mp"),
        P("dp", "mp"),
        P("mp", "dp"),
        P(("mp", "dp")),
        P(("mp", "dp")),
        P("dp"),
        P("dp", "mp"),
        P("dp", "mp"),
        P("mp", "dp"),
        P("dp"),
    )
    ring = ring_order(mesh)
    return jax.shard_map(
        functools.partial(per_device, ring=ring),
        mesh=mesh,
        in_specs=placed,
        out_specs=(
            P("dp", None),
            P("dp", None),
            P("dp", "mp"),
            P("dp", "mp"),
            P("dp", "mp"),
            P("mp", "dp"),
            P(("mp", "dp")),
            P(("mp", "dp")),
            P("dp"),
            P("dp", "mp"),
            P("dp", "mp"),
            P("mp", "dp"),
            P("dp"),
        ),
        check_vma=False,
    )
```

```python
import functools

import jax
import jax.numpy as jnp
import numpy as np
from jax import lax
from jax.sharding import PartitionSpec as P

HEAD_DIM = 128


EPS = 1e-06
THETA = 500000.0


def rope_tables(rows, head_dim):
    half = head_dim // 2
    inverse = THETA ** (-(jnp.arange(half).astype(jnp.float32) * 2.0) / head_dim)
    angles = jnp.arange(rows).astype(jnp.float32)[:, None] * inverse[None, :]
    return (jnp.cos(angles)[:, None, :], jnp.sin(angles)[:, None, :])


def rotate(value, cosine, sine):
    half = value.shape[-1] // 2
    first, second = (value[..., :half], value[..., half:])
    return jnp.concatenate(
        [first * cosine - second * sine, second * cosine + first * sine], axis=-1
    )


def rotate_back(grad, cosine, sine):
    half = grad.shape[-1] // 2
    first, second = (grad[..., :half], grad[..., half:])
    return jnp.concatenate(
        [first * cosine + second * sine, second * cosine - first * sine], axis=-1
    )


def allowed_block(start, block, seg_row, length):
    query_pos = start + jnp.arange(block)
    key_pos = jnp.arange(seg_row.shape[0])
    same = seg_row[:, None] == seg_row[None, :]
    causal = key_pos[None, :] <= query_pos[:, None]
    inside = key_pos[None, :] < length
    return same & causal & inside | (key_pos[None, :] == query_pos[:, None])


def mp_allreduce(x, carry=jnp.bfloat16):
    m = lax.axis_size("mp")
    me = lax.axis_index("mp")
    core = me % 2
    chips = m // 2
    chip = me // 2
    half = x.shape[1] // 2
    pair = [(i, i ^ 1) for i in range(m)]
    mine = lax.dynamic_slice_in_dim(x, core * half, half, 1)
    other = lax.dynamic_slice_in_dim(x, (1 - core) * half, half, 1)
    part = mine + lax.ppermute(other, "mp", pair)
    if chips == 2:
        low = part.astype(carry)
        got = lax.ppermute(low, "mp", [(i, i ^ 2) for i in range(m)])
        part = low.astype(jnp.float32) + got.astype(jnp.float32)
    elif chips > 2:
        low = part.astype(carry)
        got = [low]
        for k in range(1, chips):
            perm = [(c * 2 + r, ((c + k) % chips) * 2 + r) for c in range(chips) for r in range(2)]
            got.append(lax.ppermute(low, "mp", perm))
        stack = jnp.stack(got)
        order = (chip - jnp.arange(chips)) % chips
        ordered = jnp.take(stack, order, axis=0).astype(jnp.float32)
        part = ordered[0]
        for k in range(1, chips):
            part = part + ordered[k]
    swapped = lax.ppermute(part, "mp", pair)
    first = jnp.where(core == 0, part, swapped)
    second = jnp.where(core == 0, swapped, part)
    return jnp.concatenate([first, second], axis=1)


def branch_total(partial_sum):
    return mp_allreduce(partial_sum)


def input_total(partial_sum):
    return mp_allreduce(partial_sum)


def norm_forward(total):
    factor = lax.rsqrt(jnp.mean(total * total, axis=1, keepdims=True) + EPS)
    return (total * factor, factor)


def norm_back(grad, normed, factor, gain):
    grad_gain = jnp.sum(grad * normed, axis=0)
    scaled = grad * gain
    inner = jnp.mean(scaled * normed, axis=1, keepdims=True)
    return (factor * (scaled - normed * inner), grad_gain)


def ring_order(mesh):
    column = [mesh.devices[i, 0] for i in range(mesh.devices.shape[0])]
    count = len(column)
    try:
        coords = [tuple(d.coords) for d in column]
    except AttributeError:
        return list(range(count))
    axes = [a for a in range(len(coords[0])) if len({c[a] for c in coords}) > 1]
    if len(axes) != 2:
        return list(range(count))
    sizes = {a: len({c[a] for c in coords}) for a in axes}
    even = [a for a in axes if sizes[a] % 2 == 0]
    if not even:
        return list(range(count))
    outer = min(even, key=lambda a: sizes[a])
    inner = [a for a in axes if a != outer][0]
    lo = {a: min(c[a] for c in coords) for a in axes}
    where = {(c[outer] - lo[outer], c[inner] - lo[inner]): i for i, c in enumerate(coords)}
    order = []
    for o in range(sizes[outer]):
        steps = range(sizes[inner]) if o % 2 == 0 else reversed(range(sizes[inner]))
        for k in steps:
            order.append(where[(o, k)])
    if sorted(order) != list(range(count)):
        return list(range(count))
    return order


def ring_steps(ring):
    n = len(ring)
    pos_of = [ring.index(d) for d in range(n)]
    mypos = jnp.asarray(pos_of, jnp.int32)[lax.axis_index("dp")]
    fwd = [(ring[p], ring[(p + 1) % n]) for p in range(n)]
    bwd = [(ring[p], ring[(p - 1) % n]) for p in range(n)]
    nf = n // 2
    return n, mypos, fwd, bwd, nf, n - 1 - nf


def split_axis(ndim, axis):
    return ndim - 1 if axis != ndim - 1 else 0


def halves(values, axes, which):
    out = []
    for x, ax in zip(values, axes):
        h = x.shape[ax] // 2
        out.append(lax.slice_in_dim(x, which * h, (which + 1) * h, axis=ax))
    return tuple(out)


def joined(first, second, axes):
    return tuple(jnp.concatenate([x, y], axis=ax) for x, y, ax in zip(first, second, axes))


def gather_group(pieces, ring, after=None):
    locals_ = tuple(p.astype(jnp.bfloat16) for p, _ in pieces)
    if after is not None:
        locals_, _ = lax.optimization_barrier((locals_, after))
    n, mypos, fwd, bwd, nf, nb = ring_steps(ring)
    ring_arr = jnp.asarray(ring, jnp.int32)
    axes = [split_axis(p.ndim, axis) for p, axis in pieces]
    parts = {0: locals_}
    a = locals_
    b = locals_
    if n % 2 == 0:
        for s in range(nf - 1):
            a = lax.ppermute(a, "dp", fwd)
            b = lax.ppermute(b, "dp", bwd)
            a, b = lax.optimization_barrier((a, b))
            parts[-(s + 1)] = a
            parts[s + 1] = b
        ha = lax.ppermute(halves(a, axes, 0), "dp", fwd)
        hb = lax.ppermute(halves(b, axes, 1), "dp", bwd)
        ha, hb = lax.optimization_barrier((ha, hb))
        parts[-nf] = (ha, hb)
        last = (ha, hb)
        arrival = [0]
        for s in range(nf - 1):
            arrival += [-(s + 1), s + 1]
        arrival.append(-nf)
    else:
        for s in range(nf):
            a = lax.ppermute(a, "dp", fwd)
            if s < nb:
                b = lax.ppermute(b, "dp", bwd)
                a, b = lax.optimization_barrier((a, b))
                parts[s + 1] = b
            parts[-(s + 1)] = a
        last = (a, b)
        arrival = [0]
        for s in range(nf):
            arrival.append(-(s + 1))
            if s < nb:
                arrival.append(s + 1)
    out = []
    for i, (p, axis) in enumerate(pieces):
        shape = list(p.shape)
        width = shape[axis]
        shape[axis] *= n
        first_in = parts[arrival[1]] if len(arrival) > 1 else parts[0]
        first_in = first_in[0] if isinstance(first_in[0], tuple) else first_in
        seed = first_in[i].reshape(-1)[:1] * 0
        full = jnp.broadcast_to(seed.reshape((1,) * p.ndim), shape)
        for k in arrival:
            owner = ring_arr[(mypos + k) % n]
            if n % 2 == 0 and k == -nf:
                first, second = parts[k][0][i], parts[k][1][i]
                start = [0] * p.ndim
                start[axis] = owner * width
                full = lax.dynamic_update_slice(full, first, start)
                start[axes[i]] = first.shape[axes[i]]
                full = lax.dynamic_update_slice(full, second, start)
            else:
                full = lax.dynamic_update_slice_in_dim(full, parts[k][i], owner * width, axis)
        out.append(full)
    return out, last


def scatter_group(pieces, ring, carry=jnp.bfloat16, after=None, taps=None):
    if after is not None:
        arrays = tuple(p[1:] if isinstance(p[0], str) else (p[0],) for p in pieces)
        arrays, _ = lax.optimization_barrier((arrays, after))
        pieces = [
            ("prod",) + tuple(a) if isinstance(p[0], str) else (a[0], p[1]) for p, a in zip(pieces, arrays)
        ]
    n, mypos, fwd, bwd, nf, nb = ring_steps(ring)
    ring_arr = jnp.asarray(ring, jnp.int32)

    def chunk(piece, owner):
        if isinstance(piece[0], str):
            _, lhs, rhs = piece
            w = lhs.shape[2] // n
            part = lax.dynamic_slice_in_dim(lhs, owner * w, w, 2)
            return jnp.einsum("xrd,xrf->xdf", part, rhs, preferred_element_type=jnp.float32)
        g, axis = piece
        w = g.shape[axis] // n
        return lax.dynamic_slice_in_dim(g, owner * w, w, axis).astype(jnp.float32)

    def own(q):
        owner = ring_arr[q % n]
        return tuple(chunk(p, owner) for p in pieces)

    axes = [2 if isinstance(p[0], str) else split_axis(p[0].ndim, p[1]) for p in pieces]
    carries = carry if isinstance(carry, tuple) else (carry,) * len(pieces)

    def cast(vals):
        return tuple(v.astype(c) for v, c in zip(vals, carries))

    def wide(vals):
        return tuple(v.astype(jnp.float32) for v in vals)

    def plus(x, y):
        return tuple(u + v for u, v in zip(x, y))

    if n % 2 == 0:
        opposite = own(mypos + nf)
        got_f = lax.ppermute(cast(halves(opposite, axes, 0)), "dp", fwd)
        got_b = lax.ppermute(cast(halves(opposite, axes, 1)), "dp", bwd)
        got_f, got_b = lax.optimization_barrier((got_f, got_b))
        for s in range(1, nf):
            vf = own(mypos + nf - s)
            vb = own(mypos - nf + s)
            if s == 1:
                vf = joined(plus(halves(vf, axes, 0), wide(got_f)), halves(vf, axes, 1), axes)
                vb = joined(halves(vb, axes, 0), plus(halves(vb, axes, 1), wide(got_b)), axes)
            else:
                vf = plus(vf, wide(got_f))
                vb = plus(vb, wide(got_b))
            vf = cast(vf)
            vb = cast(vb)
            if taps is not None:
                taps.append((vf, vb))
            got_f = lax.ppermute(vf, "dp", fwd)
            got_b = lax.ppermute(vb, "dp", bwd)
            got_f, got_b = lax.optimization_barrier((got_f, got_b))
        last = (got_f, got_b)
        total = own(mypos)
        if nf == 1:
            total = plus(total, joined(wide(got_f), wide(got_b), axes))
        else:
            total = plus(plus(total, wide(got_f)), wide(got_b))
        return list(total), last

    def send(vals, got, perm):
        if got is not None:
            vals = plus(vals, wide(got))
        return lax.ppermute(cast(vals), "dp", perm)

    got_f = None
    got_b = None
    for s in range(nf):
        got_f = send(own(mypos + nf - s), got_f, fwd)
        if s < nb:
            got_b = send(own(mypos - nb + s), got_b, bwd)
            got_f, got_b = lax.optimization_barrier((got_f, got_b))
    last = (got_f, got_b)
    total = own(mypos)
    total = plus(total, wide(got_f))
    if got_b is not None:
        total = plus(total, wide(got_b))
    return list(total), last


def per_device(
    tokens,
    segment_ids,
    valid_lengths,
    cotangent,
    w_query,
    w_key,
    w_value,
    w_out,
    query_gain,
    key_gain,
    attn_gain,
    w_gate,
    w_up,
    w_down,
    mlp_gain,
    ring,
):
    f32 = jnp.float32
    bf16 = jnp.bfloat16
    rows, width = tokens.shape
    seg_row = segment_ids[0]
    length = valid_lengths[0]
    block = min(512, rows)
    count = rows // block
    scale = HEAD_DIM ** (-0.5)
    n_dp = len(ring)
    slab = attn_gain.shape[0]
    head_piece = query_gain.shape[0]

    def padded(g):
        return jnp.pad(g, (0, slab - g.shape[0]))

    gains = jnp.stack([padded(query_gain), padded(key_gain), attn_gain, mlp_gain])
    (qkvo, gains_full), seen = gather_group(
        [(jnp.stack([w_query, w_key, w_value, w_out.T]), 1), (gains, 1)], ring
    )
    wq, wk, wv, wo_t = qkvo[0], qkvo[1], qkvo[2], qkvo[3]
    gq = gains_full[0].reshape(n_dp, slab)[:, :head_piece].reshape(-1)
    gk = gains_full[1].reshape(n_dp, slab)[:, :head_piece].reshape(-1)
    ga = gains_full[2]
    gm = gains_full[3]
    (gu,), seen = gather_group([(jnp.stack([w_gate, w_up]), 1)], ring, after=seen)
    wg, wu = gu[0], gu[1]
    (wd_t,), seen = gather_group([(w_down.T, 0)], ring, after=seen)
    gq32 = gq.astype(f32)
    gk32 = gk.astype(f32)
    ga32 = ga.astype(f32)
    gm32 = gm.astype(f32)
    query = jnp.dot(tokens, wq, preferred_element_type=f32)
    keys = jnp.dot(tokens, wk, preferred_element_type=f32)
    values = jnp.dot(tokens, wv, preferred_element_type=f32).astype(bf16)
    query_sq, key_sq = lax.psum(
        (jnp.sum(query * query, axis=1), jnp.sum(keys * keys, axis=1)), "mp"
    )
    query_factor = lax.rsqrt(query_sq / width + EPS)[:, None]
    key_factor = lax.rsqrt(key_sq / width + EPS)[:, None]
    query_hat = query * query_factor
    key_hat = keys * key_factor
    heads = query.shape[1] // HEAD_DIM
    cosine, sine = rope_tables(rows, HEAD_DIM)
    query_rot = rotate((query_hat * gq32).reshape(rows, heads, HEAD_DIM), cosine, sine).astype(bf16)
    key_rot = rotate((key_hat * gk32).reshape(rows, heads, HEAD_DIM), cosine, sine).astype(bf16)
    values_h = values.reshape(rows, heads, HEAD_DIM)

    def block_scores(start):
        scores = jnp.einsum("qhe,khe->hqk", query_rot, key_rot, preferred_element_type=f32) * scale
        mask = allowed_block(start, block, seg_row, length)
        return (query_rot, jnp.where(mask[None], scores, -1e30))

    def forward_block(index):
        start = index * block
        q_blk, scores = block_scores(start)
        top = jnp.max(scores, axis=-1, keepdims=True)
        total = jnp.sum(jnp.exp(scores - top), axis=-1, keepdims=True)
        logsum = top + jnp.log(total)
        probs = jnp.exp(scores - logsum).astype(bf16)
        attended = jnp.einsum("hqk,khe->qhe", probs, values_h, preferred_element_type=f32)
        return (attended, logsum[..., 0])

    attended, logsums = lax.map(forward_block, jnp.arange(count))
    attended_b = attended.reshape(rows, heads * HEAD_DIM).astype(bf16)
    attn_partial = jnp.einsum("rc,dc->rd", attended_b, wo_t, preferred_element_type=f32)
    attn_total = branch_total(attn_partial)
    attn_hat, attn_factor = norm_forward(attn_total)
    hidden = tokens.astype(f32) + attn_hat * ga32
    hidden_b = hidden.astype(bf16)
    gate = jnp.dot(hidden_b, wg, preferred_element_type=f32)
    up = jnp.dot(hidden_b, wu, preferred_element_type=f32)
    active = jax.nn.silu(gate)
    mixed_b = (active * up).astype(bf16)
    mlp_partial = jnp.einsum("rf,df->rd", mixed_b, wd_t, preferred_element_type=f32)
    mlp_total = branch_total(mlp_partial)
    mlp_hat, mlp_factor = norm_forward(mlp_total)
    layer_out = (hidden + mlp_hat * gm32).astype(bf16)
    grad_out = cotangent.astype(f32)
    d_mlp, grad_mg = norm_back(grad_out, mlp_hat, mlp_factor, gm32)
    d_mlp_b = d_mlp.astype(bf16)
    (grad_wd_t_s,), sent = scatter_group([("prod", d_mlp_b[None], mixed_b[None])], ring)
    grad_wd_s = grad_wd_t_s[0].T
    d_mixed = jnp.einsum("rd,df->rf", d_mlp_b, wd_t, preferred_element_type=f32)
    sigma = jax.nn.sigmoid(gate)
    d_gate = (d_mixed * up * sigma * (1.0 + gate * (1.0 - sigma))).astype(bf16)
    d_up = (d_mixed * active).astype(bf16)
    grad_gu = ("prod", jnp.stack([hidden_b, hidden_b]), jnp.stack([d_gate, d_up]))
    gu_taps = []
    (grad_gu_s,), sent = scatter_group([grad_gu], ring, after=sent, taps=gu_taps)
    grad_wg_s, grad_wu_s = grad_gu_s[0], grad_gu_s[1]
    hidden_partial = jnp.einsum("rf,df->rd", d_gate, wg, preferred_element_type=f32) + jnp.einsum(
        "rf,df->rd", d_up, wu, preferred_element_type=f32
    )
    d_hidden = grad_out + input_total(hidden_partial)
    d_attn, grad_ag = norm_back(d_hidden, attn_hat, attn_factor, ga32)
    d_attn_b = d_attn.astype(bf16)
    if gu_taps:
        d_attn_b, _ = lax.optimization_barrier((d_attn_b, gu_taps[0]))
    (grad_wo_t_s,), _ = scatter_group([("prod", d_attn_b[None], attended_b[None])], ring)
    grad_wo_s = grad_wo_t_s[0].T
    d_attended = jnp.einsum("rd,dc->rc", d_attn_b, wo_t, preferred_element_type=f32).astype(bf16)
    d_attended = d_attended.reshape(rows, heads, HEAD_DIM)

    def backward_block(carry, index):
        key_acc, value_acc = carry
        start = index * block
        q_blk, scores = block_scores(start)
        logsum = lax.dynamic_index_in_dim(logsums, index, 0, keepdims=False)
        probs = jnp.exp(scores - logsum[..., None])
        value_acc = value_acc + jnp.einsum(
            "hqk,qhe->khe", probs.astype(bf16), d_attended, preferred_element_type=f32
        )
        d_probs = jnp.einsum("qhe,khe->hqk", d_attended, values_h, preferred_element_type=f32)
        delta = jnp.sum(probs * d_probs, axis=-1, keepdims=True)
        d_scores = (probs * (d_probs - delta)).astype(bf16)
        d_query_blk = (
            jnp.einsum("hqk,khe->qhe", d_scores, key_rot, preferred_element_type=f32) * scale
        )
        key_acc = (
            key_acc
            + jnp.einsum("hqk,qhe->khe", d_scores, q_blk, preferred_element_type=f32) * scale
        )
        return ((key_acc, value_acc), d_query_blk)

    empty = jnp.zeros((rows, heads, HEAD_DIM), f32)
    (d_key_rot, d_values), d_query_rot = lax.scan(backward_block, (empty, empty), jnp.arange(count))
    d_query_rot = d_query_rot.reshape(rows, heads, HEAD_DIM)
    d_values_b = d_values.reshape(rows, heads * HEAD_DIM).astype(bf16)
    d_query_n = rotate_back(d_query_rot, cosine, sine).reshape(rows, heads * HEAD_DIM)
    d_key_n = rotate_back(d_key_rot, cosine, sine).reshape(rows, heads * HEAD_DIM)
    grad_gq = jnp.sum(d_query_n * query_hat, axis=0)
    grad_gk = jnp.sum(d_key_n * key_hat, axis=0)
    d_query_hat = d_query_n * gq32
    d_key_hat = d_key_n * gk32
    query_inner, key_inner = lax.psum(
        (jnp.sum(d_query_hat * query_hat, axis=1), jnp.sum(d_key_hat * key_hat, axis=1)), "mp"
    )
    d_query_b = (query_factor * (d_query_hat - query_hat * (query_inner / width)[:, None])).astype(
        bf16
    )
    d_key_b = (key_factor * (d_key_hat - key_hat * (key_inner / width)[:, None])).astype(bf16)
    grad_qkvo = (
        "prod",
        jnp.stack([tokens, tokens, tokens]),
        jnp.stack([d_query_b, d_key_b, d_values_b]),
    )

    def spread(g):
        return jnp.pad(g.reshape(n_dp, -1), ((0, 0), (0, slab - g.shape[0] // n_dp))).reshape(-1)

    grad_gains = jnp.stack([spread(grad_gq), spread(grad_gk), grad_ag, grad_mg])
    (grad_qkvo_s, grad_gains_s), sent = scatter_group(
        [grad_qkvo, (grad_gains, 1)], ring, carry=(jnp.bfloat16, jnp.float32), after=sent
    )
    grad_wq_s, grad_wk_s, grad_wv_s = grad_qkvo_s[0], grad_qkvo_s[1], grad_qkvo_s[2]
    grad_gq_s = grad_gains_s[0, :head_piece]
    grad_gk_s = grad_gains_s[1, :head_piece]
    grad_ag_s = grad_gains_s[2]
    grad_mg_s = grad_gains_s[3]
    input_part = jnp.einsum("rc,dc->rd", d_query_b, wq, preferred_element_type=f32)
    input_part = input_part + jnp.einsum("rc,dc->rd", d_key_b, wk, preferred_element_type=f32)
    input_part = input_part + jnp.einsum("rc,dc->rd", d_values_b, wv, preferred_element_type=f32)
    input_grad = d_hidden + input_total(input_part)
    return (
        layer_out,
        input_grad,
        grad_wq_s,
        grad_wk_s,
        grad_wv_s,
        grad_wo_s,
        grad_gq_s,
        grad_gk_s,
        grad_ag_s,
        grad_wg_s,
        grad_wu_s,
        grad_wd_s,
        grad_mg_s,
    )


def solution(mesh):
    placed = (
        P("dp", None),
        P("dp", None),
        P("dp"),
        P("dp", None),
        P("dp", "mp"),
        P("dp", "mp"),
        P("dp", "mp"),
        P("mp", "dp"),
        P(("mp", "dp")),
        P(("mp", "dp")),
        P("dp"),
        P("dp", "mp"),
        P("dp", "mp"),
        P("mp", "dp"),
        P("dp"),
    )
    ring = ring_order(mesh)
    return jax.shard_map(
        functools.partial(per_device, ring=ring),
        mesh=mesh,
        in_specs=placed,
        out_specs=(
            P("dp", None),
            P("dp", None),
            P("dp", "mp"),
            P("dp", "mp"),
            P("dp", "mp"),
            P("mp", "dp"),
            P(("mp", "dp")),
            P(("mp", "dp")),
            P("dp"),
            P("dp", "mp"),
            P("dp", "mp"),
            P("mp", "dp"),
            P("dp"),
        ),
        check_vma=False,
    )
```

```python
import functools

import jax
import jax.numpy as jnp
import numpy as np
from jax import lax
from jax.sharding import PartitionSpec as P

HEAD_DIM = 128


EPS = 1e-06
THETA = 500000.0


def rope_tables(rows, head_dim):
    half = head_dim // 2
    inverse = THETA ** (-(jnp.arange(half).astype(jnp.float32) * 2.0) / head_dim)
    angles = jnp.arange(rows).astype(jnp.float32)[:, None] * inverse[None, :]
    return (jnp.cos(angles)[:, None, :], jnp.sin(angles)[:, None, :])


def rotate(value, cosine, sine):
    half = value.shape[-1] // 2
    first, second = (value[..., :half], value[..., half:])
    return jnp.concatenate(
        [first * cosine - second * sine, second * cosine + first * sine], axis=-1
    )


def rotate_back(grad, cosine, sine):
    half = grad.shape[-1] // 2
    first, second = (grad[..., :half], grad[..., half:])
    return jnp.concatenate(
        [first * cosine + second * sine, second * cosine - first * sine], axis=-1
    )


def allowed_block(start, block, seg_row, length):
    query_pos = start + jnp.arange(block)
    key_pos = jnp.arange(seg_row.shape[0])
    same = seg_row[:, None] == seg_row[None, :]
    causal = key_pos[None, :] <= query_pos[:, None]
    inside = key_pos[None, :] < length
    return same & causal & inside | (key_pos[None, :] == query_pos[:, None])


def mp_allreduce(x, carry=jnp.bfloat16):
    m = lax.axis_size("mp")
    me = lax.axis_index("mp")
    core = me % 2
    chips = m // 2
    chip = me // 2
    half = x.shape[1] // 2
    pair = [(i, i ^ 1) for i in range(m)]
    mine = lax.dynamic_slice_in_dim(x, core * half, half, 1)
    other = lax.dynamic_slice_in_dim(x, (1 - core) * half, half, 1)
    part = mine + lax.ppermute(other, "mp", pair)
    if chips == 2 and half % 256 == 0:
        quarter = half // 2
        sums, swaps = [], []
        for j in range(2):
            low = lax.slice_in_dim(part, j * quarter, (j + 1) * quarter, axis=1).astype(carry)
            got = lax.ppermute(low, "mp", [(i, i ^ 2) for i in range(m)])
            total = low.astype(jnp.float32) + got.astype(jnp.float32)
            sums.append(total)
            swaps.append(lax.ppermute(total, "mp", pair))
        part = jnp.concatenate(sums, axis=1)
        swapped = jnp.concatenate(swaps, axis=1)
        first = jnp.where(core == 0, part, swapped)
        second = jnp.where(core == 0, swapped, part)
        return jnp.concatenate([first, second], axis=1)
    if chips == 2:
        low = part.astype(carry)
        got = lax.ppermute(low, "mp", [(i, i ^ 2) for i in range(m)])
        part = low.astype(jnp.float32) + got.astype(jnp.float32)
    elif chips > 2:
        low = part.astype(carry)
        got = [low]
        for k in range(1, chips):
            perm = [(c * 2 + r, ((c + k) % chips) * 2 + r) for c in range(chips) for r in range(2)]
            got.append(lax.ppermute(low, "mp", perm))
        stack = jnp.stack(got)
        order = (chip - jnp.arange(chips)) % chips
        ordered = jnp.take(stack, order, axis=0).astype(jnp.float32)
        part = ordered[0]
        for k in range(1, chips):
            part = part + ordered[k]
    swapped = lax.ppermute(part, "mp", pair)
    first = jnp.where(core == 0, part, swapped)
    second = jnp.where(core == 0, swapped, part)
    return jnp.concatenate([first, second], axis=1)


def branch_total(partial_sum):
    return mp_allreduce(partial_sum)


def input_total(partial_sum):
    return mp_allreduce(partial_sum)


def norm_forward(total):
    factor = lax.rsqrt(jnp.mean(total * total, axis=1, keepdims=True) + EPS)
    return (total * factor, factor)


def norm_back(grad, normed, factor, gain):
    grad_gain = jnp.sum(grad * normed, axis=0)
    scaled = grad * gain
    inner = jnp.mean(scaled * normed, axis=1, keepdims=True)
    return (factor * (scaled - normed * inner), grad_gain)


def ring_order(mesh):
    column = [mesh.devices[i, 0] for i in range(mesh.devices.shape[0])]
    count = len(column)
    try:
        coords = [tuple(d.coords) for d in column]
    except AttributeError:
        return list(range(count))
    axes = [a for a in range(len(coords[0])) if len({c[a] for c in coords}) > 1]
    if len(axes) != 2:
        return list(range(count))
    sizes = {a: len({c[a] for c in coords}) for a in axes}
    even = [a for a in axes if sizes[a] % 2 == 0]
    if not even:
        return list(range(count))
    outer = min(even, key=lambda a: sizes[a])
    inner = [a for a in axes if a != outer][0]
    lo = {a: min(c[a] for c in coords) for a in axes}
    where = {(c[outer] - lo[outer], c[inner] - lo[inner]): i for i, c in enumerate(coords)}
    order = []
    for o in range(sizes[outer]):
        steps = range(sizes[inner]) if o % 2 == 0 else reversed(range(sizes[inner]))
        for k in steps:
            order.append(where[(o, k)])
    if sorted(order) != list(range(count)):
        return list(range(count))
    return order


def ring_steps(ring):
    n = len(ring)
    pos_of = [ring.index(d) for d in range(n)]
    mypos = jnp.asarray(pos_of, jnp.int32)[lax.axis_index("dp")]
    fwd = [(ring[p], ring[(p + 1) % n]) for p in range(n)]
    bwd = [(ring[p], ring[(p - 1) % n]) for p in range(n)]
    nf = n // 2
    return n, mypos, fwd, bwd, nf, n - 1 - nf


def split_axis(ndim, axis):
    return ndim - 1 if axis != ndim - 1 else 0


def halves(values, axes, which):
    out = []
    for x, ax in zip(values, axes):
        h = x.shape[ax] // 2
        out.append(lax.slice_in_dim(x, which * h, (which + 1) * h, axis=ax))
    return tuple(out)


def joined(first, second, axes):
    return tuple(jnp.concatenate([x, y], axis=ax) for x, y, ax in zip(first, second, axes))


def gather_group(pieces, ring, after=None):
    locals_ = tuple(p.astype(jnp.bfloat16) for p, _ in pieces)
    if after is not None:
        locals_, _ = lax.optimization_barrier((locals_, after))
    n, mypos, fwd, bwd, nf, nb = ring_steps(ring)
    ring_arr = jnp.asarray(ring, jnp.int32)
    axes = [split_axis(p.ndim, axis) for p, axis in pieces]
    parts = {0: locals_}
    a = locals_
    b = locals_
    if n % 2 == 0:
        for s in range(nf - 1):
            a = lax.ppermute(a, "dp", fwd)
            b = lax.ppermute(b, "dp", bwd)
            a, b = lax.optimization_barrier((a, b))
            parts[-(s + 1)] = a
            parts[s + 1] = b
        ha = lax.ppermute(halves(a, axes, 0), "dp", fwd)
        hb = lax.ppermute(halves(b, axes, 1), "dp", bwd)
        ha, hb = lax.optimization_barrier((ha, hb))
        parts[-nf] = (ha, hb)
        last = (ha, hb)
        arrival = [0]
        for s in range(nf - 1):
            arrival += [-(s + 1), s + 1]
        arrival.append(-nf)
    else:
        for s in range(nf):
            a = lax.ppermute(a, "dp", fwd)
            if s < nb:
                b = lax.ppermute(b, "dp", bwd)
                a, b = lax.optimization_barrier((a, b))
                parts[s + 1] = b
            parts[-(s + 1)] = a
        last = (a, b)
        arrival = [0]
        for s in range(nf):
            arrival.append(-(s + 1))
            if s < nb:
                arrival.append(s + 1)
    out = []
    for i, (p, axis) in enumerate(pieces):
        shape = list(p.shape)
        width = shape[axis]
        shape[axis] *= n
        first_in = parts[arrival[1]] if len(arrival) > 1 else parts[0]
        first_in = first_in[0] if isinstance(first_in[0], tuple) else first_in
        seed = first_in[i].reshape(-1)[:1] * 0
        full = jnp.broadcast_to(seed.reshape((1,) * p.ndim), shape)
        for k in arrival:
            owner = ring_arr[(mypos + k) % n]
            if n % 2 == 0 and k == -nf:
                first, second = parts[k][0][i], parts[k][1][i]
                start = [0] * p.ndim
                start[axis] = owner * width
                full = lax.dynamic_update_slice(full, first, start)
                start[axes[i]] = first.shape[axes[i]]
                full = lax.dynamic_update_slice(full, second, start)
            else:
                full = lax.dynamic_update_slice_in_dim(full, parts[k][i], owner * width, axis)
        out.append(full)
    return out, last


def scatter_group(pieces, ring, carry=jnp.bfloat16, after=None, taps=None):
    if after is not None:
        arrays = tuple(p[1:] if isinstance(p[0], str) else (p[0],) for p in pieces)
        arrays, _ = lax.optimization_barrier((arrays, after))
        pieces = [
            ("prod",) + tuple(a) if isinstance(p[0], str) else (a[0], p[1]) for p, a in zip(pieces, arrays)
        ]
    n, mypos, fwd, bwd, nf, nb = ring_steps(ring)
    ring_arr = jnp.asarray(ring, jnp.int32)

    def chunk(piece, owner):
        if isinstance(piece[0], str):
            _, lhs, rhs = piece
            w = lhs.shape[2] // n
            part = lax.dynamic_slice_in_dim(lhs, owner * w, w, 2)
            return jnp.einsum("xrd,xrf->xdf", part, rhs, preferred_element_type=jnp.float32)
        g, axis = piece
        w = g.shape[axis] // n
        return lax.dynamic_slice_in_dim(g, owner * w, w, axis).astype(jnp.float32)

    def own(q):
        owner = ring_arr[q % n]
        return tuple(chunk(p, owner) for p in pieces)

    axes = [2 if isinstance(p[0], str) else split_axis(p[0].ndim, p[1]) for p in pieces]
    carries = carry if isinstance(carry, tuple) else (carry,) * len(pieces)

    def cast(vals):
        return tuple(v.astype(c) for v, c in zip(vals, carries))

    def wide(vals):
        return tuple(v.astype(jnp.float32) for v in vals)

    def plus(x, y):
        return tuple(u + v for u, v in zip(x, y))

    if n % 2 == 0:
        opposite = own(mypos + nf)
        got_f = lax.ppermute(cast(halves(opposite, axes, 0)), "dp", fwd)
        got_b = lax.ppermute(cast(halves(opposite, axes, 1)), "dp", bwd)
        got_f, got_b = lax.optimization_barrier((got_f, got_b))
        for s in range(1, nf):
            vf = own(mypos + nf - s)
            vb = own(mypos - nf + s)
            if s == 1:
                vf = joined(plus(halves(vf, axes, 0), wide(got_f)), halves(vf, axes, 1), axes)
                vb = joined(halves(vb, axes, 0), plus(halves(vb, axes, 1), wide(got_b)), axes)
            else:
                vf = plus(vf, wide(got_f))
                vb = plus(vb, wide(got_b))
            vf = cast(vf)
            vb = cast(vb)
            if taps is not None:
                taps.append((vf, vb))
            got_f = lax.ppermute(vf, "dp", fwd)
            got_b = lax.ppermute(vb, "dp", bwd)
            got_f, got_b = lax.optimization_barrier((got_f, got_b))
        last = (got_f, got_b)
        total = own(mypos)
        if nf == 1:
            total = plus(total, joined(wide(got_f), wide(got_b), axes))
        else:
            total = plus(plus(total, wide(got_f)), wide(got_b))
        return list(total), last

    def send(vals, got, perm):
        if got is not None:
            vals = plus(vals, wide(got))
        return lax.ppermute(cast(vals), "dp", perm)

    got_f = None
    got_b = None
    for s in range(nf):
        got_f = send(own(mypos + nf - s), got_f, fwd)
        if s < nb:
            got_b = send(own(mypos - nb + s), got_b, bwd)
            got_f, got_b = lax.optimization_barrier((got_f, got_b))
    last = (got_f, got_b)
    total = own(mypos)
    total = plus(total, wide(got_f))
    if got_b is not None:
        total = plus(total, wide(got_b))
    return list(total), last


def per_device(
    tokens,
    segment_ids,
    valid_lengths,
    cotangent,
    w_query,
    w_key,
    w_value,
    w_out,
    query_gain,
    key_gain,
    attn_gain,
    w_gate,
    w_up,
    w_down,
    mlp_gain,
    ring,
):
    f32 = jnp.float32
    bf16 = jnp.bfloat16
    rows, width = tokens.shape
    seg_row = segment_ids[0]
    length = valid_lengths[0]
    block = min(512, rows)
    count = rows // block
    scale = HEAD_DIM ** (-0.5)
    n_dp = len(ring)
    slab = attn_gain.shape[0]
    head_piece = query_gain.shape[0]

    def padded(g):
        return jnp.pad(g, (0, slab - g.shape[0]))

    gains = jnp.stack([padded(query_gain), padded(key_gain), attn_gain, mlp_gain])
    (qkvo, gains_full), seen = gather_group(
        [(jnp.stack([w_query, w_key, w_value, w_out.T]), 1), (gains, 1)], ring
    )
    wq, wk, wv, wo_t = qkvo[0], qkvo[1], qkvo[2], qkvo[3]
    gq = gains_full[0].reshape(n_dp, slab)[:, :head_piece].reshape(-1)
    gk = gains_full[1].reshape(n_dp, slab)[:, :head_piece].reshape(-1)
    ga = gains_full[2]
    gm = gains_full[3]
    (gu,), seen = gather_group([(jnp.stack([w_gate, w_up]), 1)], ring, after=seen)
    wg, wu = gu[0], gu[1]
    (wd_t,), seen = gather_group([(w_down.T, 0)], ring, after=seen)
    gq32 = gq.astype(f32)
    gk32 = gk.astype(f32)
    ga32 = ga.astype(f32)
    gm32 = gm.astype(f32)
    query = jnp.dot(tokens, wq, preferred_element_type=f32)
    keys = jnp.dot(tokens, wk, preferred_element_type=f32)
    values = jnp.dot(tokens, wv, preferred_element_type=f32).astype(bf16)
    query_sq, key_sq = lax.psum(
        (jnp.sum(query * query, axis=1), jnp.sum(keys * keys, axis=1)), "mp"
    )
    query_factor = lax.rsqrt(query_sq / width + EPS)[:, None]
    key_factor = lax.rsqrt(key_sq / width + EPS)[:, None]
    query_hat = query * query_factor
    key_hat = keys * key_factor
    heads = query.shape[1] // HEAD_DIM
    cosine, sine = rope_tables(rows, HEAD_DIM)
    query_rot = rotate((query_hat * gq32).reshape(rows, heads, HEAD_DIM), cosine, sine).astype(bf16)
    key_rot = rotate((key_hat * gk32).reshape(rows, heads, HEAD_DIM), cosine, sine).astype(bf16)
    values_h = values.reshape(rows, heads, HEAD_DIM)

    def block_scores(start):
        scores = jnp.einsum("qhe,khe->hqk", query_rot, key_rot, preferred_element_type=f32) * scale
        mask = allowed_block(start, block, seg_row, length)
        return (query_rot, jnp.where(mask[None], scores, -1e30))

    def forward_block(index):
        start = index * block
        q_blk, scores = block_scores(start)
        top = jnp.max(scores, axis=-1, keepdims=True)
        total = jnp.sum(jnp.exp(scores - top), axis=-1, keepdims=True)
        logsum = top + jnp.log(total)
        probs = jnp.exp(scores - logsum).astype(bf16)
        attended = jnp.einsum("hqk,khe->qhe", probs, values_h, preferred_element_type=f32)
        return (attended, logsum[..., 0])

    attended, logsums = lax.map(forward_block, jnp.arange(count))
    attended_b = attended.reshape(rows, heads * HEAD_DIM).astype(bf16)
    attn_partial = jnp.einsum("rc,dc->rd", attended_b, wo_t, preferred_element_type=f32)
    attn_total = branch_total(attn_partial)
    attn_hat, attn_factor = norm_forward(attn_total)
    hidden = tokens.astype(f32) + attn_hat * ga32
    hidden_b = hidden.astype(bf16)
    gate = jnp.dot(hidden_b, wg, preferred_element_type=f32)
    up = jnp.dot(hidden_b, wu, preferred_element_type=f32)
    active = jax.nn.silu(gate)
    mixed_b = (active * up).astype(bf16)
    mlp_partial = jnp.einsum("rf,df->rd", mixed_b, wd_t, preferred_element_type=f32)
    mlp_total = branch_total(mlp_partial)
    mlp_hat, mlp_factor = norm_forward(mlp_total)
    layer_out = (hidden + mlp_hat * gm32).astype(bf16)
    grad_out = cotangent.astype(f32)
    d_mlp, grad_mg = norm_back(grad_out, mlp_hat, mlp_factor, gm32)
    d_mlp_b = d_mlp.astype(bf16)
    (grad_wd_t_s,), sent = scatter_group([("prod", d_mlp_b[None], mixed_b[None])], ring)
    grad_wd_s = grad_wd_t_s[0].T
    d_mixed = jnp.einsum("rd,df->rf", d_mlp_b, wd_t, preferred_element_type=f32)
    sigma = jax.nn.sigmoid(gate)
    d_gate = (d_mixed * up * sigma * (1.0 + gate * (1.0 - sigma))).astype(bf16)
    d_up = (d_mixed * active).astype(bf16)
    grad_gu = ("prod", jnp.stack([hidden_b, hidden_b]), jnp.stack([d_gate, d_up]))
    gu_taps = []
    (grad_gu_s,), sent = scatter_group([grad_gu], ring, after=sent, taps=gu_taps)
    grad_wg_s, grad_wu_s = grad_gu_s[0], grad_gu_s[1]
    hidden_partial = jnp.einsum("rf,df->rd", d_gate, wg, preferred_element_type=f32) + jnp.einsum(
        "rf,df->rd", d_up, wu, preferred_element_type=f32
    )
    d_hidden = grad_out + input_total(hidden_partial)
    d_attn, grad_ag = norm_back(d_hidden, attn_hat, attn_factor, ga32)
    d_attn_b = d_attn.astype(bf16)
    if gu_taps:
        d_attn_b, _ = lax.optimization_barrier((d_attn_b, gu_taps[0]))
    d_attended = jnp.einsum("rd,dc->rc", d_attn_b, wo_t, preferred_element_type=f32).astype(bf16)
    d_attended = d_attended.reshape(rows, heads, HEAD_DIM)

    def backward_block(carry, index):
        key_acc, value_acc = carry
        start = index * block
        q_blk, scores = block_scores(start)
        logsum = lax.dynamic_index_in_dim(logsums, index, 0, keepdims=False)
        probs = jnp.exp(scores - logsum[..., None])
        value_acc = value_acc + jnp.einsum(
            "hqk,qhe->khe", probs.astype(bf16), d_attended, preferred_element_type=f32
        )
        d_probs = jnp.einsum("qhe,khe->hqk", d_attended, values_h, preferred_element_type=f32)
        delta = jnp.sum(probs * d_probs, axis=-1, keepdims=True)
        d_scores = (probs * (d_probs - delta)).astype(bf16)
        d_query_blk = (
            jnp.einsum("hqk,khe->qhe", d_scores, key_rot, preferred_element_type=f32) * scale
        )
        key_acc = (
            key_acc
            + jnp.einsum("hqk,qhe->khe", d_scores, q_blk, preferred_element_type=f32) * scale
        )
        return ((key_acc, value_acc), d_query_blk)

    empty = jnp.zeros((rows, heads, HEAD_DIM), f32)
    (d_key_rot, d_values), d_query_rot = lax.scan(backward_block, (empty, empty), jnp.arange(count))
    d_query_rot = d_query_rot.reshape(rows, heads, HEAD_DIM)
    d_values_b = d_values.reshape(rows, heads * HEAD_DIM).astype(bf16)
    d_query_n = rotate_back(d_query_rot, cosine, sine).reshape(rows, heads * HEAD_DIM)
    d_key_n = rotate_back(d_key_rot, cosine, sine).reshape(rows, heads * HEAD_DIM)
    grad_gq = jnp.sum(d_query_n * query_hat, axis=0)
    grad_gk = jnp.sum(d_key_n * key_hat, axis=0)
    d_query_hat = d_query_n * gq32
    d_key_hat = d_key_n * gk32
    query_inner, key_inner = lax.psum(
        (jnp.sum(d_query_hat * query_hat, axis=1), jnp.sum(d_key_hat * key_hat, axis=1)), "mp"
    )
    d_query_b = (query_factor * (d_query_hat - query_hat * (query_inner / width)[:, None])).astype(
        bf16
    )
    d_key_b = (key_factor * (d_key_hat - key_hat * (key_inner / width)[:, None])).astype(bf16)
    grad_qkvo = (
        "prod",
        jnp.stack([tokens, tokens, tokens, d_attn_b]),
        jnp.stack([d_query_b, d_key_b, d_values_b, attended_b]),
    )

    def spread(g):
        return jnp.pad(g.reshape(n_dp, -1), ((0, 0), (0, slab - g.shape[0] // n_dp))).reshape(-1)

    grad_gains = jnp.stack([spread(grad_gq), spread(grad_gk), grad_ag, grad_mg])
    (grad_qkvo_s, grad_gains_s), sent = scatter_group(
        [grad_qkvo, (grad_gains, 1)], ring, carry=(jnp.bfloat16, jnp.float32), after=sent
    )
    grad_wq_s, grad_wk_s, grad_wv_s = grad_qkvo_s[0], grad_qkvo_s[1], grad_qkvo_s[2]
    grad_wo_s = grad_qkvo_s[3].T
    grad_gq_s = grad_gains_s[0, :head_piece]
    grad_gk_s = grad_gains_s[1, :head_piece]
    grad_ag_s = grad_gains_s[2]
    grad_mg_s = grad_gains_s[3]
    input_part = jnp.einsum("rc,dc->rd", d_query_b, wq, preferred_element_type=f32)
    input_part = input_part + jnp.einsum("rc,dc->rd", d_key_b, wk, preferred_element_type=f32)
    input_part = input_part + jnp.einsum("rc,dc->rd", d_values_b, wv, preferred_element_type=f32)
    input_grad = d_hidden + input_total(input_part)
    return (
        layer_out,
        input_grad,
        grad_wq_s,
        grad_wk_s,
        grad_wv_s,
        grad_wo_s,
        grad_gq_s,
        grad_gk_s,
        grad_ag_s,
        grad_wg_s,
        grad_wu_s,
        grad_wd_s,
        grad_mg_s,
    )


def solution(mesh):
    placed = (
        P("dp", None),
        P("dp", None),
        P("dp"),
        P("dp", None),
        P("dp", "mp"),
        P("dp", "mp"),
        P("dp", "mp"),
        P("mp", "dp"),
        P(("mp", "dp")),
        P(("mp", "dp")),
        P("dp"),
        P("dp", "mp"),
        P("dp", "mp"),
        P("mp", "dp"),
        P("dp"),
    )
    ring = ring_order(mesh)
    return jax.shard_map(
        functools.partial(per_device, ring=ring),
        mesh=mesh,
        in_specs=placed,
        out_specs=(
            P("dp", None),
            P("dp", None),
            P("dp", "mp"),
            P("dp", "mp"),
            P("dp", "mp"),
            P("mp", "dp"),
            P(("mp", "dp")),
            P(("mp", "dp")),
            P("dp"),
            P("dp", "mp"),
            P("dp", "mp"),
            P("mp", "dp"),
            P("dp"),
        ),
        check_vma=False,
    )
```
